32 devices in a mesh: groups: 2 (over y), cand: 4 (over z), query: 2 (over x), mp: 2 (over core).
Axes of the slice: x: 2, y: 2, z: 4, core: 2. Of those that a mesh axis runs over, the one named last changes fastest.
Arguments:
- tokens: bfloat16 [4, 4, 256, 1024], P(('groups', 'query'), 'cand'), parts along dimension 0, may hold values from -6 to 6
- lengths: int32 [4, 4], P(('groups', 'query'), 'cand'), parts along dimension 0, may hold values from 64 to 256, as said below
- teacher: float32 [4, 4], P(('groups', 'query'), 'cand'), parts along dimension 0, may hold values from -15 to 291, as said below
- w_first: bfloat16 [3, 1024, 512], P(None, None, 'mp'), may hold values from -0.1875 to 0.1875
- w_out_first: bfloat16 [512, 1024], P('mp'), may hold values from -0.25 to 0.25
- gain_first: float32 [1024], replicated, may hold values from 0.5 to 1.5
- w_last: bfloat16 [3, 1024, 512], P(None, None, 'mp'), may hold values from -0.1875 to 0.1875
- w_out_last: bfloat16 [512, 1024], P('mp'), may hold values from -0.25 to 0.25
- gain_last: float32 [1024], replicated, may hold values from 0.5 to 1.5
- w_score: float32 [1024], replicated, may hold values from -0.5 to 0.5
Outputs:
- grad_first: float32 [2048, 3, 512], P(('groups', 'cand'), None, 'mp'), parts along dimension 0
The draws below stay inside these ranges and needn't reach their ends.
There are 2 independent parts, one for each index of `groups`. The reference program is written for one: setup_inputs(seed, part) draws one part's arguments, and reference() takes and returns one part's arrays. A program takes and returns all parts, laid end to end along the dimension named above; an argument that names none is the same for every part. Nothing has to cross between parts.
Inputs may be any that keep to these rules, and one draw needn't show every extreme that they name: `lengths`: valid tokens of each pair; in every list some pair fills all 256 positions. Within each list the teacher's scores span at most 30.
All inputs are finite; a program needn't handle non-finite values.
Results may differ from the reference program's by a relative error of at most 0.012.
Values may be sent and summed in bfloat16 or wider, within the bound.
No kernel may reach another device: no remote copies, remote signals or barrier semaphores. Data moves between devices by JAX's collectives and lax.ppermute only.
A program may use at most 64 MiB of HBM per device.

```python
import jax
import jax.numpy as jnp
from jax import lax

D = 1024
HEADS = 8
HEAD_DIM = 64
SEQ = 256
HD = 512
CANDS = 4
QUERIES = 2


def draw_lengths(key, part):
    first_key, second_key = jax.random.split(jax.random.fold_in(key, 7))
    drawn = jax.random.randint(first_key, (QUERIES, CANDS), SEQ // 4, SEQ + 1)
    filled = jax.random.randint(second_key, (QUERIES, 1), 0, CANDS)
    return jnp.where(jnp.arange(CANDS)[None, :] == filled, SEQ, drawn).astype(jnp.int32)


def draw_teacher(key, part):
    first_key = jax.random.fold_in(jax.random.fold_in(key, 11), 0)
    values = jnp.clip(3.0 * jax.random.normal(first_key, (QUERIES, CANDS), jnp.float32), -15.0, 15.0)
    return values.astype(jnp.float32)


def steps_of(stream_key, shape, cuts, low, largest):
    def one(axis_at, blocks):
        heights = jax.random.uniform(jax.random.fold_in(jax.random.fold_in(stream_key, 6), axis_at), (blocks,), jnp.float32, low / len(cuts), largest / len(cuts))
        return jnp.repeat(jnp.exp(heights), shape[axis_at] // blocks).reshape((-1,) + (1,) * (len(shape) - axis_at - 1))

    factor_of = one(*cuts[0])
    for cut in cuts[1:]:
        factor_of = factor_of * one(*cut)
    return factor_of


def scatter_about(key, extent, spread, limit, cuts=(), dtype=jnp.bfloat16):
    factor_of = steps_of(key, extent, cuts, -0.22, 0.18) if cuts else 1.0
    array = jax.random.normal(key, extent, jnp.float32) * spread * factor_of
    return jnp.minimum(jnp.maximum(array, -limit), limit).astype(dtype)


def setup_inputs(seed: int = 0, part: int = 0) -> dict:
    seeds = jax.random.split(jax.random.key(seed), 11)
    own_keys = jax.random.split(jax.random.fold_in(seeds[10], part), 11)
    return {
        "tokens": scatter_about(own_keys[0], (QUERIES, CANDS, SEQ, D), 1.0, 6.0, ((0, 2), (1, 4))),
        "lengths": draw_lengths(jax.random.fold_in(jax.random.fold_in(seeds[10], part), 71), part),
        "teacher": draw_teacher(jax.random.fold_in(jax.random.fold_in(seeds[10], part), 71), part),
        "w_first": scatter_about(seeds[3], (3, D, HD), D ** -0.5, 0.1875, ((2, 2),)),
        "w_out_first": scatter_about(seeds[4], (HD, D), HD ** -0.5, 0.25, ((0, 2),)),
        "gain_first": jnp.clip(1.0 + 0.1 * jax.random.normal(seeds[5], (D,), jnp.float32), 0.5, 1.5),
        "w_last": scatter_about(seeds[6], (3, D, HD), D ** -0.5, 0.1875, ((2, 2),)),
        "w_out_last": scatter_about(seeds[7], (HD, D), HD ** -0.5, 0.25, ((0, 2),)),
        "gain_last": jnp.clip(1.0 + 0.1 * jax.random.normal(seeds[8], (D,), jnp.float32), 0.5, 1.5),
        "w_score": scatter_about(seeds[9], (D,), 0.09, 0.5, (), jnp.float32),
    }


EPSILON = 1e-05
LOSS_SCALE = 1024.0
NEGATIVE = -1e+30

def product(pattern, former, latter):
    return jnp.einsum(pattern, former.astype(jnp.float32), latter.astype(jnp.float32), precision=lax.Precision.HIGHEST)

def norm_forward(matrix, scales):
    center = matrix - lax.optimization_barrier(jnp.mean(matrix, -1, keepdims=True))
    inverse = lax.rsqrt(lax.optimization_barrier(jnp.mean(center * center, -1, keepdims=True)) + EPSILON)
    normed = center * inverse
    return (normed * scales, normed, inverse)

def norm_backward(incoming, normed, inverse, scales):
    scaled = incoming * scales
    return inverse * (scaled - lax.optimization_barrier(jnp.mean(scaled, -1, keepdims=True)) - normed * lax.optimization_barrier(jnp.mean(scaled * normed, -1, keepdims=True)))

def split_softmax(own_scores, cross_scores, first_mask):
    own_peak = lax.optimization_barrier(jnp.max(own_scores, -1))
    row_peak = jnp.maximum(own_peak[..., 0], lax.optimization_barrier(jnp.max(cross_scores, -1)))
    peak = jnp.where(first_mask, row_peak[..., None], own_peak)
    own_exp = jnp.exp(own_scores - peak[..., None])
    cross_exp = jnp.exp(cross_scores - row_peak[..., None])
    own_totals = lax.optimization_barrier(jnp.sum(own_exp, -1))
    row_totals = own_totals[..., 0] + lax.optimization_barrier(jnp.sum(cross_exp, -1))
    totals = jnp.where(first_mask, row_totals[..., None], own_totals)
    return (own_exp / totals[..., None], cross_exp / row_totals[..., None])

def row_softmax(own_scores, cross_scores):
    peak = jnp.maximum(lax.optimization_barrier(jnp.max(own_scores, -1)), lax.optimization_barrier(jnp.max(cross_scores, -1)))[..., None]
    own_exp = jnp.exp(own_scores - peak)
    cross_exp = jnp.exp(cross_scores - peak)
    totals = (lax.optimization_barrier(jnp.sum(own_exp, -1)) + lax.optimization_barrier(jnp.sum(cross_exp, -1)))[..., None]
    return (own_exp / totals, cross_exp / totals)

def one_list(tokens, lengths, teacher, w_first, w_out_first, gain_first, w_last, w_out_last, gain_last, w_score):
    lists, cands, seq_len, model_width = tokens.shape
    full_width = w_first.shape[2]
    score_scale = HEAD_DIM ** (-0.5)
    positions = jnp.arange(seq_len)
    first_mask = positions == 0
    own_valid = positions[None, None, :] < lengths[:, :, None]
    cand_ids = jnp.arange(cands)
    cross_valid = cand_ids[:, None] != cand_ids[None, :]
    head_shape = (lists, cands, seq_len, HEADS, HEAD_DIM)
    projected = product('qcsd,kdf->kqcsf', tokens, w_first).astype(jnp.bfloat16)
    first_query = projected[0].reshape(head_shape)
    first_keys = projected[1].reshape(head_shape)
    first_vals = projected[2].reshape(head_shape)
    cls_keys = first_keys[:, :, 0]
    cls_vals = first_vals[:, :, 0]
    own_scores = product('qcshe,qcthe->qchst', first_query, first_keys) * score_scale
    own_scores = jnp.where(own_valid[:, :, None, None, :], own_scores, NEGATIVE)
    cross_scores = product('qche,qdhe->qchd', first_query[:, :, 0], cls_keys) * score_scale
    cross_scores = jnp.where(cross_valid[None, :, None, :], cross_scores, NEGATIVE)
    own_prob, cross_prob = split_softmax(own_scores, cross_scores, first_mask)
    own_weight = own_prob.astype(jnp.bfloat16)
    cross_weight = cross_prob.astype(jnp.bfloat16)
    attended = product('qchst,qcthe->qcshe', own_weight, first_vals)
    attended_cls = product('qchd,qdhe->qche', cross_weight, cls_vals)
    attended = jnp.where(first_mask[None, None, :, None, None], attended + attended_cls[:, :, None], attended)
    first_mixed = attended.reshape(lists, cands, seq_len, full_width).astype(jnp.bfloat16)
    residual_first = tokens.astype(jnp.float32) + product('qcsf,fd->qcsd', first_mixed, w_out_first)
    normed_first, unit_first, inverse_first = norm_forward(residual_first, gain_first)
    hidden = normed_first.astype(jnp.bfloat16)
    last_query = product('qcd,df->qcf', hidden[:, :, 0], w_last[0]).astype(jnp.bfloat16)
    last_kv = product('qcsd,kdf->kqcsf', hidden, w_last[1:]).astype(jnp.bfloat16)
    last_heads = last_query.reshape(lists, cands, HEADS, HEAD_DIM)
    last_keys = last_kv[0].reshape(head_shape)
    last_vals = last_kv[1].reshape(head_shape)
    cls_keys_last = last_keys[:, :, 0]
    cls_vals_last = last_vals[:, :, 0]
    own_last = product('qche,qcthe->qcht', last_heads, last_keys) * score_scale
    own_last = jnp.where(own_valid[:, :, None, :], own_last, NEGATIVE)
    cross_last = product('qche,qdhe->qchd', last_heads, cls_keys_last) * score_scale
    cross_last = jnp.where(cross_valid[None, :, None, :], cross_last, NEGATIVE)
    own_last_prob, cross_last_prob = row_softmax(own_last, cross_last)
    own_last_weight = own_last_prob.astype(jnp.bfloat16)
    cross_last_weight = cross_last_prob.astype(jnp.bfloat16)
    attended_last = product('qcht,qcthe->qche', own_last_weight, last_vals) + product('qchd,qdhe->qche', cross_last_weight, cls_vals_last)
    last_mixed = attended_last.reshape(lists, cands, full_width).astype(jnp.bfloat16)
    residual_last = hidden[:, :, 0].astype(jnp.float32) + product('qcf,fd->qcd', last_mixed, w_out_last)
    normed_last, unit_last, inverse_last = norm_forward(residual_last, gain_last)
    scores = product('qcd,d->qc', normed_last, w_score)
    score_exp = jnp.exp(scores)
    student_prob = score_exp / lax.optimization_barrier(jnp.sum(score_exp, 1, keepdims=True))
    teacher_exp = jnp.exp(teacher - lax.optimization_barrier(jnp.max(teacher, 1, keepdims=True)))
    teacher_prob = teacher_exp / lax.optimization_barrier(jnp.sum(teacher_exp, 1, keepdims=True))
    score_grad = LOSS_SCALE * (student_prob - teacher_prob) / QUERIES
    grad_last = norm_backward(score_grad[..., None] * w_score, unit_last, inverse_last, gain_last)
    grad_last_low = grad_last.astype(jnp.bfloat16)
    grad_mixed_last = product('qcd,fd->qcf', grad_last_low, w_out_last).astype(jnp.bfloat16).reshape(lists, cands, HEADS, HEAD_DIM)
    own_dot = product('qche,qcthe->qcht', grad_mixed_last, last_vals)
    cross_dot = product('qche,qdhe->qchd', grad_mixed_last, cls_vals_last)
    centre = lax.optimization_barrier(jnp.sum(own_last_prob * own_dot, -1, keepdims=True)) + lax.optimization_barrier(jnp.sum(cross_last_prob * cross_dot, -1, keepdims=True))
    own_slope = (own_last_prob * (own_dot - centre)).astype(jnp.bfloat16)
    cross_slope = (cross_last_prob * (cross_dot - centre)).astype(jnp.bfloat16)
    grad_query_last = ((product('qcht,qcthe->qche', own_slope, last_keys) + product('qchd,qdhe->qche', cross_slope, cls_keys_last)) * score_scale).astype(jnp.bfloat16).reshape(lists, cands, full_width)
    own_key_grad = (product('qcht,qche->qcthe', own_slope, last_heads) * score_scale).reshape(lists, cands, seq_len, full_width)
    own_val_grad = product('qcht,qche->qcthe', own_last_weight, grad_mixed_last).reshape(lists, cands, seq_len, full_width)
    back_keys = (product('qchd,qche->qdhe', cross_slope, last_heads) * score_scale).reshape(lists, cands, full_width)
    back_vals = product('qchd,qche->qdhe', cross_last_weight, grad_mixed_last).reshape(lists, cands, full_width)
    first_cols = first_mask[None, None, :, None]
    key_grad = jnp.where(first_cols, own_key_grad + back_keys[:, :, None], own_key_grad).astype(jnp.bfloat16)
    val_grad = jnp.where(first_cols, own_val_grad + back_vals[:, :, None], own_val_grad).astype(jnp.bfloat16)
    partial_term = product('qcsf,df->qcsd', key_grad, w_last[1]) + product('qcsf,df->qcsd', val_grad, w_last[2])
    query_term = product('qcf,df->qcd', grad_query_last, w_last[0])
    partial_term = jnp.where(first_cols, partial_term + query_term[:, :, None], partial_term)
    grad_hidden = jnp.where(first_cols, partial_term + grad_last[:, :, None], partial_term)
    grad_first = norm_backward(grad_hidden, unit_first, inverse_first, gain_first).astype(jnp.bfloat16)
    grad_mixed_first = product('qcsd,fd->qcsf', grad_first, w_out_first).astype(jnp.bfloat16).reshape(head_shape)
    own_dot_first = product('qcshe,qcthe->qchst', grad_mixed_first, first_vals)
    cross_dot_first = product('qche,qdhe->qchd', grad_mixed_first[:, :, 0], cls_vals)
    own_part = lax.optimization_barrier(jnp.sum(own_prob * own_dot_first, -1))
    row_part = own_part[..., 0] + lax.optimization_barrier(jnp.sum(cross_prob * cross_dot_first, -1))
    centre_first = jnp.where(first_mask, row_part[..., None], own_part)
    own_slope_first = (own_prob * (own_dot_first - centre_first[..., None])).astype(jnp.bfloat16)
    cross_slope_first = (cross_prob * (cross_dot_first - row_part[..., None])).astype(jnp.bfloat16)
    query_grad = product('qchst,qcthe->qcshe', own_slope_first, first_keys)
    query_cls = product('qchd,qdhe->qche', cross_slope_first, cls_keys)
    query_grad = jnp.where(first_mask[None, None, :, None, None], query_grad + query_cls[:, :, None], query_grad)
    query_grad = (query_grad * score_scale).astype(jnp.bfloat16).reshape(lists, cands, seq_len, full_width)
    key_first = (product('qchst,qcshe->qcthe', own_slope_first, first_query) * score_scale).reshape(lists, cands, seq_len, full_width)
    val_first = product('qchst,qcshe->qcthe', own_weight, grad_mixed_first).reshape(lists, cands, seq_len, full_width)
    back_key_first = (product('qchd,qche->qdhe', cross_slope_first, first_query[:, :, 0]) * score_scale).reshape(lists, cands, full_width)
    back_val_first = product('qchd,qche->qdhe', cross_weight, grad_mixed_first[:, :, 0]).reshape(lists, cands, full_width)
    key_first = jnp.where(first_cols, key_first + back_key_first[:, :, None], key_first).astype(jnp.bfloat16)
    val_first = jnp.where(first_cols, val_first + back_val_first[:, :, None], val_first).astype(jnp.bfloat16)
    stacked = jnp.stack([query_grad, key_first, val_first], 3).reshape(lists * cands * seq_len, 3, full_width)
    flat_tokens = tokens.reshape(lists * cands * seq_len, model_width)
    return product('rd,rkf->dkf', flat_tokens, stacked)

def reference(tokens, lengths, teacher, w_first, w_out_first, gain_first, w_last, w_out_last, gain_last, w_score):

    def single(pieces):
        return one_list(pieces[0][None], pieces[1][None], pieces[2][None], w_first, w_out_first, gain_first, w_last, w_out_last, gain_last, w_score)
    grads = lax.map(single, (tokens, lengths, teacher))
    return lax.optimization_barrier(jnp.sum(grads, 0))
```

```python
import jax
import jax.numpy as jnp
from jax import lax
from jax.sharding import PartitionSpec as P

HEAD_DIM = 64


EPSILON = 1e-05
LOSS_SCALE = 1024.0
NEGATIVE = -1e30


def mixed(pattern, former, latter):
    return jnp.einsum(pattern, former, latter, preferred_element_type=jnp.float32)


def norm_forward(matrix, scales):
    center = matrix - jnp.mean(matrix, -1, keepdims=True)
    inverse = lax.rsqrt(jnp.mean(center * center, -1, keepdims=True) + EPSILON)
    normed = center * inverse
    return (normed * scales, normed, inverse)


def norm_backward(incoming, normed, inverse, scales):
    scaled = incoming * scales
    return inverse * (
        scaled
        - jnp.mean(scaled, -1, keepdims=True)
        - normed * jnp.mean(scaled * normed, -1, keepdims=True)
    )


def split_softmax(own_scores, cross_scores, first_mask):
    own_peak = jnp.max(own_scores, -1)
    row_peak = jnp.maximum(own_peak[..., 0], jnp.max(cross_scores, -1))
    peak = jnp.where(first_mask, row_peak[..., None], own_peak)
    own_exp = jnp.exp(own_scores - peak[..., None])
    cross_exp = jnp.exp(cross_scores - row_peak[..., None])
    own_totals = jnp.sum(own_exp, -1)
    row_totals = own_totals[..., 0] + jnp.sum(cross_exp, -1)
    totals = jnp.where(first_mask, row_totals[..., None], own_totals)
    return (own_exp / totals[..., None], cross_exp / row_totals[..., None])


def row_softmax(own_scores, cross_scores):
    peak = jnp.maximum(jnp.max(own_scores, -1), jnp.max(cross_scores, -1))[..., None]
    own_exp = jnp.exp(own_scores - peak)
    cross_exp = jnp.exp(cross_scores - peak)
    totals = (jnp.sum(own_exp, -1) + jnp.sum(cross_exp, -1))[..., None]
    return (own_exp / totals, cross_exp / totals)


def local(
    tokens,
    lengths,
    teacher,
    w_first,
    w_out_first,
    gain_first,
    w_last,
    w_out_last,
    gain_last,
    w_score,
):
    lists, local_cands, seq_len, model_width = tokens.shape
    local_width = w_first.shape[2]
    local_heads = local_width // HEAD_DIM
    cand_count = local_cands * lax.axis_size("cand")
    query_count = lists * lax.axis_size("query")
    score_scale = HEAD_DIM ** (-0.5)
    positions = jnp.arange(seq_len)
    first_mask = positions == 0
    own_valid = positions[None, None, :] < lengths[:, :, None]
    local_ids = lax.axis_index("cand") * local_cands + jnp.arange(local_cands)
    cross_valid = local_ids[:, None] != jnp.arange(cand_count)[None, :]
    head_shape = (lists, local_cands, seq_len, local_heads, HEAD_DIM)
    cls_shape = (lists, cand_count, local_heads, HEAD_DIM)
    out_first_full = lax.all_gather(w_out_first, "mp", axis=0, tiled=True)
    last_full = lax.all_gather(w_last, "mp", axis=2, tiled=True)
    out_last_full = lax.all_gather(w_out_last, "mp", axis=0, tiled=True)
    teacher_all = lax.all_gather(teacher, "cand", axis=1, tiled=True)
    projected = mixed("qcsd,kdf->kqcsf", tokens, w_first).astype(jnp.bfloat16)
    gathered_kv = lax.all_gather(
        jnp.concatenate([projected[1][:, :, 0], projected[2][:, :, 0]], -1),
        "cand",
        axis=1,
        tiled=True,
    )
    gathered_keys = gathered_kv[..., :local_width]
    gathered_vals = gathered_kv[..., local_width:]
    first_query = projected[0].reshape(head_shape)
    first_keys = projected[1].reshape(head_shape)
    first_vals = projected[2].reshape(head_shape)
    cls_keys = gathered_keys.reshape(cls_shape)
    cls_vals = gathered_vals.reshape(cls_shape)
    own_scores = mixed("qcshe,qcthe->qchst", first_query, first_keys) * score_scale
    own_scores = jnp.where(own_valid[:, :, None, None, :], own_scores, NEGATIVE)
    cross_scores = mixed("qche,qdhe->qchd", first_query[:, :, 0], cls_keys) * score_scale
    cross_scores = jnp.where(cross_valid[None, :, None, :], cross_scores, NEGATIVE)
    own_prob, cross_prob = split_softmax(own_scores, cross_scores, first_mask)
    own_weight = own_prob.astype(jnp.bfloat16)
    cross_weight = cross_prob.astype(jnp.bfloat16)
    attended = mixed("qchst,qcthe->qcshe", own_weight, first_vals)
    attended_cls = mixed("qchd,qdhe->qche", cross_weight, cls_vals)
    attended = jnp.where(
        first_mask[None, None, :, None, None], attended + attended_cls[:, :, None], attended
    )
    first_mixed = attended.reshape(lists, local_cands, seq_len, local_width).astype(jnp.bfloat16)
    first_joined = lax.all_gather(first_mixed, "mp", axis=3, tiled=True)
    residual_first = tokens.astype(jnp.float32) + mixed(
        "qcsf,fd->qcsd", first_joined, out_first_full
    )
    normed_first, unit_first, inverse_first = norm_forward(residual_first, gain_first)
    hidden = normed_first.astype(jnp.bfloat16)
    last_query = mixed("qcd,df->qcf", hidden[:, :, 0], w_last[0]).astype(jnp.bfloat16)
    last_kv = mixed("qcsd,kdf->kqcsf", hidden, w_last[1:]).astype(jnp.bfloat16)
    gathered_kv_last = lax.all_gather(
        jnp.concatenate([last_kv[0][:, :, 0], last_kv[1][:, :, 0]], -1),
        "cand",
        axis=1,
        tiled=True,
    )
    gathered_keys_last = gathered_kv_last[..., :local_width]
    gathered_vals_last = gathered_kv_last[..., local_width:]
    last_heads = last_query.reshape(lists, local_cands, local_heads, HEAD_DIM)
    last_keys = last_kv[0].reshape(head_shape)
    last_vals = last_kv[1].reshape(head_shape)
    cls_keys_last = gathered_keys_last.reshape(cls_shape)
    cls_vals_last = gathered_vals_last.reshape(cls_shape)
    own_last = mixed("qche,qcthe->qcht", last_heads, last_keys) * score_scale
    own_last = jnp.where(own_valid[:, :, None, :], own_last, NEGATIVE)
    cross_last = mixed("qche,qdhe->qchd", last_heads, cls_keys_last) * score_scale
    cross_last = jnp.where(cross_valid[None, :, None, :], cross_last, NEGATIVE)
    own_last_prob, cross_last_prob = row_softmax(own_last, cross_last)
    own_last_weight = own_last_prob.astype(jnp.bfloat16)
    cross_last_weight = cross_last_prob.astype(jnp.bfloat16)
    attended_last = mixed("qcht,qcthe->qche", own_last_weight, last_vals) + mixed(
        "qchd,qdhe->qche", cross_last_weight, cls_vals_last
    )
    last_mixed = attended_last.reshape(lists, local_cands, local_width).astype(jnp.bfloat16)
    last_joined = lax.all_gather(last_mixed, "mp", axis=2, tiled=True)
    residual_last = hidden[:, :, 0].astype(jnp.float32) + mixed(
        "qcf,fd->qcd", last_joined, out_last_full
    )
    normed_last, unit_last, inverse_last = norm_forward(residual_last, gain_last)
    scores = jnp.einsum("qcd,d->qc", normed_last, w_score, precision=lax.Precision.HIGHEST)
    score_exp = jnp.exp(scores)
    teacher_peak = jnp.max(teacher_all, 1)
    teacher_exp = jnp.exp(teacher - teacher_peak[:, None])
    teacher_totals = jnp.sum(jnp.exp(teacher_all - teacher_peak[:, None]), 1)
    score_totals = lax.psum(jnp.sum(score_exp, 1), "cand")
    student_prob = score_exp / score_totals[:, None]
    teacher_prob = teacher_exp / teacher_totals[:, None]
    score_grad = LOSS_SCALE * (student_prob - teacher_prob) / query_count
    grad_last = norm_backward(score_grad[..., None] * w_score, unit_last, inverse_last, gain_last)
    grad_last_low = grad_last.astype(jnp.bfloat16)
    grad_mixed_last = (
        mixed("qcd,fd->qcf", grad_last_low, w_out_last)
        .astype(jnp.bfloat16)
        .reshape(lists, local_cands, local_heads, HEAD_DIM)
    )
    own_dot = mixed("qche,qcthe->qcht", grad_mixed_last, last_vals)
    cross_dot = mixed("qche,qdhe->qchd", grad_mixed_last, cls_vals_last)
    centre = jnp.sum(own_last_prob * own_dot, -1, keepdims=True) + jnp.sum(
        cross_last_prob * cross_dot, -1, keepdims=True
    )
    own_slope = (own_last_prob * (own_dot - centre)).astype(jnp.bfloat16)
    cross_slope = (cross_last_prob * (cross_dot - centre)).astype(jnp.bfloat16)
    grad_query_last = (
        (
            (
                mixed("qcht,qcthe->qche", own_slope, last_keys)
                + mixed("qchd,qdhe->qche", cross_slope, cls_keys_last)
            )
            * score_scale
        )
        .astype(jnp.bfloat16)
        .reshape(lists, local_cands, local_width)
    )
    own_key_grad = (mixed("qcht,qche->qcthe", own_slope, last_heads) * score_scale).reshape(
        lists, local_cands, seq_len, local_width
    )
    own_val_grad = mixed("qcht,qche->qcthe", own_last_weight, grad_mixed_last).reshape(
        lists, local_cands, seq_len, local_width
    )
    cls_key_terms = (mixed("qchd,qche->qdhe", cross_slope, last_heads) * score_scale).reshape(
        lists, cand_count, local_width
    )
    cls_val_terms = mixed("qchd,qche->qdhe", cross_last_weight, grad_mixed_last).reshape(
        lists, cand_count, local_width
    )
    back_keys, back_vals = (
        lax.psum_scatter(cls_key_terms, "cand", scatter_dimension=1, tiled=True),
        lax.psum_scatter(cls_val_terms, "cand", scatter_dimension=1, tiled=True),
    )
    first_cols = first_mask[None, None, :, None]
    key_grad = jnp.where(first_cols, own_key_grad + back_keys[:, :, None], own_key_grad).astype(
        jnp.bfloat16
    )
    val_grad = jnp.where(first_cols, own_val_grad + back_vals[:, :, None], own_val_grad).astype(
        jnp.bfloat16
    )
    joined = lax.all_gather(
        jnp.concatenate([key_grad, val_grad, grad_query_last[:, :, None]], 2),
        "mp",
        axis=3,
        tiled=True,
    )
    key_joined = joined[:, :, :seq_len]
    val_joined = joined[:, :, seq_len : 2 * seq_len]
    query_joined = joined[:, :, 2 * seq_len]
    summed_term = mixed("qcsf,df->qcsd", key_joined, last_full[1]) + mixed(
        "qcsf,df->qcsd", val_joined, last_full[2]
    )
    query_term = mixed("qcf,df->qcd", query_joined, last_full[0])
    summed_term = jnp.where(first_cols, summed_term + query_term[:, :, None], summed_term)
    grad_hidden = jnp.where(first_cols, summed_term + grad_last[:, :, None], summed_term)
    grad_first = norm_backward(grad_hidden, unit_first, inverse_first, gain_first).astype(
        jnp.bfloat16
    )
    grad_mixed_first = (
        mixed("qcsd,fd->qcsf", grad_first, w_out_first).astype(jnp.bfloat16).reshape(head_shape)
    )
    own_dot_first = mixed("qcshe,qcthe->qchst", grad_mixed_first, first_vals)
    cross_dot_first = mixed("qche,qdhe->qchd", grad_mixed_first[:, :, 0], cls_vals)
    own_part = jnp.sum(own_prob * own_dot_first, -1)
    row_part = own_part[..., 0] + jnp.sum(cross_prob * cross_dot_first, -1)
    centre_first = jnp.where(first_mask, row_part[..., None], own_part)
    own_slope_first = (own_prob * (own_dot_first - centre_first[..., None])).astype(jnp.bfloat16)
    cross_slope_first = (cross_prob * (cross_dot_first - row_part[..., None])).astype(jnp.bfloat16)
    query_grad = mixed("qchst,qcthe->qcshe", own_slope_first, first_keys)
    query_cls = mixed("qchd,qdhe->qche", cross_slope_first, cls_keys)
    query_grad = jnp.where(
        first_mask[None, None, :, None, None], query_grad + query_cls[:, :, None], query_grad
    )
    query_grad = (
        (query_grad * score_scale)
        .astype(jnp.bfloat16)
        .reshape(lists, local_cands, seq_len, local_width)
    )
    key_first = (mixed("qchst,qcshe->qcthe", own_slope_first, first_query) * score_scale).reshape(
        lists, local_cands, seq_len, local_width
    )
    val_first = mixed("qchst,qcshe->qcthe", own_weight, grad_mixed_first).reshape(
        lists, local_cands, seq_len, local_width
    )
    cls_key_first = (
        mixed("qchd,qche->qdhe", cross_slope_first, first_query[:, :, 0]) * score_scale
    ).reshape(lists, cand_count, local_width)
    cls_val_first = mixed("qchd,qche->qdhe", cross_weight, grad_mixed_first[:, :, 0]).reshape(
        lists, cand_count, local_width
    )
    back_key_first, back_val_first = (
        lax.psum_scatter(cls_key_first, "cand", scatter_dimension=1, tiled=True),
        lax.psum_scatter(cls_val_first, "cand", scatter_dimension=1, tiled=True),
    )
    key_first = jnp.where(first_cols, key_first + back_key_first[:, :, None], key_first).astype(
        jnp.bfloat16
    )
    val_first = jnp.where(first_cols, val_first + back_val_first[:, :, None], val_first).astype(
        jnp.bfloat16
    )
    row_count = lists * local_cands * seq_len
    stacked = jnp.stack([query_grad, key_first, val_first], 3).reshape(row_count, 3, local_width)
    flat_tokens = tokens.reshape(row_count, model_width)
    partial_grad = lax.psum_scatter(
        mixed("rd,rkf->dkf", flat_tokens, stacked).astype(jnp.bfloat16),
        "cand",
        scatter_dimension=0,
        tiled=True,
    )
    result = lax.psum(partial_grad, "query")
    return result.astype(jnp.float32)


def solution(mesh):
    return jax.shard_map(
        local,
        mesh=mesh,
        in_specs=(
            P(("groups", "query"), "cand", None, None),
            P(("groups", "query"), "cand"),
            P(("groups", "query"), "cand"),
            P(None, None, "mp"),
            P("mp", None),
            P(),
            P(None, None, "mp"),
            P("mp", None),
            P(),
            P(),
        ),
        out_specs=P(("groups", "cand"), None, "mp"),
        check_vma=False,
    )
```

```python
import jax
import jax.numpy as jnp
from jax import lax
from jax.sharding import PartitionSpec as P

HEAD_DIM = 64


EPSILON = 1e-05
LOSS_SCALE = 1024.0
NEGATIVE = -1e30


def mixed(pattern, former, latter):
    return jnp.einsum(pattern, former, latter, preferred_element_type=jnp.float32)


def norm_forward(matrix, scales):
    center = matrix - jnp.mean(matrix, -1, keepdims=True)
    inverse = lax.rsqrt(jnp.mean(center * center, -1, keepdims=True) + EPSILON)
    normed = center * inverse
    return (normed * scales, normed, inverse)


def norm_backward(incoming, normed, inverse, scales):
    scaled = incoming * scales
    return inverse * (
        scaled
        - jnp.mean(scaled, -1, keepdims=True)
        - normed * jnp.mean(scaled * normed, -1, keepdims=True)
    )


def split_softmax(own_scores, cross_scores, first_mask):
    own_peak = jnp.max(own_scores, -1)
    row_peak = jnp.maximum(own_peak[..., 0], jnp.max(cross_scores, -1))
    peak = jnp.where(first_mask, row_peak[..., None], own_peak)
    own_exp = jnp.exp(own_scores - peak[..., None])
    cross_exp = jnp.exp(cross_scores - row_peak[..., None])
    own_totals = jnp.sum(own_exp, -1)
    row_totals = own_totals[..., 0] + jnp.sum(cross_exp, -1)
    totals = jnp.where(first_mask, row_totals[..., None], own_totals)
    return (own_exp / totals[..., None], cross_exp / row_totals[..., None])


def row_softmax(own_scores, cross_scores):
    peak = jnp.maximum(jnp.max(own_scores, -1), jnp.max(cross_scores, -1))[..., None]
    own_exp = jnp.exp(own_scores - peak)
    cross_exp = jnp.exp(cross_scores - peak)
    totals = (jnp.sum(own_exp, -1) + jnp.sum(cross_exp, -1))[..., None]
    return (own_exp / totals, cross_exp / totals)


def gather_cand(block, axis):
    count = lax.axis_size("cand")
    if count > 8:
        return lax.all_gather(block, "cand", axis=axis, tiled=True)
    me = lax.axis_index("cand")
    parts = [block] + [
        lax.ppermute(block, "cand", [(j, (j + k) % count) for j in range(count)])
        for k in range(1, count)
    ]
    ordered = jnp.take(jnp.stack(parts, 0), (me - jnp.arange(count)) % count, axis=0)
    ordered = jnp.moveaxis(ordered, 0, axis)
    shape = block.shape[:axis] + (count * block.shape[axis],) + block.shape[axis + 1 :]
    return ordered.reshape(shape)


def sum_query(block):
    if lax.axis_size("query") != 2:
        return lax.psum(block, "query")
    other = lax.ppermute(block, "query", [(0, 1), (1, 0)])
    return block.astype(jnp.float32) + other.astype(jnp.float32)


def local(
    tokens,
    lengths,
    teacher,
    w_first,
    w_out_first,
    gain_first,
    w_last,
    w_out_last,
    gain_last,
    w_score,
):
    lists, local_cands, seq_len, model_width = tokens.shape
    local_width = w_first.shape[2]
    local_heads = local_width // HEAD_DIM
    cand_count = local_cands * lax.axis_size("cand")
    query_count = lists * lax.axis_size("query")
    score_scale = HEAD_DIM ** (-0.5)
    positions = jnp.arange(seq_len)
    first_mask = positions == 0
    own_valid = positions[None, None, :] < lengths[:, :, None]
    local_ids = lax.axis_index("cand") * local_cands + jnp.arange(local_cands)
    cross_valid = local_ids[:, None] != jnp.arange(cand_count)[None, :]
    head_shape = (lists, local_cands, seq_len, local_heads, HEAD_DIM)
    cls_shape = (lists, cand_count, local_heads, HEAD_DIM)
    out_first_full = lax.all_gather(w_out_first, "mp", axis=0, tiled=True)
    last_full = lax.all_gather(w_last, "mp", axis=2, tiled=True)
    out_last_full = lax.all_gather(w_out_last, "mp", axis=0, tiled=True)
    teacher_all = lax.all_gather(teacher, "cand", axis=1, tiled=True)
    cls_tokens = gather_cand(tokens[:, :, 0], 1)
    projected = mixed("qcsd,kdf->kqcsf", tokens, w_first).astype(jnp.bfloat16)
    cls_projected = mixed("qcd,kdf->kqcf", cls_tokens, w_first[1:]).astype(jnp.bfloat16)
    gathered_keys = cls_projected[0]
    gathered_vals = cls_projected[1]
    first_query = projected[0].reshape(head_shape)
    first_keys = projected[1].reshape(head_shape)
    first_vals = projected[2].reshape(head_shape)
    cls_keys = gathered_keys.reshape(cls_shape)
    cls_vals = gathered_vals.reshape(cls_shape)
    own_scores = mixed("qcshe,qcthe->qchst", first_query, first_keys) * score_scale
    own_scores = jnp.where(own_valid[:, :, None, None, :], own_scores, NEGATIVE)
    cross_scores = mixed("qche,qdhe->qchd", first_query[:, :, 0], cls_keys) * score_scale
    cross_scores = jnp.where(cross_valid[None, :, None, :], cross_scores, NEGATIVE)
    own_prob, cross_prob = split_softmax(own_scores, cross_scores, first_mask)
    own_weight = own_prob.astype(jnp.bfloat16)
    cross_weight = cross_prob.astype(jnp.bfloat16)
    attended = mixed("qchst,qcthe->qcshe", own_weight, first_vals)
    attended_cls = mixed("qchd,qdhe->qche", cross_weight, cls_vals)
    attended = jnp.where(
        first_mask[None, None, :, None, None], attended + attended_cls[:, :, None], attended
    )
    first_mixed = attended.reshape(lists, local_cands, seq_len, local_width).astype(jnp.bfloat16)
    first_joined = lax.all_gather(first_mixed, "mp", axis=3, tiled=True)
    residual_first = tokens.astype(jnp.float32) + mixed(
        "qcsf,fd->qcsd", first_joined, out_first_full
    )
    normed_first, unit_first, inverse_first = norm_forward(residual_first, gain_first)
    hidden = normed_first.astype(jnp.bfloat16)
    last_query = mixed("qcd,df->qcf", hidden[:, :, 0], w_last[0]).astype(jnp.bfloat16)
    last_kv = mixed("qcsd,kdf->kqcsf", hidden, w_last[1:]).astype(jnp.bfloat16)
    gathered_kv_last = lax.all_gather(
        jnp.concatenate([last_kv[0][:, :, 0], last_kv[1][:, :, 0]], -1),
        "cand",
        axis=1,
        tiled=True,
    )
    gathered_keys_last = gathered_kv_last[..., :local_width]
    gathered_vals_last = gathered_kv_last[..., local_width:]
    last_heads = last_query.reshape(lists, local_cands, local_heads, HEAD_DIM)
    last_keys = last_kv[0].reshape(head_shape)
    last_vals = last_kv[1].reshape(head_shape)
    cls_keys_last = gathered_keys_last.reshape(cls_shape)
    cls_vals_last = gathered_vals_last.reshape(cls_shape)
    own_last = mixed("qche,qcthe->qcht", last_heads, last_keys) * score_scale
    own_last = jnp.where(own_valid[:, :, None, :], own_last, NEGATIVE)
    cross_last = mixed("qche,qdhe->qchd", last_heads, cls_keys_last) * score_scale
    cross_last = jnp.where(cross_valid[None, :, None, :], cross_last, NEGATIVE)
    own_last_prob, cross_last_prob = row_softmax(own_last, cross_last)
    own_last_weight = own_last_prob.astype(jnp.bfloat16)
    cross_last_weight = cross_last_prob.astype(jnp.bfloat16)
    attended_last = mixed("qcht,qcthe->qche", own_last_weight, last_vals) + mixed(
        "qchd,qdhe->qche", cross_last_weight, cls_vals_last
    )
    last_mixed = attended_last.reshape(lists, local_cands, local_width).astype(jnp.bfloat16)
    last_joined = lax.all_gather(last_mixed, "mp", axis=2, tiled=True)
    residual_last = hidden[:, :, 0].astype(jnp.float32) + mixed(
        "qcf,fd->qcd", last_joined, out_last_full
    )
    normed_last, unit_last, inverse_last = norm_forward(residual_last, gain_last)
    scores = jnp.einsum("qcd,d->qc", normed_last, w_score, precision=lax.Precision.HIGHEST)
    score_exp = jnp.exp(scores)
    teacher_peak = jnp.max(teacher_all, 1)
    teacher_exp = jnp.exp(teacher - teacher_peak[:, None])
    teacher_totals = jnp.sum(jnp.exp(teacher_all - teacher_peak[:, None]), 1)
    score_totals = lax.psum(jnp.sum(score_exp, 1), "cand")
    student_prob = score_exp / score_totals[:, None]
    teacher_prob = teacher_exp / teacher_totals[:, None]
    score_grad = LOSS_SCALE * (student_prob - teacher_prob) / query_count
    grad_last = norm_backward(score_grad[..., None] * w_score, unit_last, inverse_last, gain_last)
    grad_last_low = grad_last.astype(jnp.bfloat16)
    grad_mixed_last = (
        mixed("qcd,fd->qcf", grad_last_low, w_out_last)
        .astype(jnp.bfloat16)
        .reshape(lists, local_cands, local_heads, HEAD_DIM)
    )
    own_dot = mixed("qche,qcthe->qcht", grad_mixed_last, last_vals)
    cross_dot = mixed("qche,qdhe->qchd", grad_mixed_last, cls_vals_last)
    centre = jnp.sum(own_last_prob * own_dot, -1, keepdims=True) + jnp.sum(
        cross_last_prob * cross_dot, -1, keepdims=True
    )
    own_slope = (own_last_prob * (own_dot - centre)).astype(jnp.bfloat16)
    cross_slope = (cross_last_prob * (cross_dot - centre)).astype(jnp.bfloat16)
    grad_query_last = (
        (
            (
                mixed("qcht,qcthe->qche", own_slope, last_keys)
                + mixed("qchd,qdhe->qche", cross_slope, cls_keys_last)
            )
            * score_scale
        )
        .astype(jnp.bfloat16)
        .reshape(lists, local_cands, local_width)
    )
    own_key_grad = (mixed("qcht,qche->qcthe", own_slope, last_heads) * score_scale).reshape(
        lists, local_cands, seq_len, local_width
    )
    own_val_grad = mixed("qcht,qche->qcthe", own_last_weight, grad_mixed_last).reshape(
        lists, local_cands, seq_len, local_width
    )
    cls_key_terms = (mixed("qchd,qche->qdhe", cross_slope, last_heads) * score_scale).reshape(
        lists, cand_count, local_width
    )
    cls_val_terms = mixed("qchd,qche->qdhe", cross_last_weight, grad_mixed_last).reshape(
        lists, cand_count, local_width
    )
    back_keys, back_vals = (
        lax.psum_scatter(cls_key_terms, "cand", scatter_dimension=1, tiled=True),
        lax.psum_scatter(cls_val_terms, "cand", scatter_dimension=1, tiled=True),
    )
    first_cols = first_mask[None, None, :, None]
    key_grad = jnp.where(first_cols, own_key_grad + back_keys[:, :, None], own_key_grad).astype(
        jnp.bfloat16
    )
    val_grad = jnp.where(first_cols, own_val_grad + back_vals[:, :, None], own_val_grad).astype(
        jnp.bfloat16
    )
    joined = lax.all_gather(
        jnp.concatenate([key_grad, val_grad, grad_query_last[:, :, None]], 2),
        "mp",
        axis=3,
        tiled=True,
    )
    key_joined = joined[:, :, :seq_len]
    val_joined = joined[:, :, seq_len : 2 * seq_len]
    query_joined = joined[:, :, 2 * seq_len]
    summed_term = mixed("qcsf,df->qcsd", key_joined, last_full[1]) + mixed(
        "qcsf,df->qcsd", val_joined, last_full[2]
    )
    query_term = mixed("qcf,df->qcd", query_joined, last_full[0])
    summed_term = jnp.where(first_cols, summed_term + query_term[:, :, None], summed_term)
    grad_hidden = jnp.where(first_cols, summed_term + grad_last[:, :, None], summed_term)
    grad_first = norm_backward(grad_hidden, unit_first, inverse_first, gain_first).astype(
        jnp.bfloat16
    )
    grad_mixed_first = (
        mixed("qcsd,fd->qcsf", grad_first, w_out_first).astype(jnp.bfloat16).reshape(head_shape)
    )
    own_dot_first = mixed("qcshe,qcthe->qchst", grad_mixed_first, first_vals)
    cross_dot_first = mixed("qche,qdhe->qchd", grad_mixed_first[:, :, 0], cls_vals)
    own_part = jnp.sum(own_prob * own_dot_first, -1)
    row_part = own_part[..., 0] + jnp.sum(cross_prob * cross_dot_first, -1)
    centre_first = jnp.where(first_mask, row_part[..., None], own_part)
    own_slope_first = (own_prob * (own_dot_first - centre_first[..., None])).astype(jnp.bfloat16)
    cross_slope_first = (cross_prob * (cross_dot_first - row_part[..., None])).astype(jnp.bfloat16)
    query_grad = mixed("qchst,qcthe->qcshe", own_slope_first, first_keys)
    query_cls = mixed("qchd,qdhe->qche", cross_slope_first, cls_keys)
    query_grad = jnp.where(
        first_mask[None, None, :, None, None], query_grad + query_cls[:, :, None], query_grad
    )
    query_grad = (
        (query_grad * score_scale)
        .astype(jnp.bfloat16)
        .reshape(lists, local_cands, seq_len, local_width)
    )
    key_first = (mixed("qchst,qcshe->qcthe", own_slope_first, first_query) * score_scale).reshape(
        lists, local_cands, seq_len, local_width
    )
    val_first = mixed("qchst,qcshe->qcthe", own_weight, grad_mixed_first).reshape(
        lists, local_cands, seq_len, local_width
    )
    cls_key_first = (
        mixed("qchd,qche->qdhe", cross_slope_first, first_query[:, :, 0]) * score_scale
    ).reshape(lists, cand_count, local_width)
    cls_val_first = mixed("qchd,qche->qdhe", cross_weight, grad_mixed_first[:, :, 0]).reshape(
        lists, cand_count, local_width
    )
    key_first = key_first.astype(jnp.bfloat16)
    val_first = val_first.astype(jnp.bfloat16)
    row_count = lists * local_cands * seq_len
    stacked = jnp.stack([query_grad, key_first, val_first], 3).reshape(row_count, 3, local_width)
    cross_rows = lists * cand_count
    cross_stacked = jnp.stack(
        [jnp.zeros_like(cls_key_first), cls_key_first, cls_val_first], 2
    ).astype(jnp.bfloat16)
    all_rows = jnp.concatenate(
        [stacked, cross_stacked.reshape(cross_rows, 3, local_width)], 0
    )
    all_tokens = jnp.concatenate(
        [tokens.reshape(row_count, model_width), cls_tokens.reshape(cross_rows, model_width)], 0
    )
    partial_grad = lax.psum_scatter(
        mixed("rd,rkf->dkf", all_tokens, all_rows).astype(jnp.bfloat16),
        "cand",
        scatter_dimension=0,
        tiled=True,
    )
    return sum_query(partial_grad).astype(jnp.float32)


def solution(mesh):
    return jax.shard_map(
        local,
        mesh=mesh,
        in_specs=(
            P(("groups", "query"), "cand", None, None),
            P(("groups", "query"), "cand"),
            P(("groups", "query"), "cand"),
            P(None, None, "mp"),
            P("mp", None),
            P(),
            P(None, None, "mp"),
            P("mp", None),
            P(),
            P(),
        ),
        out_specs=P(("groups", "cand"), None, "mp"),
        check_vma=False,
    )
```

```python
import jax
import jax.numpy as jnp
from jax import lax
from jax.sharding import PartitionSpec as P

HEAD_DIM = 64


EPSILON = 1e-05
LOSS_SCALE = 1024.0
NEGATIVE = -1e30


def mixed(pattern, former, latter):
    return jnp.einsum(pattern, former, latter, preferred_element_type=jnp.float32)


def norm_forward(matrix, scales):
    center = matrix - jnp.mean(matrix, -1, keepdims=True)
    inverse = lax.rsqrt(jnp.mean(center * center, -1, keepdims=True) + EPSILON)
    normed = center * inverse
    return (normed * scales, normed, inverse)


def norm_backward(incoming, normed, inverse, scales):
    scaled = incoming * scales
    return inverse * (
        scaled
        - jnp.mean(scaled, -1, keepdims=True)
        - normed * jnp.mean(scaled * normed, -1, keepdims=True)
    )


def split_softmax(own_scores, cross_scores, first_mask):
    own_peak = jnp.max(own_scores, -1)
    row_peak = jnp.maximum(own_peak[..., 0], jnp.max(cross_scores, -1))
    peak = jnp.where(first_mask, row_peak[..., None], own_peak)
    own_exp = jnp.exp(own_scores - peak[..., None])
    cross_exp = jnp.exp(cross_scores - row_peak[..., None])
    own_totals = jnp.sum(own_exp, -1)
    row_totals = own_totals[..., 0] + jnp.sum(cross_exp, -1)
    totals = jnp.where(first_mask, row_totals[..., None], own_totals)
    return (own_exp / totals[..., None], cross_exp / row_totals[..., None])


def row_softmax(own_scores, cross_scores):
    peak = jnp.maximum(jnp.max(own_scores, -1), jnp.max(cross_scores, -1))[..., None]
    own_exp = jnp.exp(own_scores - peak)
    cross_exp = jnp.exp(cross_scores - peak)
    totals = (jnp.sum(own_exp, -1) + jnp.sum(cross_exp, -1))[..., None]
    return (own_exp / totals, cross_exp / totals)


def gather_cand(block, axis):
    count = lax.axis_size("cand")
    if count > 8:
        return lax.all_gather(block, "cand", axis=axis, tiled=True)
    me = lax.axis_index("cand")
    parts = [block] + [
        lax.ppermute(block, "cand", [(j, (j + k) % count) for j in range(count)])
        for k in range(1, count)
    ]
    ordered = jnp.take(jnp.stack(parts, 0), (me - jnp.arange(count)) % count, axis=0)
    ordered = jnp.moveaxis(ordered, 0, axis)
    shape = block.shape[:axis] + (count * block.shape[axis],) + block.shape[axis + 1 :]
    return ordered.reshape(shape)


def sum_cand(block):
    count = lax.axis_size("cand")
    if count > 8:
        return lax.psum(block, "cand")
    total = block
    for k in range(1, count):
        total = total + lax.ppermute(block, "cand", [(j, (j + k) % count) for j in range(count)])
    return total


def scatter_cand(block, axis):
    count = lax.axis_size("cand")
    if count > 8:
        return lax.psum_scatter(block, "cand", scatter_dimension=axis, tiled=True)
    me = lax.axis_index("cand")
    width = block.shape[axis] // count
    total = lax.dynamic_slice_in_dim(block, me * width, width, axis)
    for k in range(1, count):
        piece = lax.dynamic_slice_in_dim(block, ((me + k) % count) * width, width, axis)
        total = total + lax.ppermute(piece, "cand", [(j, (j + k) % count) for j in range(count)])
    return total


def sum_query(block):
    if lax.axis_size("query") != 2:
        return lax.psum(block, "query")
    other = lax.ppermute(block, "query", [(0, 1), (1, 0)])
    return block.astype(jnp.float32) + other.astype(jnp.float32)


def local(
    tokens,
    lengths,
    teacher,
    w_first,
    w_out_first,
    gain_first,
    w_last,
    w_out_last,
    gain_last,
    w_score,
):
    lists, local_cands, seq_len, model_width = tokens.shape
    local_width = w_first.shape[2]
    local_heads = local_width // HEAD_DIM
    cand_count = local_cands * lax.axis_size("cand")
    query_count = lists * lax.axis_size("query")
    score_scale = HEAD_DIM ** (-0.5)
    positions = jnp.arange(seq_len)
    first_mask = positions == 0
    own_valid = positions[None, None, :] < lengths[:, :, None]
    local_ids = lax.axis_index("cand") * local_cands + jnp.arange(local_cands)
    cross_valid = local_ids[:, None] != jnp.arange(cand_count)[None, :]
    head_shape = (lists, local_cands, seq_len, local_heads, HEAD_DIM)
    cls_shape = (lists, cand_count, local_heads, HEAD_DIM)
    out_first_full = lax.all_gather(w_out_first, "mp", axis=0, tiled=True)
    last_full = lax.all_gather(w_last, "mp", axis=2, tiled=True)
    out_last_full = lax.all_gather(w_out_last, "mp", axis=0, tiled=True)
    teacher_all = gather_cand(teacher, 1)
    cls_tokens = gather_cand(tokens[:, :, 0], 1)
    projected = mixed("qcsd,kdf->kqcsf", tokens, w_first).astype(jnp.bfloat16)
    cls_projected = mixed("qcd,kdf->kqcf", cls_tokens, w_first[1:]).astype(jnp.bfloat16)
    gathered_keys = cls_projected[0]
    gathered_vals = cls_projected[1]
    first_query = projected[0].reshape(head_shape)
    first_keys = projected[1].reshape(head_shape)
    first_vals = projected[2].reshape(head_shape)
    cls_keys = gathered_keys.reshape(cls_shape)
    cls_vals = gathered_vals.reshape(cls_shape)
    own_scores = mixed("qcshe,qcthe->qchst", first_query, first_keys) * score_scale
    own_scores = jnp.where(own_valid[:, :, None, None, :], own_scores, NEGATIVE)
    cross_scores = mixed("qche,qdhe->qchd", first_query[:, :, 0], cls_keys) * score_scale
    cross_scores = jnp.where(cross_valid[None, :, None, :], cross_scores, NEGATIVE)
    own_prob, cross_prob = split_softmax(own_scores, cross_scores, first_mask)
    own_weight = own_prob.astype(jnp.bfloat16)
    cross_weight = cross_prob.astype(jnp.bfloat16)
    attended = mixed("qchst,qcthe->qcshe", own_weight, first_vals)
    attended_cls = mixed("qchd,qdhe->qche", cross_weight, cls_vals)
    attended = jnp.where(
        first_mask[None, None, :, None, None], attended + attended_cls[:, :, None], attended
    )
    first_mixed = attended.reshape(lists, local_cands, seq_len, local_width).astype(jnp.bfloat16)
    first_joined = lax.all_gather(first_mixed, "mp", axis=3, tiled=True)
    residual_first = tokens.astype(jnp.float32) + mixed(
        "qcsf,fd->qcsd", first_joined, out_first_full
    )
    normed_first, unit_first, inverse_first = norm_forward(residual_first, gain_first)
    hidden = normed_first.astype(jnp.bfloat16)
    last_query = mixed("qcd,df->qcf", hidden[:, :, 0], w_last[0]).astype(jnp.bfloat16)
    last_kv = mixed("qcsd,kdf->kqcsf", hidden, w_last[1:]).astype(jnp.bfloat16)
    gathered_kv_last = gather_cand(
        jnp.concatenate([last_kv[0][:, :, 0], last_kv[1][:, :, 0]], -1), 1
    )
    gathered_keys_last = gathered_kv_last[..., :local_width]
    gathered_vals_last = gathered_kv_last[..., local_width:]
    last_heads = last_query.reshape(lists, local_cands, local_heads, HEAD_DIM)
    last_keys = last_kv[0].reshape(head_shape)
    last_vals = last_kv[1].reshape(head_shape)
    cls_keys_last = gathered_keys_last.reshape(cls_shape)
    cls_vals_last = gathered_vals_last.reshape(cls_shape)
    own_last = mixed("qche,qcthe->qcht", last_heads, last_keys) * score_scale
    own_last = jnp.where(own_valid[:, :, None, :], own_last, NEGATIVE)
    cross_last = mixed("qche,qdhe->qchd", last_heads, cls_keys_last) * score_scale
    cross_last = jnp.where(cross_valid[None, :, None, :], cross_last, NEGATIVE)
    own_last_prob, cross_last_prob = row_softmax(own_last, cross_last)
    own_last_weight = own_last_prob.astype(jnp.bfloat16)
    cross_last_weight = cross_last_prob.astype(jnp.bfloat16)
    attended_last = mixed("qcht,qcthe->qche", own_last_weight, last_vals) + mixed(
        "qchd,qdhe->qche", cross_last_weight, cls_vals_last
    )
    last_mixed = attended_last.reshape(lists, local_cands, local_width).astype(jnp.bfloat16)
    last_joined = lax.all_gather(last_mixed, "mp", axis=2, tiled=True)
    residual_last = hidden[:, :, 0].astype(jnp.float32) + mixed(
        "qcf,fd->qcd", last_joined, out_last_full
    )
    normed_last, unit_last, inverse_last = norm_forward(residual_last, gain_last)
    scores = jnp.einsum("qcd,d->qc", normed_last, w_score, precision=lax.Precision.HIGHEST)
    score_exp = jnp.exp(scores)
    teacher_peak = jnp.max(teacher_all, 1)
    teacher_exp = jnp.exp(teacher - teacher_peak[:, None])
    teacher_totals = jnp.sum(jnp.exp(teacher_all - teacher_peak[:, None]), 1)
    score_totals = sum_cand(jnp.sum(score_exp, 1))
    student_prob = score_exp / score_totals[:, None]
    teacher_prob = teacher_exp / teacher_totals[:, None]
    score_grad = LOSS_SCALE * (student_prob - teacher_prob) / query_count
    grad_last = norm_backward(score_grad[..., None] * w_score, unit_last, inverse_last, gain_last)
    grad_last_low = grad_last.astype(jnp.bfloat16)
    grad_mixed_last = (
        mixed("qcd,fd->qcf", grad_last_low, w_out_last)
        .astype(jnp.bfloat16)
        .reshape(lists, local_cands, local_heads, HEAD_DIM)
    )
    own_dot = mixed("qche,qcthe->qcht", grad_mixed_last, last_vals)
    cross_dot = mixed("qche,qdhe->qchd", grad_mixed_last, cls_vals_last)
    centre = jnp.sum(own_last_prob * own_dot, -1, keepdims=True) + jnp.sum(
        cross_last_prob * cross_dot, -1, keepdims=True
    )
    own_slope = (own_last_prob * (own_dot - centre)).astype(jnp.bfloat16)
    cross_slope = (cross_last_prob * (cross_dot - centre)).astype(jnp.bfloat16)
    grad_query_last = (
        (
            (
                mixed("qcht,qcthe->qche", own_slope, last_keys)
                + mixed("qchd,qdhe->qche", cross_slope, cls_keys_last)
            )
            * score_scale
        )
        .astype(jnp.bfloat16)
        .reshape(lists, local_cands, local_width)
    )
    own_key_grad = (mixed("qcht,qche->qcthe", own_slope, last_heads) * score_scale).reshape(
        lists, local_cands, seq_len, local_width
    )
    own_val_grad = mixed("qcht,qche->qcthe", own_last_weight, grad_mixed_last).reshape(
        lists, local_cands, seq_len, local_width
    )
    cls_key_terms = (mixed("qchd,qche->qdhe", cross_slope, last_heads) * score_scale).reshape(
        lists, cand_count, local_width
    )
    cls_val_terms = mixed("qchd,qche->qdhe", cross_last_weight, grad_mixed_last).reshape(
        lists, cand_count, local_width
    )
    back_terms = scatter_cand(jnp.concatenate([cls_key_terms, cls_val_terms], -1), 1)
    back_keys = back_terms[..., :local_width]
    back_vals = back_terms[..., local_width:]
    first_cols = first_mask[None, None, :, None]
    key_grad = jnp.where(first_cols, own_key_grad + back_keys[:, :, None], own_key_grad).astype(
        jnp.bfloat16
    )
    val_grad = jnp.where(first_cols, own_val_grad + back_vals[:, :, None], own_val_grad).astype(
        jnp.bfloat16
    )
    joined = lax.all_gather(
        jnp.concatenate([key_grad, val_grad, grad_query_last[:, :, None]], 2),
        "mp",
        axis=3,
        tiled=True,
    )
    key_joined = joined[:, :, :seq_len]
    val_joined = joined[:, :, seq_len : 2 * seq_len]
    query_joined = joined[:, :, 2 * seq_len]
    summed_term = mixed("qcsf,df->qcsd", key_joined, last_full[1]) + mixed(
        "qcsf,df->qcsd", val_joined, last_full[2]
    )
    query_term = mixed("qcf,df->qcd", query_joined, last_full[0])
    summed_term = jnp.where(first_cols, summed_term + query_term[:, :, None], summed_term)
    grad_hidden = jnp.where(first_cols, summed_term + grad_last[:, :, None], summed_term)
    grad_first = norm_backward(grad_hidden, unit_first, inverse_first, gain_first).astype(
        jnp.bfloat16
    )
    grad_mixed_first = (
        mixed("qcsd,fd->qcsf", grad_first, w_out_first).astype(jnp.bfloat16).reshape(head_shape)
    )
    own_dot_first = mixed("qcshe,qcthe->qchst", grad_mixed_first, first_vals)
    cross_dot_first = mixed("qche,qdhe->qchd", grad_mixed_first[:, :, 0], cls_vals)
    own_part = jnp.sum(own_prob * own_dot_first, -1)
    row_part = own_part[..., 0] + jnp.sum(cross_prob * cross_dot_first, -1)
    centre_first = jnp.where(first_mask, row_part[..., None], own_part)
    own_slope_first = (own_prob * (own_dot_first - centre_first[..., None])).astype(jnp.bfloat16)
    cross_slope_first = (cross_prob * (cross_dot_first - row_part[..., None])).astype(jnp.bfloat16)
    query_grad = mixed("qchst,qcthe->qcshe", own_slope_first, first_keys)
    query_cls = mixed("qchd,qdhe->qche", cross_slope_first, cls_keys)
    query_grad = jnp.where(
        first_mask[None, None, :, None, None], query_grad + query_cls[:, :, None], query_grad
    )
    query_grad = (
        (query_grad * score_scale)
        .astype(jnp.bfloat16)
        .reshape(lists, local_cands, seq_len, local_width)
    )
    key_first = (mixed("qchst,qcshe->qcthe", own_slope_first, first_query) * score_scale).reshape(
        lists, local_cands, seq_len, local_width
    )
    val_first = mixed("qchst,qcshe->qcthe", own_weight, grad_mixed_first).reshape(
        lists, local_cands, seq_len, local_width
    )
    cls_key_first = (
        mixed("qchd,qche->qdhe", cross_slope_first, first_query[:, :, 0]) * score_scale
    ).reshape(lists, cand_count, local_width)
    cls_val_first = mixed("qchd,qche->qdhe", cross_weight, grad_mixed_first[:, :, 0]).reshape(
        lists, cand_count, local_width
    )
    key_first = key_first.astype(jnp.bfloat16)
    val_first = val_first.astype(jnp.bfloat16)
    row_count = lists * local_cands * seq_len
    stacked = jnp.stack([query_grad, key_first, val_first], 3).reshape(row_count, 3, local_width)
    cross_rows = lists * cand_count
    cross_stacked = jnp.stack(
        [jnp.zeros_like(cls_key_first), cls_key_first, cls_val_first], 2
    ).astype(jnp.bfloat16)
    all_rows = jnp.concatenate(
        [stacked, cross_stacked.reshape(cross_rows, 3, local_width)], 0
    )
    all_tokens = jnp.concatenate(
        [tokens.reshape(row_count, model_width), cls_tokens.reshape(cross_rows, model_width)], 0
    )
    partial_grad = lax.psum_scatter(
        mixed("rd,rkf->dkf", all_tokens, all_rows).astype(jnp.bfloat16),
        "cand",
        scatter_dimension=0,
        tiled=True,
    )
    return sum_query(partial_grad).astype(jnp.float32)


def solution(mesh):
    return jax.shard_map(
        local,
        mesh=mesh,
        in_specs=(
            P(("groups", "query"), "cand", None, None),
            P(("groups", "query"), "cand"),
            P(("groups", "query"), "cand"),
            P(None, None, "mp"),
            P("mp", None),
            P(),
            P(None, None, "mp"),
            P("mp", None),
            P(),
            P(),
        ),
        out_specs=P(("groups", "cand"), None, "mp"),
        check_vma=False,
    )
```

```python
import jax
import jax.numpy as jnp
from jax import lax
from jax.sharding import PartitionSpec as P

HEAD_DIM = 64


EPSILON = 1e-05
LOSS_SCALE = 1024.0
NEGATIVE = -1e30


def mixed(pattern, former, latter):
    return jnp.einsum(pattern, former, latter, preferred_element_type=jnp.float32)


def norm_forward(matrix, scales):
    center = matrix - jnp.mean(matrix, -1, keepdims=True)
    inverse = lax.rsqrt(jnp.mean(center * center, -1, keepdims=True) + EPSILON)
    normed = center * inverse
    return (normed * scales, normed, inverse)


def norm_backward(incoming, normed, inverse, scales):
    scaled = incoming * scales
    return inverse * (
        scaled
        - jnp.mean(scaled, -1, keepdims=True)
        - normed * jnp.mean(scaled * normed, -1, keepdims=True)
    )


def split_softmax(own_scores, cross_scores, first_mask):
    own_peak = jnp.max(own_scores, -1)
    row_peak = jnp.maximum(own_peak[..., 0], jnp.max(cross_scores, -1))
    peak = jnp.where(first_mask, row_peak[..., None], own_peak)
    own_exp = jnp.exp(own_scores - peak[..., None])
    cross_exp = jnp.exp(cross_scores - row_peak[..., None])
    own_totals = jnp.sum(own_exp, -1)
    row_totals = own_totals[..., 0] + jnp.sum(cross_exp, -1)
    totals = jnp.where(first_mask, row_totals[..., None], own_totals)
    return (own_exp / totals[..., None], cross_exp / row_totals[..., None])


def row_softmax(own_scores, cross_scores):
    peak = jnp.maximum(jnp.max(own_scores, -1), jnp.max(cross_scores, -1))[..., None]
    own_exp = jnp.exp(own_scores - peak)
    cross_exp = jnp.exp(cross_scores - peak)
    totals = (jnp.sum(own_exp, -1) + jnp.sum(cross_exp, -1))[..., None]
    return (own_exp / totals, cross_exp / totals)


def gather_cand(block, axis):
    count = lax.axis_size("cand")
    if count > 8:
        return lax.all_gather(block, "cand", axis=axis, tiled=True)
    me = lax.axis_index("cand")
    parts = [block] + [
        lax.ppermute(block, "cand", [(j, (j + k) % count) for j in range(count)])
        for k in range(1, count)
    ]
    ordered = jnp.take(jnp.stack(parts, 0), (me - jnp.arange(count)) % count, axis=0)
    ordered = jnp.moveaxis(ordered, 0, axis)
    shape = block.shape[:axis] + (count * block.shape[axis],) + block.shape[axis + 1 :]
    return ordered.reshape(shape)


def sum_cand(block):
    count = lax.axis_size("cand")
    if count > 8:
        return lax.psum(block, "cand")
    total = block
    for k in range(1, count):
        total = total + lax.ppermute(block, "cand", [(j, (j + k) % count) for j in range(count)])
    return total


def scatter_cand(block, axis):
    count = lax.axis_size("cand")
    if count > 8:
        return lax.psum_scatter(block, "cand", scatter_dimension=axis, tiled=True)
    me = lax.axis_index("cand")
    width = block.shape[axis] // count
    total = lax.dynamic_slice_in_dim(block, me * width, width, axis)
    for k in range(1, count):
        piece = lax.dynamic_slice_in_dim(block, ((me + k) % count) * width, width, axis)
        total = total + lax.ppermute(piece, "cand", [(j, (j + k) % count) for j in range(count)])
    return total


def sum_query(block):
    if lax.axis_size("query") != 2:
        return lax.psum(block, "query")
    other = lax.ppermute(block, "query", [(0, 1), (1, 0)])
    return block.astype(jnp.float32) + other.astype(jnp.float32)


def local(
    tokens,
    lengths,
    teacher,
    w_first,
    w_out_first,
    gain_first,
    w_last,
    w_out_last,
    gain_last,
    w_score,
):
    lists, local_cands, seq_len, model_width = tokens.shape
    local_width = w_first.shape[2]
    local_heads = local_width // HEAD_DIM
    cand_count = local_cands * lax.axis_size("cand")
    query_count = lists * lax.axis_size("query")
    score_scale = HEAD_DIM ** (-0.5)
    positions = jnp.arange(seq_len)
    first_mask = positions == 0
    own_valid = positions[None, None, :] < lengths[:, :, None]
    local_ids = lax.axis_index("cand") * local_cands + jnp.arange(local_cands)
    cross_valid = local_ids[:, None] != jnp.arange(cand_count)[None, :]
    head_shape = (lists, local_cands, seq_len, local_heads, HEAD_DIM)
    cls_shape = (lists, cand_count, local_heads, HEAD_DIM)
    out_first_full = lax.all_gather(w_out_first, "mp", axis=0, tiled=True)
    last_full = lax.all_gather(w_last, "mp", axis=2, tiled=True)
    out_last_full = lax.all_gather(w_out_last, "mp", axis=0, tiled=True)
    teacher_all = gather_cand(teacher, 1)
    cls_tokens = gather_cand(tokens[:, :, 0], 1)
    projected = mixed("qcsd,kdf->kqcsf", tokens, w_first).astype(jnp.bfloat16)
    cls_projected = mixed("qcd,kdf->kqcf", cls_tokens, w_first[1:]).astype(jnp.bfloat16)
    gathered_keys = cls_projected[0]
    gathered_vals = cls_projected[1]
    first_query = projected[0].reshape(head_shape)
    first_keys = projected[1].reshape(head_shape)
    first_vals = projected[2].reshape(head_shape)
    cls_keys = gathered_keys.reshape(cls_shape)
    cls_vals = gathered_vals.reshape(cls_shape)
    own_scores = mixed("qcshe,qcthe->qchst", first_query, first_keys) * score_scale
    own_scores = jnp.where(own_valid[:, :, None, None, :], own_scores, NEGATIVE)
    cross_scores = mixed("qche,qdhe->qchd", first_query[:, :, 0], cls_keys) * score_scale
    cross_scores = jnp.where(cross_valid[None, :, None, :], cross_scores, NEGATIVE)
    own_prob, cross_prob = split_softmax(own_scores, cross_scores, first_mask)
    own_weight = own_prob.astype(jnp.bfloat16)
    cross_weight = cross_prob.astype(jnp.bfloat16)
    attended = mixed("qchst,qcthe->qcshe", own_weight, first_vals)
    attended_cls = mixed("qchd,qdhe->qche", cross_weight, cls_vals)
    attended = jnp.where(
        first_mask[None, None, :, None, None], attended + attended_cls[:, :, None], attended
    )
    first_mixed = attended.reshape(lists, local_cands, seq_len, local_width).astype(jnp.bfloat16)
    first_joined = lax.all_gather(first_mixed, "mp", axis=3, tiled=True)
    residual_first = tokens.astype(jnp.float32) + mixed(
        "qcsf,fd->qcsd", first_joined, out_first_full
    )
    normed_first, unit_first, inverse_first = norm_forward(residual_first, gain_first)
    hidden = normed_first.astype(jnp.bfloat16)
    last_query = mixed("qcd,df->qcf", hidden[:, :, 0], w_last[0]).astype(jnp.bfloat16)
    last_kv = mixed("qcsd,kdf->kqcsf", hidden, w_last[1:]).astype(jnp.bfloat16)
    gathered_kv_last = gather_cand(
        jnp.concatenate([last_kv[0][:, :, 0], last_kv[1][:, :, 0]], -1), 1
    )
    gathered_keys_last = gathered_kv_last[..., :local_width]
    gathered_vals_last = gathered_kv_last[..., local_width:]
    last_heads = last_query.reshape(lists, local_cands, local_heads, HEAD_DIM)
    last_keys = last_kv[0].reshape(head_shape)
    last_vals = last_kv[1].reshape(head_shape)
    cls_keys_last = gathered_keys_last.reshape(cls_shape)
    cls_vals_last = gathered_vals_last.reshape(cls_shape)
    own_last = mixed("qche,qcthe->qcht", last_heads, last_keys) * score_scale
    own_last = jnp.where(own_valid[:, :, None, :], own_last, NEGATIVE)
    cross_last = mixed("qche,qdhe->qchd", last_heads, cls_keys_last) * score_scale
    cross_last = jnp.where(cross_valid[None, :, None, :], cross_last, NEGATIVE)
    own_last_prob, cross_last_prob = row_softmax(own_last, cross_last)
    own_last_weight = own_last_prob.astype(jnp.bfloat16)
    cross_last_weight = cross_last_prob.astype(jnp.bfloat16)
    attended_last = mixed("qcht,qcthe->qche", own_last_weight, last_vals) + mixed(
        "qchd,qdhe->qche", cross_last_weight, cls_vals_last
    )
    last_mixed = attended_last.reshape(lists, local_cands, local_width).astype(jnp.bfloat16)
    last_joined = lax.all_gather(last_mixed, "mp", axis=2, tiled=True)
    residual_last = hidden[:, :, 0].astype(jnp.float32) + mixed(
        "qcf,fd->qcd", last_joined, out_last_full
    )
    normed_last, unit_last, inverse_last = norm_forward(residual_last, gain_last)
    scores = jnp.einsum("qcd,d->qc", normed_last, w_score, precision=lax.Precision.HIGHEST)
    score_exp = jnp.exp(scores)
    teacher_peak = jnp.max(teacher_all, 1)
    teacher_exp = jnp.exp(teacher - teacher_peak[:, None])
    teacher_totals = jnp.sum(jnp.exp(teacher_all - teacher_peak[:, None]), 1)
    score_totals = sum_cand(jnp.sum(score_exp, 1))
    student_prob = score_exp / score_totals[:, None]
    teacher_prob = teacher_exp / teacher_totals[:, None]
    score_grad = LOSS_SCALE * (student_prob - teacher_prob) / query_count
    grad_last = norm_backward(score_grad[..., None] * w_score, unit_last, inverse_last, gain_last)
    grad_last_low = grad_last.astype(jnp.bfloat16)
    grad_mixed_last = (
        mixed("qcd,fd->qcf", grad_last_low, w_out_last)
        .astype(jnp.bfloat16)
        .reshape(lists, local_cands, local_heads, HEAD_DIM)
    )
    own_dot = mixed("qche,qcthe->qcht", grad_mixed_last, last_vals)
    cross_dot = mixed("qche,qdhe->qchd", grad_mixed_last, cls_vals_last)
    centre = jnp.sum(own_last_prob * own_dot, -1, keepdims=True) + jnp.sum(
        cross_last_prob * cross_dot, -1, keepdims=True
    )
    own_slope = (own_last_prob * (own_dot - centre)).astype(jnp.bfloat16)
    cross_slope = (cross_last_prob * (cross_dot - centre)).astype(jnp.bfloat16)
    grad_query_last = (
        (
            (
                mixed("qcht,qcthe->qche", own_slope, last_keys)
                + mixed("qchd,qdhe->qche", cross_slope, cls_keys_last)
            )
            * score_scale
        )
        .astype(jnp.bfloat16)
        .reshape(lists, local_cands, local_width)
    )
    own_key_grad = (mixed("qcht,qche->qcthe", own_slope, last_heads) * score_scale).reshape(
        lists, local_cands, seq_len, local_width
    )
    own_val_grad = mixed("qcht,qche->qcthe", own_last_weight, grad_mixed_last).reshape(
        lists, local_cands, seq_len, local_width
    )
    cls_key_terms = (mixed("qchd,qche->qdhe", cross_slope, last_heads) * score_scale).reshape(
        lists, cand_count, local_width
    )
    cls_val_terms = mixed("qchd,qche->qdhe", cross_last_weight, grad_mixed_last).reshape(
        lists, cand_count, local_width
    )
    back_terms = scatter_cand(jnp.concatenate([cls_key_terms, cls_val_terms], -1), 1)
    back_keys = back_terms[..., :local_width]
    back_vals = back_terms[..., local_width:]
    first_cols = first_mask[None, None, :, None]
    key_grad = jnp.where(first_cols, own_key_grad + back_keys[:, :, None], own_key_grad).astype(
        jnp.bfloat16
    )
    val_grad = jnp.where(first_cols, own_val_grad + back_vals[:, :, None], own_val_grad).astype(
        jnp.bfloat16
    )
    joined = lax.all_gather(
        jnp.concatenate([key_grad, val_grad, grad_query_last[:, :, None]], 2),
        "mp",
        axis=3,
        tiled=True,
    )
    key_joined = joined[:, :, :seq_len]
    val_joined = joined[:, :, seq_len : 2 * seq_len]
    query_joined = joined[:, :, 2 * seq_len]
    summed_term = mixed("qcsf,df->qcsd", key_joined, last_full[1]) + mixed(
        "qcsf,df->qcsd", val_joined, last_full[2]
    )
    query_term = mixed("qcf,df->qcd", query_joined, last_full[0])
    summed_term = jnp.where(first_cols, summed_term + query_term[:, :, None], summed_term)
    grad_hidden = jnp.where(first_cols, summed_term + grad_last[:, :, None], summed_term)
    grad_first = norm_backward(grad_hidden, unit_first, inverse_first, gain_first).astype(
        jnp.bfloat16
    )
    grad_mixed_first = (
        mixed("qcsd,fd->qcsf", grad_first, w_out_first).astype(jnp.bfloat16).reshape(head_shape)
    )
    own_dot_first = mixed("qcshe,qcthe->qchst", grad_mixed_first, first_vals)
    cross_dot_first = mixed("qche,qdhe->qchd", grad_mixed_first[:, :, 0], cls_vals)
    own_part = jnp.sum(own_prob * own_dot_first, -1)
    row_part = own_part[..., 0] + jnp.sum(cross_prob * cross_dot_first, -1)
    centre_first = jnp.where(first_mask, row_part[..., None], own_part)
    own_slope_first = (own_prob * (own_dot_first - centre_first[..., None])).astype(jnp.bfloat16)
    cross_slope_first = (cross_prob * (cross_dot_first - row_part[..., None])).astype(jnp.bfloat16)
    query_grad = mixed("qchst,qcthe->qcshe", own_slope_first, first_keys)
    query_cls = mixed("qchd,qdhe->qche", cross_slope_first, cls_keys)
    query_grad = jnp.where(
        first_mask[None, None, :, None, None], query_grad + query_cls[:, :, None], query_grad
    )
    query_grad = (
        (query_grad * score_scale)
        .astype(jnp.bfloat16)
        .reshape(lists, local_cands, seq_len, local_width)
    )
    key_first = (mixed("qchst,qcshe->qcthe", own_slope_first, first_query) * score_scale).reshape(
        lists, local_cands, seq_len, local_width
    )
    val_first = mixed("qchst,qcshe->qcthe", own_weight, grad_mixed_first).reshape(
        lists, local_cands, seq_len, local_width
    )
    cls_key_first = (
        mixed("qchd,qche->qdhe", cross_slope_first, first_query[:, :, 0]) * score_scale
    ).reshape(lists, cand_count, local_width)
    cls_val_first = mixed("qchd,qche->qdhe", cross_weight, grad_mixed_first[:, :, 0]).reshape(
        lists, cand_count, local_width
    )
    key_first = key_first.astype(jnp.bfloat16)
    val_first = val_first.astype(jnp.bfloat16)
    row_count = lists * local_cands * seq_len
    stacked = jnp.stack([query_grad, key_first, val_first], 3).reshape(row_count, 3, local_width)
    cross_rows = lists * cand_count
    cross_stacked = jnp.stack(
        [jnp.zeros_like(cls_key_first), cls_key_first, cls_val_first], 2
    ).astype(jnp.bfloat16)
    all_rows = jnp.concatenate(
        [stacked, cross_stacked.reshape(cross_rows, 3, local_width)], 0
    )
    all_tokens = jnp.concatenate(
        [tokens.reshape(row_count, model_width), cls_tokens.reshape(cross_rows, model_width)], 0
    )
    if lax.axis_size("query") != 2:
        partial_grad = lax.psum_scatter(
            mixed("rd,rkf->dkf", all_tokens, all_rows).astype(jnp.bfloat16),
            "cand",
            scatter_dimension=0,
            tiled=True,
        )
        return sum_query(partial_grad).astype(jnp.float32)
    swap = [(0, 1), (1, 0)]
    half = 3 * local_width // 2
    side = lax.axis_index("query")
    other_tokens = lax.ppermute(all_tokens, "query", swap)
    flat_rows = all_rows.reshape(all_rows.shape[0], 3 * local_width)
    other_rows = lax.ppermute(flat_rows, "query", swap)
    own_half = lax.dynamic_slice_in_dim(flat_rows, side * half, half, 1)
    other_half = lax.dynamic_slice_in_dim(other_rows, side * half, half, 1)
    paired = mixed("rd,rf->df", all_tokens, own_half) + mixed("rd,rf->df", other_tokens, other_half)
    reduced = lax.psum_scatter(
        paired.astype(jnp.bfloat16), "cand", scatter_dimension=0, tiled=True
    )
    partner = lax.ppermute(reduced, "query", swap)
    joined = jnp.where(
        side == 0,
        jnp.concatenate([reduced, partner], 1),
        jnp.concatenate([partner, reduced], 1),
    )
    return joined.reshape(joined.shape[0], 3, local_width).astype(jnp.float32)


def solution(mesh):
    return jax.shard_map(
        local,
        mesh=mesh,
        in_specs=(
            P(("groups", "query"), "cand", None, None),
            P(("groups", "query"), "cand"),
            P(("groups", "query"), "cand"),
            P(None, None, "mp"),
            P("mp", None),
            P(),
            P(None, None, "mp"),
            P("mp", None),
            P(),
            P(),
        ),
        out_specs=P(("groups", "cand"), None, "mp"),
        check_vma=False,
    )
```

```python
import jax
import jax.numpy as jnp
from jax import lax
from jax.sharding import PartitionSpec as P

HEAD_DIM = 64


EPSILON = 1e-05
LOSS_SCALE = 1024.0
NEGATIVE = -1e30


def mixed(pattern, former, latter):
    return jnp.einsum(pattern, former, latter, preferred_element_type=jnp.float32)


def norm_forward(matrix, scales):
    center = matrix - jnp.mean(matrix, -1, keepdims=True)
    inverse = lax.rsqrt(jnp.mean(center * center, -1, keepdims=True) + EPSILON)
    normed = center * inverse
    return (normed * scales, normed, inverse)


def norm_backward(incoming, normed, inverse, scales):
    scaled = incoming * scales
    return inverse * (
        scaled
        - jnp.mean(scaled, -1, keepdims=True)
        - normed * jnp.mean(scaled * normed, -1, keepdims=True)
    )


def split_softmax(own_scores, cross_scores, first_mask):
    own_peak = jnp.max(own_scores, -1)
    row_peak = jnp.maximum(own_peak[..., 0], jnp.max(cross_scores, -1))
    peak = jnp.where(first_mask, row_peak[..., None], own_peak)
    own_exp = jnp.exp(own_scores - peak[..., None])
    cross_exp = jnp.exp(cross_scores - row_peak[..., None])
    own_totals = jnp.sum(own_exp, -1)
    row_totals = own_totals[..., 0] + jnp.sum(cross_exp, -1)
    totals = jnp.where(first_mask, row_totals[..., None], own_totals)
    return (own_exp / totals[..., None], cross_exp / row_totals[..., None])


def row_softmax(own_scores, cross_scores):
    peak = jnp.maximum(jnp.max(own_scores, -1), jnp.max(cross_scores, -1))[..., None]
    own_exp = jnp.exp(own_scores - peak)
    cross_exp = jnp.exp(cross_scores - peak)
    totals = (jnp.sum(own_exp, -1) + jnp.sum(cross_exp, -1))[..., None]
    return (own_exp / totals, cross_exp / totals)


def gather_cand(block, axis):
    count = lax.axis_size("cand")
    if count > 8:
        return lax.all_gather(block, "cand", axis=axis, tiled=True)
    me = lax.axis_index("cand")
    parts = [block] + [
        lax.ppermute(block, "cand", [(j, (j + k) % count) for j in range(count)])
        for k in range(1, count)
    ]
    ordered = jnp.take(jnp.stack(parts, 0), (me - jnp.arange(count)) % count, axis=0)
    ordered = jnp.moveaxis(ordered, 0, axis)
    shape = block.shape[:axis] + (count * block.shape[axis],) + block.shape[axis + 1 :]
    return ordered.reshape(shape)


def sum_cand(block):
    count = lax.axis_size("cand")
    if count > 8:
        return lax.psum(block, "cand")
    total = block
    for k in range(1, count):
        total = total + lax.ppermute(block, "cand", [(j, (j + k) % count) for j in range(count)])
    return total


def scatter_cand(block, axis):
    count = lax.axis_size("cand")
    if count > 8:
        return lax.psum_scatter(block, "cand", scatter_dimension=axis, tiled=True)
    me = lax.axis_index("cand")
    width = block.shape[axis] // count
    total = lax.dynamic_slice_in_dim(block, me * width, width, axis)
    for k in range(1, count):
        piece = lax.dynamic_slice_in_dim(block, ((me + k) % count) * width, width, axis)
        total = total + lax.ppermute(piece, "cand", [(j, (j + k) % count) for j in range(count)])
    return total


def sum_query(block):
    if lax.axis_size("query") != 2:
        return lax.psum(block, "query")
    other = lax.ppermute(block, "query", [(0, 1), (1, 0)])
    return block.astype(jnp.float32) + other.astype(jnp.float32)


def local(
    tokens,
    lengths,
    teacher,
    w_first,
    w_out_first,
    gain_first,
    w_last,
    w_out_last,
    gain_last,
    w_score,
):
    lists, local_cands, seq_len, model_width = tokens.shape
    local_width = w_first.shape[2]
    local_heads = local_width // HEAD_DIM
    cand_count = local_cands * lax.axis_size("cand")
    query_count = lists * lax.axis_size("query")
    score_scale = HEAD_DIM ** (-0.5)
    positions = jnp.arange(seq_len)
    first_mask = positions == 0
    own_valid = positions[None, None, :] < lengths[:, :, None]
    local_ids = lax.axis_index("cand") * local_cands + jnp.arange(local_cands)
    cross_valid = local_ids[:, None] != jnp.arange(cand_count)[None, :]
    head_shape = (lists, local_cands, seq_len, local_heads, HEAD_DIM)
    cls_shape = (lists, cand_count, local_heads, HEAD_DIM)
    out_first_full = lax.all_gather(w_out_first, "mp", axis=0, tiled=True)
    last_full = lax.all_gather(w_last, "mp", axis=2, tiled=True)
    out_last_full = lax.all_gather(w_out_last, "mp", axis=0, tiled=True)
    teacher_all = gather_cand(teacher, 1)
    cls_tokens = gather_cand(tokens[:, :, 0], 1)
    row_count = lists * local_cands * seq_len
    swap = [(0, 1), (1, 0)]
    paired_lists = lax.axis_size("query") == 2
    if paired_lists:
        other_tokens = lax.ppermute(tokens.reshape(row_count, model_width), "query", swap)
    projected = mixed("qcsd,kdf->kqcsf", tokens, w_first).astype(jnp.bfloat16)
    cls_projected = mixed("qcd,kdf->kqcf", cls_tokens, w_first[1:]).astype(jnp.bfloat16)
    gathered_keys = cls_projected[0]
    gathered_vals = cls_projected[1]
    first_query = projected[0].reshape(head_shape)
    first_keys = projected[1].reshape(head_shape)
    first_vals = projected[2].reshape(head_shape)
    cls_keys = gathered_keys.reshape(cls_shape)
    cls_vals = gathered_vals.reshape(cls_shape)
    own_scores = mixed("qcshe,qcthe->qchst", first_query, first_keys) * score_scale
    own_scores = jnp.where(own_valid[:, :, None, None, :], own_scores, NEGATIVE)
    cross_scores = mixed("qche,qdhe->qchd", first_query[:, :, 0], cls_keys) * score_scale
    cross_scores = jnp.where(cross_valid[None, :, None, :], cross_scores, NEGATIVE)
    own_prob, cross_prob = split_softmax(own_scores, cross_scores, first_mask)
    own_weight = own_prob.astype(jnp.bfloat16)
    cross_weight = cross_prob.astype(jnp.bfloat16)
    attended = mixed("qchst,qcthe->qcshe", own_weight, first_vals)
    attended_cls = mixed("qchd,qdhe->qche", cross_weight, cls_vals)
    attended = jnp.where(
        first_mask[None, None, :, None, None], attended + attended_cls[:, :, None], attended
    )
    first_mixed = attended.reshape(lists, local_cands, seq_len, local_width).astype(jnp.bfloat16)
    first_joined = lax.all_gather(first_mixed, "mp", axis=3, tiled=True)
    residual_first = tokens.astype(jnp.float32) + mixed(
        "qcsf,fd->qcsd", first_joined, out_first_full
    )
    normed_first, unit_first, inverse_first = norm_forward(residual_first, gain_first)
    hidden = normed_first.astype(jnp.bfloat16)
    last_query = mixed("qcd,df->qcf", hidden[:, :, 0], w_last[0]).astype(jnp.bfloat16)
    last_kv = mixed("qcsd,kdf->kqcsf", hidden, w_last[1:]).astype(jnp.bfloat16)
    gathered_kv_last = gather_cand(
        jnp.concatenate([last_kv[0][:, :, 0], last_kv[1][:, :, 0]], -1), 1
    )
    gathered_keys_last = gathered_kv_last[..., :local_width]
    gathered_vals_last = gathered_kv_last[..., local_width:]
    last_heads = last_query.reshape(lists, local_cands, local_heads, HEAD_DIM)
    last_keys = last_kv[0].reshape(head_shape)
    last_vals = last_kv[1].reshape(head_shape)
    cls_keys_last = gathered_keys_last.reshape(cls_shape)
    cls_vals_last = gathered_vals_last.reshape(cls_shape)
    own_last = mixed("qche,qcthe->qcht", last_heads, last_keys) * score_scale
    own_last = jnp.where(own_valid[:, :, None, :], own_last, NEGATIVE)
    cross_last = mixed("qche,qdhe->qchd", last_heads, cls_keys_last) * score_scale
    cross_last = jnp.where(cross_valid[None, :, None, :], cross_last, NEGATIVE)
    own_last_prob, cross_last_prob = row_softmax(own_last, cross_last)
    own_last_weight = own_last_prob.astype(jnp.bfloat16)
    cross_last_weight = cross_last_prob.astype(jnp.bfloat16)
    attended_last = mixed("qcht,qcthe->qche", own_last_weight, last_vals) + mixed(
        "qchd,qdhe->qche", cross_last_weight, cls_vals_last
    )
    last_mixed = attended_last.reshape(lists, local_cands, local_width).astype(jnp.bfloat16)
    last_joined = lax.all_gather(last_mixed, "mp", axis=2, tiled=True)
    residual_last = hidden[:, :, 0].astype(jnp.float32) + mixed(
        "qcf,fd->qcd", last_joined, out_last_full
    )
    normed_last, unit_last, inverse_last = norm_forward(residual_last, gain_last)
    scores = jnp.einsum("qcd,d->qc", normed_last, w_score, precision=lax.Precision.HIGHEST)
    score_exp = jnp.exp(scores)
    teacher_peak = jnp.max(teacher_all, 1)
    teacher_exp = jnp.exp(teacher - teacher_peak[:, None])
    teacher_totals = jnp.sum(jnp.exp(teacher_all - teacher_peak[:, None]), 1)
    score_totals = sum_cand(jnp.sum(score_exp, 1))
    student_prob = score_exp / score_totals[:, None]
    teacher_prob = teacher_exp / teacher_totals[:, None]
    score_grad = LOSS_SCALE * (student_prob - teacher_prob) / query_count
    grad_last = norm_backward(score_grad[..., None] * w_score, unit_last, inverse_last, gain_last)
    grad_last_low = grad_last.astype(jnp.bfloat16)
    grad_mixed_last = (
        mixed("qcd,fd->qcf", grad_last_low, w_out_last)
        .astype(jnp.bfloat16)
        .reshape(lists, local_cands, local_heads, HEAD_DIM)
    )
    own_dot = mixed("qche,qcthe->qcht", grad_mixed_last, last_vals)
    cross_dot = mixed("qche,qdhe->qchd", grad_mixed_last, cls_vals_last)
    centre = jnp.sum(own_last_prob * own_dot, -1, keepdims=True) + jnp.sum(
        cross_last_prob * cross_dot, -1, keepdims=True
    )
    own_slope = (own_last_prob * (own_dot - centre)).astype(jnp.bfloat16)
    cross_slope = (cross_last_prob * (cross_dot - centre)).astype(jnp.bfloat16)
    grad_query_last = (
        (
            (
                mixed("qcht,qcthe->qche", own_slope, last_keys)
                + mixed("qchd,qdhe->qche", cross_slope, cls_keys_last)
            )
            * score_scale
        )
        .astype(jnp.bfloat16)
        .reshape(lists, local_cands, local_width)
    )
    own_key_grad = (mixed("qcht,qche->qcthe", own_slope, last_heads) * score_scale).reshape(
        lists, local_cands, seq_len, local_width
    )
    own_val_grad = mixed("qcht,qche->qcthe", own_last_weight, grad_mixed_last).reshape(
        lists, local_cands, seq_len, local_width
    )
    cls_key_terms = (mixed("qchd,qche->qdhe", cross_slope, last_heads) * score_scale).reshape(
        lists, cand_count, local_width
    )
    cls_val_terms = mixed("qchd,qche->qdhe", cross_last_weight, grad_mixed_last).reshape(
        lists, cand_count, local_width
    )
    back_terms = scatter_cand(jnp.concatenate([cls_key_terms, cls_val_terms], -1), 1)
    back_keys = back_terms[..., :local_width]
    back_vals = back_terms[..., local_width:]
    first_cols = first_mask[None, None, :, None]
    key_grad = jnp.where(first_cols, own_key_grad + back_keys[:, :, None], own_key_grad).astype(
        jnp.bfloat16
    )
    val_grad = jnp.where(first_cols, own_val_grad + back_vals[:, :, None], own_val_grad).astype(
        jnp.bfloat16
    )
    joined = lax.all_gather(
        jnp.concatenate([key_grad, val_grad, grad_query_last[:, :, None]], 2),
        "mp",
        axis=3,
        tiled=True,
    )
    key_joined = joined[:, :, :seq_len]
    val_joined = joined[:, :, seq_len : 2 * seq_len]
    query_joined = joined[:, :, 2 * seq_len]
    summed_term = mixed("qcsf,df->qcsd", key_joined, last_full[1]) + mixed(
        "qcsf,df->qcsd", val_joined, last_full[2]
    )
    query_term = mixed("qcf,df->qcd", query_joined, last_full[0])
    summed_term = jnp.where(first_cols, summed_term + query_term[:, :, None], summed_term)
    grad_hidden = jnp.where(first_cols, summed_term + grad_last[:, :, None], summed_term)
    grad_first = norm_backward(grad_hidden, unit_first, inverse_first, gain_first).astype(
        jnp.bfloat16
    )
    grad_mixed_first = (
        mixed("qcsd,fd->qcsf", grad_first, w_out_first).astype(jnp.bfloat16).reshape(head_shape)
    )
    own_dot_first = mixed("qcshe,qcthe->qchst", grad_mixed_first, first_vals)
    cross_dot_first = mixed("qche,qdhe->qchd", grad_mixed_first[:, :, 0], cls_vals)
    own_part = jnp.sum(own_prob * own_dot_first, -1)
    row_part = own_part[..., 0] + jnp.sum(cross_prob * cross_dot_first, -1)
    centre_first = jnp.where(first_mask, row_part[..., None], own_part)
    own_slope_first = (own_prob * (own_dot_first - centre_first[..., None])).astype(jnp.bfloat16)
    cross_slope_first = (cross_prob * (cross_dot_first - row_part[..., None])).astype(jnp.bfloat16)
    query_grad = mixed("qchst,qcthe->qcshe", own_slope_first, first_keys)
    query_cls = mixed("qchd,qdhe->qche", cross_slope_first, cls_keys)
    query_grad = jnp.where(
        first_mask[None, None, :, None, None], query_grad + query_cls[:, :, None], query_grad
    )
    query_grad = (
        (query_grad * score_scale)
        .astype(jnp.bfloat16)
        .reshape(lists, local_cands, seq_len, local_width)
    )
    key_first = (mixed("qchst,qcshe->qcthe", own_slope_first, first_query) * score_scale).reshape(
        lists, local_cands, seq_len, local_width
    )
    val_first = mixed("qchst,qcshe->qcthe", own_weight, grad_mixed_first).reshape(
        lists, local_cands, seq_len, local_width
    )
    cls_key_first = (
        mixed("qchd,qche->qdhe", cross_slope_first, first_query[:, :, 0]) * score_scale
    ).reshape(lists, cand_count, local_width)
    cls_val_first = mixed("qchd,qche->qdhe", cross_weight, grad_mixed_first[:, :, 0]).reshape(
        lists, cand_count, local_width
    )
    key_first = key_first.astype(jnp.bfloat16)
    val_first = val_first.astype(jnp.bfloat16)
    stacked = jnp.stack([query_grad, key_first, val_first], 3).reshape(row_count, 3, local_width)
    cross_rows = lists * cand_count
    cross_stacked = jnp.stack(
        [jnp.zeros_like(cls_key_first), cls_key_first, cls_val_first], 2
    ).astype(jnp.bfloat16)
    all_rows = jnp.concatenate(
        [stacked, cross_stacked.reshape(cross_rows, 3, local_width)], 0
    )
    all_tokens = jnp.concatenate(
        [tokens.reshape(row_count, model_width), cls_tokens.reshape(cross_rows, model_width)], 0
    )
    if not paired_lists:
        partial_grad = lax.psum_scatter(
            mixed("rd,rkf->dkf", all_tokens, all_rows).astype(jnp.bfloat16),
            "cand",
            scatter_dimension=0,
            tiled=True,
        )
        return sum_query(partial_grad).astype(jnp.float32)
    half = 3 * local_width // 2
    side = lax.axis_index("query")
    flat_rows = all_rows.reshape(all_rows.shape[0], 3 * local_width)
    cls_flat = cls_tokens.reshape(cross_rows, model_width)
    sent = lax.ppermute(
        jnp.concatenate([flat_rows.reshape(-1), cls_flat.reshape(-1)]), "query", swap
    )
    other_rows = sent[: flat_rows.size].reshape(flat_rows.shape)
    other_cls = sent[flat_rows.size :].reshape(cls_flat.shape)
    own_half = lax.dynamic_slice_in_dim(flat_rows, side * half, half, 1)
    other_half = lax.dynamic_slice_in_dim(other_rows, side * half, half, 1)
    paired = (
        mixed("rd,rf->df", all_tokens, own_half)
        + mixed("rd,rf->df", other_tokens, other_half[:row_count])
        + mixed("rd,rf->df", other_cls, other_half[row_count:])
    )
    reduced = lax.psum_scatter(
        paired.astype(jnp.bfloat16), "cand", scatter_dimension=0, tiled=True
    )
    partner = lax.ppermute(reduced, "query", swap)
    joined = jnp.where(
        side == 0,
        jnp.concatenate([reduced, partner], 1),
        jnp.concatenate([partner, reduced], 1),
    )
    return joined.reshape(joined.shape[0], 3, local_width).astype(jnp.float32)


def solution(mesh):
    return jax.shard_map(
        local,
        mesh=mesh,
        in_specs=(
            P(("groups", "query"), "cand", None, None),
            P(("groups", "query"), "cand"),
            P(("groups", "query"), "cand"),
            P(None, None, "mp"),
            P("mp", None),
            P(),
            P(None, None, "mp"),
            P("mp", None),
            P(),
            P(),
        ),
        out_specs=P(("groups", "cand"), None, "mp"),
        check_vma=False,
    )
```

```python
import jax
import jax.numpy as jnp
from jax import lax
from jax.sharding import PartitionSpec as P

HEAD_DIM = 64


EPSILON = 1e-05
LOSS_SCALE = 1024.0
NEGATIVE = -1e30


def mixed(pattern, former, latter):
    return jnp.einsum(pattern, former, latter, preferred_element_type=jnp.float32)


def norm_forward(matrix, scales):
    center = matrix - jnp.mean(matrix, -1, keepdims=True)
    inverse = lax.rsqrt(jnp.mean(center * center, -1, keepdims=True) + EPSILON)
    normed = center * inverse
    return (normed * scales, normed, inverse)


def norm_backward(incoming, normed, inverse, scales):
    scaled = incoming * scales
    return inverse * (
        scaled
        - jnp.mean(scaled, -1, keepdims=True)
        - normed * jnp.mean(scaled * normed, -1, keepdims=True)
    )


def split_softmax(own_scores, cross_scores, first_mask):
    own_peak = jnp.max(own_scores, -1)
    row_peak = jnp.maximum(own_peak[..., 0], jnp.max(cross_scores, -1))
    peak = jnp.where(first_mask, row_peak[..., None], own_peak)
    own_exp = jnp.exp(own_scores - peak[..., None])
    cross_exp = jnp.exp(cross_scores - row_peak[..., None])
    own_totals = jnp.sum(own_exp, -1)
    row_totals = own_totals[..., 0] + jnp.sum(cross_exp, -1)
    totals = jnp.where(first_mask, row_totals[..., None], own_totals)
    return (own_exp / totals[..., None], cross_exp / row_totals[..., None])


def row_softmax(own_scores, cross_scores):
    peak = jnp.maximum(jnp.max(own_scores, -1), jnp.max(cross_scores, -1))[..., None]
    own_exp = jnp.exp(own_scores - peak)
    cross_exp = jnp.exp(cross_scores - peak)
    totals = (jnp.sum(own_exp, -1) + jnp.sum(cross_exp, -1))[..., None]
    return (own_exp / totals, cross_exp / totals)


def gather_cand(block, axis):
    count = lax.axis_size("cand")
    if count > 8:
        return lax.all_gather(block, "cand", axis=axis, tiled=True)
    me = lax.axis_index("cand")
    parts = [block] + [
        lax.ppermute(block, "cand", [(j, (j + k) % count) for j in range(count)])
        for k in range(1, count)
    ]
    ordered = jnp.take(jnp.stack(parts, 0), (me - jnp.arange(count)) % count, axis=0)
    ordered = jnp.moveaxis(ordered, 0, axis)
    shape = block.shape[:axis] + (count * block.shape[axis],) + block.shape[axis + 1 :]
    return ordered.reshape(shape)


def sum_cand(block):
    count = lax.axis_size("cand")
    if count > 8:
        return lax.psum(block, "cand")
    total = block
    for k in range(1, count):
        total = total + lax.ppermute(block, "cand", [(j, (j + k) % count) for j in range(count)])
    return total


def scatter_cand(block, axis):
    count = lax.axis_size("cand")
    if count > 8:
        return lax.psum_scatter(block, "cand", scatter_dimension=axis, tiled=True)
    me = lax.axis_index("cand")
    width = block.shape[axis] // count
    total = lax.dynamic_slice_in_dim(block, me * width, width, axis)
    for k in range(1, count):
        piece = lax.dynamic_slice_in_dim(block, ((me + k) % count) * width, width, axis)
        total = total + lax.ppermute(piece, "cand", [(j, (j + k) % count) for j in range(count)])
    return total


def sum_query(block):
    if lax.axis_size("query") != 2:
        return lax.psum(block, "query")
    other = lax.ppermute(block, "query", [(0, 1), (1, 0)])
    return block.astype(jnp.float32) + other.astype(jnp.float32)


def local(
    tokens,
    lengths,
    teacher,
    w_first,
    w_out_first,
    gain_first,
    w_last,
    w_out_last,
    gain_last,
    w_score,
):
    lists, local_cands, seq_len, model_width = tokens.shape
    local_width = w_first.shape[2]
    local_heads = local_width // HEAD_DIM
    cand_count = local_cands * lax.axis_size("cand")
    query_count = lists * lax.axis_size("query")
    score_scale = HEAD_DIM ** (-0.5)
    positions = jnp.arange(seq_len)
    first_mask = positions == 0
    own_valid = positions[None, None, :] < lengths[:, :, None]
    local_ids = lax.axis_index("cand") * local_cands + jnp.arange(local_cands)
    cross_valid = local_ids[:, None] != jnp.arange(cand_count)[None, :]
    head_shape = (lists, local_cands, seq_len, local_heads, HEAD_DIM)
    cls_shape = (lists, cand_count, local_heads, HEAD_DIM)
    out_first_full = lax.all_gather(w_out_first, "mp", axis=0, tiled=True)
    last_full = lax.all_gather(w_last, "mp", axis=2, tiled=True)
    out_last_full = lax.all_gather(w_out_last, "mp", axis=0, tiled=True)
    cls_and_teacher = gather_cand(
        jnp.concatenate([tokens[:, :, 0].astype(jnp.float32), teacher[..., None]], -1), 1
    )
    cls_tokens = cls_and_teacher[..., :model_width].astype(jnp.bfloat16)
    teacher_all = cls_and_teacher[..., model_width]
    row_count = lists * local_cands * seq_len
    swap = [(0, 1), (1, 0)]
    paired_lists = lax.axis_size("query") == 2
    if paired_lists:
        other_tokens = lax.ppermute(tokens.reshape(row_count, model_width), "query", swap)
    projected = mixed("qcsd,kdf->kqcsf", tokens, w_first).astype(jnp.bfloat16)
    cls_projected = mixed("qcd,kdf->kqcf", cls_tokens, w_first[1:]).astype(jnp.bfloat16)
    gathered_keys = cls_projected[0]
    gathered_vals = cls_projected[1]
    first_query = projected[0].reshape(head_shape)
    first_keys = projected[1].reshape(head_shape)
    first_vals = projected[2].reshape(head_shape)
    cls_keys = gathered_keys.reshape(cls_shape)
    cls_vals = gathered_vals.reshape(cls_shape)
    own_scores = mixed("qcshe,qcthe->qchst", first_query, first_keys) * score_scale
    own_scores = jnp.where(own_valid[:, :, None, None, :], own_scores, NEGATIVE)
    cross_scores = mixed("qche,qdhe->qchd", first_query[:, :, 0], cls_keys) * score_scale
    cross_scores = jnp.where(cross_valid[None, :, None, :], cross_scores, NEGATIVE)
    own_prob, cross_prob = split_softmax(own_scores, cross_scores, first_mask)
    own_weight = own_prob.astype(jnp.bfloat16)
    cross_weight = cross_prob.astype(jnp.bfloat16)
    attended = mixed("qchst,qcthe->qcshe", own_weight, first_vals)
    attended_cls = mixed("qchd,qdhe->qche", cross_weight, cls_vals)
    attended = jnp.where(
        first_mask[None, None, :, None, None], attended + attended_cls[:, :, None], attended
    )
    first_mixed = attended.reshape(lists, local_cands, seq_len, local_width).astype(jnp.bfloat16)
    first_joined = lax.all_gather(first_mixed, "mp", axis=3, tiled=True)
    residual_first = tokens.astype(jnp.float32) + mixed(
        "qcsf,fd->qcsd", first_joined, out_first_full
    )
    normed_first, unit_first, inverse_first = norm_forward(residual_first, gain_first)
    hidden = normed_first.astype(jnp.bfloat16)
    last_query = mixed("qcd,df->qcf", hidden[:, :, 0], w_last[0]).astype(jnp.bfloat16)
    last_kv = mixed("qcsd,kdf->kqcsf", hidden, w_last[1:]).astype(jnp.bfloat16)
    gathered_kv_last = gather_cand(
        jnp.concatenate([last_kv[0][:, :, 0], last_kv[1][:, :, 0]], -1), 1
    )
    gathered_keys_last = gathered_kv_last[..., :local_width]
    gathered_vals_last = gathered_kv_last[..., local_width:]
    last_heads = last_query.reshape(lists, local_cands, local_heads, HEAD_DIM)
    last_keys = last_kv[0].reshape(head_shape)
    last_vals = last_kv[1].reshape(head_shape)
    cls_keys_last = gathered_keys_last.reshape(cls_shape)
    cls_vals_last = gathered_vals_last.reshape(cls_shape)
    own_last = mixed("qche,qcthe->qcht", last_heads, last_keys) * score_scale
    own_last = jnp.where(own_valid[:, :, None, :], own_last, NEGATIVE)
    cross_last = mixed("qche,qdhe->qchd", last_heads, cls_keys_last) * score_scale
    cross_last = jnp.where(cross_valid[None, :, None, :], cross_last, NEGATIVE)
    own_last_prob, cross_last_prob = row_softmax(own_last, cross_last)
    own_last_weight = own_last_prob.astype(jnp.bfloat16)
    cross_last_weight = cross_last_prob.astype(jnp.bfloat16)
    attended_last = mixed("qcht,qcthe->qche", own_last_weight, last_vals) + mixed(
        "qchd,qdhe->qche", cross_last_weight, cls_vals_last
    )
    last_mixed = attended_last.reshape(lists, local_cands, local_width).astype(jnp.bfloat16)
    last_joined = lax.all_gather(last_mixed, "mp", axis=2, tiled=True)
    residual_last = hidden[:, :, 0].astype(jnp.float32) + mixed(
        "qcf,fd->qcd", last_joined, out_last_full
    )
    normed_last, unit_last, inverse_last = norm_forward(residual_last, gain_last)
    scores = jnp.einsum("qcd,d->qc", normed_last, w_score, precision=lax.Precision.HIGHEST)
    score_exp = jnp.exp(scores)
    teacher_peak = jnp.max(teacher_all, 1)
    teacher_exp = jnp.exp(teacher - teacher_peak[:, None])
    teacher_totals = jnp.sum(jnp.exp(teacher_all - teacher_peak[:, None]), 1)
    score_totals = sum_cand(jnp.sum(score_exp, 1))
    student_prob = score_exp / score_totals[:, None]
    teacher_prob = teacher_exp / teacher_totals[:, None]
    score_grad = LOSS_SCALE * (student_prob - teacher_prob) / query_count
    grad_last = norm_backward(score_grad[..., None] * w_score, unit_last, inverse_last, gain_last)
    grad_last_low = grad_last.astype(jnp.bfloat16)
    grad_mixed_last = (
        mixed("qcd,fd->qcf", grad_last_low, w_out_last)
        .astype(jnp.bfloat16)
        .reshape(lists, local_cands, local_heads, HEAD_DIM)
    )
    own_dot = mixed("qche,qcthe->qcht", grad_mixed_last, last_vals)
    cross_dot = mixed("qche,qdhe->qchd", grad_mixed_last, cls_vals_last)
    centre = jnp.sum(own_last_prob * own_dot, -1, keepdims=True) + jnp.sum(
        cross_last_prob * cross_dot, -1, keepdims=True
    )
    own_slope = (own_last_prob * (own_dot - centre)).astype(jnp.bfloat16)
    cross_slope = (cross_last_prob * (cross_dot - centre)).astype(jnp.bfloat16)
    grad_query_last = (
        (
            (
                mixed("qcht,qcthe->qche", own_slope, last_keys)
                + mixed("qchd,qdhe->qche", cross_slope, cls_keys_last)
            )
            * score_scale
        )
        .astype(jnp.bfloat16)
        .reshape(lists, local_cands, local_width)
    )
    own_key_grad = (mixed("qcht,qche->qcthe", own_slope, last_heads) * score_scale).reshape(
        lists, local_cands, seq_len, local_width
    )
    own_val_grad = mixed("qcht,qche->qcthe", own_last_weight, grad_mixed_last).reshape(
        lists, local_cands, seq_len, local_width
    )
    cls_key_terms = (mixed("qchd,qche->qdhe", cross_slope, last_heads) * score_scale).reshape(
        lists, cand_count, local_width
    )
    cls_val_terms = mixed("qchd,qche->qdhe", cross_last_weight, grad_mixed_last).reshape(
        lists, cand_count, local_width
    )
    back_terms = scatter_cand(jnp.concatenate([cls_key_terms, cls_val_terms], -1), 1)
    back_keys = back_terms[..., :local_width]
    back_vals = back_terms[..., local_width:]
    first_cols = first_mask[None, None, :, None]
    key_grad = jnp.where(first_cols, own_key_grad + back_keys[:, :, None], own_key_grad).astype(
        jnp.bfloat16
    )
    val_grad = jnp.where(first_cols, own_val_grad + back_vals[:, :, None], own_val_grad).astype(
        jnp.bfloat16
    )
    joined = lax.all_gather(
        jnp.concatenate([key_grad, val_grad, grad_query_last[:, :, None]], 2),
        "mp",
        axis=3,
        tiled=True,
    )
    key_joined = joined[:, :, :seq_len]
    val_joined = joined[:, :, seq_len : 2 * seq_len]
    query_joined = joined[:, :, 2 * seq_len]
    summed_term = mixed("qcsf,df->qcsd", key_joined, last_full[1]) + mixed(
        "qcsf,df->qcsd", val_joined, last_full[2]
    )
    query_term = mixed("qcf,df->qcd", query_joined, last_full[0])
    summed_term = jnp.where(first_cols, summed_term + query_term[:, :, None], summed_term)
    grad_hidden = jnp.where(first_cols, summed_term + grad_last[:, :, None], summed_term)
    grad_first = norm_backward(grad_hidden, unit_first, inverse_first, gain_first).astype(
        jnp.bfloat16
    )
    grad_mixed_first = (
        mixed("qcsd,fd->qcsf", grad_first, w_out_first).astype(jnp.bfloat16).reshape(head_shape)
    )
    own_dot_first = mixed("qcshe,qcthe->qchst", grad_mixed_first, first_vals)
    cross_dot_first = mixed("qche,qdhe->qchd", grad_mixed_first[:, :, 0], cls_vals)
    own_part = jnp.sum(own_prob * own_dot_first, -1)
    row_part = own_part[..., 0] + jnp.sum(cross_prob * cross_dot_first, -1)
    centre_first = jnp.where(first_mask, row_part[..., None], own_part)
    own_slope_first = (own_prob * (own_dot_first - centre_first[..., None])).astype(jnp.bfloat16)
    cross_slope_first = (cross_prob * (cross_dot_first - row_part[..., None])).astype(jnp.bfloat16)
    query_grad = mixed("qchst,qcthe->qcshe", own_slope_first, first_keys)
    query_cls = mixed("qchd,qdhe->qche", cross_slope_first, cls_keys)
    query_grad = jnp.where(
        first_mask[None, None, :, None, None], query_grad + query_cls[:, :, None], query_grad
    )
    query_grad = (
        (query_grad * score_scale)
        .astype(jnp.bfloat16)
        .reshape(lists, local_cands, seq_len, local_width)
    )
    key_first = (mixed("qchst,qcshe->qcthe", own_slope_first, first_query) * score_scale).reshape(
        lists, local_cands, seq_len, local_width
    )
    val_first = mixed("qchst,qcshe->qcthe", own_weight, grad_mixed_first).reshape(
        lists, local_cands, seq_len, local_width
    )
    cls_key_first = (
        mixed("qchd,qche->qdhe", cross_slope_first, first_query[:, :, 0]) * score_scale
    ).reshape(lists, cand_count, local_width)
    cls_val_first = mixed("qchd,qche->qdhe", cross_weight, grad_mixed_first[:, :, 0]).reshape(
        lists, cand_count, local_width
    )
    key_first = key_first.astype(jnp.bfloat16)
    val_first = val_first.astype(jnp.bfloat16)
    stacked = jnp.stack([query_grad, key_first, val_first], 3).reshape(row_count, 3, local_width)
    cross_rows = lists * cand_count
    cross_stacked = jnp.stack(
        [jnp.zeros_like(cls_key_first), cls_key_first, cls_val_first], 2
    ).astype(jnp.bfloat16)
    all_rows = jnp.concatenate(
        [stacked, cross_stacked.reshape(cross_rows, 3, local_width)], 0
    )
    all_tokens = jnp.concatenate(
        [tokens.reshape(row_count, model_width), cls_tokens.reshape(cross_rows, model_width)], 0
    )
    if not paired_lists:
        partial_grad = lax.psum_scatter(
            mixed("rd,rkf->dkf", all_tokens, all_rows).astype(jnp.bfloat16),
            "cand",
            scatter_dimension=0,
            tiled=True,
        )
        return sum_query(partial_grad).astype(jnp.float32)
    half = 3 * local_width // 2
    side = lax.axis_index("query")
    flat_rows = all_rows.reshape(all_rows.shape[0], 3 * local_width)
    cls_flat = cls_tokens.reshape(cross_rows, model_width)
    own_half = lax.dynamic_slice_in_dim(flat_rows, side * half, half, 1)
    given_half = lax.dynamic_slice_in_dim(flat_rows, (1 - side) * half, half, 1)
    sent = lax.ppermute(
        jnp.concatenate([given_half.reshape(-1), cls_flat.reshape(-1)]), "query", swap
    )
    other_half = sent[: given_half.size].reshape(given_half.shape)
    other_cls = sent[given_half.size :].reshape(cls_flat.shape)
    paired = (
        mixed("rd,rf->df", all_tokens, own_half)
        + mixed("rd,rf->df", other_tokens, other_half[:row_count])
        + mixed("rd,rf->df", other_cls, other_half[row_count:])
    )
    reduced = lax.psum_scatter(
        paired.astype(jnp.bfloat16), "cand", scatter_dimension=0, tiled=True
    )
    partner = lax.ppermute(reduced, "query", swap)
    joined = jnp.where(
        side == 0,
        jnp.concatenate([reduced, partner], 1),
        jnp.concatenate([partner, reduced], 1),
    )
    return joined.reshape(joined.shape[0], 3, local_width).astype(jnp.float32)


def solution(mesh):
    return jax.shard_map(
        local,
        mesh=mesh,
        in_specs=(
            P(("groups", "query"), "cand", None, None),
            P(("groups", "query"), "cand"),
            P(("groups", "query"), "cand"),
            P(None, None, "mp"),
            P("mp", None),
            P(),
            P(None, None, "mp"),
            P("mp", None),
            P(),
            P(),
        ),
        out_specs=P(("groups", "cand"), None, "mp"),
        check_vma=False,
    )
```

```python
import jax
import jax.numpy as jnp
from jax import lax
from jax.sharding import PartitionSpec as P

HEAD_DIM = 64


EPSILON = 1e-05
LOSS_SCALE = 1024.0
NEGATIVE = -1e30


def mixed(pattern, former, latter):
    return jnp.einsum(pattern, former, latter, preferred_element_type=jnp.float32)


def norm_forward(matrix, scales):
    center = matrix - jnp.mean(matrix, -1, keepdims=True)
    inverse = lax.rsqrt(jnp.mean(center * center, -1, keepdims=True) + EPSILON)
    normed = center * inverse
    return (normed * scales, normed, inverse)


def norm_backward(incoming, normed, inverse, scales):
    scaled = incoming * scales
    return inverse * (
        scaled
        - jnp.mean(scaled, -1, keepdims=True)
        - normed * jnp.mean(scaled * normed, -1, keepdims=True)
    )


def split_softmax(own_scores, cross_scores, first_mask):
    own_peak = jnp.max(own_scores, -1)
    row_peak = jnp.maximum(own_peak[..., 0], jnp.max(cross_scores, -1))
    peak = jnp.where(first_mask, row_peak[..., None], own_peak)
    own_exp = jnp.exp(own_scores - peak[..., None])
    cross_exp = jnp.exp(cross_scores - row_peak[..., None])
    own_totals = jnp.sum(own_exp, -1)
    row_totals = own_totals[..., 0] + jnp.sum(cross_exp, -1)
    totals = jnp.where(first_mask, row_totals[..., None], own_totals)
    return (own_exp / totals[..., None], cross_exp / row_totals[..., None])


def row_softmax(own_scores, cross_scores):
    peak = jnp.maximum(jnp.max(own_scores, -1), jnp.max(cross_scores, -1))[..., None]
    own_exp = jnp.exp(own_scores - peak)
    cross_exp = jnp.exp(cross_scores - peak)
    totals = (jnp.sum(own_exp, -1) + jnp.sum(cross_exp, -1))[..., None]
    return (own_exp / totals, cross_exp / totals)


def gather_cand(block, axis):
    count = lax.axis_size("cand")
    if count > 8:
        return lax.all_gather(block, "cand", axis=axis, tiled=True)
    me = lax.axis_index("cand")
    parts = [block] + [
        lax.ppermute(block, "cand", [(j, (j + k) % count) for j in range(count)])
        for k in range(1, count)
    ]
    ordered = jnp.take(jnp.stack(parts, 0), (me - jnp.arange(count)) % count, axis=0)
    ordered = jnp.moveaxis(ordered, 0, axis)
    shape = block.shape[:axis] + (count * block.shape[axis],) + block.shape[axis + 1 :]
    return ordered.reshape(shape)


def sum_cand(block):
    count = lax.axis_size("cand")
    if count > 8:
        return lax.psum(block, "cand")
    total = block
    for k in range(1, count):
        total = total + lax.ppermute(block, "cand", [(j, (j + k) % count) for j in range(count)])
    return total


def scatter_cand(block, axis, total_type=None):
    count = lax.axis_size("cand")
    if count > 8:
        return lax.psum_scatter(block, "cand", scatter_dimension=axis, tiled=True)
    total_type = total_type or block.dtype
    me = lax.axis_index("cand")
    width = block.shape[axis] // count
    total = lax.dynamic_slice_in_dim(block, me * width, width, axis).astype(total_type)
    for k in range(1, count):
        piece = lax.dynamic_slice_in_dim(block, ((me + k) % count) * width, width, axis)
        moved = lax.ppermute(piece, "cand", [(j, (j + k) % count) for j in range(count)])
        total = total + moved.astype(total_type)
    return total


def sum_query(block):
    if lax.axis_size("query") != 2:
        return lax.psum(block, "query")
    other = lax.ppermute(block, "query", [(0, 1), (1, 0)])
    return block.astype(jnp.float32) + other.astype(jnp.float32)


def local(
    tokens,
    lengths,
    teacher,
    w_first,
    w_out_first,
    gain_first,
    w_last,
    w_out_last,
    gain_last,
    w_score,
):
    lists, local_cands, seq_len, model_width = tokens.shape
    local_width = w_first.shape[2]
    local_heads = local_width // HEAD_DIM
    cand_count = local_cands * lax.axis_size("cand")
    query_count = lists * lax.axis_size("query")
    score_scale = HEAD_DIM ** (-0.5)
    positions = jnp.arange(seq_len)
    first_mask = positions == 0
    own_valid = positions[None, None, :] < lengths[:, :, None]
    local_ids = lax.axis_index("cand") * local_cands + jnp.arange(local_cands)
    cross_valid = local_ids[:, None] != jnp.arange(cand_count)[None, :]
    head_shape = (lists, local_cands, seq_len, local_heads, HEAD_DIM)
    cls_shape = (lists, cand_count, local_heads, HEAD_DIM)
    out_first_full = lax.all_gather(w_out_first, "mp", axis=0, tiled=True)
    last_full = lax.all_gather(w_last, "mp", axis=2, tiled=True)
    out_last_full = lax.all_gather(w_out_last, "mp", axis=0, tiled=True)
    cls_and_teacher = gather_cand(
        jnp.concatenate([tokens[:, :, 0].astype(jnp.float32), teacher[..., None]], -1), 1
    )
    cls_tokens = cls_and_teacher[..., :model_width].astype(jnp.bfloat16)
    teacher_all = cls_and_teacher[..., model_width]
    row_count = lists * local_cands * seq_len
    swap = [(0, 1), (1, 0)]
    paired_lists = lax.axis_size("query") == 2
    if paired_lists:
        other_tokens = lax.ppermute(tokens.reshape(row_count, model_width), "query", swap)
    projected = mixed("qcsd,kdf->kqcsf", tokens, w_first).astype(jnp.bfloat16)
    cls_projected = mixed("qcd,kdf->kqcf", cls_tokens, w_first[1:]).astype(jnp.bfloat16)
    gathered_keys = cls_projected[0]
    gathered_vals = cls_projected[1]
    first_query = projected[0].reshape(head_shape)
    first_keys = projected[1].reshape(head_shape)
    first_vals = projected[2].reshape(head_shape)
    cls_keys = gathered_keys.reshape(cls_shape)
    cls_vals = gathered_vals.reshape(cls_shape)
    own_scores = mixed("qcshe,qcthe->qchst", first_query, first_keys) * score_scale
    own_scores = jnp.where(own_valid[:, :, None, None, :], own_scores, NEGATIVE)
    cross_scores = mixed("qche,qdhe->qchd", first_query[:, :, 0], cls_keys) * score_scale
    cross_scores = jnp.where(cross_valid[None, :, None, :], cross_scores, NEGATIVE)
    own_prob, cross_prob = split_softmax(own_scores, cross_scores, first_mask)
    own_weight = own_prob.astype(jnp.bfloat16)
    cross_weight = cross_prob.astype(jnp.bfloat16)
    attended = mixed("qchst,qcthe->qcshe", own_weight, first_vals)
    attended_cls = mixed("qchd,qdhe->qche", cross_weight, cls_vals)
    attended = jnp.where(
        first_mask[None, None, :, None, None], attended + attended_cls[:, :, None], attended
    )
    first_mixed = attended.reshape(lists, local_cands, seq_len, local_width).astype(jnp.bfloat16)
    first_joined = lax.all_gather(first_mixed, "mp", axis=3, tiled=True)
    residual_first = tokens.astype(jnp.float32) + mixed(
        "qcsf,fd->qcsd", first_joined, out_first_full
    )
    normed_first, unit_first, inverse_first = norm_forward(residual_first, gain_first)
    hidden = normed_first.astype(jnp.bfloat16)
    last_query = mixed("qcd,df->qcf", hidden[:, :, 0], w_last[0]).astype(jnp.bfloat16)
    last_kv = mixed("qcsd,kdf->kqcsf", hidden, w_last[1:]).astype(jnp.bfloat16)
    gathered_kv_last = gather_cand(
        jnp.concatenate([last_kv[0][:, :, 0], last_kv[1][:, :, 0]], -1), 1
    )
    gathered_keys_last = gathered_kv_last[..., :local_width]
    gathered_vals_last = gathered_kv_last[..., local_width:]
    last_heads = last_query.reshape(lists, local_cands, local_heads, HEAD_DIM)
    last_keys = last_kv[0].reshape(head_shape)
    last_vals = last_kv[1].reshape(head_shape)
    cls_keys_last = gathered_keys_last.reshape(cls_shape)
    cls_vals_last = gathered_vals_last.reshape(cls_shape)
    own_last = mixed("qche,qcthe->qcht", last_heads, last_keys) * score_scale
    own_last = jnp.where(own_valid[:, :, None, :], own_last, NEGATIVE)
    cross_last = mixed("qche,qdhe->qchd", last_heads, cls_keys_last) * score_scale
    cross_last = jnp.where(cross_valid[None, :, None, :], cross_last, NEGATIVE)
    own_last_prob, cross_last_prob = row_softmax(own_last, cross_last)
    own_last_weight = own_last_prob.astype(jnp.bfloat16)
    cross_last_weight = cross_last_prob.astype(jnp.bfloat16)
    attended_last = mixed("qcht,qcthe->qche", own_last_weight, last_vals) + mixed(
        "qchd,qdhe->qche", cross_last_weight, cls_vals_last
    )
    last_mixed = attended_last.reshape(lists, local_cands, local_width).astype(jnp.bfloat16)
    last_joined = lax.all_gather(last_mixed, "mp", axis=2, tiled=True)
    residual_last = hidden[:, :, 0].astype(jnp.float32) + mixed(
        "qcf,fd->qcd", last_joined, out_last_full
    )
    normed_last, unit_last, inverse_last = norm_forward(residual_last, gain_last)
    scores = jnp.einsum("qcd,d->qc", normed_last, w_score, precision=lax.Precision.HIGHEST)
    score_exp = jnp.exp(scores)
    teacher_peak = jnp.max(teacher_all, 1)
    teacher_exp = jnp.exp(teacher - teacher_peak[:, None])
    teacher_totals = jnp.sum(jnp.exp(teacher_all - teacher_peak[:, None]), 1)
    score_totals = sum_cand(jnp.sum(score_exp, 1))
    student_prob = score_exp / score_totals[:, None]
    teacher_prob = teacher_exp / teacher_totals[:, None]
    score_grad = LOSS_SCALE * (student_prob - teacher_prob) / query_count
    grad_last = norm_backward(score_grad[..., None] * w_score, unit_last, inverse_last, gain_last)
    grad_last_low = grad_last.astype(jnp.bfloat16)
    grad_mixed_last = (
        mixed("qcd,fd->qcf", grad_last_low, w_out_last)
        .astype(jnp.bfloat16)
        .reshape(lists, local_cands, local_heads, HEAD_DIM)
    )
    own_dot = mixed("qche,qcthe->qcht", grad_mixed_last, last_vals)
    cross_dot = mixed("qche,qdhe->qchd", grad_mixed_last, cls_vals_last)
    centre = jnp.sum(own_last_prob * own_dot, -1, keepdims=True) + jnp.sum(
        cross_last_prob * cross_dot, -1, keepdims=True
    )
    own_slope = (own_last_prob * (own_dot - centre)).astype(jnp.bfloat16)
    cross_slope = (cross_last_prob * (cross_dot - centre)).astype(jnp.bfloat16)
    grad_query_last = (
        (
            (
                mixed("qcht,qcthe->qche", own_slope, last_keys)
                + mixed("qchd,qdhe->qche", cross_slope, cls_keys_last)
            )
            * score_scale
        )
        .astype(jnp.bfloat16)
        .reshape(lists, local_cands, local_width)
    )
    own_key_grad = (mixed("qcht,qche->qcthe", own_slope, last_heads) * score_scale).reshape(
        lists, local_cands, seq_len, local_width
    )
    own_val_grad = mixed("qcht,qche->qcthe", own_last_weight, grad_mixed_last).reshape(
        lists, local_cands, seq_len, local_width
    )
    cls_key_terms = (mixed("qchd,qche->qdhe", cross_slope, last_heads) * score_scale).reshape(
        lists, cand_count, local_width
    )
    cls_val_terms = mixed("qchd,qche->qdhe", cross_last_weight, grad_mixed_last).reshape(
        lists, cand_count, local_width
    )
    back_terms = scatter_cand(jnp.concatenate([cls_key_terms, cls_val_terms], -1), 1)
    back_keys = back_terms[..., :local_width]
    back_vals = back_terms[..., local_width:]
    first_cols = first_mask[None, None, :, None]
    key_grad = jnp.where(first_cols, own_key_grad + back_keys[:, :, None], own_key_grad).astype(
        jnp.bfloat16
    )
    val_grad = jnp.where(first_cols, own_val_grad + back_vals[:, :, None], own_val_grad).astype(
        jnp.bfloat16
    )
    joined = lax.all_gather(
        jnp.concatenate([key_grad, val_grad, grad_query_last[:, :, None]], 2),
        "mp",
        axis=3,
        tiled=True,
    )
    key_joined = joined[:, :, :seq_len]
    val_joined = joined[:, :, seq_len : 2 * seq_len]
    query_joined = joined[:, :, 2 * seq_len]
    summed_term = mixed("qcsf,df->qcsd", key_joined, last_full[1]) + mixed(
        "qcsf,df->qcsd", val_joined, last_full[2]
    )
    query_term = mixed("qcf,df->qcd", query_joined, last_full[0])
    summed_term = jnp.where(first_cols, summed_term + query_term[:, :, None], summed_term)
    grad_hidden = jnp.where(first_cols, summed_term + grad_last[:, :, None], summed_term)
    grad_first = norm_backward(grad_hidden, unit_first, inverse_first, gain_first).astype(
        jnp.bfloat16
    )
    grad_mixed_first = (
        mixed("qcsd,fd->qcsf", grad_first, w_out_first).astype(jnp.bfloat16).reshape(head_shape)
    )
    own_dot_first = mixed("qcshe,qcthe->qchst", grad_mixed_first, first_vals)
    cross_dot_first = mixed("qche,qdhe->qchd", grad_mixed_first[:, :, 0], cls_vals)
    own_part = jnp.sum(own_prob * own_dot_first, -1)
    row_part = own_part[..., 0] + jnp.sum(cross_prob * cross_dot_first, -1)
    centre_first = jnp.where(first_mask, row_part[..., None], own_part)
    own_slope_first = (own_prob * (own_dot_first - centre_first[..., None])).astype(jnp.bfloat16)
    cross_slope_first = (cross_prob * (cross_dot_first - row_part[..., None])).astype(jnp.bfloat16)
    query_grad = mixed("qchst,qcthe->qcshe", own_slope_first, first_keys)
    query_cls = mixed("qchd,qdhe->qche", cross_slope_first, cls_keys)
    query_grad = jnp.where(
        first_mask[None, None, :, None, None], query_grad + query_cls[:, :, None], query_grad
    )
    query_grad = (
        (query_grad * score_scale)
        .astype(jnp.bfloat16)
        .reshape(lists, local_cands, seq_len, local_width)
    )
    key_first = (mixed("qchst,qcshe->qcthe", own_slope_first, first_query) * score_scale).reshape(
        lists, local_cands, seq_len, local_width
    )
    val_first = mixed("qchst,qcshe->qcthe", own_weight, grad_mixed_first).reshape(
        lists, local_cands, seq_len, local_width
    )
    cls_key_first = (
        mixed("qchd,qche->qdhe", cross_slope_first, first_query[:, :, 0]) * score_scale
    ).reshape(lists, cand_count, local_width)
    cls_val_first = mixed("qchd,qche->qdhe", cross_weight, grad_mixed_first[:, :, 0]).reshape(
        lists, cand_count, local_width
    )
    key_first = key_first.astype(jnp.bfloat16)
    val_first = val_first.astype(jnp.bfloat16)
    stacked = jnp.stack([query_grad, key_first, val_first], 3).reshape(row_count, 3, local_width)
    cross_rows = lists * cand_count
    cross_stacked = jnp.stack(
        [jnp.zeros_like(cls_key_first), cls_key_first, cls_val_first], 2
    ).astype(jnp.bfloat16)
    all_rows = jnp.concatenate(
        [stacked, cross_stacked.reshape(cross_rows, 3, local_width)], 0
    )
    all_tokens = jnp.concatenate(
        [tokens.reshape(row_count, model_width), cls_tokens.reshape(cross_rows, model_width)], 0
    )
    if not paired_lists:
        partial_grad = lax.psum_scatter(
            mixed("rd,rkf->dkf", all_tokens, all_rows).astype(jnp.bfloat16),
            "cand",
            scatter_dimension=0,
            tiled=True,
        )
        return sum_query(partial_grad).astype(jnp.float32)
    half = 3 * local_width // 2
    side = lax.axis_index("query")
    flat_rows = all_rows.reshape(all_rows.shape[0], 3 * local_width)
    cls_flat = cls_tokens.reshape(cross_rows, model_width)
    own_half = lax.dynamic_slice_in_dim(flat_rows, side * half, half, 1)
    given_half = lax.dynamic_slice_in_dim(flat_rows, (1 - side) * half, half, 1)
    sent = lax.ppermute(
        jnp.concatenate([given_half.reshape(-1), cls_flat.reshape(-1)]), "query", swap
    )
    other_half = sent[: given_half.size].reshape(given_half.shape)
    other_cls = sent[given_half.size :].reshape(cls_flat.shape)
    paired = (
        mixed("rd,rf->df", all_tokens, own_half)
        + mixed("rd,rf->df", other_tokens, other_half[:row_count])
        + mixed("rd,rf->df", other_cls, other_half[row_count:])
    )
    reduced = scatter_cand(paired.astype(jnp.bfloat16), 0, jnp.float32).astype(jnp.bfloat16)
    partner = lax.ppermute(reduced, "query", swap)
    joined = jnp.where(
        side == 0,
        jnp.concatenate([reduced, partner], 1),
        jnp.concatenate([partner, reduced], 1),
    )
    return joined.reshape(joined.shape[0], 3, local_width).astype(jnp.float32)


def solution(mesh):
    return jax.shard_map(
        local,
        mesh=mesh,
        in_specs=(
            P(("groups", "query"), "cand", None, None),
            P(("groups", "query"), "cand"),
            P(("groups", "query"), "cand"),
            P(None, None, "mp"),
            P("mp", None),
            P(),
            P(None, None, "mp"),
            P("mp", None),
            P(),
            P(),
        ),
        out_specs=P(("groups", "cand"), None, "mp"),
        check_vma=False,
    )
```

```python
import jax
import jax.numpy as jnp
from jax import lax
from jax.sharding import PartitionSpec as P

HEAD_DIM = 64


EPSILON = 1e-05
LOSS_SCALE = 1024.0
NEGATIVE = -1e30


def mixed(pattern, former, latter):
    return jnp.einsum(pattern, former, latter, preferred_element_type=jnp.float32)


def norm_forward(matrix, scales):
    center = matrix - jnp.mean(matrix, -1, keepdims=True)
    inverse = lax.rsqrt(jnp.mean(center * center, -1, keepdims=True) + EPSILON)
    normed = center * inverse
    return (normed * scales, normed, inverse)


def norm_backward(incoming, normed, inverse, scales):
    scaled = incoming * scales
    return inverse * (
        scaled
        - jnp.mean(scaled, -1, keepdims=True)
        - normed * jnp.mean(scaled * normed, -1, keepdims=True)
    )


def split_softmax(own_scores, cross_scores, first_mask):
    own_peak = jnp.max(own_scores, -1)
    row_peak = jnp.maximum(own_peak[..., 0], jnp.max(cross_scores, -1))
    peak = jnp.where(first_mask, row_peak[..., None], own_peak)
    own_exp = jnp.exp(own_scores - peak[..., None])
    cross_exp = jnp.exp(cross_scores - row_peak[..., None])
    own_totals = jnp.sum(own_exp, -1)
    row_totals = own_totals[..., 0] + jnp.sum(cross_exp, -1)
    totals = jnp.where(first_mask, row_totals[..., None], own_totals)
    return (own_exp / totals[..., None], cross_exp / row_totals[..., None])


def row_softmax(own_scores, cross_scores):
    peak = jnp.maximum(jnp.max(own_scores, -1), jnp.max(cross_scores, -1))[..., None]
    own_exp = jnp.exp(own_scores - peak)
    cross_exp = jnp.exp(cross_scores - peak)
    totals = (jnp.sum(own_exp, -1) + jnp.sum(cross_exp, -1))[..., None]
    return (own_exp / totals, cross_exp / totals)


def gather_cand(block, axis):
    count = lax.axis_size("cand")
    if count > 8:
        return lax.all_gather(block, "cand", axis=axis, tiled=True)
    me = lax.axis_index("cand")
    parts = [block] + [
        lax.ppermute(block, "cand", [(j, (j + k) % count) for j in range(count)])
        for k in range(1, count)
    ]
    ordered = jnp.take(jnp.stack(parts, 0), (me - jnp.arange(count)) % count, axis=0)
    ordered = jnp.moveaxis(ordered, 0, axis)
    shape = block.shape[:axis] + (count * block.shape[axis],) + block.shape[axis + 1 :]
    return ordered.reshape(shape)


def sum_cand(block):
    count = lax.axis_size("cand")
    if count > 8:
        return lax.psum(block, "cand")
    total = block
    for k in range(1, count):
        total = total + lax.ppermute(block, "cand", [(j, (j + k) % count) for j in range(count)])
    return total


def scatter_cand(block, axis, total_type=None):
    count = lax.axis_size("cand")
    if count > 8:
        return lax.psum_scatter(block, "cand", scatter_dimension=axis, tiled=True)
    total_type = total_type or block.dtype
    me = lax.axis_index("cand")
    width = block.shape[axis] // count
    total = lax.dynamic_slice_in_dim(block, me * width, width, axis).astype(total_type)
    for k in range(1, count):
        piece = lax.dynamic_slice_in_dim(block, ((me + k) % count) * width, width, axis)
        moved = lax.ppermute(piece, "cand", [(j, (j + k) % count) for j in range(count)])
        total = total + moved.astype(total_type)
    return total


def gather_mp(block, axis):
    if lax.axis_size("mp") != 2:
        return lax.all_gather(block, "mp", axis=axis, tiled=True)
    other = lax.ppermute(block, "mp", [(0, 1), (1, 0)])
    return jnp.where(
        lax.axis_index("mp") == 0,
        jnp.concatenate([block, other], axis),
        jnp.concatenate([other, block], axis),
    )


def sum_query(block):
    if lax.axis_size("query") != 2:
        return lax.psum(block, "query")
    other = lax.ppermute(block, "query", [(0, 1), (1, 0)])
    return block.astype(jnp.float32) + other.astype(jnp.float32)


def local(
    tokens,
    lengths,
    teacher,
    w_first,
    w_out_first,
    gain_first,
    w_last,
    w_out_last,
    gain_last,
    w_score,
):
    lists, local_cands, seq_len, model_width = tokens.shape
    local_width = w_first.shape[2]
    local_heads = local_width // HEAD_DIM
    cand_count = local_cands * lax.axis_size("cand")
    query_count = lists * lax.axis_size("query")
    score_scale = HEAD_DIM ** (-0.5)
    positions = jnp.arange(seq_len)
    first_mask = positions == 0
    own_valid = positions[None, None, :] < lengths[:, :, None]
    local_ids = lax.axis_index("cand") * local_cands + jnp.arange(local_cands)
    cross_valid = local_ids[:, None] != jnp.arange(cand_count)[None, :]
    head_shape = (lists, local_cands, seq_len, local_heads, HEAD_DIM)
    cls_shape = (lists, cand_count, local_heads, HEAD_DIM)
    out_first_full = gather_mp(w_out_first, 0)
    last_full = gather_mp(w_last, 2)
    out_last_full = gather_mp(w_out_last, 0)
    cls_and_teacher = gather_cand(
        jnp.concatenate([tokens[:, :, 0].astype(jnp.float32), teacher[..., None]], -1), 1
    )
    cls_tokens = cls_and_teacher[..., :model_width].astype(jnp.bfloat16)
    teacher_all = cls_and_teacher[..., model_width]
    row_count = lists * local_cands * seq_len
    swap = [(0, 1), (1, 0)]
    paired_lists = lax.axis_size("query") == 2
    if paired_lists:
        other_tokens = lax.ppermute(tokens.reshape(row_count, model_width), "query", swap)
    projected = mixed("qcsd,kdf->kqcsf", tokens, w_first).astype(jnp.bfloat16)
    cls_projected = mixed("qcd,kdf->kqcf", cls_tokens, w_first[1:]).astype(jnp.bfloat16)
    gathered_keys = cls_projected[0]
    gathered_vals = cls_projected[1]
    first_query = projected[0].reshape(head_shape)
    first_keys = projected[1].reshape(head_shape)
    first_vals = projected[2].reshape(head_shape)
    cls_keys = gathered_keys.reshape(cls_shape)
    cls_vals = gathered_vals.reshape(cls_shape)
    own_scores = mixed("qcshe,qcthe->qchst", first_query, first_keys) * score_scale
    own_scores = jnp.where(own_valid[:, :, None, None, :], own_scores, NEGATIVE)
    cross_scores = mixed("qche,qdhe->qchd", first_query[:, :, 0], cls_keys) * score_scale
    cross_scores = jnp.where(cross_valid[None, :, None, :], cross_scores, NEGATIVE)
    own_prob, cross_prob = split_softmax(own_scores, cross_scores, first_mask)
    own_weight = own_prob.astype(jnp.bfloat16)
    cross_weight = cross_prob.astype(jnp.bfloat16)
    attended = mixed("qchst,qcthe->qcshe", own_weight, first_vals)
    attended_cls = mixed("qchd,qdhe->qche", cross_weight, cls_vals)
    attended = jnp.where(
        first_mask[None, None, :, None, None], attended + attended_cls[:, :, None], attended
    )
    first_mixed = attended.reshape(lists, local_cands, seq_len, local_width).astype(jnp.bfloat16)
    first_joined = lax.all_gather(first_mixed, "mp", axis=3, tiled=True)
    residual_first = tokens.astype(jnp.float32) + mixed(
        "qcsf,fd->qcsd", first_joined, out_first_full
    )
    normed_first, unit_first, inverse_first = norm_forward(residual_first, gain_first)
    hidden = normed_first.astype(jnp.bfloat16)
    last_query = mixed("qcd,df->qcf", hidden[:, :, 0], w_last[0]).astype(jnp.bfloat16)
    last_kv = mixed("qcsd,kdf->kqcsf", hidden, w_last[1:]).astype(jnp.bfloat16)
    gathered_kv_last = gather_cand(
        jnp.concatenate([last_kv[0][:, :, 0], last_kv[1][:, :, 0]], -1), 1
    )
    gathered_keys_last = gathered_kv_last[..., :local_width]
    gathered_vals_last = gathered_kv_last[..., local_width:]
    last_heads = last_query.reshape(lists, local_cands, local_heads, HEAD_DIM)
    last_keys = last_kv[0].reshape(head_shape)
    last_vals = last_kv[1].reshape(head_shape)
    cls_keys_last = gathered_keys_last.reshape(cls_shape)
    cls_vals_last = gathered_vals_last.reshape(cls_shape)
    own_last = mixed("qche,qcthe->qcht", last_heads, last_keys) * score_scale
    own_last = jnp.where(own_valid[:, :, None, :], own_last, NEGATIVE)
    cross_last = mixed("qche,qdhe->qchd", last_heads, cls_keys_last) * score_scale
    cross_last = jnp.where(cross_valid[None, :, None, :], cross_last, NEGATIVE)
    own_last_prob, cross_last_prob = row_softmax(own_last, cross_last)
    own_last_weight = own_last_prob.astype(jnp.bfloat16)
    cross_last_weight = cross_last_prob.astype(jnp.bfloat16)
    attended_last = mixed("qcht,qcthe->qche", own_last_weight, last_vals) + mixed(
        "qchd,qdhe->qche", cross_last_weight, cls_vals_last
    )
    last_mixed = attended_last.reshape(lists, local_cands, local_width).astype(jnp.bfloat16)
    last_joined = lax.all_gather(last_mixed, "mp", axis=2, tiled=True)
    residual_last = hidden[:, :, 0].astype(jnp.float32) + mixed(
        "qcf,fd->qcd", last_joined, out_last_full
    )
    normed_last, unit_last, inverse_last = norm_forward(residual_last, gain_last)
    scores = jnp.einsum("qcd,d->qc", normed_last, w_score, precision=lax.Precision.HIGHEST)
    score_exp = jnp.exp(scores)
    teacher_peak = jnp.max(teacher_all, 1)
    teacher_exp = jnp.exp(teacher - teacher_peak[:, None])
    teacher_totals = jnp.sum(jnp.exp(teacher_all - teacher_peak[:, None]), 1)
    score_totals = sum_cand(jnp.sum(score_exp, 1))
    student_prob = score_exp / score_totals[:, None]
    teacher_prob = teacher_exp / teacher_totals[:, None]
    score_grad = LOSS_SCALE * (student_prob - teacher_prob) / query_count
    grad_last = norm_backward(score_grad[..., None] * w_score, unit_last, inverse_last, gain_last)
    grad_last_low = grad_last.astype(jnp.bfloat16)
    grad_mixed_last = (
        mixed("qcd,fd->qcf", grad_last_low, w_out_last)
        .astype(jnp.bfloat16)
        .reshape(lists, local_cands, local_heads, HEAD_DIM)
    )
    own_dot = mixed("qche,qcthe->qcht", grad_mixed_last, last_vals)
    cross_dot = mixed("qche,qdhe->qchd", grad_mixed_last, cls_vals_last)
    centre = jnp.sum(own_last_prob * own_dot, -1, keepdims=True) + jnp.sum(
        cross_last_prob * cross_dot, -1, keepdims=True
    )
    own_slope = (own_last_prob * (own_dot - centre)).astype(jnp.bfloat16)
    cross_slope = (cross_last_prob * (cross_dot - centre)).astype(jnp.bfloat16)
    grad_query_last = (
        (
            (
                mixed("qcht,qcthe->qche", own_slope, last_keys)
                + mixed("qchd,qdhe->qche", cross_slope, cls_keys_last)
            )
            * score_scale
        )
        .astype(jnp.bfloat16)
        .reshape(lists, local_cands, local_width)
    )
    own_key_grad = (mixed("qcht,qche->qcthe", own_slope, last_heads) * score_scale).reshape(
        lists, local_cands, seq_len, local_width
    )
    own_val_grad = mixed("qcht,qche->qcthe", own_last_weight, grad_mixed_last).reshape(
        lists, local_cands, seq_len, local_width
    )
    cls_key_terms = (mixed("qchd,qche->qdhe", cross_slope, last_heads) * score_scale).reshape(
        lists, cand_count, local_width
    )
    cls_val_terms = mixed("qchd,qche->qdhe", cross_last_weight, grad_mixed_last).reshape(
        lists, cand_count, local_width
    )
    back_terms = scatter_cand(jnp.concatenate([cls_key_terms, cls_val_terms], -1), 1)
    back_keys = back_terms[..., :local_width]
    back_vals = back_terms[..., local_width:]
    first_cols = first_mask[None, None, :, None]
    key_grad = jnp.where(first_cols, own_key_grad + back_keys[:, :, None], own_key_grad).astype(
        jnp.bfloat16
    )
    val_grad = jnp.where(first_cols, own_val_grad + back_vals[:, :, None], own_val_grad).astype(
        jnp.bfloat16
    )
    joined = lax.all_gather(
        jnp.concatenate([key_grad, val_grad, grad_query_last[:, :, None]], 2),
        "mp",
        axis=3,
        tiled=True,
    )
    key_joined = joined[:, :, :seq_len]
    val_joined = joined[:, :, seq_len : 2 * seq_len]
    query_joined = joined[:, :, 2 * seq_len]
    summed_term = mixed("qcsf,df->qcsd", key_joined, last_full[1]) + mixed(
        "qcsf,df->qcsd", val_joined, last_full[2]
    )
    query_term = mixed("qcf,df->qcd", query_joined, last_full[0])
    summed_term = jnp.where(first_cols, summed_term + query_term[:, :, None], summed_term)
    grad_hidden = jnp.where(first_cols, summed_term + grad_last[:, :, None], summed_term)
    grad_first = norm_backward(grad_hidden, unit_first, inverse_first, gain_first).astype(
        jnp.bfloat16
    )
    grad_mixed_first = (
        mixed("qcsd,fd->qcsf", grad_first, w_out_first).astype(jnp.bfloat16).reshape(head_shape)
    )
    own_dot_first = mixed("qcshe,qcthe->qchst", grad_mixed_first, first_vals)
    cross_dot_first = mixed("qche,qdhe->qchd", grad_mixed_first[:, :, 0], cls_vals)
    own_part = jnp.sum(own_prob * own_dot_first, -1)
    row_part = own_part[..., 0] + jnp.sum(cross_prob * cross_dot_first, -1)
    centre_first = jnp.where(first_mask, row_part[..., None], own_part)
    own_slope_first = (own_prob * (own_dot_first - centre_first[..., None])).astype(jnp.bfloat16)
    cross_slope_first = (cross_prob * (cross_dot_first - row_part[..., None])).astype(jnp.bfloat16)
    query_grad = mixed("qchst,qcthe->qcshe", own_slope_first, first_keys)
    query_cls = mixed("qchd,qdhe->qche", cross_slope_first, cls_keys)
    query_grad = jnp.where(
        first_mask[None, None, :, None, None], query_grad + query_cls[:, :, None], query_grad
    )
    query_grad = (
        (query_grad * score_scale)
        .astype(jnp.bfloat16)
        .reshape(lists, local_cands, seq_len, local_width)
    )
    key_first = (mixed("qchst,qcshe->qcthe", own_slope_first, first_query) * score_scale).reshape(
        lists, local_cands, seq_len, local_width
    )
    val_first = mixed("qchst,qcshe->qcthe", own_weight, grad_mixed_first).reshape(
        lists, local_cands, seq_len, local_width
    )
    cls_key_first = (
        mixed("qchd,qche->qdhe", cross_slope_first, first_query[:, :, 0]) * score_scale
    ).reshape(lists, cand_count, local_width)
    cls_val_first = mixed("qchd,qche->qdhe", cross_weight, grad_mixed_first[:, :, 0]).reshape(
        lists, cand_count, local_width
    )
    key_first = key_first.astype(jnp.bfloat16)
    val_first = val_first.astype(jnp.bfloat16)
    stacked = jnp.stack([query_grad, key_first, val_first], 3).reshape(row_count, 3, local_width)
    cross_rows = lists * cand_count
    cross_stacked = jnp.stack(
        [jnp.zeros_like(cls_key_first), cls_key_first, cls_val_first], 2
    ).astype(jnp.bfloat16)
    all_rows = jnp.concatenate(
        [stacked, cross_stacked.reshape(cross_rows, 3, local_width)], 0
    )
    all_tokens = jnp.concatenate(
        [tokens.reshape(row_count, model_width), cls_tokens.reshape(cross_rows, model_width)], 0
    )
    if not paired_lists:
        partial_grad = lax.psum_scatter(
            mixed("rd,rkf->dkf", all_tokens, all_rows).astype(jnp.bfloat16),
            "cand",
            scatter_dimension=0,
            tiled=True,
        )
        return sum_query(partial_grad).astype(jnp.float32)
    half = 3 * local_width // 2
    side = lax.axis_index("query")
    flat_rows = all_rows.reshape(all_rows.shape[0], 3 * local_width)
    cls_flat = cls_tokens.reshape(cross_rows, model_width)
    own_half = lax.dynamic_slice_in_dim(flat_rows, side * half, half, 1)
    given_half = lax.dynamic_slice_in_dim(flat_rows, (1 - side) * half, half, 1)
    sent = lax.ppermute(
        jnp.concatenate([given_half.reshape(-1), cls_flat.reshape(-1)]), "query", swap
    )
    other_half = sent[: given_half.size].reshape(given_half.shape)
    other_cls = sent[given_half.size :].reshape(cls_flat.shape)
    paired = (
        mixed("rd,rf->df", all_tokens, own_half)
        + mixed("rd,rf->df", other_tokens, other_half[:row_count])
        + mixed("rd,rf->df", other_cls, other_half[row_count:])
    )
    reduced = scatter_cand(paired.astype(jnp.bfloat16), 0, jnp.float32).astype(jnp.bfloat16)
    partner = lax.ppermute(reduced, "query", swap)
    joined = jnp.where(
        side == 0,
        jnp.concatenate([reduced, partner], 1),
        jnp.concatenate([partner, reduced], 1),
    )
    return joined.reshape(joined.shape[0], 3, local_width).astype(jnp.float32)


def solution(mesh):
    return jax.shard_map(
        local,
        mesh=mesh,
        in_specs=(
            P(("groups", "query"), "cand", None, None),
            P(("groups", "query"), "cand"),
            P(("groups", "query"), "cand"),
            P(None, None, "mp"),
            P("mp", None),
            P(),
            P(None, None, "mp"),
            P("mp", None),
            P(),
            P(),
        ),
        out_specs=P(("groups", "cand"), None, "mp"),
        check_vma=False,
    )
```

```python
import jax
import jax.numpy as jnp
from jax import lax
from jax.sharding import PartitionSpec as P

HEAD_DIM = 64


EPSILON = 1e-05
LOSS_SCALE = 1024.0
NEGATIVE = -1e30


def mixed(pattern, former, latter):
    return jnp.einsum(pattern, former, latter, preferred_element_type=jnp.float32)


def norm_forward(matrix, scales):
    center = matrix - jnp.mean(matrix, -1, keepdims=True)
    inverse = lax.rsqrt(jnp.mean(center * center, -1, keepdims=True) + EPSILON)
    normed = center * inverse
    return (normed * scales, normed, inverse)


def norm_backward(incoming, normed, inverse, scales):
    scaled = incoming * scales
    return inverse * (
        scaled
        - jnp.mean(scaled, -1, keepdims=True)
        - normed * jnp.mean(scaled * normed, -1, keepdims=True)
    )


def split_softmax(own_scores, cross_scores, first_mask):
    own_peak = jnp.max(own_scores, -1)
    row_peak = jnp.maximum(own_peak[..., 0], jnp.max(cross_scores, -1))
    peak = jnp.where(first_mask, row_peak[..., None], own_peak)
    own_exp = jnp.exp(own_scores - peak[..., None])
    cross_exp = jnp.exp(cross_scores - row_peak[..., None])
    own_totals = jnp.sum(own_exp, -1)
    row_totals = own_totals[..., 0] + jnp.sum(cross_exp, -1)
    totals = jnp.where(first_mask, row_totals[..., None], own_totals)
    return (own_exp / totals[..., None], cross_exp / row_totals[..., None])


def row_softmax(own_scores, cross_scores):
    peak = jnp.maximum(jnp.max(own_scores, -1), jnp.max(cross_scores, -1))[..., None]
    own_exp = jnp.exp(own_scores - peak)
    cross_exp = jnp.exp(cross_scores - peak)
    totals = (jnp.sum(own_exp, -1) + jnp.sum(cross_exp, -1))[..., None]
    return (own_exp / totals, cross_exp / totals)


def gather_cand(block, axis):
    count = lax.axis_size("cand")
    if count > 8:
        return lax.all_gather(block, "cand", axis=axis, tiled=True)
    me = lax.axis_index("cand")
    parts = [block] + [
        lax.ppermute(block, "cand", [(j, (j + k) % count) for j in range(count)])
        for k in range(1, count)
    ]
    ordered = jnp.take(jnp.stack(parts, 0), (me - jnp.arange(count)) % count, axis=0)
    ordered = jnp.moveaxis(ordered, 0, axis)
    shape = block.shape[:axis] + (count * block.shape[axis],) + block.shape[axis + 1 :]
    return ordered.reshape(shape)


def sum_cand(block):
    count = lax.axis_size("cand")
    if count > 8:
        return lax.psum(block, "cand")
    total = block
    for k in range(1, count):
        total = total + lax.ppermute(block, "cand", [(j, (j + k) % count) for j in range(count)])
    return total


def scatter_cand(block, axis, total_type=None):
    count = lax.axis_size("cand")
    if count > 8:
        return lax.psum_scatter(block, "cand", scatter_dimension=axis, tiled=True)
    total_type = total_type or block.dtype
    me = lax.axis_index("cand")
    width = block.shape[axis] // count
    total = lax.dynamic_slice_in_dim(block, me * width, width, axis).astype(total_type)
    for k in range(1, count):
        piece = lax.dynamic_slice_in_dim(block, ((me + k) % count) * width, width, axis)
        moved = lax.ppermute(piece, "cand", [(j, (j + k) % count) for j in range(count)])
        total = total + moved.astype(total_type)
    return total


def gather_mp(block, axis):
    if lax.axis_size("mp") != 2:
        return lax.all_gather(block, "mp", axis=axis, tiled=True)
    other = lax.ppermute(block, "mp", [(0, 1), (1, 0)])
    return jnp.where(
        lax.axis_index("mp") == 0,
        jnp.concatenate([block, other], axis),
        jnp.concatenate([other, block], axis),
    )


def sum_query(block):
    if lax.axis_size("query") != 2:
        return lax.psum(block, "query")
    other = lax.ppermute(block, "query", [(0, 1), (1, 0)])
    return block.astype(jnp.float32) + other.astype(jnp.float32)


def local(
    tokens,
    lengths,
    teacher,
    w_first,
    w_out_first,
    gain_first,
    w_last,
    w_out_last,
    gain_last,
    w_score,
):
    lists, local_cands, seq_len, model_width = tokens.shape
    local_width = w_first.shape[2]
    local_heads = local_width // HEAD_DIM
    cand_count = local_cands * lax.axis_size("cand")
    query_count = lists * lax.axis_size("query")
    score_scale = HEAD_DIM ** (-0.5)
    positions = jnp.arange(seq_len)
    first_mask = positions == 0
    own_valid = positions[None, None, :] < lengths[:, :, None]
    local_ids = lax.axis_index("cand") * local_cands + jnp.arange(local_cands)
    cross_valid = local_ids[:, None] != jnp.arange(cand_count)[None, :]
    head_shape = (lists, local_cands, seq_len, local_heads, HEAD_DIM)
    cls_shape = (lists, cand_count, local_heads, HEAD_DIM)
    out_first_full = gather_mp(w_out_first, 0)
    last_full = gather_mp(w_last, 2)
    out_last_full = gather_mp(w_out_last, 0)
    cls_and_teacher = gather_cand(
        jnp.concatenate([tokens[:, :, 0].astype(jnp.float32), teacher[..., None]], -1), 1
    )
    cls_tokens = cls_and_teacher[..., :model_width].astype(jnp.bfloat16)
    teacher_all = cls_and_teacher[..., model_width]
    row_count = lists * local_cands * seq_len
    swap = [(0, 1), (1, 0)]
    paired_lists = lax.axis_size("query") == 2
    if paired_lists:
        other_tokens = lax.ppermute(tokens.reshape(row_count, model_width), "query", swap)
    projected = mixed("qcsd,kdf->kqcsf", tokens, w_first).astype(jnp.bfloat16)
    cls_projected = mixed("qcd,kdf->kqcf", cls_tokens, w_first[1:]).astype(jnp.bfloat16)
    gathered_keys = cls_projected[0]
    gathered_vals = cls_projected[1]
    first_query = projected[0].reshape(head_shape)
    first_keys = projected[1].reshape(head_shape)
    first_vals = projected[2].reshape(head_shape)
    cls_keys = gathered_keys.reshape(cls_shape)
    cls_vals = gathered_vals.reshape(cls_shape)
    own_scores = mixed("qcshe,qcthe->qchst", first_query, first_keys) * score_scale
    own_scores = jnp.where(own_valid[:, :, None, None, :], own_scores, NEGATIVE)
    cross_scores = mixed("qche,qdhe->qchd", first_query[:, :, 0], cls_keys) * score_scale
    cross_scores = jnp.where(cross_valid[None, :, None, :], cross_scores, NEGATIVE)
    own_prob, cross_prob = split_softmax(own_scores, cross_scores, first_mask)
    own_weight = own_prob.astype(jnp.bfloat16)
    cross_weight = cross_prob.astype(jnp.bfloat16)
    attended = mixed("qchst,qcthe->qcshe", own_weight, first_vals)
    attended_cls = mixed("qchd,qdhe->qche", cross_weight, cls_vals)
    attended = jnp.where(
        first_mask[None, None, :, None, None], attended + attended_cls[:, :, None], attended
    )
    first_mixed = attended.reshape(lists, local_cands, seq_len, local_width).astype(jnp.bfloat16)
    first_joined = lax.all_gather(first_mixed, "mp", axis=3, tiled=True)
    residual_first = tokens.astype(jnp.float32) + mixed(
        "qcsf,fd->qcsd", first_joined, out_first_full
    )
    normed_first, unit_first, inverse_first = norm_forward(residual_first, gain_first)
    hidden = normed_first.astype(jnp.bfloat16)
    last_query = mixed("qcd,df->qcf", hidden[:, :, 0], w_last[0]).astype(jnp.bfloat16)
    last_kv = mixed("qcsd,kdf->kqcsf", hidden, w_last[1:]).astype(jnp.bfloat16)
    gathered_kv_last = gather_cand(
        jnp.concatenate([last_kv[0][:, :, 0], last_kv[1][:, :, 0], last_query], -1), 1
    )
    gathered_keys_last = gathered_kv_last[..., :local_width]
    gathered_vals_last = gathered_kv_last[..., local_width : 2 * local_width]
    cls_queries_last = gathered_kv_last[..., 2 * local_width :].reshape(cls_shape)
    last_heads = last_query.reshape(lists, local_cands, local_heads, HEAD_DIM)
    last_keys = last_kv[0].reshape(head_shape)
    last_vals = last_kv[1].reshape(head_shape)
    cls_keys_last = gathered_keys_last.reshape(cls_shape)
    cls_vals_last = gathered_vals_last.reshape(cls_shape)
    own_last = mixed("qche,qcthe->qcht", last_heads, last_keys) * score_scale
    own_last = jnp.where(own_valid[:, :, None, :], own_last, NEGATIVE)
    cross_last = mixed("qche,qdhe->qchd", last_heads, cls_keys_last) * score_scale
    cross_last = jnp.where(cross_valid[None, :, None, :], cross_last, NEGATIVE)
    own_last_prob, cross_last_prob = row_softmax(own_last, cross_last)
    own_last_weight = own_last_prob.astype(jnp.bfloat16)
    cross_last_weight = cross_last_prob.astype(jnp.bfloat16)
    attended_last = mixed("qcht,qcthe->qche", own_last_weight, last_vals) + mixed(
        "qchd,qdhe->qche", cross_last_weight, cls_vals_last
    )
    last_mixed = attended_last.reshape(lists, local_cands, local_width).astype(jnp.bfloat16)
    last_joined = lax.all_gather(last_mixed, "mp", axis=2, tiled=True)
    residual_last = hidden[:, :, 0].astype(jnp.float32) + mixed(
        "qcf,fd->qcd", last_joined, out_last_full
    )
    exact = lax.Precision.HIGHEST
    mean_last = jnp.einsum(
        "qcht,qcthe->qche", own_last_prob, last_vals.astype(jnp.float32), precision=exact
    ) + jnp.einsum(
        "qchd,qdhe->qche", cross_last_prob, cls_vals_last.astype(jnp.float32), precision=exact
    )
    shared_last = gather_cand(
        jnp.concatenate(
            [
                residual_last,
                mean_last.reshape(lists, local_cands, local_width),
                cross_last_prob.reshape(lists, local_cands, local_heads * cand_count),
            ],
            -1,
        ),
        1,
    )
    all_residual = shared_last[..., :model_width]
    all_mean = shared_last[..., model_width : model_width + local_width].reshape(cls_shape)
    all_cross_prob = shared_last[..., model_width + local_width :].reshape(
        lists, cand_count, local_heads, cand_count
    )
    normed_last, unit_last, inverse_last = norm_forward(all_residual, gain_last)
    scores = jnp.einsum("qcd,d->qc", normed_last, w_score, precision=exact)
    score_exp = jnp.exp(scores)
    teacher_peak = jnp.max(teacher_all, 1)
    teacher_exp = jnp.exp(teacher_all - teacher_peak[:, None])
    student_prob = score_exp / jnp.sum(score_exp, 1)[:, None]
    teacher_prob = teacher_exp / jnp.sum(teacher_exp, 1)[:, None]
    score_grad = LOSS_SCALE * (student_prob - teacher_prob) / query_count
    grad_last_all = norm_backward(
        score_grad[..., None] * w_score, unit_last, inverse_last, gain_last
    )
    grad_mixed_all = (
        mixed("qcd,fd->qcf", grad_last_all.astype(jnp.bfloat16), w_out_last)
        .astype(jnp.bfloat16)
        .reshape(cls_shape)
    )
    grad_last = jnp.take(grad_last_all, local_ids, axis=1)
    grad_mixed_last = jnp.take(grad_mixed_all, local_ids, axis=1)
    own_dot = mixed("qche,qcthe->qcht", grad_mixed_last, last_vals)
    cross_dot = mixed("qche,qdhe->qchd", grad_mixed_last, cls_vals_last)
    centre = jnp.sum(own_last_prob * own_dot, -1, keepdims=True) + jnp.sum(
        cross_last_prob * cross_dot, -1, keepdims=True
    )
    own_slope = (own_last_prob * (own_dot - centre)).astype(jnp.bfloat16)
    cross_slope = (cross_last_prob * (cross_dot - centre)).astype(jnp.bfloat16)
    grad_query_last = (
        (
            (
                mixed("qcht,qcthe->qche", own_slope, last_keys)
                + mixed("qchd,qdhe->qche", cross_slope, cls_keys_last)
            )
            * score_scale
        )
        .astype(jnp.bfloat16)
        .reshape(lists, local_cands, local_width)
    )
    own_key_grad = (mixed("qcht,qche->qcthe", own_slope, last_heads) * score_scale).reshape(
        lists, local_cands, seq_len, local_width
    )
    own_val_grad = mixed("qcht,qche->qcthe", own_last_weight, grad_mixed_last).reshape(
        lists, local_cands, seq_len, local_width
    )
    own_cls_vals = last_vals[:, :, 0]
    dot_in = mixed("qche,qdhe->qchd", grad_mixed_all, own_cls_vals)
    centre_all = jnp.sum(grad_mixed_all.astype(jnp.float32) * all_mean, -1)
    prob_in = jnp.take(all_cross_prob, local_ids, axis=3)
    slope_in = (prob_in * (dot_in - centre_all[..., None])).astype(jnp.bfloat16)
    back_keys = (
        mixed("qchd,qche->qdhe", slope_in, cls_queries_last) * score_scale
    ).reshape(lists, local_cands, local_width)
    back_vals = mixed(
        "qchd,qche->qdhe", prob_in.astype(jnp.bfloat16), grad_mixed_all
    ).reshape(lists, local_cands, local_width)
    first_cols = first_mask[None, None, :, None]
    key_grad = jnp.where(first_cols, own_key_grad + back_keys[:, :, None], own_key_grad).astype(
        jnp.bfloat16
    )
    val_grad = jnp.where(first_cols, own_val_grad + back_vals[:, :, None], own_val_grad).astype(
        jnp.bfloat16
    )
    joined = lax.all_gather(
        jnp.concatenate([key_grad, val_grad, grad_query_last[:, :, None]], 2),
        "mp",
        axis=3,
        tiled=True,
    )
    key_joined = joined[:, :, :seq_len]
    val_joined = joined[:, :, seq_len : 2 * seq_len]
    query_joined = joined[:, :, 2 * seq_len]
    summed_term = mixed("qcsf,df->qcsd", key_joined, last_full[1]) + mixed(
        "qcsf,df->qcsd", val_joined, last_full[2]
    )
    query_term = mixed("qcf,df->qcd", query_joined, last_full[0])
    summed_term = jnp.where(first_cols, summed_term + query_term[:, :, None], summed_term)
    grad_hidden = jnp.where(first_cols, summed_term + grad_last[:, :, None], summed_term)
    grad_first = norm_backward(grad_hidden, unit_first, inverse_first, gain_first).astype(
        jnp.bfloat16
    )
    grad_mixed_first = (
        mixed("qcsd,fd->qcsf", grad_first, w_out_first).astype(jnp.bfloat16).reshape(head_shape)
    )
    own_dot_first = mixed("qcshe,qcthe->qchst", grad_mixed_first, first_vals)
    cross_dot_first = mixed("qche,qdhe->qchd", grad_mixed_first[:, :, 0], cls_vals)
    own_part = jnp.sum(own_prob * own_dot_first, -1)
    row_part = own_part[..., 0] + jnp.sum(cross_prob * cross_dot_first, -1)
    centre_first = jnp.where(first_mask, row_part[..., None], own_part)
    own_slope_first = (own_prob * (own_dot_first - centre_first[..., None])).astype(jnp.bfloat16)
    cross_slope_first = (cross_prob * (cross_dot_first - row_part[..., None])).astype(jnp.bfloat16)
    query_grad = mixed("qchst,qcthe->qcshe", own_slope_first, first_keys)
    query_cls = mixed("qchd,qdhe->qche", cross_slope_first, cls_keys)
    query_grad = jnp.where(
        first_mask[None, None, :, None, None], query_grad + query_cls[:, :, None], query_grad
    )
    query_grad = (
        (query_grad * score_scale)
        .astype(jnp.bfloat16)
        .reshape(lists, local_cands, seq_len, local_width)
    )
    key_first = (mixed("qchst,qcshe->qcthe", own_slope_first, first_query) * score_scale).reshape(
        lists, local_cands, seq_len, local_width
    )
    val_first = mixed("qchst,qcshe->qcthe", own_weight, grad_mixed_first).reshape(
        lists, local_cands, seq_len, local_width
    )
    cls_key_first = (
        mixed("qchd,qche->qdhe", cross_slope_first, first_query[:, :, 0]) * score_scale
    ).reshape(lists, cand_count, local_width)
    cls_val_first = mixed("qchd,qche->qdhe", cross_weight, grad_mixed_first[:, :, 0]).reshape(
        lists, cand_count, local_width
    )
    key_first = key_first.astype(jnp.bfloat16)
    val_first = val_first.astype(jnp.bfloat16)
    stacked = jnp.stack([query_grad, key_first, val_first], 3).reshape(row_count, 3, local_width)
    cross_rows = lists * cand_count
    cross_stacked = jnp.stack(
        [jnp.zeros_like(cls_key_first), cls_key_first, cls_val_first], 2
    ).astype(jnp.bfloat16)
    all_rows = jnp.concatenate(
        [stacked, cross_stacked.reshape(cross_rows, 3, local_width)], 0
    )
    all_tokens = jnp.concatenate(
        [tokens.reshape(row_count, model_width), cls_tokens.reshape(cross_rows, model_width)], 0
    )
    if not paired_lists:
        partial_grad = lax.psum_scatter(
            mixed("rd,rkf->dkf", all_tokens, all_rows).astype(jnp.bfloat16),
            "cand",
            scatter_dimension=0,
            tiled=True,
        )
        return sum_query(partial_grad).astype(jnp.float32)
    half = 3 * local_width // 2
    side = lax.axis_index("query")
    flat_rows = all_rows.reshape(all_rows.shape[0], 3 * local_width)
    cls_flat = cls_tokens.reshape(cross_rows, model_width)
    own_half = lax.dynamic_slice_in_dim(flat_rows, side * half, half, 1)
    given_half = lax.dynamic_slice_in_dim(flat_rows, (1 - side) * half, half, 1)
    sent = lax.ppermute(
        jnp.concatenate([given_half.reshape(-1), cls_flat.reshape(-1)]), "query", swap
    )
    other_half = sent[: given_half.size].reshape(given_half.shape)
    other_cls = sent[given_half.size :].reshape(cls_flat.shape)
    paired = (
        mixed("rd,rf->df", all_tokens, own_half)
        + mixed("rd,rf->df", other_tokens, other_half[:row_count])
        + mixed("rd,rf->df", other_cls, other_half[row_count:])
    )
    reduced = scatter_cand(paired.astype(jnp.bfloat16), 0, jnp.float32).astype(jnp.bfloat16)
    partner = lax.ppermute(reduced, "query", swap)
    joined = jnp.where(
        side == 0,
        jnp.concatenate([reduced, partner], 1),
        jnp.concatenate([partner, reduced], 1),
    )
    return joined.reshape(joined.shape[0], 3, local_width).astype(jnp.float32)


def solution(mesh):
    return jax.shard_map(
        local,
        mesh=mesh,
        in_specs=(
            P(("groups", "query"), "cand", None, None),
            P(("groups", "query"), "cand"),
            P(("groups", "query"), "cand"),
            P(None, None, "mp"),
            P("mp", None),
            P(),
            P(None, None, "mp"),
            P("mp", None),
            P(),
            P(),
        ),
        out_specs=P(("groups", "cand"), None, "mp"),
        check_vma=False,
    )
```

```python
import jax
import jax.numpy as jnp
from jax import lax
from jax.sharding import PartitionSpec as P

HEAD_DIM = 64


EPSILON = 1e-05
LOSS_SCALE = 1024.0
NEGATIVE = -1e30


def mixed(pattern, former, latter):
    return jnp.einsum(pattern, former, latter, preferred_element_type=jnp.float32)


def norm_forward(matrix, scales):
    center = matrix - jnp.mean(matrix, -1, keepdims=True)
    inverse = lax.rsqrt(jnp.mean(center * center, -1, keepdims=True) + EPSILON)
    normed = center * inverse
    return (normed * scales, normed, inverse)


def norm_backward(incoming, normed, inverse, scales):
    scaled = incoming * scales
    return inverse * (
        scaled
        - jnp.mean(scaled, -1, keepdims=True)
        - normed * jnp.mean(scaled * normed, -1, keepdims=True)
    )


def split_softmax(own_scores, cross_scores, first_mask):
    own_peak = jnp.max(own_scores, -1)
    row_peak = jnp.maximum(own_peak[..., 0], jnp.max(cross_scores, -1))
    peak = jnp.where(first_mask, row_peak[..., None], own_peak)
    own_exp = jnp.exp(own_scores - peak[..., None])
    cross_exp = jnp.exp(cross_scores - row_peak[..., None])
    own_totals = jnp.sum(own_exp, -1)
    row_totals = own_totals[..., 0] + jnp.sum(cross_exp, -1)
    totals = jnp.where(first_mask, row_totals[..., None], own_totals)
    return (own_exp / totals[..., None], cross_exp / row_totals[..., None])


def row_softmax(own_scores, cross_scores):
    peak = jnp.maximum(jnp.max(own_scores, -1), jnp.max(cross_scores, -1))[..., None]
    own_exp = jnp.exp(own_scores - peak)
    cross_exp = jnp.exp(cross_scores - peak)
    totals = (jnp.sum(own_exp, -1) + jnp.sum(cross_exp, -1))[..., None]
    return (own_exp / totals, cross_exp / totals)


def gather_cand(block, axis):
    count = lax.axis_size("cand")
    if count > 8:
        return lax.all_gather(block, "cand", axis=axis, tiled=True)
    me = lax.axis_index("cand")
    parts = [block] + [
        lax.ppermute(block, "cand", [(j, (j + k) % count) for j in range(count)])
        for k in range(1, count)
    ]
    ordered = jnp.take(jnp.stack(parts, 0), (me - jnp.arange(count)) % count, axis=0)
    ordered = jnp.moveaxis(ordered, 0, axis)
    shape = block.shape[:axis] + (count * block.shape[axis],) + block.shape[axis + 1 :]
    return ordered.reshape(shape)


def sum_cand(block):
    count = lax.axis_size("cand")
    if count > 8:
        return lax.psum(block, "cand")
    total = block
    for k in range(1, count):
        total = total + lax.ppermute(block, "cand", [(j, (j + k) % count) for j in range(count)])
    return total


def scatter_cand(block, axis, total_type=None):
    count = lax.axis_size("cand")
    if count > 8:
        return lax.psum_scatter(block, "cand", scatter_dimension=axis, tiled=True)
    total_type = total_type or block.dtype
    me = lax.axis_index("cand")
    width = block.shape[axis] // count
    total = lax.dynamic_slice_in_dim(block, me * width, width, axis).astype(total_type)
    for k in range(1, count):
        piece = lax.dynamic_slice_in_dim(block, ((me + k) % count) * width, width, axis)
        moved = lax.ppermute(piece, "cand", [(j, (j + k) % count) for j in range(count)])
        total = total + moved.astype(total_type)
    return total


def swap_core(block):
    return lax.ppermute(block, "mp", [(0, 1), (1, 0)])


def sum_query(block):
    if lax.axis_size("query") != 2:
        return lax.psum(block, "query")
    other = lax.ppermute(block, "query", [(0, 1), (1, 0)])
    return block.astype(jnp.float32) + other.astype(jnp.float32)


def local(
    tokens,
    lengths,
    teacher,
    w_first,
    w_out_first,
    gain_first,
    w_last,
    w_out_last,
    gain_last,
    w_score,
):
    lists, local_cands, seq_len, model_width = tokens.shape
    local_width = w_first.shape[2]
    local_heads = local_width // HEAD_DIM
    cand_count = local_cands * lax.axis_size("cand")
    query_count = lists * lax.axis_size("query")
    score_scale = HEAD_DIM ** (-0.5)
    positions = jnp.arange(seq_len)
    first_mask = positions == 0
    own_valid = positions[None, None, :] < lengths[:, :, None]
    local_ids = lax.axis_index("cand") * local_cands + jnp.arange(local_cands)
    cross_valid = local_ids[:, None] != jnp.arange(cand_count)[None, :]
    head_shape = (lists, local_cands, seq_len, local_heads, HEAD_DIM)
    cls_shape = (lists, cand_count, local_heads, HEAD_DIM)
    other_out_first = swap_core(w_out_first)
    other_last = swap_core(w_last)
    other_out_last = swap_core(w_out_last)
    cls_and_teacher = gather_cand(
        jnp.concatenate([tokens[:, :, 0].astype(jnp.float32), teacher[..., None]], -1), 1
    )
    cls_tokens = cls_and_teacher[..., :model_width].astype(jnp.bfloat16)
    teacher_all = cls_and_teacher[..., model_width]
    row_count = lists * local_cands * seq_len
    swap = [(0, 1), (1, 0)]
    paired_lists = lax.axis_size("query") == 2
    if paired_lists:
        other_tokens = lax.ppermute(tokens.reshape(row_count, model_width), "query", swap)
    projected = mixed("qcsd,kdf->kqcsf", tokens, w_first).astype(jnp.bfloat16)
    cls_projected = mixed("qcd,kdf->kqcf", cls_tokens, w_first[1:]).astype(jnp.bfloat16)
    gathered_keys = cls_projected[0]
    gathered_vals = cls_projected[1]
    first_query = projected[0].reshape(head_shape)
    first_keys = projected[1].reshape(head_shape)
    first_vals = projected[2].reshape(head_shape)
    cls_keys = gathered_keys.reshape(cls_shape)
    cls_vals = gathered_vals.reshape(cls_shape)
    own_scores = mixed("qcshe,qcthe->qchst", first_query, first_keys) * score_scale
    own_scores = jnp.where(own_valid[:, :, None, None, :], own_scores, NEGATIVE)
    cross_scores = mixed("qche,qdhe->qchd", first_query[:, :, 0], cls_keys) * score_scale
    cross_scores = jnp.where(cross_valid[None, :, None, :], cross_scores, NEGATIVE)
    own_prob, cross_prob = split_softmax(own_scores, cross_scores, first_mask)
    own_weight = own_prob.astype(jnp.bfloat16)
    cross_weight = cross_prob.astype(jnp.bfloat16)
    attended = mixed("qchst,qcthe->qcshe", own_weight, first_vals)
    attended_cls = mixed("qchd,qdhe->qche", cross_weight, cls_vals)
    attended = jnp.where(
        first_mask[None, None, :, None, None], attended + attended_cls[:, :, None], attended
    )
    first_mixed = attended.reshape(lists, local_cands, seq_len, local_width).astype(jnp.bfloat16)
    residual_first = (
        tokens.astype(jnp.float32)
        + mixed("qcsf,fd->qcsd", first_mixed, w_out_first)
        + mixed("qcsf,fd->qcsd", swap_core(first_mixed), other_out_first)
    )
    normed_first, unit_first, inverse_first = norm_forward(residual_first, gain_first)
    hidden = normed_first.astype(jnp.bfloat16)
    last_query = mixed("qcd,df->qcf", hidden[:, :, 0], w_last[0]).astype(jnp.bfloat16)
    last_kv = mixed("qcsd,kdf->kqcsf", hidden, w_last[1:]).astype(jnp.bfloat16)
    gathered_kv_last = gather_cand(
        jnp.concatenate([last_kv[0][:, :, 0], last_kv[1][:, :, 0]], -1), 1
    )
    gathered_keys_last = gathered_kv_last[..., :local_width]
    gathered_vals_last = gathered_kv_last[..., local_width:]
    last_heads = last_query.reshape(lists, local_cands, local_heads, HEAD_DIM)
    last_keys = last_kv[0].reshape(head_shape)
    last_vals = last_kv[1].reshape(head_shape)
    cls_keys_last = gathered_keys_last.reshape(cls_shape)
    cls_vals_last = gathered_vals_last.reshape(cls_shape)
    own_last = mixed("qche,qcthe->qcht", last_heads, last_keys) * score_scale
    own_last = jnp.where(own_valid[:, :, None, :], own_last, NEGATIVE)
    cross_last = mixed("qche,qdhe->qchd", last_heads, cls_keys_last) * score_scale
    cross_last = jnp.where(cross_valid[None, :, None, :], cross_last, NEGATIVE)
    own_last_prob, cross_last_prob = row_softmax(own_last, cross_last)
    own_last_weight = own_last_prob.astype(jnp.bfloat16)
    cross_last_weight = cross_last_prob.astype(jnp.bfloat16)
    attended_last = mixed("qcht,qcthe->qche", own_last_weight, last_vals) + mixed(
        "qchd,qdhe->qche", cross_last_weight, cls_vals_last
    )
    last_mixed = attended_last.reshape(lists, local_cands, local_width).astype(jnp.bfloat16)
    residual_last = (
        hidden[:, :, 0].astype(jnp.float32)
        + mixed("qcf,fd->qcd", last_mixed, w_out_last)
        + mixed("qcf,fd->qcd", swap_core(last_mixed), other_out_last)
    )
    normed_last, unit_last, inverse_last = norm_forward(residual_last, gain_last)
    scores = jnp.einsum("qcd,d->qc", normed_last, w_score, precision=lax.Precision.HIGHEST)
    score_exp = jnp.exp(scores)
    teacher_peak = jnp.max(teacher_all, 1)
    teacher_exp = jnp.exp(teacher - teacher_peak[:, None])
    teacher_totals = jnp.sum(jnp.exp(teacher_all - teacher_peak[:, None]), 1)
    score_totals = sum_cand(jnp.sum(score_exp, 1))
    student_prob = score_exp / score_totals[:, None]
    teacher_prob = teacher_exp / teacher_totals[:, None]
    score_grad = LOSS_SCALE * (student_prob - teacher_prob) / query_count
    grad_last = norm_backward(score_grad[..., None] * w_score, unit_last, inverse_last, gain_last)
    grad_last_low = grad_last.astype(jnp.bfloat16)
    grad_mixed_last = (
        mixed("qcd,fd->qcf", grad_last_low, w_out_last)
        .astype(jnp.bfloat16)
        .reshape(lists, local_cands, local_heads, HEAD_DIM)
    )
    own_dot = mixed("qche,qcthe->qcht", grad_mixed_last, last_vals)
    cross_dot = mixed("qche,qdhe->qchd", grad_mixed_last, cls_vals_last)
    centre = jnp.sum(own_last_prob * own_dot, -1, keepdims=True) + jnp.sum(
        cross_last_prob * cross_dot, -1, keepdims=True
    )
    own_slope = (own_last_prob * (own_dot - centre)).astype(jnp.bfloat16)
    cross_slope = (cross_last_prob * (cross_dot - centre)).astype(jnp.bfloat16)
    grad_query_last = (
        (
            (
                mixed("qcht,qcthe->qche", own_slope, last_keys)
                + mixed("qchd,qdhe->qche", cross_slope, cls_keys_last)
            )
            * score_scale
        )
        .astype(jnp.bfloat16)
        .reshape(lists, local_cands, local_width)
    )
    own_key_grad = (mixed("qcht,qche->qcthe", own_slope, last_heads) * score_scale).reshape(
        lists, local_cands, seq_len, local_width
    )
    own_val_grad = mixed("qcht,qche->qcthe", own_last_weight, grad_mixed_last).reshape(
        lists, local_cands, seq_len, local_width
    )
    cls_key_terms = (mixed("qchd,qche->qdhe", cross_slope, last_heads) * score_scale).reshape(
        lists, cand_count, local_width
    )
    cls_val_terms = mixed("qchd,qche->qdhe", cross_last_weight, grad_mixed_last).reshape(
        lists, cand_count, local_width
    )
    back_terms = scatter_cand(jnp.concatenate([cls_key_terms, cls_val_terms], -1), 1)
    back_keys = back_terms[..., :local_width]
    back_vals = back_terms[..., local_width:]
    first_cols = first_mask[None, None, :, None]
    key_grad = jnp.where(first_cols, own_key_grad + back_keys[:, :, None], own_key_grad).astype(
        jnp.bfloat16
    )
    val_grad = jnp.where(first_cols, own_val_grad + back_vals[:, :, None], own_val_grad).astype(
        jnp.bfloat16
    )
    other = swap_core(jnp.concatenate([key_grad, val_grad, grad_query_last[:, :, None]], 2))
    other_key = other[:, :, :seq_len]
    other_val = other[:, :, seq_len : 2 * seq_len]
    other_query = other[:, :, 2 * seq_len]
    summed_term = (
        mixed("qcsf,df->qcsd", key_grad, w_last[1])
        + mixed("qcsf,df->qcsd", val_grad, w_last[2])
        + mixed("qcsf,df->qcsd", other_key, other_last[1])
        + mixed("qcsf,df->qcsd", other_val, other_last[2])
    )
    query_term = mixed("qcf,df->qcd", grad_query_last, w_last[0]) + mixed(
        "qcf,df->qcd", other_query, other_last[0]
    )
    summed_term = jnp.where(first_cols, summed_term + query_term[:, :, None], summed_term)
    grad_hidden = jnp.where(first_cols, summed_term + grad_last[:, :, None], summed_term)
    grad_first = norm_backward(grad_hidden, unit_first, inverse_first, gain_first).astype(
        jnp.bfloat16
    )
    grad_mixed_first = (
        mixed("qcsd,fd->qcsf", grad_first, w_out_first).astype(jnp.bfloat16).reshape(head_shape)
    )
    own_dot_first = mixed("qcshe,qcthe->qchst", grad_mixed_first, first_vals)
    cross_dot_first = mixed("qche,qdhe->qchd", grad_mixed_first[:, :, 0], cls_vals)
    own_part = jnp.sum(own_prob * own_dot_first, -1)
    row_part = own_part[..., 0] + jnp.sum(cross_prob * cross_dot_first, -1)
    centre_first = jnp.where(first_mask, row_part[..., None], own_part)
    own_slope_first = (own_prob * (own_dot_first - centre_first[..., None])).astype(jnp.bfloat16)
    cross_slope_first = (cross_prob * (cross_dot_first - row_part[..., None])).astype(jnp.bfloat16)
    query_grad = mixed("qchst,qcthe->qcshe", own_slope_first, first_keys)
    query_cls = mixed("qchd,qdhe->qche", cross_slope_first, cls_keys)
    query_grad = jnp.where(
        first_mask[None, None, :, None, None], query_grad + query_cls[:, :, None], query_grad
    )
    query_grad = (
        (query_grad * score_scale)
        .astype(jnp.bfloat16)
        .reshape(lists, local_cands, seq_len, local_width)
    )
    key_first = (mixed("qchst,qcshe->qcthe", own_slope_first, first_query) * score_scale).reshape(
        lists, local_cands, seq_len, local_width
    )
    val_first = mixed("qchst,qcshe->qcthe", own_weight, grad_mixed_first).reshape(
        lists, local_cands, seq_len, local_width
    )
    cls_key_first = (
        mixed("qchd,qche->qdhe", cross_slope_first, first_query[:, :, 0]) * score_scale
    ).reshape(lists, cand_count, local_width)
    cls_val_first = mixed("qchd,qche->qdhe", cross_weight, grad_mixed_first[:, :, 0]).reshape(
        lists, cand_count, local_width
    )
    key_first = key_first.astype(jnp.bfloat16)
    val_first = val_first.astype(jnp.bfloat16)
    stacked = jnp.stack([query_grad, key_first, val_first], 3).reshape(row_count, 3, local_width)
    cross_rows = lists * cand_count
    cross_stacked = jnp.stack(
        [jnp.zeros_like(cls_key_first), cls_key_first, cls_val_first], 2
    ).astype(jnp.bfloat16)
    all_rows = jnp.concatenate(
        [stacked, cross_stacked.reshape(cross_rows, 3, local_width)], 0
    )
    all_tokens = jnp.concatenate(
        [tokens.reshape(row_count, model_width), cls_tokens.reshape(cross_rows, model_width)], 0
    )
    if not paired_lists:
        partial_grad = lax.psum_scatter(
            mixed("rd,rkf->dkf", all_tokens, all_rows).astype(jnp.bfloat16),
            "cand",
            scatter_dimension=0,
            tiled=True,
        )
        return sum_query(partial_grad).astype(jnp.float32)
    half = 3 * local_width // 2
    side = lax.axis_index("query")
    flat_rows = all_rows.reshape(all_rows.shape[0], 3 * local_width)
    cls_flat = cls_tokens.reshape(cross_rows, model_width)
    own_half = lax.dynamic_slice_in_dim(flat_rows, side * half, half, 1)
    given_half = lax.dynamic_slice_in_dim(flat_rows, (1 - side) * half, half, 1)
    sent = lax.ppermute(
        jnp.concatenate([given_half.reshape(-1), cls_flat.reshape(-1)]), "query", swap
    )
    other_half = sent[: given_half.size].reshape(given_half.shape)
    other_cls = sent[given_half.size :].reshape(cls_flat.shape)
    paired = (
        mixed("rd,rf->df", all_tokens, own_half)
        + mixed("rd,rf->df", other_tokens, other_half[:row_count])
        + mixed("rd,rf->df", other_cls, other_half[row_count:])
    )
    reduced = scatter_cand(paired.astype(jnp.bfloat16), 0, jnp.float32).astype(jnp.bfloat16)
    partner = lax.ppermute(reduced, "query", swap)
    joined = jnp.where(
        side == 0,
        jnp.concatenate([reduced, partner], 1),
        jnp.concatenate([partner, reduced], 1),
    )
    return joined.reshape(joined.shape[0], 3, local_width).astype(jnp.float32)


def solution(mesh):
    return jax.shard_map(
        local,
        mesh=mesh,
        in_specs=(
            P(("groups", "query"), "cand", None, None),
            P(("groups", "query"), "cand"),
            P(("groups", "query"), "cand"),
            P(None, None, "mp"),
            P("mp", None),
            P(),
            P(None, None, "mp"),
            P("mp", None),
            P(),
            P(),
        ),
        out_specs=P(("groups", "cand"), None, "mp"),
        check_vma=False,
    )
```

```python
import jax
import jax.numpy as jnp
from jax import lax
from jax.sharding import PartitionSpec as P

HEAD_DIM = 64


EPSILON = 1e-05
LOSS_SCALE = 1024.0
NEGATIVE = -1e30


def mixed(pattern, former, latter):
    return jnp.einsum(pattern, former, latter, preferred_element_type=jnp.float32)


def norm_forward(matrix, scales):
    center = matrix - jnp.mean(matrix, -1, keepdims=True)
    inverse = lax.rsqrt(jnp.mean(center * center, -1, keepdims=True) + EPSILON)
    normed = center * inverse
    return (normed * scales, normed, inverse)


def norm_backward(incoming, normed, inverse, scales):
    scaled = incoming * scales
    return inverse * (
        scaled
        - jnp.mean(scaled, -1, keepdims=True)
        - normed * jnp.mean(scaled * normed, -1, keepdims=True)
    )


def split_softmax(own_scores, cross_scores, first_mask):
    own_peak = jnp.max(own_scores, -1)
    row_peak = jnp.maximum(own_peak[..., 0], jnp.max(cross_scores, -1))
    peak = jnp.where(first_mask, row_peak[..., None], own_peak)
    own_exp = jnp.exp(own_scores - peak[..., None])
    cross_exp = jnp.exp(cross_scores - row_peak[..., None])
    own_totals = jnp.sum(own_exp, -1)
    row_totals = own_totals[..., 0] + jnp.sum(cross_exp, -1)
    totals = jnp.where(first_mask, row_totals[..., None], own_totals)
    return (own_exp / totals[..., None], cross_exp / row_totals[..., None])


def row_softmax(own_scores, cross_scores):
    peak = jnp.maximum(jnp.max(own_scores, -1), jnp.max(cross_scores, -1))[..., None]
    own_exp = jnp.exp(own_scores - peak)
    cross_exp = jnp.exp(cross_scores - peak)
    totals = (jnp.sum(own_exp, -1) + jnp.sum(cross_exp, -1))[..., None]
    return (own_exp / totals, cross_exp / totals)


def gather_cand(block, axis):
    count = lax.axis_size("cand")
    if count > 8:
        return lax.all_gather(block, "cand", axis=axis, tiled=True)
    me = lax.axis_index("cand")
    parts = [block] + [
        lax.ppermute(block, "cand", [(j, (j + k) % count) for j in range(count)])
        for k in range(1, count)
    ]
    ordered = jnp.take(jnp.stack(parts, 0), (me - jnp.arange(count)) % count, axis=0)
    ordered = jnp.moveaxis(ordered, 0, axis)
    shape = block.shape[:axis] + (count * block.shape[axis],) + block.shape[axis + 1 :]
    return ordered.reshape(shape)


def sum_cand(block):
    count = lax.axis_size("cand")
    if count > 8:
        return lax.psum(block, "cand")
    total = block
    for k in range(1, count):
        total = total + lax.ppermute(block, "cand", [(j, (j + k) % count) for j in range(count)])
    return total


def scatter_cand(block, axis, total_type=None):
    count = lax.axis_size("cand")
    if count > 8:
        return lax.psum_scatter(block, "cand", scatter_dimension=axis, tiled=True)
    total_type = total_type or block.dtype
    me = lax.axis_index("cand")
    width = block.shape[axis] // count
    total = lax.dynamic_slice_in_dim(block, me * width, width, axis).astype(total_type)
    for k in range(1, count):
        piece = lax.dynamic_slice_in_dim(block, ((me + k) % count) * width, width, axis)
        moved = lax.ppermute(piece, "cand", [(j, (j + k) % count) for j in range(count)])
        total = total + moved.astype(total_type)
    return total


def swap_core(block):
    return lax.ppermute(block, "mp", [(0, 1), (1, 0)])


def sum_query(block):
    if lax.axis_size("query") != 2:
        return lax.psum(block, "query")
    other = lax.ppermute(block, "query", [(0, 1), (1, 0)])
    return block.astype(jnp.float32) + other.astype(jnp.float32)


def local(
    tokens,
    lengths,
    teacher,
    w_first,
    w_out_first,
    gain_first,
    w_last,
    w_out_last,
    gain_last,
    w_score,
):
    lists, local_cands, seq_len, model_width = tokens.shape
    local_width = w_first.shape[2]
    local_heads = local_width // HEAD_DIM
    cand_count = local_cands * lax.axis_size("cand")
    query_count = lists * lax.axis_size("query")
    score_scale = HEAD_DIM ** (-0.5)
    positions = jnp.arange(seq_len)
    first_mask = positions == 0
    own_valid = positions[None, None, :] < lengths[:, :, None]
    local_ids = lax.axis_index("cand") * local_cands + jnp.arange(local_cands)
    cross_valid = local_ids[:, None] != jnp.arange(cand_count)[None, :]
    head_shape = (lists, local_cands, seq_len, local_heads, HEAD_DIM)
    cls_shape = (lists, cand_count, local_heads, HEAD_DIM)
    other_out_first = swap_core(w_out_first)
    other_last = swap_core(w_last)
    other_out_last = swap_core(w_out_last)
    projected = mixed("qcsd,kdf->kqcsf", tokens, w_first).astype(jnp.bfloat16)
    cls_rows, projected = lax.optimization_barrier(
        (jnp.concatenate([tokens[:, :, 0].astype(jnp.float32), teacher[..., None]], -1), projected)
    )
    cls_and_teacher = gather_cand(cls_rows, 1)
    cls_tokens = cls_and_teacher[..., :model_width].astype(jnp.bfloat16)
    teacher_all = cls_and_teacher[..., model_width]
    row_count = lists * local_cands * seq_len
    swap = [(0, 1), (1, 0)]
    paired_lists = lax.axis_size("query") == 2
    if paired_lists:
        other_tokens = lax.ppermute(tokens.reshape(row_count, model_width), "query", swap)
    cls_projected = mixed("qcd,kdf->kqcf", cls_tokens, w_first[1:]).astype(jnp.bfloat16)
    gathered_keys = cls_projected[0]
    gathered_vals = cls_projected[1]
    first_query = projected[0].reshape(head_shape)
    first_keys = projected[1].reshape(head_shape)
    first_vals = projected[2].reshape(head_shape)
    cls_keys = gathered_keys.reshape(cls_shape)
    cls_vals = gathered_vals.reshape(cls_shape)
    own_scores = mixed("qcshe,qcthe->qchst", first_query, first_keys) * score_scale
    own_scores = jnp.where(own_valid[:, :, None, None, :], own_scores, NEGATIVE)
    cross_scores = mixed("qche,qdhe->qchd", first_query[:, :, 0], cls_keys) * score_scale
    cross_scores = jnp.where(cross_valid[None, :, None, :], cross_scores, NEGATIVE)
    own_prob, cross_prob = split_softmax(own_scores, cross_scores, first_mask)
    own_weight = own_prob.astype(jnp.bfloat16)
    cross_weight = cross_prob.astype(jnp.bfloat16)
    attended = mixed("qchst,qcthe->qcshe", own_weight, first_vals)
    attended_cls = mixed("qchd,qdhe->qche", cross_weight, cls_vals)
    attended = jnp.where(
        first_mask[None, None, :, None, None], attended + attended_cls[:, :, None], attended
    )
    first_mixed = attended.reshape(lists, local_cands, seq_len, local_width).astype(jnp.bfloat16)
    residual_first = (
        tokens.astype(jnp.float32)
        + mixed("qcsf,fd->qcsd", first_mixed, w_out_first)
        + mixed("qcsf,fd->qcsd", swap_core(first_mixed), other_out_first)
    )
    normed_first, unit_first, inverse_first = norm_forward(residual_first, gain_first)
    hidden = normed_first.astype(jnp.bfloat16)
    last_query = mixed("qcd,df->qcf", hidden[:, :, 0], w_last[0]).astype(jnp.bfloat16)
    last_kv = mixed("qcsd,kdf->kqcsf", hidden, w_last[1:]).astype(jnp.bfloat16)
    gathered_kv_last = gather_cand(
        jnp.concatenate([last_kv[0][:, :, 0], last_kv[1][:, :, 0]], -1), 1
    )
    gathered_keys_last = gathered_kv_last[..., :local_width]
    gathered_vals_last = gathered_kv_last[..., local_width:]
    last_heads = last_query.reshape(lists, local_cands, local_heads, HEAD_DIM)
    last_keys = last_kv[0].reshape(head_shape)
    last_vals = last_kv[1].reshape(head_shape)
    cls_keys_last = gathered_keys_last.reshape(cls_shape)
    cls_vals_last = gathered_vals_last.reshape(cls_shape)
    own_last = mixed("qche,qcthe->qcht", last_heads, last_keys) * score_scale
    own_last = jnp.where(own_valid[:, :, None, :], own_last, NEGATIVE)
    cross_last = mixed("qche,qdhe->qchd", last_heads, cls_keys_last) * score_scale
    cross_last = jnp.where(cross_valid[None, :, None, :], cross_last, NEGATIVE)
    own_last_prob, cross_last_prob = row_softmax(own_last, cross_last)
    own_last_weight = own_last_prob.astype(jnp.bfloat16)
    cross_last_weight = cross_last_prob.astype(jnp.bfloat16)
    attended_last = mixed("qcht,qcthe->qche", own_last_weight, last_vals) + mixed(
        "qchd,qdhe->qche", cross_last_weight, cls_vals_last
    )
    last_mixed = attended_last.reshape(lists, local_cands, local_width).astype(jnp.bfloat16)
    residual_last = (
        hidden[:, :, 0].astype(jnp.float32)
        + mixed("qcf,fd->qcd", last_mixed, w_out_last)
        + mixed("qcf,fd->qcd", swap_core(last_mixed), other_out_last)
    )
    normed_last, unit_last, inverse_last = norm_forward(residual_last, gain_last)
    scores = jnp.einsum("qcd,d->qc", normed_last, w_score, precision=lax.Precision.HIGHEST)
    score_exp = jnp.exp(scores)
    teacher_peak = jnp.max(teacher_all, 1)
    teacher_exp = jnp.exp(teacher - teacher_peak[:, None])
    teacher_totals = jnp.sum(jnp.exp(teacher_all - teacher_peak[:, None]), 1)
    score_totals = sum_cand(jnp.sum(score_exp, 1))
    student_prob = score_exp / score_totals[:, None]
    teacher_prob = teacher_exp / teacher_totals[:, None]
    score_grad = LOSS_SCALE * (student_prob - teacher_prob) / query_count
    grad_last = norm_backward(score_grad[..., None] * w_score, unit_last, inverse_last, gain_last)
    grad_last_low = grad_last.astype(jnp.bfloat16)
    grad_mixed_last = (
        mixed("qcd,fd->qcf", grad_last_low, w_out_last)
        .astype(jnp.bfloat16)
        .reshape(lists, local_cands, local_heads, HEAD_DIM)
    )
    own_dot = mixed("qche,qcthe->qcht", grad_mixed_last, last_vals)
    cross_dot = mixed("qche,qdhe->qchd", grad_mixed_last, cls_vals_last)
    centre = jnp.sum(own_last_prob * own_dot, -1, keepdims=True) + jnp.sum(
        cross_last_prob * cross_dot, -1, keepdims=True
    )
    own_slope = (own_last_prob * (own_dot - centre)).astype(jnp.bfloat16)
    cross_slope = (cross_last_prob * (cross_dot - centre)).astype(jnp.bfloat16)
    grad_query_last = (
        (
            (
                mixed("qcht,qcthe->qche", own_slope, last_keys)
                + mixed("qchd,qdhe->qche", cross_slope, cls_keys_last)
            )
            * score_scale
        )
        .astype(jnp.bfloat16)
        .reshape(lists, local_cands, local_width)
    )
    own_key_grad = (mixed("qcht,qche->qcthe", own_slope, last_heads) * score_scale).reshape(
        lists, local_cands, seq_len, local_width
    )
    own_val_grad = mixed("qcht,qche->qcthe", own_last_weight, grad_mixed_last).reshape(
        lists, local_cands, seq_len, local_width
    )
    cls_key_terms = (mixed("qchd,qche->qdhe", cross_slope, last_heads) * score_scale).reshape(
        lists, cand_count, local_width
    )
    cls_val_terms = mixed("qchd,qche->qdhe", cross_last_weight, grad_mixed_last).reshape(
        lists, cand_count, local_width
    )
    back_terms = scatter_cand(jnp.concatenate([cls_key_terms, cls_val_terms], -1), 1)
    back_keys = back_terms[..., :local_width]
    back_vals = back_terms[..., local_width:]
    first_cols = first_mask[None, None, :, None]
    key_grad = jnp.where(first_cols, own_key_grad + back_keys[:, :, None], own_key_grad).astype(
        jnp.bfloat16
    )
    val_grad = jnp.where(first_cols, own_val_grad + back_vals[:, :, None], own_val_grad).astype(
        jnp.bfloat16
    )
    other = swap_core(jnp.concatenate([key_grad, val_grad, grad_query_last[:, :, None]], 2))
    other_key = other[:, :, :seq_len]
    other_val = other[:, :, seq_len : 2 * seq_len]
    other_query = other[:, :, 2 * seq_len]
    summed_term = (
        mixed("qcsf,df->qcsd", key_grad, w_last[1])
        + mixed("qcsf,df->qcsd", val_grad, w_last[2])
        + mixed("qcsf,df->qcsd", other_key, other_last[1])
        + mixed("qcsf,df->qcsd", other_val, other_last[2])
    )
    query_term = mixed("qcf,df->qcd", grad_query_last, w_last[0]) + mixed(
        "qcf,df->qcd", other_query, other_last[0]
    )
    summed_term = jnp.where(first_cols, summed_term + query_term[:, :, None], summed_term)
    grad_hidden = jnp.where(first_cols, summed_term + grad_last[:, :, None], summed_term)
    grad_first = norm_backward(grad_hidden, unit_first, inverse_first, gain_first).astype(
        jnp.bfloat16
    )
    grad_mixed_first = (
        mixed("qcsd,fd->qcsf", grad_first, w_out_first).astype(jnp.bfloat16).reshape(head_shape)
    )
    own_dot_first = mixed("qcshe,qcthe->qchst", grad_mixed_first, first_vals)
    cross_dot_first = mixed("qche,qdhe->qchd", grad_mixed_first[:, :, 0], cls_vals)
    own_part = jnp.sum(own_prob * own_dot_first, -1)
    row_part = own_part[..., 0] + jnp.sum(cross_prob * cross_dot_first, -1)
    centre_first = jnp.where(first_mask, row_part[..., None], own_part)
    own_slope_first = (own_prob * (own_dot_first - centre_first[..., None])).astype(jnp.bfloat16)
    cross_slope_first = (cross_prob * (cross_dot_first - row_part[..., None])).astype(jnp.bfloat16)
    query_grad = mixed("qchst,qcthe->qcshe", own_slope_first, first_keys)
    query_cls = mixed("qchd,qdhe->qche", cross_slope_first, cls_keys)
    query_grad = jnp.where(
        first_mask[None, None, :, None, None], query_grad + query_cls[:, :, None], query_grad
    )
    query_grad = (
        (query_grad * score_scale)
        .astype(jnp.bfloat16)
        .reshape(lists, local_cands, seq_len, local_width)
    )
    key_first = (mixed("qchst,qcshe->qcthe", own_slope_first, first_query) * score_scale).reshape(
        lists, local_cands, seq_len, local_width
    )
    val_first = mixed("qchst,qcshe->qcthe", own_weight, grad_mixed_first).reshape(
        lists, local_cands, seq_len, local_width
    )
    cls_key_first = (
        mixed("qchd,qche->qdhe", cross_slope_first, first_query[:, :, 0]) * score_scale
    ).reshape(lists, cand_count, local_width)
    cls_val_first = mixed("qchd,qche->qdhe", cross_weight, grad_mixed_first[:, :, 0]).reshape(
        lists, cand_count, local_width
    )
    key_first = key_first.astype(jnp.bfloat16)
    val_first = val_first.astype(jnp.bfloat16)
    stacked = jnp.stack([query_grad, key_first, val_first], 3).reshape(row_count, 3, local_width)
    cross_rows = lists * cand_count
    cross_stacked = jnp.stack(
        [jnp.zeros_like(cls_key_first), cls_key_first, cls_val_first], 2
    ).astype(jnp.bfloat16)
    all_rows = jnp.concatenate(
        [stacked, cross_stacked.reshape(cross_rows, 3, local_width)], 0
    )
    all_tokens = jnp.concatenate(
        [tokens.reshape(row_count, model_width), cls_tokens.reshape(cross_rows, model_width)], 0
    )
    if not paired_lists:
        partial_grad = lax.psum_scatter(
            mixed("rd,rkf->dkf", all_tokens, all_rows).astype(jnp.bfloat16),
            "cand",
            scatter_dimension=0,
            tiled=True,
        )
        return sum_query(partial_grad).astype(jnp.float32)
    half = 3 * local_width // 2
    side = lax.axis_index("query")
    flat_rows = all_rows.reshape(all_rows.shape[0], 3 * local_width)
    cls_flat = cls_tokens.reshape(cross_rows, model_width)
    own_half = lax.dynamic_slice_in_dim(flat_rows, side * half, half, 1)
    given_half = lax.dynamic_slice_in_dim(flat_rows, (1 - side) * half, half, 1)
    sent = lax.ppermute(
        jnp.concatenate([given_half.reshape(-1), cls_flat.reshape(-1)]), "query", swap
    )
    other_half = sent[: given_half.size].reshape(given_half.shape)
    other_cls = sent[given_half.size :].reshape(cls_flat.shape)
    paired = (
        mixed("rd,rf->df", all_tokens, own_half)
        + mixed("rd,rf->df", other_tokens, other_half[:row_count])
        + mixed("rd,rf->df", other_cls, other_half[row_count:])
    )
    reduced = scatter_cand(paired.astype(jnp.bfloat16), 0, jnp.float32).astype(jnp.bfloat16)
    partner = lax.ppermute(reduced, "query", swap)
    joined = jnp.where(
        side == 0,
        jnp.concatenate([reduced, partner], 1),
        jnp.concatenate([partner, reduced], 1),
    )
    return joined.reshape(joined.shape[0], 3, local_width).astype(jnp.float32)


def solution(mesh):
    return jax.shard_map(
        local,
        mesh=mesh,
        in_specs=(
            P(("groups", "query"), "cand", None, None),
            P(("groups", "query"), "cand"),
            P(("groups", "query"), "cand"),
            P(None, None, "mp"),
            P("mp", None),
            P(),
            P(None, None, "mp"),
            P("mp", None),
            P(),
            P(),
        ),
        out_specs=P(("groups", "cand"), None, "mp"),
        check_vma=False,
    )
```

```python
import jax
import jax.numpy as jnp
from jax import lax
from jax.sharding import PartitionSpec as P

HEAD_DIM = 64


EPSILON = 1e-05
LOSS_SCALE = 1024.0
NEGATIVE = -1e30


def mixed(pattern, former, latter):
    return jnp.einsum(pattern, former, latter, preferred_element_type=jnp.float32)


def norm_forward(matrix, scales):
    center = matrix - jnp.mean(matrix, -1, keepdims=True)
    inverse = lax.rsqrt(jnp.mean(center * center, -1, keepdims=True) + EPSILON)
    normed = center * inverse
    return (normed * scales, normed, inverse)


def norm_backward(incoming, normed, inverse, scales):
    scaled = incoming * scales
    return inverse * (
        scaled
        - jnp.mean(scaled, -1, keepdims=True)
        - normed * jnp.mean(scaled * normed, -1, keepdims=True)
    )


def split_softmax(own_scores, cross_scores, first_mask):
    own_peak = jnp.max(own_scores, -1)
    row_peak = jnp.maximum(own_peak[..., 0], jnp.max(cross_scores, -1))
    peak = jnp.where(first_mask, row_peak[..., None], own_peak)
    own_exp = jnp.exp(own_scores - peak[..., None])
    cross_exp = jnp.exp(cross_scores - row_peak[..., None])
    own_totals = jnp.sum(own_exp, -1)
    row_totals = own_totals[..., 0] + jnp.sum(cross_exp, -1)
    totals = jnp.where(first_mask, row_totals[..., None], own_totals)
    return (own_exp / totals[..., None], cross_exp / row_totals[..., None])


def row_softmax(own_scores, cross_scores):
    peak = jnp.maximum(jnp.max(own_scores, -1), jnp.max(cross_scores, -1))[..., None]
    own_exp = jnp.exp(own_scores - peak)
    cross_exp = jnp.exp(cross_scores - peak)
    totals = (jnp.sum(own_exp, -1) + jnp.sum(cross_exp, -1))[..., None]
    return (own_exp / totals, cross_exp / totals)


def gather_cand(block, axis):
    count = lax.axis_size("cand")
    if count > 8:
        return lax.all_gather(block, "cand", axis=axis, tiled=True)
    me = lax.axis_index("cand")
    parts = [block] + [
        lax.ppermute(block, "cand", [(j, (j + k) % count) for j in range(count)])
        for k in range(1, count)
    ]
    ordered = jnp.take(jnp.stack(parts, 0), (me - jnp.arange(count)) % count, axis=0)
    ordered = jnp.moveaxis(ordered, 0, axis)
    shape = block.shape[:axis] + (count * block.shape[axis],) + block.shape[axis + 1 :]
    return ordered.reshape(shape)


def sum_cand(block):
    count = lax.axis_size("cand")
    if count > 8:
        return lax.psum(block, "cand")
    total = block
    for k in range(1, count):
        total = total + lax.ppermute(block, "cand", [(j, (j + k) % count) for j in range(count)])
    return total


def scatter_cand(block, axis, total_type=None):
    count = lax.axis_size("cand")
    if count > 8:
        return lax.psum_scatter(block, "cand", scatter_dimension=axis, tiled=True)
    total_type = total_type or block.dtype
    me = lax.axis_index("cand")
    width = block.shape[axis] // count
    total = lax.dynamic_slice_in_dim(block, me * width, width, axis).astype(total_type)
    for k in range(1, count):
        piece = lax.dynamic_slice_in_dim(block, ((me + k) % count) * width, width, axis)
        moved = lax.ppermute(piece, "cand", [(j, (j + k) % count) for j in range(count)])
        total = total + moved.astype(total_type)
    return total


def swap_core(block):
    return lax.ppermute(block, "mp", [(0, 1), (1, 0)])


def sum_query(block):
    if lax.axis_size("query") != 2:
        return lax.psum(block, "query")
    other = lax.ppermute(block, "query", [(0, 1), (1, 0)])
    return block.astype(jnp.float32) + other.astype(jnp.float32)


def local(
    tokens,
    lengths,
    teacher,
    w_first,
    w_out_first,
    gain_first,
    w_last,
    w_out_last,
    gain_last,
    w_score,
):
    lists, local_cands, seq_len, model_width = tokens.shape
    local_width = w_first.shape[2]
    local_heads = local_width // HEAD_DIM
    cand_count = local_cands * lax.axis_size("cand")
    query_count = lists * lax.axis_size("query")
    score_scale = HEAD_DIM ** (-0.5)
    positions = jnp.arange(seq_len)
    first_mask = positions == 0
    own_valid = positions[None, None, :] < lengths[:, :, None]
    local_ids = lax.axis_index("cand") * local_cands + jnp.arange(local_cands)
    cross_valid = local_ids[:, None] != jnp.arange(cand_count)[None, :]
    head_shape = (lists, local_cands, seq_len, local_heads, HEAD_DIM)
    cls_shape = (lists, cand_count, local_heads, HEAD_DIM)
    other_out_first = swap_core(w_out_first)
    other_last = swap_core(w_last)
    other_out_last = swap_core(w_out_last)
    cls_and_teacher = gather_cand(
        jnp.concatenate([tokens[:, :, 0].astype(jnp.float32), teacher[..., None]], -1), 1
    )
    cls_tokens = cls_and_teacher[..., :model_width].astype(jnp.bfloat16)
    teacher_all = cls_and_teacher[..., model_width]
    row_count = lists * local_cands * seq_len
    swap = [(0, 1), (1, 0)]
    paired_lists = lax.axis_size("query") == 2
    if paired_lists:
        other_tokens = lax.ppermute(tokens.reshape(row_count, model_width), "query", swap)
    projected = mixed("qcsd,kdf->kqcsf", tokens, w_first).astype(jnp.bfloat16)
    cls_projected = mixed("qcd,kdf->kqcf", cls_tokens, w_first[1:]).astype(jnp.bfloat16)
    gathered_keys = cls_projected[0]
    gathered_vals = cls_projected[1]
    first_query = projected[0].reshape(head_shape)
    first_keys = projected[1].reshape(head_shape)
    first_vals = projected[2].reshape(head_shape)
    cls_keys = gathered_keys.reshape(cls_shape)
    cls_vals = gathered_vals.reshape(cls_shape)
    own_scores = mixed("qcshe,qcthe->qchst", first_query, first_keys) * score_scale
    own_scores = jnp.where(own_valid[:, :, None, None, :], own_scores, NEGATIVE)
    cross_scores = mixed("qche,qdhe->qchd", first_query[:, :, 0], cls_keys) * score_scale
    cross_scores = jnp.where(cross_valid[None, :, None, :], cross_scores, NEGATIVE)
    own_prob, cross_prob = split_softmax(own_scores, cross_scores, first_mask)
    own_weight = own_prob.astype(jnp.bfloat16)
    cross_weight = cross_prob.astype(jnp.bfloat16)
    attended = mixed("qchst,qcthe->qcshe", own_weight, first_vals)
    attended_cls = mixed("qchd,qdhe->qche", cross_weight, cls_vals)
    attended = jnp.where(
        first_mask[None, None, :, None, None], attended + attended_cls[:, :, None], attended
    )
    first_mixed = attended.reshape(lists, local_cands, seq_len, local_width).astype(jnp.bfloat16)
    residual_first = (
        tokens.astype(jnp.float32)
        + mixed("qcsf,fd->qcsd", first_mixed, w_out_first)
        + mixed("qcsf,fd->qcsd", swap_core(first_mixed), other_out_first)
    )
    normed_first, unit_first, inverse_first = norm_forward(residual_first, gain_first)
    hidden = normed_first.astype(jnp.bfloat16)
    last_query = mixed("qcd,df->qcf", hidden[:, :, 0], w_last[0]).astype(jnp.bfloat16)
    last_kv = mixed("qcsd,kdf->kqcsf", hidden, w_last[1:]).astype(jnp.bfloat16)
    gathered_kv_last = gather_cand(
        jnp.concatenate([last_kv[0][:, :, 0], last_kv[1][:, :, 0]], -1), 1
    )
    gathered_keys_last = gathered_kv_last[..., :local_width]
    gathered_vals_last = gathered_kv_last[..., local_width:]
    last_heads = last_query.reshape(lists, local_cands, local_heads, HEAD_DIM)
    last_keys = last_kv[0].reshape(head_shape)
    last_vals = last_kv[1].reshape(head_shape)
    cls_keys_last = gathered_keys_last.reshape(cls_shape)
    cls_vals_last = gathered_vals_last.reshape(cls_shape)
    own_last = mixed("qche,qcthe->qcht", last_heads, last_keys) * score_scale
    own_last = jnp.where(own_valid[:, :, None, :], own_last, NEGATIVE)
    cross_last = mixed("qche,qdhe->qchd", last_heads, cls_keys_last) * score_scale
    cross_last = jnp.where(cross_valid[None, :, None, :], cross_last, NEGATIVE)
    own_last_prob, cross_last_prob = row_softmax(own_last, cross_last)
    own_last_weight = own_last_prob.astype(jnp.bfloat16)
    cross_last_weight = cross_last_prob.astype(jnp.bfloat16)
    attended_last = mixed("qcht,qcthe->qche", own_last_weight, last_vals) + mixed(
        "qchd,qdhe->qche", cross_last_weight, cls_vals_last
    )
    last_mixed = attended_last.reshape(lists, local_cands, local_width).astype(jnp.bfloat16)
    residual_last = (
        hidden[:, :, 0].astype(jnp.float32)
        + mixed("qcf,fd->qcd", last_mixed, w_out_last)
        + mixed("qcf,fd->qcd", swap_core(last_mixed), other_out_last)
    )
    normed_last, unit_last, inverse_last = norm_forward(residual_last, gain_last)
    scores = jnp.einsum("qcd,d->qc", normed_last, w_score, precision=lax.Precision.HIGHEST)
    score_exp_all = gather_cand(jnp.exp(scores), 1)
    teacher_peak = jnp.max(teacher_all, 1)
    teacher_exp = jnp.exp(teacher_all - teacher_peak[:, None])
    student_prob = score_exp_all / jnp.sum(score_exp_all, 1)[:, None]
    teacher_prob = teacher_exp / jnp.sum(teacher_exp, 1)[:, None]
    score_grad_all = LOSS_SCALE * (student_prob - teacher_prob) / query_count
    score_grad = jnp.take(score_grad_all, local_ids, axis=1)
    unit_grad_last = norm_backward(
        jnp.broadcast_to(w_score, normed_last.shape), unit_last, inverse_last, gain_last
    )
    grad_last = score_grad[..., None] * unit_grad_last
    grad_last_low = unit_grad_last.astype(jnp.bfloat16)
    grad_mixed_last = (
        mixed("qcd,fd->qcf", grad_last_low, w_out_last)
        .astype(jnp.bfloat16)
        .reshape(lists, local_cands, local_heads, HEAD_DIM)
    )
    own_dot = mixed("qche,qcthe->qcht", grad_mixed_last, last_vals)
    cross_dot = mixed("qche,qdhe->qchd", grad_mixed_last, cls_vals_last)
    centre = jnp.sum(own_last_prob * own_dot, -1, keepdims=True) + jnp.sum(
        cross_last_prob * cross_dot, -1, keepdims=True
    )
    own_slope = (own_last_prob * (own_dot - centre)).astype(jnp.bfloat16)
    cross_slope = (cross_last_prob * (cross_dot - centre)).astype(jnp.bfloat16)
    own_scale = score_grad[:, :, None, None]
    grad_query_last = (
        (
            (
                mixed("qcht,qcthe->qche", own_slope, last_keys)
                + mixed("qchd,qdhe->qche", cross_slope, cls_keys_last)
            )
            * score_scale
            * own_scale
        )
        .astype(jnp.bfloat16)
        .reshape(lists, local_cands, local_width)
    )
    own_key_grad = (
        mixed("qcht,qche->qcthe", own_slope, last_heads) * score_scale * own_scale[..., None]
    ).reshape(lists, local_cands, seq_len, local_width)
    own_val_grad = (
        mixed("qcht,qche->qcthe", own_last_weight, grad_mixed_last) * own_scale[..., None]
    ).reshape(lists, local_cands, seq_len, local_width)
    cls_key_terms = mixed("qchd,qche->qcdhe", cross_slope, last_heads) * score_scale
    cls_val_terms = mixed("qchd,qche->qcdhe", cross_last_weight, grad_mixed_last)
    cls_terms = jnp.concatenate(
        [
            cls_key_terms.reshape(lists, local_cands, cand_count, local_width),
            cls_val_terms.reshape(lists, local_cands, cand_count, local_width),
        ],
        -1,
    )
    count = lax.axis_size("cand")
    if count <= 8 and local_cands == 1:
        me = lax.axis_index("cand")
        block = cls_terms[:, 0]
        back_terms = lax.dynamic_slice_in_dim(block, me, 1, 1) * score_grad[:, :, None]
        for k in range(1, count):
            piece = lax.dynamic_slice_in_dim(block, (me + k) % count, 1, 1)
            moved = lax.ppermute(piece, "cand", [(j, (j + k) % count) for j in range(count)])
            source = lax.dynamic_slice_in_dim(score_grad_all, (me - k) % count, 1, 1)
            back_terms = back_terms + moved * source[:, :, None]
    else:
        back_terms = scatter_cand(jnp.sum(cls_terms * score_grad[:, :, None, None], 1), 1)
    back_keys = back_terms[..., :local_width]
    back_vals = back_terms[..., local_width:]
    first_cols = first_mask[None, None, :, None]
    key_grad = jnp.where(first_cols, own_key_grad + back_keys[:, :, None], own_key_grad).astype(
        jnp.bfloat16
    )
    val_grad = jnp.where(first_cols, own_val_grad + back_vals[:, :, None], own_val_grad).astype(
        jnp.bfloat16
    )
    other = swap_core(jnp.concatenate([key_grad, val_grad, grad_query_last[:, :, None]], 2))
    other_key = other[:, :, :seq_len]
    other_val = other[:, :, seq_len : 2 * seq_len]
    other_query = other[:, :, 2 * seq_len]
    summed_term = (
        mixed("qcsf,df->qcsd", key_grad, w_last[1])
        + mixed("qcsf,df->qcsd", val_grad, w_last[2])
        + mixed("qcsf,df->qcsd", other_key, other_last[1])
        + mixed("qcsf,df->qcsd", other_val, other_last[2])
    )
    query_term = mixed("qcf,df->qcd", grad_query_last, w_last[0]) + mixed(
        "qcf,df->qcd", other_query, other_last[0]
    )
    summed_term = jnp.where(first_cols, summed_term + query_term[:, :, None], summed_term)
    grad_hidden = jnp.where(first_cols, summed_term + grad_last[:, :, None], summed_term)
    grad_first = norm_backward(grad_hidden, unit_first, inverse_first, gain_first).astype(
        jnp.bfloat16
    )
    grad_mixed_first = (
        mixed("qcsd,fd->qcsf", grad_first, w_out_first).astype(jnp.bfloat16).reshape(head_shape)
    )
    own_dot_first = mixed("qcshe,qcthe->qchst", grad_mixed_first, first_vals)
    cross_dot_first = mixed("qche,qdhe->qchd", grad_mixed_first[:, :, 0], cls_vals)
    own_part = jnp.sum(own_prob * own_dot_first, -1)
    row_part = own_part[..., 0] + jnp.sum(cross_prob * cross_dot_first, -1)
    centre_first = jnp.where(first_mask, row_part[..., None], own_part)
    own_slope_first = (own_prob * (own_dot_first - centre_first[..., None])).astype(jnp.bfloat16)
    cross_slope_first = (cross_prob * (cross_dot_first - row_part[..., None])).astype(jnp.bfloat16)
    query_grad = mixed("qchst,qcthe->qcshe", own_slope_first, first_keys)
    query_cls = mixed("qchd,qdhe->qche", cross_slope_first, cls_keys)
    query_grad = jnp.where(
        first_mask[None, None, :, None, None], query_grad + query_cls[:, :, None], query_grad
    )
    query_grad = (
        (query_grad * score_scale)
        .astype(jnp.bfloat16)
        .reshape(lists, local_cands, seq_len, local_width)
    )
    key_first = (mixed("qchst,qcshe->qcthe", own_slope_first, first_query) * score_scale).reshape(
        lists, local_cands, seq_len, local_width
    )
    val_first = mixed("qchst,qcshe->qcthe", own_weight, grad_mixed_first).reshape(
        lists, local_cands, seq_len, local_width
    )
    cls_key_first = (
        mixed("qchd,qche->qdhe", cross_slope_first, first_query[:, :, 0]) * score_scale
    ).reshape(lists, cand_count, local_width)
    cls_val_first = mixed("qchd,qche->qdhe", cross_weight, grad_mixed_first[:, :, 0]).reshape(
        lists, cand_count, local_width
    )
    key_first = key_first.astype(jnp.bfloat16)
    val_first = val_first.astype(jnp.bfloat16)
    stacked = jnp.stack([query_grad, key_first, val_first], 3).reshape(row_count, 3, local_width)
    cross_rows = lists * cand_count
    cross_stacked = jnp.stack(
        [jnp.zeros_like(cls_key_first), cls_key_first, cls_val_first], 2
    ).astype(jnp.bfloat16)
    all_rows = jnp.concatenate(
        [stacked, cross_stacked.reshape(cross_rows, 3, local_width)], 0
    )
    all_tokens = jnp.concatenate(
        [tokens.reshape(row_count, model_width), cls_tokens.reshape(cross_rows, model_width)], 0
    )
    if not paired_lists:
        partial_grad = lax.psum_scatter(
            mixed("rd,rkf->dkf", all_tokens, all_rows).astype(jnp.bfloat16),
            "cand",
            scatter_dimension=0,
            tiled=True,
        )
        return sum_query(partial_grad).astype(jnp.float32)
    half = 3 * local_width // 2
    side = lax.axis_index("query")
    flat_rows = all_rows.reshape(all_rows.shape[0], 3 * local_width)
    cls_flat = cls_tokens.reshape(cross_rows, model_width)
    own_half = lax.dynamic_slice_in_dim(flat_rows, side * half, half, 1)
    given_half = lax.dynamic_slice_in_dim(flat_rows, (1 - side) * half, half, 1)
    sent = lax.ppermute(
        jnp.concatenate([given_half.reshape(-1), cls_flat.reshape(-1)]), "query", swap
    )
    other_half = sent[: given_half.size].reshape(given_half.shape)
    other_cls = sent[given_half.size :].reshape(cls_flat.shape)
    paired = (
        mixed("rd,rf->df", all_tokens, own_half)
        + mixed("rd,rf->df", other_tokens, other_half[:row_count])
        + mixed("rd,rf->df", other_cls, other_half[row_count:])
    )
    reduced = scatter_cand(paired.astype(jnp.bfloat16), 0, jnp.float32).astype(jnp.bfloat16)
    partner = lax.ppermute(reduced, "query", swap)
    joined = jnp.where(
        side == 0,
        jnp.concatenate([reduced, partner], 1),
        jnp.concatenate([partner, reduced], 1),
    )
    return joined.reshape(joined.shape[0], 3, local_width).astype(jnp.float32)


def solution(mesh):
    return jax.shard_map(
        local,
        mesh=mesh,
        in_specs=(
            P(("groups", "query"), "cand", None, None),
            P(("groups", "query"), "cand"),
            P(("groups", "query"), "cand"),
            P(None, None, "mp"),
            P("mp", None),
            P(),
            P(None, None, "mp"),
            P("mp", None),
            P(),
            P(),
        ),
        out_specs=P(("groups", "cand"), None, "mp"),
        check_vma=False,
    )
```

```python
import jax
import jax.numpy as jnp
from jax import lax
from jax.sharding import PartitionSpec as P

HEAD_DIM = 64


EPSILON = 1e-05
LOSS_SCALE = 1024.0
NEGATIVE = -1e30


def mixed(pattern, former, latter):
    return jnp.einsum(pattern, former, latter, preferred_element_type=jnp.float32)


def norm_forward(matrix, scales):
    center = matrix - jnp.mean(matrix, -1, keepdims=True)
    inverse = lax.rsqrt(jnp.mean(center * center, -1, keepdims=True) + EPSILON)
    normed = center * inverse
    return (normed * scales, normed, inverse)


def norm_backward(incoming, normed, inverse, scales):
    scaled = incoming * scales
    return inverse * (
        scaled
        - jnp.mean(scaled, -1, keepdims=True)
        - normed * jnp.mean(scaled * normed, -1, keepdims=True)
    )


def split_softmax(own_scores, cross_scores, first_mask):
    own_peak = jnp.max(own_scores, -1)
    row_peak = jnp.maximum(own_peak[..., 0], jnp.max(cross_scores, -1))
    peak = jnp.where(first_mask, row_peak[..., None], own_peak)
    own_exp = jnp.exp(own_scores - peak[..., None])
    cross_exp = jnp.exp(cross_scores - row_peak[..., None])
    own_totals = jnp.sum(own_exp, -1)
    row_totals = own_totals[..., 0] + jnp.sum(cross_exp, -1)
    totals = jnp.where(first_mask, row_totals[..., None], own_totals)
    return (own_exp / totals[..., None], cross_exp / row_totals[..., None])


def row_softmax(own_scores, cross_scores):
    peak = jnp.maximum(jnp.max(own_scores, -1), jnp.max(cross_scores, -1))[..., None]
    own_exp = jnp.exp(own_scores - peak)
    cross_exp = jnp.exp(cross_scores - peak)
    totals = (jnp.sum(own_exp, -1) + jnp.sum(cross_exp, -1))[..., None]
    return (own_exp / totals, cross_exp / totals)


def gather_cand(block, axis):
    count = lax.axis_size("cand")
    if count > 8:
        return lax.all_gather(block, "cand", axis=axis, tiled=True)
    me = lax.axis_index("cand")
    parts = [block] + [
        lax.ppermute(block, "cand", [(j, (j + k) % count) for j in range(count)])
        for k in range(1, count)
    ]
    ordered = jnp.take(jnp.stack(parts, 0), (me - jnp.arange(count)) % count, axis=0)
    ordered = jnp.moveaxis(ordered, 0, axis)
    shape = block.shape[:axis] + (count * block.shape[axis],) + block.shape[axis + 1 :]
    return ordered.reshape(shape)


def sum_cand(block):
    count = lax.axis_size("cand")
    if count > 8:
        return lax.psum(block, "cand")
    total = block
    for k in range(1, count):
        total = total + lax.ppermute(block, "cand", [(j, (j + k) % count) for j in range(count)])
    return total


def scatter_cand(block, axis, total_type=None):
    count = lax.axis_size("cand")
    if count > 8:
        return lax.psum_scatter(block, "cand", scatter_dimension=axis, tiled=True)
    total_type = total_type or block.dtype
    me = lax.axis_index("cand")
    width = block.shape[axis] // count
    total = lax.dynamic_slice_in_dim(block, me * width, width, axis).astype(total_type)
    for k in range(1, count):
        piece = lax.dynamic_slice_in_dim(block, ((me + k) % count) * width, width, axis)
        moved = lax.ppermute(piece, "cand", [(j, (j + k) % count) for j in range(count)])
        total = total + moved.astype(total_type)
    return total


def gather_mp(block, axis):
    if lax.axis_size("mp") != 2:
        return lax.all_gather(block, "mp", axis=axis, tiled=True)
    other = lax.ppermute(block, "mp", [(0, 1), (1, 0)])
    return jnp.where(
        lax.axis_index("mp") == 0,
        jnp.concatenate([block, other], axis),
        jnp.concatenate([other, block], axis),
    )


def sum_query(block):
    if lax.axis_size("query") != 2:
        return lax.psum(block, "query")
    other = lax.ppermute(block, "query", [(0, 1), (1, 0)])
    return block.astype(jnp.float32) + other.astype(jnp.float32)


def local(
    tokens,
    lengths,
    teacher,
    w_first,
    w_out_first,
    gain_first,
    w_last,
    w_out_last,
    gain_last,
    w_score,
):
    lists, local_cands, seq_len, model_width = tokens.shape
    local_width = w_first.shape[2]
    local_heads = local_width // HEAD_DIM
    cand_count = local_cands * lax.axis_size("cand")
    query_count = lists * lax.axis_size("query")
    score_scale = HEAD_DIM ** (-0.5)
    positions = jnp.arange(seq_len)
    first_mask = positions == 0
    own_valid = positions[None, None, :] < lengths[:, :, None]
    local_ids = lax.axis_index("cand") * local_cands + jnp.arange(local_cands)
    cross_valid = local_ids[:, None] != jnp.arange(cand_count)[None, :]
    head_shape = (lists, local_cands, seq_len, local_heads, HEAD_DIM)
    cls_shape = (lists, cand_count, local_heads, HEAD_DIM)
    out_first_full = gather_mp(w_out_first, 0)
    last_full = gather_mp(w_last, 2)
    out_last_full = gather_mp(w_out_last, 0)
    cls_and_teacher = gather_cand(
        jnp.concatenate([tokens[:, :, 0].astype(jnp.float32), teacher[..., None]], -1), 1
    )
    cls_tokens = cls_and_teacher[..., :model_width].astype(jnp.bfloat16)
    teacher_all = cls_and_teacher[..., model_width]
    row_count = lists * local_cands * seq_len
    swap = [(0, 1), (1, 0)]
    paired_lists = lax.axis_size("query") == 2
    if paired_lists:
        other_tokens = lax.ppermute(tokens.reshape(row_count, model_width), "query", swap)
    projected = mixed("qcsd,kdf->kqcsf", tokens, w_first).astype(jnp.bfloat16)
    cls_projected = mixed("qcd,kdf->kqcf", cls_tokens, w_first[1:]).astype(jnp.bfloat16)
    gathered_keys = cls_projected[0]
    gathered_vals = cls_projected[1]
    first_query = projected[0].reshape(head_shape)
    first_keys = projected[1].reshape(head_shape)
    first_vals = projected[2].reshape(head_shape)
    cls_keys = gathered_keys.reshape(cls_shape)
    cls_vals = gathered_vals.reshape(cls_shape)
    own_scores = mixed("qcshe,qcthe->qchst", first_query, first_keys) * score_scale
    own_scores = jnp.where(own_valid[:, :, None, None, :], own_scores, NEGATIVE)
    cross_scores = mixed("qche,qdhe->qchd", first_query[:, :, 0], cls_keys) * score_scale
    cross_scores = jnp.where(cross_valid[None, :, None, :], cross_scores, NEGATIVE)
    own_prob, cross_prob = split_softmax(own_scores, cross_scores, first_mask)
    own_weight = own_prob.astype(jnp.bfloat16)
    cross_weight = cross_prob.astype(jnp.bfloat16)
    attended = mixed("qchst,qcthe->qcshe", own_weight, first_vals)
    attended_cls = mixed("qchd,qdhe->qche", cross_weight, cls_vals)
    attended = jnp.where(
        first_mask[None, None, :, None, None], attended + attended_cls[:, :, None], attended
    )
    first_mixed = attended.reshape(lists, local_cands, seq_len, local_width).astype(jnp.bfloat16)
    first_joined = gather_mp(first_mixed, 3)
    residual_first = tokens.astype(jnp.float32) + mixed(
        "qcsf,fd->qcsd", first_joined, out_first_full
    )
    normed_first, unit_first, inverse_first = norm_forward(residual_first, gain_first)
    hidden = normed_first.astype(jnp.bfloat16)
    last_query = mixed("qcd,df->qcf", hidden[:, :, 0], w_last[0]).astype(jnp.bfloat16)
    last_kv = mixed("qcsd,kdf->kqcsf", hidden, w_last[1:]).astype(jnp.bfloat16)
    gathered_kv_last = gather_cand(
        jnp.concatenate([last_kv[0][:, :, 0], last_kv[1][:, :, 0]], -1), 1
    )
    gathered_keys_last = gathered_kv_last[..., :local_width]
    gathered_vals_last = gathered_kv_last[..., local_width:]
    last_heads = last_query.reshape(lists, local_cands, local_heads, HEAD_DIM)
    last_keys = last_kv[0].reshape(head_shape)
    last_vals = last_kv[1].reshape(head_shape)
    cls_keys_last = gathered_keys_last.reshape(cls_shape)
    cls_vals_last = gathered_vals_last.reshape(cls_shape)
    own_last = mixed("qche,qcthe->qcht", last_heads, last_keys) * score_scale
    own_last = jnp.where(own_valid[:, :, None, :], own_last, NEGATIVE)
    cross_last = mixed("qche,qdhe->qchd", last_heads, cls_keys_last) * score_scale
    cross_last = jnp.where(cross_valid[None, :, None, :], cross_last, NEGATIVE)
    own_last_prob, cross_last_prob = row_softmax(own_last, cross_last)
    own_last_weight = own_last_prob.astype(jnp.bfloat16)
    cross_last_weight = cross_last_prob.astype(jnp.bfloat16)
    attended_last = mixed("qcht,qcthe->qche", own_last_weight, last_vals) + mixed(
        "qchd,qdhe->qche", cross_last_weight, cls_vals_last
    )
    last_mixed = attended_last.reshape(lists, local_cands, local_width).astype(jnp.bfloat16)
    last_joined = gather_mp(last_mixed, 2)
    residual_last = hidden[:, :, 0].astype(jnp.float32) + mixed(
        "qcf,fd->qcd", last_joined, out_last_full
    )
    normed_last, unit_last, inverse_last = norm_forward(residual_last, gain_last)
    scores = jnp.einsum("qcd,d->qc", normed_last, w_score, precision=lax.Precision.HIGHEST)
    score_exp = jnp.exp(scores)
    teacher_peak = jnp.max(teacher_all, 1)
    teacher_exp = jnp.exp(teacher - teacher_peak[:, None])
    teacher_totals = jnp.sum(jnp.exp(teacher_all - teacher_peak[:, None]), 1)
    score_totals = sum_cand(jnp.sum(score_exp, 1))
    student_prob = score_exp / score_totals[:, None]
    teacher_prob = teacher_exp / teacher_totals[:, None]
    score_grad = LOSS_SCALE * (student_prob - teacher_prob) / query_count
    grad_last = norm_backward(score_grad[..., None] * w_score, unit_last, inverse_last, gain_last)
    grad_last_low = grad_last.astype(jnp.bfloat16)
    grad_mixed_last = (
        mixed("qcd,fd->qcf", grad_last_low, w_out_last)
        .astype(jnp.bfloat16)
        .reshape(lists, local_cands, local_heads, HEAD_DIM)
    )
    own_dot = mixed("qche,qcthe->qcht", grad_mixed_last, last_vals)
    cross_dot = mixed("qche,qdhe->qchd", grad_mixed_last, cls_vals_last)
    centre = jnp.sum(own_last_prob * own_dot, -1, keepdims=True) + jnp.sum(
        cross_last_prob * cross_dot, -1, keepdims=True
    )
    own_slope = (own_last_prob * (own_dot - centre)).astype(jnp.bfloat16)
    cross_slope = (cross_last_prob * (cross_dot - centre)).astype(jnp.bfloat16)
    grad_query_last = (
        (
            (
                mixed("qcht,qcthe->qche", own_slope, last_keys)
                + mixed("qchd,qdhe->qche", cross_slope, cls_keys_last)
            )
            * score_scale
        )
        .astype(jnp.bfloat16)
        .reshape(lists, local_cands, local_width)
    )
    own_key_grad = (mixed("qcht,qche->qcthe", own_slope, last_heads) * score_scale).reshape(
        lists, local_cands, seq_len, local_width
    )
    own_val_grad = mixed("qcht,qche->qcthe", own_last_weight, grad_mixed_last).reshape(
        lists, local_cands, seq_len, local_width
    )
    cls_key_terms = (mixed("qchd,qche->qdhe", cross_slope, last_heads) * score_scale).reshape(
        lists, cand_count, local_width
    )
    cls_val_terms = mixed("qchd,qche->qdhe", cross_last_weight, grad_mixed_last).reshape(
        lists, cand_count, local_width
    )
    back_terms = scatter_cand(jnp.concatenate([cls_key_terms, cls_val_terms], -1), 1)
    back_keys = back_terms[..., :local_width]
    back_vals = back_terms[..., local_width:]
    first_cols = first_mask[None, None, :, None]
    key_grad = jnp.where(first_cols, own_key_grad + back_keys[:, :, None], own_key_grad).astype(
        jnp.bfloat16
    )
    val_grad = jnp.where(first_cols, own_val_grad + back_vals[:, :, None], own_val_grad).astype(
        jnp.bfloat16
    )
    joined = gather_mp(jnp.concatenate([key_grad, val_grad, grad_query_last[:, :, None]], 2), 3)
    key_joined = joined[:, :, :seq_len]
    val_joined = joined[:, :, seq_len : 2 * seq_len]
    query_joined = joined[:, :, 2 * seq_len]
    summed_term = mixed("qcsf,df->qcsd", key_joined, last_full[1]) + mixed(
        "qcsf,df->qcsd", val_joined, last_full[2]
    )
    query_term = mixed("qcf,df->qcd", query_joined, last_full[0])
    summed_term = jnp.where(first_cols, summed_term + query_term[:, :, None], summed_term)
    grad_hidden = jnp.where(first_cols, summed_term + grad_last[:, :, None], summed_term)
    grad_first = norm_backward(grad_hidden, unit_first, inverse_first, gain_first).astype(
        jnp.bfloat16
    )
    grad_mixed_first = (
        mixed("qcsd,fd->qcsf", grad_first, w_out_first).astype(jnp.bfloat16).reshape(head_shape)
    )
    own_dot_first = mixed("qcshe,qcthe->qchst", grad_mixed_first, first_vals)
    cross_dot_first = mixed("qche,qdhe->qchd", grad_mixed_first[:, :, 0], cls_vals)
    own_part = jnp.sum(own_prob * own_dot_first, -1)
    row_part = own_part[..., 0] + jnp.sum(cross_prob * cross_dot_first, -1)
    centre_first = jnp.where(first_mask, row_part[..., None], own_part)
    own_slope_first = (own_prob * (own_dot_first - centre_first[..., None])).astype(jnp.bfloat16)
    cross_slope_first = (cross_prob * (cross_dot_first - row_part[..., None])).astype(jnp.bfloat16)
    query_grad = mixed("qchst,qcthe->qcshe", own_slope_first, first_keys)
    query_cls = mixed("qchd,qdhe->qche", cross_slope_first, cls_keys)
    query_grad = jnp.where(
        first_mask[None, None, :, None, None], query_grad + query_cls[:, :, None], query_grad
    )
    query_grad = (
        (query_grad * score_scale)
        .astype(jnp.bfloat16)
        .reshape(lists, local_cands, seq_len, local_width)
    )
    key_first = (mixed("qchst,qcshe->qcthe", own_slope_first, first_query) * score_scale).reshape(
        lists, local_cands, seq_len, local_width
    )
    val_first = mixed("qchst,qcshe->qcthe", own_weight, grad_mixed_first).reshape(
        lists, local_cands, seq_len, local_width
    )
    cls_key_first = (
        mixed("qchd,qche->qdhe", cross_slope_first, first_query[:, :, 0]) * score_scale
    ).reshape(lists, cand_count, local_width)
    cls_val_first = mixed("qchd,qche->qdhe", cross_weight, grad_mixed_first[:, :, 0]).reshape(
        lists, cand_count, local_width
    )
    key_first = key_first.astype(jnp.bfloat16)
    val_first = val_first.astype(jnp.bfloat16)
    stacked = jnp.stack([query_grad, key_first, val_first], 3).reshape(row_count, 3, local_width)
    cross_rows = lists * cand_count
    cross_stacked = jnp.stack(
        [jnp.zeros_like(cls_key_first), cls_key_first, cls_val_first], 2
    ).astype(jnp.bfloat16)
    all_rows = jnp.concatenate(
        [stacked, cross_stacked.reshape(cross_rows, 3, local_width)], 0
    )
    all_tokens = jnp.concatenate(
        [tokens.reshape(row_count, model_width), cls_tokens.reshape(cross_rows, model_width)], 0
    )
    if not paired_lists:
        partial_grad = lax.psum_scatter(
            mixed("rd,rkf->dkf", all_tokens, all_rows).astype(jnp.bfloat16),
            "cand",
            scatter_dimension=0,
            tiled=True,
        )
        return sum_query(partial_grad).astype(jnp.float32)
    half = 3 * local_width // 2
    side = lax.axis_index("query")
    flat_rows = all_rows.reshape(all_rows.shape[0], 3 * local_width)
    cls_flat = cls_tokens.reshape(cross_rows, model_width)
    own_half = lax.dynamic_slice_in_dim(flat_rows, side * half, half, 1)
    given_half = lax.dynamic_slice_in_dim(flat_rows, (1 - side) * half, half, 1)
    sent = lax.ppermute(
        jnp.concatenate([given_half.reshape(-1), cls_flat.reshape(-1)]), "query", swap
    )
    other_half = sent[: given_half.size].reshape(given_half.shape)
    other_cls = sent[given_half.size :].reshape(cls_flat.shape)
    paired = (
        mixed("rd,rf->df", all_tokens, own_half)
        + mixed("rd,rf->df", other_tokens, other_half[:row_count])
        + mixed("rd,rf->df", other_cls, other_half[row_count:])
    )
    reduced = scatter_cand(paired.astype(jnp.bfloat16), 0, jnp.float32).astype(jnp.bfloat16)
    partner = lax.ppermute(reduced, "query", swap)
    joined = jnp.where(
        side == 0,
        jnp.concatenate([reduced, partner], 1),
        jnp.concatenate([partner, reduced], 1),
    )
    return joined.reshape(joined.shape[0], 3, local_width).astype(jnp.float32)


def solution(mesh):
    return jax.shard_map(
        local,
        mesh=mesh,
        in_specs=(
            P(("groups", "query"), "cand", None, None),
            P(("groups", "query"), "cand"),
            P(("groups", "query"), "cand"),
            P(None, None, "mp"),
            P("mp", None),
            P(),
            P(None, None, "mp"),
            P("mp", None),
            P(),
            P(),
        ),
        out_specs=P(("groups", "cand"), None, "mp"),
        check_vma=False,
    )
```

```python
import jax
import jax.numpy as jnp
from jax import lax
from jax.sharding import PartitionSpec as P

HEAD_DIM = 64


EPSILON = 1e-05
LOSS_SCALE = 1024.0
NEGATIVE = -1e30


def mixed(pattern, former, latter):
    return jnp.einsum(pattern, former, latter, preferred_element_type=jnp.float32)


def norm_forward(matrix, scales):
    center = matrix - jnp.mean(matrix, -1, keepdims=True)
    inverse = lax.rsqrt(jnp.mean(center * center, -1, keepdims=True) + EPSILON)
    normed = center * inverse
    return (normed * scales, normed, inverse)


def norm_backward(incoming, normed, inverse, scales):
    scaled = incoming * scales
    return inverse * (
        scaled
        - jnp.mean(scaled, -1, keepdims=True)
        - normed * jnp.mean(scaled * normed, -1, keepdims=True)
    )


def split_softmax(own_scores, cross_scores, first_mask):
    own_peak = jnp.max(own_scores, -1)
    row_peak = jnp.maximum(own_peak[..., 0], jnp.max(cross_scores, -1))
    peak = jnp.where(first_mask, row_peak[..., None], own_peak)
    own_exp = jnp.exp(own_scores - peak[..., None])
    cross_exp = jnp.exp(cross_scores - row_peak[..., None])
    own_totals = jnp.sum(own_exp, -1)
    row_totals = own_totals[..., 0] + jnp.sum(cross_exp, -1)
    totals = jnp.where(first_mask, row_totals[..., None], own_totals)
    return (own_exp / totals[..., None], cross_exp / row_totals[..., None])


def row_softmax(own_scores, cross_scores):
    peak = jnp.maximum(jnp.max(own_scores, -1), jnp.max(cross_scores, -1))[..., None]
    own_exp = jnp.exp(own_scores - peak)
    cross_exp = jnp.exp(cross_scores - peak)
    totals = (jnp.sum(own_exp, -1) + jnp.sum(cross_exp, -1))[..., None]
    return (own_exp / totals, cross_exp / totals)


def gather_cand(block, axis):
    count = lax.axis_size("cand")
    if count > 8:
        return lax.all_gather(block, "cand", axis=axis, tiled=True)
    me = lax.axis_index("cand")
    parts = [block] + [
        lax.ppermute(block, "cand", [(j, (j + k) % count) for j in range(count)])
        for k in range(1, count)
    ]
    ordered = jnp.take(jnp.stack(parts, 0), (me - jnp.arange(count)) % count, axis=0)
    ordered = jnp.moveaxis(ordered, 0, axis)
    shape = block.shape[:axis] + (count * block.shape[axis],) + block.shape[axis + 1 :]
    return ordered.reshape(shape)


def sum_cand(block):
    count = lax.axis_size("cand")
    if count > 8:
        return lax.psum(block, "cand")
    total = block
    for k in range(1, count):
        total = total + lax.ppermute(block, "cand", [(j, (j + k) % count) for j in range(count)])
    return total


def scatter_cand(block, axis, total_type=None):
    count = lax.axis_size("cand")
    if count > 8:
        return lax.psum_scatter(block, "cand", scatter_dimension=axis, tiled=True)
    total_type = total_type or block.dtype
    me = lax.axis_index("cand")
    width = block.shape[axis] // count
    total = lax.dynamic_slice_in_dim(block, me * width, width, axis).astype(total_type)
    for k in range(1, count):
        piece = lax.dynamic_slice_in_dim(block, ((me + k) % count) * width, width, axis)
        moved = lax.ppermute(piece, "cand", [(j, (j + k) % count) for j in range(count)])
        total = total + moved.astype(total_type)
    return total


def sum_mp(block):
    if lax.axis_size("mp") != 2:
        return lax.psum(block, "mp")
    return block + lax.ppermute(block, "mp", [(0, 1), (1, 0)])


def sum_query(block):
    if lax.axis_size("query") != 2:
        return lax.psum(block, "query")
    other = lax.ppermute(block, "query", [(0, 1), (1, 0)])
    return block.astype(jnp.float32) + other.astype(jnp.float32)


def local(
    tokens,
    lengths,
    teacher,
    w_first,
    w_out_first,
    gain_first,
    w_last,
    w_out_last,
    gain_last,
    w_score,
):
    lists, local_cands, seq_len, model_width = tokens.shape
    local_width = w_first.shape[2]
    local_heads = local_width // HEAD_DIM
    cand_count = local_cands * lax.axis_size("cand")
    query_count = lists * lax.axis_size("query")
    score_scale = HEAD_DIM ** (-0.5)
    positions = jnp.arange(seq_len)
    first_mask = positions == 0
    own_valid = positions[None, None, :] < lengths[:, :, None]
    local_ids = lax.axis_index("cand") * local_cands + jnp.arange(local_cands)
    cross_valid = local_ids[:, None] != jnp.arange(cand_count)[None, :]
    head_shape = (lists, local_cands, seq_len, local_heads, HEAD_DIM)
    cls_shape = (lists, cand_count, local_heads, HEAD_DIM)
    cls_and_teacher = gather_cand(
        jnp.concatenate([tokens[:, :, 0].astype(jnp.float32), teacher[..., None]], -1), 1
    )
    cls_tokens = cls_and_teacher[..., :model_width].astype(jnp.bfloat16)
    teacher_all = cls_and_teacher[..., model_width]
    row_count = lists * local_cands * seq_len
    swap = [(0, 1), (1, 0)]
    paired_lists = lax.axis_size("query") == 2
    if paired_lists:
        other_tokens = lax.ppermute(tokens.reshape(row_count, model_width), "query", swap)
    projected = mixed("qcsd,kdf->kqcsf", tokens, w_first).astype(jnp.bfloat16)
    cls_projected = mixed("qcd,kdf->kqcf", cls_tokens, w_first[1:]).astype(jnp.bfloat16)
    gathered_keys = cls_projected[0]
    gathered_vals = cls_projected[1]
    first_query = projected[0].reshape(head_shape)
    first_keys = projected[1].reshape(head_shape)
    first_vals = projected[2].reshape(head_shape)
    cls_keys = gathered_keys.reshape(cls_shape)
    cls_vals = gathered_vals.reshape(cls_shape)
    own_scores = mixed("qcshe,qcthe->qchst", first_query, first_keys) * score_scale
    own_scores = jnp.where(own_valid[:, :, None, None, :], own_scores, NEGATIVE)
    cross_scores = mixed("qche,qdhe->qchd", first_query[:, :, 0], cls_keys) * score_scale
    cross_scores = jnp.where(cross_valid[None, :, None, :], cross_scores, NEGATIVE)
    own_prob, cross_prob = split_softmax(own_scores, cross_scores, first_mask)
    own_weight = own_prob.astype(jnp.bfloat16)
    cross_weight = cross_prob.astype(jnp.bfloat16)
    attended = mixed("qchst,qcthe->qcshe", own_weight, first_vals)
    attended_cls = mixed("qchd,qdhe->qche", cross_weight, cls_vals)
    attended = jnp.where(
        first_mask[None, None, :, None, None], attended + attended_cls[:, :, None], attended
    )
    first_mixed = attended.reshape(lists, local_cands, seq_len, local_width).astype(jnp.bfloat16)
    residual_first = tokens.astype(jnp.float32) + sum_mp(
        mixed("qcsf,fd->qcsd", first_mixed, w_out_first)
    )
    normed_first, unit_first, inverse_first = norm_forward(residual_first, gain_first)
    hidden = normed_first.astype(jnp.bfloat16)
    last_query = mixed("qcd,df->qcf", hidden[:, :, 0], w_last[0]).astype(jnp.bfloat16)
    last_kv = mixed("qcsd,kdf->kqcsf", hidden, w_last[1:]).astype(jnp.bfloat16)
    gathered_kv_last = gather_cand(
        jnp.concatenate([last_kv[0][:, :, 0], last_kv[1][:, :, 0]], -1), 1
    )
    gathered_keys_last = gathered_kv_last[..., :local_width]
    gathered_vals_last = gathered_kv_last[..., local_width:]
    last_heads = last_query.reshape(lists, local_cands, local_heads, HEAD_DIM)
    last_keys = last_kv[0].reshape(head_shape)
    last_vals = last_kv[1].reshape(head_shape)
    cls_keys_last = gathered_keys_last.reshape(cls_shape)
    cls_vals_last = gathered_vals_last.reshape(cls_shape)
    own_last = mixed("qche,qcthe->qcht", last_heads, last_keys) * score_scale
    own_last = jnp.where(own_valid[:, :, None, :], own_last, NEGATIVE)
    cross_last = mixed("qche,qdhe->qchd", last_heads, cls_keys_last) * score_scale
    cross_last = jnp.where(cross_valid[None, :, None, :], cross_last, NEGATIVE)
    own_last_prob, cross_last_prob = row_softmax(own_last, cross_last)
    own_last_weight = own_last_prob.astype(jnp.bfloat16)
    cross_last_weight = cross_last_prob.astype(jnp.bfloat16)
    attended_last = mixed("qcht,qcthe->qche", own_last_weight, last_vals) + mixed(
        "qchd,qdhe->qche", cross_last_weight, cls_vals_last
    )
    last_mixed = attended_last.reshape(lists, local_cands, local_width).astype(jnp.bfloat16)
    residual_last = hidden[:, :, 0].astype(jnp.float32) + sum_mp(
        mixed("qcf,fd->qcd", last_mixed, w_out_last)
    )
    normed_last, unit_last, inverse_last = norm_forward(residual_last, gain_last)
    scores = jnp.einsum("qcd,d->qc", normed_last, w_score, precision=lax.Precision.HIGHEST)
    score_exp = jnp.exp(scores)
    teacher_peak = jnp.max(teacher_all, 1)
    teacher_exp = jnp.exp(teacher - teacher_peak[:, None])
    teacher_totals = jnp.sum(jnp.exp(teacher_all - teacher_peak[:, None]), 1)
    score_totals = sum_cand(jnp.sum(score_exp, 1))
    student_prob = score_exp / score_totals[:, None]
    teacher_prob = teacher_exp / teacher_totals[:, None]
    score_grad = LOSS_SCALE * (student_prob - teacher_prob) / query_count
    grad_last = norm_backward(score_grad[..., None] * w_score, unit_last, inverse_last, gain_last)
    grad_last_low = grad_last.astype(jnp.bfloat16)
    grad_mixed_last = (
        mixed("qcd,fd->qcf", grad_last_low, w_out_last)
        .astype(jnp.bfloat16)
        .reshape(lists, local_cands, local_heads, HEAD_DIM)
    )
    own_dot = mixed("qche,qcthe->qcht", grad_mixed_last, last_vals)
    cross_dot = mixed("qche,qdhe->qchd", grad_mixed_last, cls_vals_last)
    centre = jnp.sum(own_last_prob * own_dot, -1, keepdims=True) + jnp.sum(
        cross_last_prob * cross_dot, -1, keepdims=True
    )
    own_slope = (own_last_prob * (own_dot - centre)).astype(jnp.bfloat16)
    cross_slope = (cross_last_prob * (cross_dot - centre)).astype(jnp.bfloat16)
    grad_query_last = (
        (
            (
                mixed("qcht,qcthe->qche", own_slope, last_keys)
                + mixed("qchd,qdhe->qche", cross_slope, cls_keys_last)
            )
            * score_scale
        )
        .astype(jnp.bfloat16)
        .reshape(lists, local_cands, local_width)
    )
    own_key_grad = (mixed("qcht,qche->qcthe", own_slope, last_heads) * score_scale).reshape(
        lists, local_cands, seq_len, local_width
    )
    own_val_grad = mixed("qcht,qche->qcthe", own_last_weight, grad_mixed_last).reshape(
        lists, local_cands, seq_len, local_width
    )
    cls_key_terms = (mixed("qchd,qche->qdhe", cross_slope, last_heads) * score_scale).reshape(
        lists, cand_count, local_width
    )
    cls_val_terms = mixed("qchd,qche->qdhe", cross_last_weight, grad_mixed_last).reshape(
        lists, cand_count, local_width
    )
    back_terms = scatter_cand(jnp.concatenate([cls_key_terms, cls_val_terms], -1), 1)
    back_keys = back_terms[..., :local_width]
    back_vals = back_terms[..., local_width:]
    first_cols = first_mask[None, None, :, None]
    key_grad = jnp.where(first_cols, own_key_grad + back_keys[:, :, None], own_key_grad).astype(
        jnp.bfloat16
    )
    val_grad = jnp.where(first_cols, own_val_grad + back_vals[:, :, None], own_val_grad).astype(
        jnp.bfloat16
    )
    partial_term = mixed("qcsf,df->qcsd", key_grad, w_last[1]) + mixed(
        "qcsf,df->qcsd", val_grad, w_last[2]
    )
    query_term = mixed("qcf,df->qcd", grad_query_last, w_last[0])
    partial_term = jnp.where(first_cols, partial_term + query_term[:, :, None], partial_term)
    summed_term = sum_mp(partial_term)
    grad_hidden = jnp.where(first_cols, summed_term + grad_last[:, :, None], summed_term)
    grad_first = norm_backward(grad_hidden, unit_first, inverse_first, gain_first).astype(
        jnp.bfloat16
    )
    grad_mixed_first = (
        mixed("qcsd,fd->qcsf", grad_first, w_out_first).astype(jnp.bfloat16).reshape(head_shape)
    )
    own_dot_first = mixed("qcshe,qcthe->qchst", grad_mixed_first, first_vals)
    cross_dot_first = mixed("qche,qdhe->qchd", grad_mixed_first[:, :, 0], cls_vals)
    own_part = jnp.sum(own_prob * own_dot_first, -1)
    row_part = own_part[..., 0] + jnp.sum(cross_prob * cross_dot_first, -1)
    centre_first = jnp.where(first_mask, row_part[..., None], own_part)
    own_slope_first = (own_prob * (own_dot_first - centre_first[..., None])).astype(jnp.bfloat16)
    cross_slope_first = (cross_prob * (cross_dot_first - row_part[..., None])).astype(jnp.bfloat16)
    query_grad = mixed("qchst,qcthe->qcshe", own_slope_first, first_keys)
    query_cls = mixed("qchd,qdhe->qche", cross_slope_first, cls_keys)
    query_grad = jnp.where(
        first_mask[None, None, :, None, None], query_grad + query_cls[:, :, None], query_grad
    )
    query_grad = (
        (query_grad * score_scale)
        .astype(jnp.bfloat16)
        .reshape(lists, local_cands, seq_len, local_width)
    )
    key_first = (mixed("qchst,qcshe->qcthe", own_slope_first, first_query) * score_scale).reshape(
        lists, local_cands, seq_len, local_width
    )
    val_first = mixed("qchst,qcshe->qcthe", own_weight, grad_mixed_first).reshape(
        lists, local_cands, seq_len, local_width
    )
    cls_key_first = (
        mixed("qchd,qche->qdhe", cross_slope_first, first_query[:, :, 0]) * score_scale
    ).reshape(lists, cand_count, local_width)
    cls_val_first = mixed("qchd,qche->qdhe", cross_weight, grad_mixed_first[:, :, 0]).reshape(
        lists, cand_count, local_width
    )
    key_first = key_first.astype(jnp.bfloat16)
    val_first = val_first.astype(jnp.bfloat16)
    stacked = jnp.stack([query_grad, key_first, val_first], 3).reshape(row_count, 3, local_width)
    cross_rows = lists * cand_count
    cross_stacked = jnp.stack(
        [jnp.zeros_like(cls_key_first), cls_key_first, cls_val_first], 2
    ).astype(jnp.bfloat16)
    all_rows = jnp.concatenate(
        [stacked, cross_stacked.reshape(cross_rows, 3, local_width)], 0
    )
    all_tokens = jnp.concatenate(
        [tokens.reshape(row_count, model_width), cls_tokens.reshape(cross_rows, model_width)], 0
    )
    if not paired_lists:
        partial_grad = lax.psum_scatter(
            mixed("rd,rkf->dkf", all_tokens, all_rows).astype(jnp.bfloat16),
            "cand",
            scatter_dimension=0,
            tiled=True,
        )
        return sum_query(partial_grad).astype(jnp.float32)
    half = 3 * local_width // 2
    side = lax.axis_index("query")
    flat_rows = all_rows.reshape(all_rows.shape[0], 3 * local_width)
    cls_flat = cls_tokens.reshape(cross_rows, model_width)
    own_half = lax.dynamic_slice_in_dim(flat_rows, side * half, half, 1)
    given_half = lax.dynamic_slice_in_dim(flat_rows, (1 - side) * half, half, 1)
    sent = lax.ppermute(
        jnp.concatenate([given_half.reshape(-1), cls_flat.reshape(-1)]), "query", swap
    )
    other_half = sent[: given_half.size].reshape(given_half.shape)
    other_cls = sent[given_half.size :].reshape(cls_flat.shape)
    paired = (
        mixed("rd,rf->df", all_tokens, own_half)
        + mixed("rd,rf->df", other_tokens, other_half[:row_count])
        + mixed("rd,rf->df", other_cls, other_half[row_count:])
    )
    reduced = scatter_cand(paired.astype(jnp.bfloat16), 0, jnp.float32).astype(jnp.bfloat16)
    partner = lax.ppermute(reduced, "query", swap)
    joined = jnp.where(
        side == 0,
        jnp.concatenate([reduced, partner], 1),
        jnp.concatenate([partner, reduced], 1),
    )
    return joined.reshape(joined.shape[0], 3, local_width).astype(jnp.float32)


def solution(mesh):
    return jax.shard_map(
        local,
        mesh=mesh,
        in_specs=(
            P(("groups", "query"), "cand", None, None),
            P(("groups", "query"), "cand"),
            P(("groups", "query"), "cand"),
            P(None, None, "mp"),
            P("mp", None),
            P(),
            P(None, None, "mp"),
            P("mp", None),
            P(),
            P(),
        ),
        out_specs=P(("groups", "cand"), None, "mp"),
        check_vma=False,
    )
```

```python
import jax
import jax.numpy as jnp
from jax import lax
from jax.sharding import PartitionSpec as P

HEAD_DIM = 64


EPSILON = 1e-05
LOSS_SCALE = 1024.0
NEGATIVE = -1e30


def mixed(pattern, former, latter):
    return jnp.einsum(pattern, former, latter, preferred_element_type=jnp.float32)


def norm_forward(matrix, scales):
    center = matrix - jnp.mean(matrix, -1, keepdims=True)
    inverse = lax.rsqrt(jnp.mean(center * center, -1, keepdims=True) + EPSILON)
    normed = center * inverse
    return (normed * scales, normed, inverse)


def norm_backward(incoming, normed, inverse, scales):
    scaled = incoming * scales
    return inverse * (
        scaled
        - jnp.mean(scaled, -1, keepdims=True)
        - normed * jnp.mean(scaled * normed, -1, keepdims=True)
    )


def split_softmax(own_scores, cross_scores, first_mask):
    own_peak = jnp.max(own_scores, -1)
    row_peak = jnp.maximum(own_peak[..., 0], jnp.max(cross_scores, -1))
    peak = jnp.where(first_mask, row_peak[..., None], own_peak)
    own_exp = jnp.exp(own_scores - peak[..., None])
    cross_exp = jnp.exp(cross_scores - row_peak[..., None])
    own_totals = jnp.sum(own_exp, -1)
    row_totals = own_totals[..., 0] + jnp.sum(cross_exp, -1)
    totals = jnp.where(first_mask, row_totals[..., None], own_totals)
    return (own_exp / totals[..., None], cross_exp / row_totals[..., None])


def row_softmax(own_scores, cross_scores):
    peak = jnp.maximum(jnp.max(own_scores, -1), jnp.max(cross_scores, -1))[..., None]
    own_exp = jnp.exp(own_scores - peak)
    cross_exp = jnp.exp(cross_scores - peak)
    totals = (jnp.sum(own_exp, -1) + jnp.sum(cross_exp, -1))[..., None]
    return (own_exp / totals, cross_exp / totals)


def shift_order(count):
    return sorted(range(1, count), key=lambda k: min(k, count - k), reverse=True)


def gather_cand(block, axis):
    count = lax.axis_size("cand")
    if count > 8:
        return lax.all_gather(block, "cand", axis=axis, tiled=True)
    me = lax.axis_index("cand")
    moved = {
        k: lax.ppermute(block, "cand", [(j, (j + k) % count) for j in range(count)])
        for k in shift_order(count)
    }
    parts = [block] + [moved[k] for k in range(1, count)]
    ordered = jnp.take(jnp.stack(parts, 0), (me - jnp.arange(count)) % count, axis=0)
    ordered = jnp.moveaxis(ordered, 0, axis)
    shape = block.shape[:axis] + (count * block.shape[axis],) + block.shape[axis + 1 :]
    return ordered.reshape(shape)


def sum_cand(block):
    count = lax.axis_size("cand")
    if count > 8:
        return lax.psum(block, "cand")
    total = block
    for k in shift_order(count):
        total = total + lax.ppermute(block, "cand", [(j, (j + k) % count) for j in range(count)])
    return total


def scatter_cand(block, axis, total_type=None):
    count = lax.axis_size("cand")
    if count > 8:
        return lax.psum_scatter(block, "cand", scatter_dimension=axis, tiled=True)
    total_type = total_type or block.dtype
    me = lax.axis_index("cand")
    width = block.shape[axis] // count
    total = lax.dynamic_slice_in_dim(block, me * width, width, axis).astype(total_type)
    for k in shift_order(count):
        piece = lax.dynamic_slice_in_dim(block, ((me + k) % count) * width, width, axis)
        moved = lax.ppermute(piece, "cand", [(j, (j + k) % count) for j in range(count)])
        total = total + moved.astype(total_type)
    return total


def gather_mp(block, axis):
    if lax.axis_size("mp") != 2:
        return lax.all_gather(block, "mp", axis=axis, tiled=True)
    other = lax.ppermute(block, "mp", [(0, 1), (1, 0)])
    return jnp.where(
        lax.axis_index("mp") == 0,
        jnp.concatenate([block, other], axis),
        jnp.concatenate([other, block], axis),
    )


def sum_query(block):
    if lax.axis_size("query") != 2:
        return lax.psum(block, "query")
    other = lax.ppermute(block, "query", [(0, 1), (1, 0)])
    return block.astype(jnp.float32) + other.astype(jnp.float32)


def local(
    tokens,
    lengths,
    teacher,
    w_first,
    w_out_first,
    gain_first,
    w_last,
    w_out_last,
    gain_last,
    w_score,
):
    lists, local_cands, seq_len, model_width = tokens.shape
    local_width = w_first.shape[2]
    local_heads = local_width // HEAD_DIM
    cand_count = local_cands * lax.axis_size("cand")
    query_count = lists * lax.axis_size("query")
    score_scale = HEAD_DIM ** (-0.5)
    positions = jnp.arange(seq_len)
    first_mask = positions == 0
    own_valid = positions[None, None, :] < lengths[:, :, None]
    local_ids = lax.axis_index("cand") * local_cands + jnp.arange(local_cands)
    cross_valid = local_ids[:, None] != jnp.arange(cand_count)[None, :]
    head_shape = (lists, local_cands, seq_len, local_heads, HEAD_DIM)
    cls_shape = (lists, cand_count, local_heads, HEAD_DIM)
    out_first_full = gather_mp(w_out_first, 0)
    last_full = gather_mp(w_last, 2)
    out_last_full = gather_mp(w_out_last, 0)
    cls_and_teacher = gather_cand(
        jnp.concatenate([tokens[:, :, 0].astype(jnp.float32), teacher[..., None]], -1), 1
    )
    cls_tokens = cls_and_teacher[..., :model_width].astype(jnp.bfloat16)
    teacher_all = cls_and_teacher[..., model_width]
    row_count = lists * local_cands * seq_len
    swap = [(0, 1), (1, 0)]
    paired_lists = lax.axis_size("query") == 2
    if paired_lists:
        other_tokens = lax.ppermute(tokens.reshape(row_count, model_width), "query", swap)
    projected = mixed("qcsd,kdf->kqcsf", tokens, w_first).astype(jnp.bfloat16)
    cls_projected = mixed("qcd,kdf->kqcf", cls_tokens, w_first[1:]).astype(jnp.bfloat16)
    gathered_keys = cls_projected[0]
    gathered_vals = cls_projected[1]
    first_query = projected[0].reshape(head_shape)
    first_keys = projected[1].reshape(head_shape)
    first_vals = projected[2].reshape(head_shape)
    cls_keys = gathered_keys.reshape(cls_shape)
    cls_vals = gathered_vals.reshape(cls_shape)
    own_scores = mixed("qcshe,qcthe->qchst", first_query, first_keys) * score_scale
    own_scores = jnp.where(own_valid[:, :, None, None, :], own_scores, NEGATIVE)
    cross_scores = mixed("qche,qdhe->qchd", first_query[:, :, 0], cls_keys) * score_scale
    cross_scores = jnp.where(cross_valid[None, :, None, :], cross_scores, NEGATIVE)
    own_prob, cross_prob = split_softmax(own_scores, cross_scores, first_mask)
    own_weight = own_prob.astype(jnp.bfloat16)
    cross_weight = cross_prob.astype(jnp.bfloat16)
    attended = mixed("qchst,qcthe->qcshe", own_weight, first_vals)
    attended_cls = mixed("qchd,qdhe->qche", cross_weight, cls_vals)
    attended = jnp.where(
        first_mask[None, None, :, None, None], attended + attended_cls[:, :, None], attended
    )
    first_mixed = attended.reshape(lists, local_cands, seq_len, local_width).astype(jnp.bfloat16)
    first_joined = lax.all_gather(first_mixed, "mp", axis=3, tiled=True)
    residual_first = tokens.astype(jnp.float32) + mixed(
        "qcsf,fd->qcsd", first_joined, out_first_full
    )
    normed_first, unit_first, inverse_first = norm_forward(residual_first, gain_first)
    hidden = normed_first.astype(jnp.bfloat16)
    last_query = mixed("qcd,df->qcf", hidden[:, :, 0], w_last[0]).astype(jnp.bfloat16)
    last_kv = mixed("qcsd,kdf->kqcsf", hidden, w_last[1:]).astype(jnp.bfloat16)
    gathered_kv_last = gather_cand(
        jnp.concatenate([last_kv[0][:, :, 0], last_kv[1][:, :, 0]], -1), 1
    )
    gathered_keys_last = gathered_kv_last[..., :local_width]
    gathered_vals_last = gathered_kv_last[..., local_width:]
    last_heads = last_query.reshape(lists, local_cands, local_heads, HEAD_DIM)
    last_keys = last_kv[0].reshape(head_shape)
    last_vals = last_kv[1].reshape(head_shape)
    cls_keys_last = gathered_keys_last.reshape(cls_shape)
    cls_vals_last = gathered_vals_last.reshape(cls_shape)
    own_last = mixed("qche,qcthe->qcht", last_heads, last_keys) * score_scale
    own_last = jnp.where(own_valid[:, :, None, :], own_last, NEGATIVE)
    cross_last = mixed("qche,qdhe->qchd", last_heads, cls_keys_last) * score_scale
    cross_last = jnp.where(cross_valid[None, :, None, :], cross_last, NEGATIVE)
    own_last_prob, cross_last_prob = row_softmax(own_last, cross_last)
    own_last_weight = own_last_prob.astype(jnp.bfloat16)
    cross_last_weight = cross_last_prob.astype(jnp.bfloat16)
    attended_last = mixed("qcht,qcthe->qche", own_last_weight, last_vals) + mixed(
        "qchd,qdhe->qche", cross_last_weight, cls_vals_last
    )
    last_mixed = attended_last.reshape(lists, local_cands, local_width).astype(jnp.bfloat16)
    last_joined = lax.all_gather(last_mixed, "mp", axis=2, tiled=True)
    residual_last = hidden[:, :, 0].astype(jnp.float32) + mixed(
        "qcf,fd->qcd", last_joined, out_last_full
    )
    normed_last, unit_last, inverse_last = norm_forward(residual_last, gain_last)
    scores = jnp.einsum("qcd,d->qc", normed_last, w_score, precision=lax.Precision.HIGHEST)
    score_exp = jnp.exp(scores)
    teacher_peak = jnp.max(teacher_all, 1)
    teacher_exp = jnp.exp(teacher - teacher_peak[:, None])
    teacher_totals = jnp.sum(jnp.exp(teacher_all - teacher_peak[:, None]), 1)
    score_totals = sum_cand(jnp.sum(score_exp, 1))
    student_prob = score_exp / score_totals[:, None]
    teacher_prob = teacher_exp / teacher_totals[:, None]
    score_grad = LOSS_SCALE * (student_prob - teacher_prob) / query_count
    grad_last = norm_backward(score_grad[..., None] * w_score, unit_last, inverse_last, gain_last)
    grad_last_low = grad_last.astype(jnp.bfloat16)
    grad_mixed_last = (
        mixed("qcd,fd->qcf", grad_last_low, w_out_last)
        .astype(jnp.bfloat16)
        .reshape(lists, local_cands, local_heads, HEAD_DIM)
    )
    own_dot = mixed("qche,qcthe->qcht", grad_mixed_last, last_vals)
    cross_dot = mixed("qche,qdhe->qchd", grad_mixed_last, cls_vals_last)
    centre = jnp.sum(own_last_prob * own_dot, -1, keepdims=True) + jnp.sum(
        cross_last_prob * cross_dot, -1, keepdims=True
    )
    own_slope = (own_last_prob * (own_dot - centre)).astype(jnp.bfloat16)
    cross_slope = (cross_last_prob * (cross_dot - centre)).astype(jnp.bfloat16)
    grad_query_last = (
        (
            (
                mixed("qcht,qcthe->qche", own_slope, last_keys)
                + mixed("qchd,qdhe->qche", cross_slope, cls_keys_last)
            )
            * score_scale
        )
        .astype(jnp.bfloat16)
        .reshape(lists, local_cands, local_width)
    )
    own_key_grad = (mixed("qcht,qche->qcthe", own_slope, last_heads) * score_scale).reshape(
        lists, local_cands, seq_len, local_width
    )
    own_val_grad = mixed("qcht,qche->qcthe", own_last_weight, grad_mixed_last).reshape(
        lists, local_cands, seq_len, local_width
    )
    cls_key_terms = (mixed("qchd,qche->qdhe", cross_slope, last_heads) * score_scale).reshape(
        lists, cand_count, local_width
    )
    cls_val_terms = mixed("qchd,qche->qdhe", cross_last_weight, grad_mixed_last).reshape(
        lists, cand_count, local_width
    )
    back_terms = scatter_cand(jnp.concatenate([cls_key_terms, cls_val_terms], -1), 1)
    back_keys = back_terms[..., :local_width]
    back_vals = back_terms[..., local_width:]
    first_cols = first_mask[None, None, :, None]
    key_grad = jnp.where(first_cols, own_key_grad + back_keys[:, :, None], own_key_grad).astype(
        jnp.bfloat16
    )
    val_grad = jnp.where(first_cols, own_val_grad + back_vals[:, :, None], own_val_grad).astype(
        jnp.bfloat16
    )
    joined = lax.all_gather(
        jnp.concatenate([key_grad, val_grad, grad_query_last[:, :, None]], 2),
        "mp",
        axis=3,
        tiled=True,
    )
    key_joined = joined[:, :, :seq_len]
    val_joined = joined[:, :, seq_len : 2 * seq_len]
    query_joined = joined[:, :, 2 * seq_len]
    summed_term = mixed("qcsf,df->qcsd", key_joined, last_full[1]) + mixed(
        "qcsf,df->qcsd", val_joined, last_full[2]
    )
    query_term = mixed("qcf,df->qcd", query_joined, last_full[0])
    summed_term = jnp.where(first_cols, summed_term + query_term[:, :, None], summed_term)
    grad_hidden = jnp.where(first_cols, summed_term + grad_last[:, :, None], summed_term)
    grad_first = norm_backward(grad_hidden, unit_first, inverse_first, gain_first).astype(
        jnp.bfloat16
    )
    grad_mixed_first = (
        mixed("qcsd,fd->qcsf", grad_first, w_out_first).astype(jnp.bfloat16).reshape(head_shape)
    )
    own_dot_first = mixed("qcshe,qcthe->qchst", grad_mixed_first, first_vals)
    cross_dot_first = mixed("qche,qdhe->qchd", grad_mixed_first[:, :, 0], cls_vals)
    own_part = jnp.sum(own_prob * own_dot_first, -1)
    row_part = own_part[..., 0] + jnp.sum(cross_prob * cross_dot_first, -1)
    centre_first = jnp.where(first_mask, row_part[..., None], own_part)
    own_slope_first = (own_prob * (own_dot_first - centre_first[..., None])).astype(jnp.bfloat16)
    cross_slope_first = (cross_prob * (cross_dot_first - row_part[..., None])).astype(jnp.bfloat16)
    query_grad = mixed("qchst,qcthe->qcshe", own_slope_first, first_keys)
    query_cls = mixed("qchd,qdhe->qche", cross_slope_first, cls_keys)
    query_grad = jnp.where(
        first_mask[None, None, :, None, None], query_grad + query_cls[:, :, None], query_grad
    )
    query_grad = (
        (query_grad * score_scale)
        .astype(jnp.bfloat16)
        .reshape(lists, local_cands, seq_len, local_width)
    )
    key_first = (mixed("qchst,qcshe->qcthe", own_slope_first, first_query) * score_scale).reshape(
        lists, local_cands, seq_len, local_width
    )
    val_first = mixed("qchst,qcshe->qcthe", own_weight, grad_mixed_first).reshape(
        lists, local_cands, seq_len, local_width
    )
    cls_key_first = (
        mixed("qchd,qche->qdhe", cross_slope_first, first_query[:, :, 0]) * score_scale
    ).reshape(lists, cand_count, local_width)
    cls_val_first = mixed("qchd,qche->qdhe", cross_weight, grad_mixed_first[:, :, 0]).reshape(
        lists, cand_count, local_width
    )
    key_first = key_first.astype(jnp.bfloat16)
    val_first = val_first.astype(jnp.bfloat16)
    stacked = jnp.stack([query_grad, key_first, val_first], 3).reshape(row_count, 3, local_width)
    cross_rows = lists * cand_count
    cross_stacked = jnp.stack(
        [jnp.zeros_like(cls_key_first), cls_key_first, cls_val_first], 2
    ).astype(jnp.bfloat16)
    all_rows = jnp.concatenate(
        [stacked, cross_stacked.reshape(cross_rows, 3, local_width)], 0
    )
    all_tokens = jnp.concatenate(
        [tokens.reshape(row_count, model_width), cls_tokens.reshape(cross_rows, model_width)], 0
    )
    if not paired_lists:
        partial_grad = lax.psum_scatter(
            mixed("rd,rkf->dkf", all_tokens, all_rows).astype(jnp.bfloat16),
            "cand",
            scatter_dimension=0,
            tiled=True,
        )
        return sum_query(partial_grad).astype(jnp.float32)
    half = 3 * local_width // 2
    side = lax.axis_index("query")
    flat_rows = all_rows.reshape(all_rows.shape[0], 3 * local_width)
    cls_flat = cls_tokens.reshape(cross_rows, model_width)
    own_half = lax.dynamic_slice_in_dim(flat_rows, side * half, half, 1)
    given_half = lax.dynamic_slice_in_dim(flat_rows, (1 - side) * half, half, 1)
    sent = lax.ppermute(
        jnp.concatenate([given_half.reshape(-1), cls_flat.reshape(-1)]), "query", swap
    )
    other_half = sent[: given_half.size].reshape(given_half.shape)
    other_cls = sent[given_half.size :].reshape(cls_flat.shape)
    paired = (
        mixed("rd,rf->df", all_tokens, own_half)
        + mixed("rd,rf->df", other_tokens, other_half[:row_count])
        + mixed("rd,rf->df", other_cls, other_half[row_count:])
    )
    reduced = scatter_cand(paired.astype(jnp.bfloat16), 0, jnp.float32).astype(jnp.bfloat16)
    partner = lax.ppermute(reduced, "query", swap)
    joined = jnp.where(
        side == 0,
        jnp.concatenate([reduced, partner], 1),
        jnp.concatenate([partner, reduced], 1),
    )
    return joined.reshape(joined.shape[0], 3, local_width).astype(jnp.float32)


def solution(mesh):
    return jax.shard_map(
        local,
        mesh=mesh,
        in_specs=(
            P(("groups", "query"), "cand", None, None),
            P(("groups", "query"), "cand"),
            P(("groups", "query"), "cand"),
            P(None, None, "mp"),
            P("mp", None),
            P(),
            P(None, None, "mp"),
            P("mp", None),
            P(),
            P(),
        ),
        out_specs=P(("groups", "cand"), None, "mp"),
        check_vma=False,
    )
```

```python
import jax
import jax.numpy as jnp
from jax import lax
from jax.sharding import PartitionSpec as P

HEAD_DIM = 64


EPSILON = 1e-05
LOSS_SCALE = 1024.0
NEGATIVE = -1e30


def mixed(pattern, former, latter):
    return jnp.einsum(pattern, former, latter, preferred_element_type=jnp.float32)


def norm_forward(matrix, scales):
    center = matrix - jnp.mean(matrix, -1, keepdims=True)
    inverse = lax.rsqrt(jnp.mean(center * center, -1, keepdims=True) + EPSILON)
    normed = center * inverse
    return (normed * scales, normed, inverse)


def norm_backward(incoming, normed, inverse, scales):
    scaled = incoming * scales
    return inverse * (
        scaled
        - jnp.mean(scaled, -1, keepdims=True)
        - normed * jnp.mean(scaled * normed, -1, keepdims=True)
    )


def split_softmax(own_scores, cross_scores, first_mask):
    own_peak = jnp.max(own_scores, -1)
    row_peak = jnp.maximum(own_peak[..., 0], jnp.max(cross_scores, -1))
    peak = jnp.where(first_mask, row_peak[..., None], own_peak)
    own_exp = jnp.exp(own_scores - peak[..., None])
    cross_exp = jnp.exp(cross_scores - row_peak[..., None])
    own_totals = jnp.sum(own_exp, -1)
    row_totals = own_totals[..., 0] + jnp.sum(cross_exp, -1)
    totals = jnp.where(first_mask, row_totals[..., None], own_totals)
    return (own_exp / totals[..., None], cross_exp / row_totals[..., None])


def row_softmax(own_scores, cross_scores):
    peak = jnp.maximum(jnp.max(own_scores, -1), jnp.max(cross_scores, -1))[..., None]
    own_exp = jnp.exp(own_scores - peak)
    cross_exp = jnp.exp(cross_scores - peak)
    totals = (jnp.sum(own_exp, -1) + jnp.sum(cross_exp, -1))[..., None]
    return (own_exp / totals, cross_exp / totals)


def shift_order(count):
    return sorted(range(1, count), key=lambda k: min(k, count - k), reverse=True)


def gather_cand(block, axis):
    count = lax.axis_size("cand")
    if count > 8:
        return lax.all_gather(block, "cand", axis=axis, tiled=True)
    me = lax.axis_index("cand")
    moved = {
        k: lax.ppermute(block, "cand", [(j, (j + k) % count) for j in range(count)])
        for k in shift_order(count)
    }
    parts = [block] + [moved[k] for k in range(1, count)]
    ordered = jnp.take(jnp.stack(parts, 0), (me - jnp.arange(count)) % count, axis=0)
    ordered = jnp.moveaxis(ordered, 0, axis)
    shape = block.shape[:axis] + (count * block.shape[axis],) + block.shape[axis + 1 :]
    return ordered.reshape(shape)


def sum_cand(block):
    count = lax.axis_size("cand")
    if count > 8:
        return lax.psum(block, "cand")
    total = block
    for k in shift_order(count):
        total = total + lax.ppermute(block, "cand", [(j, (j + k) % count) for j in range(count)])
    return total


def scatter_cand(block, axis, total_type=None):
    count = lax.axis_size("cand")
    if count > 8:
        return lax.psum_scatter(block, "cand", scatter_dimension=axis, tiled=True)
    total_type = total_type or block.dtype
    me = lax.axis_index("cand")
    width = block.shape[axis] // count
    total = lax.dynamic_slice_in_dim(block, me * width, width, axis).astype(total_type)
    for k in shift_order(count):
        piece = lax.dynamic_slice_in_dim(block, ((me + k) % count) * width, width, axis)
        moved = lax.ppermute(piece, "cand", [(j, (j + k) % count) for j in range(count)])
        total = total + moved.astype(total_type)
    return total


def gather_mp(block, axis):
    if lax.axis_size("mp") != 2:
        return lax.all_gather(block, "mp", axis=axis, tiled=True)
    other = lax.ppermute(block, "mp", [(0, 1), (1, 0)])
    return jnp.where(
        lax.axis_index("mp") == 0,
        jnp.concatenate([block, other], axis),
        jnp.concatenate([other, block], axis),
    )


def sum_query(block):
    if lax.axis_size("query") != 2:
        return lax.psum(block, "query")
    other = lax.ppermute(block, "query", [(0, 1), (1, 0)])
    return block.astype(jnp.float32) + other.astype(jnp.float32)


def local(
    tokens,
    lengths,
    teacher,
    w_first,
    w_out_first,
    gain_first,
    w_last,
    w_out_last,
    gain_last,
    w_score,
):
    lists, local_cands, seq_len, model_width = tokens.shape
    local_width = w_first.shape[2]
    local_heads = local_width // HEAD_DIM
    cand_count = local_cands * lax.axis_size("cand")
    query_count = lists * lax.axis_size("query")
    score_scale = HEAD_DIM ** (-0.5)
    positions = jnp.arange(seq_len)
    first_mask = positions == 0
    own_valid = positions[None, None, :] < lengths[:, :, None]
    local_ids = lax.axis_index("cand") * local_cands + jnp.arange(local_cands)
    cross_valid = local_ids[:, None] != jnp.arange(cand_count)[None, :]
    head_shape = (lists, local_cands, seq_len, local_heads, HEAD_DIM)
    cls_shape = (lists, cand_count, local_heads, HEAD_DIM)
    out_first_full = gather_mp(w_out_first, 0)
    last_full = gather_mp(w_last, 2)
    out_last_full = gather_mp(w_out_last, 0)
    cls_and_teacher = gather_cand(
        jnp.concatenate([tokens[:, :, 0].astype(jnp.float32), teacher[..., None]], -1), 1
    )
    cls_tokens = cls_and_teacher[..., :model_width].astype(jnp.bfloat16)
    teacher_all = cls_and_teacher[..., model_width]
    row_count = lists * local_cands * seq_len
    swap = [(0, 1), (1, 0)]
    paired_lists = lax.axis_size("query") == 2
    if paired_lists:
        other_tokens = lax.ppermute(tokens.reshape(row_count, model_width), "query", swap)
    projected = mixed("qcsd,kdf->kqcsf", tokens, w_first).astype(jnp.bfloat16)
    cls_projected = mixed("qcd,kdf->kqcf", cls_tokens, w_first[1:]).astype(jnp.bfloat16)
    gathered_keys = cls_projected[0]
    gathered_vals = cls_projected[1]
    first_query = projected[0].reshape(head_shape)
    first_keys = projected[1].reshape(head_shape)
    first_vals = projected[2].reshape(head_shape)
    cls_keys = gathered_keys.reshape(cls_shape)
    cls_vals = gathered_vals.reshape(cls_shape)
    own_scores = mixed("qcshe,qcthe->qchst", first_query, first_keys) * score_scale
    own_scores = jnp.where(own_valid[:, :, None, None, :], own_scores, NEGATIVE)
    cross_scores = mixed("qche,qdhe->qchd", first_query[:, :, 0], cls_keys) * score_scale
    cross_scores = jnp.where(cross_valid[None, :, None, :], cross_scores, NEGATIVE)
    own_prob, cross_prob = split_softmax(own_scores, cross_scores, first_mask)
    own_weight = own_prob.astype(jnp.bfloat16)
    cross_weight = cross_prob.astype(jnp.bfloat16)
    attended = mixed("qchst,qcthe->qcshe", own_weight, first_vals)
    attended_cls = mixed("qchd,qdhe->qche", cross_weight, cls_vals)
    attended = jnp.where(
        first_mask[None, None, :, None, None], attended + attended_cls[:, :, None], attended
    )
    first_mixed = attended.reshape(lists, local_cands, seq_len, local_width).astype(jnp.bfloat16)
    first_joined = lax.all_gather(first_mixed, "mp", axis=3, tiled=True)
    residual_first = tokens.astype(jnp.float32) + mixed(
        "qcsf,fd->qcsd", first_joined, out_first_full
    )
    normed_first, unit_first, inverse_first = norm_forward(residual_first, gain_first)
    hidden = normed_first.astype(jnp.bfloat16)
    last_query = mixed("qcd,df->qcf", hidden[:, :, 0], w_last[0]).astype(jnp.bfloat16)
    last_kv = mixed("qcsd,kdf->kqcsf", hidden, w_last[1:]).astype(jnp.bfloat16)
    gathered_kv_last = gather_cand(
        jnp.concatenate([last_kv[0][:, :, 0], last_kv[1][:, :, 0]], -1), 1
    )
    gathered_keys_last = gathered_kv_last[..., :local_width]
    gathered_vals_last = gathered_kv_last[..., local_width:]
    last_heads = last_query.reshape(lists, local_cands, local_heads, HEAD_DIM)
    last_keys = last_kv[0].reshape(head_shape)
    last_vals = last_kv[1].reshape(head_shape)
    cls_keys_last = gathered_keys_last.reshape(cls_shape)
    cls_vals_last = gathered_vals_last.reshape(cls_shape)
    own_last = mixed("qche,qcthe->qcht", last_heads, last_keys) * score_scale
    own_last = jnp.where(own_valid[:, :, None, :], own_last, NEGATIVE)
    cross_last = mixed("qche,qdhe->qchd", last_heads, cls_keys_last) * score_scale
    cross_last = jnp.where(cross_valid[None, :, None, :], cross_last, NEGATIVE)
    own_last_prob, cross_last_prob = row_softmax(own_last, cross_last)
    own_last_weight = own_last_prob.astype(jnp.bfloat16)
    cross_last_weight = cross_last_prob.astype(jnp.bfloat16)
    attended_last = mixed("qcht,qcthe->qche", own_last_weight, last_vals) + mixed(
        "qchd,qdhe->qche", cross_last_weight, cls_vals_last
    )
    last_mixed = attended_last.reshape(lists, local_cands, local_width).astype(jnp.bfloat16)
    last_joined = lax.all_gather(last_mixed, "mp", axis=2, tiled=True)
    residual_last = hidden[:, :, 0].astype(jnp.float32) + mixed(
        "qcf,fd->qcd", last_joined, out_last_full
    )
    normed_last, unit_last, inverse_last = norm_forward(residual_last, gain_last)
    scores = jnp.einsum("qcd,d->qc", normed_last, w_score, precision=lax.Precision.HIGHEST)
    score_exp = jnp.exp(scores)
    teacher_peak = jnp.max(teacher_all, 1)
    teacher_exp = jnp.exp(teacher - teacher_peak[:, None])
    teacher_totals = jnp.sum(jnp.exp(teacher_all - teacher_peak[:, None]), 1)
    score_totals = sum_cand(jnp.sum(score_exp, 1))
    student_prob = score_exp / score_totals[:, None]
    teacher_prob = teacher_exp / teacher_totals[:, None]
    score_grad = LOSS_SCALE * (student_prob - teacher_prob) / query_count
    grad_last = norm_backward(score_grad[..., None] * w_score, unit_last, inverse_last, gain_last)
    grad_last_low = grad_last.astype(jnp.bfloat16)
    grad_mixed_last = (
        mixed("qcd,fd->qcf", grad_last_low, w_out_last)
        .astype(jnp.bfloat16)
        .reshape(lists, local_cands, local_heads, HEAD_DIM)
    )
    own_dot = mixed("qche,qcthe->qcht", grad_mixed_last, last_vals)
    cross_dot = mixed("qche,qdhe->qchd", grad_mixed_last, cls_vals_last)
    centre = jnp.sum(own_last_prob * own_dot, -1, keepdims=True) + jnp.sum(
        cross_last_prob * cross_dot, -1, keepdims=True
    )
    own_slope = (own_last_prob * (own_dot - centre)).astype(jnp.bfloat16)
    cross_slope = (cross_last_prob * (cross_dot - centre)).astype(jnp.bfloat16)
    grad_query_last = (
        (
            (
                mixed("qcht,qcthe->qche", own_slope, last_keys)
                + mixed("qchd,qdhe->qche", cross_slope, cls_keys_last)
            )
            * score_scale
        )
        .astype(jnp.bfloat16)
        .reshape(lists, local_cands, local_width)
    )
    own_key_grad = (mixed("qcht,qche->qcthe", own_slope, last_heads) * score_scale).reshape(
        lists, local_cands, seq_len, local_width
    )
    own_val_grad = mixed("qcht,qche->qcthe", own_last_weight, grad_mixed_last).reshape(
        lists, local_cands, seq_len, local_width
    )
    cls_key_terms = (mixed("qchd,qche->qdhe", cross_slope, last_heads) * score_scale).reshape(
        lists, cand_count, local_width
    )
    cls_val_terms = mixed("qchd,qche->qdhe", cross_last_weight, grad_mixed_last).reshape(
        lists, cand_count, local_width
    )
    back_terms = scatter_cand(jnp.concatenate([cls_key_terms, cls_val_terms], -1), 1)
    back_keys = back_terms[..., :local_width]
    back_vals = back_terms[..., local_width:]
    first_cols = first_mask[None, None, :, None]
    key_grad = jnp.where(first_cols, own_key_grad + back_keys[:, :, None], own_key_grad).astype(
        jnp.bfloat16
    )
    val_grad = jnp.where(first_cols, own_val_grad + back_vals[:, :, None], own_val_grad).astype(
        jnp.bfloat16
    )
    joined = lax.all_gather(
        jnp.concatenate([key_grad, val_grad, grad_query_last[:, :, None]], 2),
        "mp",
        axis=3,
        tiled=True,
    )
    key_joined = joined[:, :, :seq_len]
    val_joined = joined[:, :, seq_len : 2 * seq_len]
    query_joined = joined[:, :, 2 * seq_len]
    summed_term = mixed("qcsf,df->qcsd", key_joined, last_full[1]) + mixed(
        "qcsf,df->qcsd", val_joined, last_full[2]
    )
    query_term = mixed("qcf,df->qcd", query_joined, last_full[0])
    summed_term = jnp.where(first_cols, summed_term + query_term[:, :, None], summed_term)
    grad_hidden = jnp.where(first_cols, summed_term + grad_last[:, :, None], summed_term)
    grad_first = norm_backward(grad_hidden, unit_first, inverse_first, gain_first).astype(
        jnp.bfloat16
    )
    grad_mixed_first = (
        mixed("qcsd,fd->qcsf", grad_first, w_out_first).astype(jnp.bfloat16).reshape(head_shape)
    )
    own_dot_first = mixed("qcshe,qcthe->qchst", grad_mixed_first, first_vals)
    cross_dot_first = mixed("qche,qdhe->qchd", grad_mixed_first[:, :, 0], cls_vals)
    own_part = jnp.sum(own_prob * own_dot_first, -1)
    row_part = own_part[..., 0] + jnp.sum(cross_prob * cross_dot_first, -1)
    centre_first = jnp.where(first_mask, row_part[..., None], own_part)
    own_slope_first = (own_prob * (own_dot_first - centre_first[..., None])).astype(jnp.bfloat16)
    cross_slope_first = (cross_prob * (cross_dot_first - row_part[..., None])).astype(jnp.bfloat16)
    query_grad = mixed("qchst,qcthe->qcshe", own_slope_first, first_keys)
    query_cls = mixed("qchd,qdhe->qche", cross_slope_first, cls_keys)
    query_grad = jnp.where(
        first_mask[None, None, :, None, None], query_grad + query_cls[:, :, None], query_grad
    )
    query_grad = (
        (query_grad * score_scale)
        .astype(jnp.bfloat16)
        .reshape(lists, local_cands, seq_len, local_width)
    )
    key_first = (mixed("qchst,qcshe->qcthe", own_slope_first, first_query) * score_scale).reshape(
        lists, local_cands, seq_len, local_width
    )
    val_first = mixed("qchst,qcshe->qcthe", own_weight, grad_mixed_first).reshape(
        lists, local_cands, seq_len, local_width
    )
    cls_key_first = (
        mixed("qchd,qche->qdhe", cross_slope_first, first_query[:, :, 0]) * score_scale
    ).reshape(lists, cand_count, local_width)
    cls_val_first = mixed("qchd,qche->qdhe", cross_weight, grad_mixed_first[:, :, 0]).reshape(
        lists, cand_count, local_width
    )
    key_first = key_first.astype(jnp.bfloat16)
    val_first = val_first.astype(jnp.bfloat16)
    stacked = jnp.stack([query_grad, key_first, val_first], 3).reshape(row_count, 3, local_width)
    cross_rows = lists * cand_count
    cross_stacked = jnp.stack(
        [jnp.zeros_like(cls_key_first), cls_key_first, cls_val_first], 2
    ).astype(jnp.bfloat16)
    all_rows = jnp.concatenate(
        [stacked, cross_stacked.reshape(cross_rows, 3, local_width)], 0
    )
    all_tokens = jnp.concatenate(
        [tokens.reshape(row_count, model_width), cls_tokens.reshape(cross_rows, model_width)], 0
    )
    if not paired_lists:
        partial_grad = lax.psum_scatter(
            mixed("rd,rkf->dkf", all_tokens, all_rows).astype(jnp.bfloat16),
            "cand",
            scatter_dimension=0,
            tiled=True,
        )
        return sum_query(partial_grad).astype(jnp.float32)
    half = 3 * local_width // 2
    side = lax.axis_index("query")
    flat_rows = all_rows.reshape(all_rows.shape[0], 3 * local_width)
    cls_flat = cls_tokens.reshape(cross_rows, model_width)
    own_half = lax.dynamic_slice_in_dim(flat_rows, side * half, half, 1)
    given_half = lax.dynamic_slice_in_dim(flat_rows, (1 - side) * half, half, 1)
    sent = lax.ppermute(
        jnp.concatenate([given_half.reshape(-1), cls_flat.reshape(-1)]), "query", swap
    )
    other_half = sent[: given_half.size].reshape(given_half.shape)
    other_cls = sent[given_half.size :].reshape(cls_flat.shape)
    paired = (
        mixed("rd,rf->df", all_tokens, own_half)
        + mixed("rd,rf->df", other_tokens, other_half[:row_count])
        + mixed("rd,rf->df", other_cls, other_half[row_count:])
    )
    count = lax.axis_size("cand")
    blocks = paired.astype(jnp.bfloat16).reshape(count, -1, half)
    arrived = lax.all_to_all(blocks, "cand", 0, 0, tiled=False)
    reduced = jnp.sum(arrived.astype(jnp.float32), 0).astype(jnp.bfloat16)
    partner = lax.ppermute(reduced, "query", swap)
    joined = jnp.where(
        side == 0,
        jnp.concatenate([reduced, partner], 1),
        jnp.concatenate([partner, reduced], 1),
    )
    return joined.reshape(joined.shape[0], 3, local_width).astype(jnp.float32)


def solution(mesh):
    return jax.shard_map(
        local,
        mesh=mesh,
        in_specs=(
            P(("groups", "query"), "cand", None, None),
            P(("groups", "query"), "cand"),
            P(("groups", "query"), "cand"),
            P(None, None, "mp"),
            P("mp", None),
            P(),
            P(None, None, "mp"),
            P("mp", None),
            P(),
            P(),
        ),
        out_specs=P(("groups", "cand"), None, "mp"),
        check_vma=False,
    )
```

```python
import jax
import jax.numpy as jnp
from jax import lax
from jax.sharding import PartitionSpec as P

HEAD_DIM = 64


EPSILON = 1e-05
LOSS_SCALE = 1024.0
NEGATIVE = -1e30


def mixed(pattern, former, latter):
    return jnp.einsum(pattern, former, latter, preferred_element_type=jnp.float32)


def norm_forward(matrix, scales):
    center = matrix - jnp.mean(matrix, -1, keepdims=True)
    inverse = lax.rsqrt(jnp.mean(center * center, -1, keepdims=True) + EPSILON)
    normed = center * inverse
    return (normed * scales, normed, inverse)


def norm_backward(incoming, normed, inverse, scales):
    scaled = incoming * scales
    return inverse * (
        scaled
        - jnp.mean(scaled, -1, keepdims=True)
        - normed * jnp.mean(scaled * normed, -1, keepdims=True)
    )


def split_softmax(own_scores, cross_scores, first_mask):
    own_peak = jnp.max(own_scores, -1)
    row_peak = jnp.maximum(own_peak[..., 0], jnp.max(cross_scores, -1))
    peak = jnp.where(first_mask, row_peak[..., None], own_peak)
    own_exp = jnp.exp(own_scores - peak[..., None])
    cross_exp = jnp.exp(cross_scores - row_peak[..., None])
    own_totals = jnp.sum(own_exp, -1)
    row_totals = own_totals[..., 0] + jnp.sum(cross_exp, -1)
    totals = jnp.where(first_mask, row_totals[..., None], own_totals)
    return (own_exp / totals[..., None], cross_exp / row_totals[..., None])


def row_softmax(own_scores, cross_scores):
    peak = jnp.maximum(jnp.max(own_scores, -1), jnp.max(cross_scores, -1))[..., None]
    own_exp = jnp.exp(own_scores - peak)
    cross_exp = jnp.exp(cross_scores - peak)
    totals = (jnp.sum(own_exp, -1) + jnp.sum(cross_exp, -1))[..., None]
    return (own_exp / totals, cross_exp / totals)


def slotted(block, axis):
    return lax.axis_size("cand") <= 8 and block.shape[axis] == 1


def gather_slots(block, axis):
    if not slotted(block, axis):
        return lax.all_gather(block, "cand", axis=axis, tiled=True)
    count = lax.axis_size("cand")
    parts = [block] + [
        lax.ppermute(block, "cand", [(j, (j + k) % count) for j in range(count)])
        for k in range(1, count)
    ]
    return jnp.concatenate(parts, axis)


def scatter_slots(block, axis):
    count = lax.axis_size("cand")
    if count > 8 or block.shape[axis] != count:
        return lax.psum_scatter(block, "cand", scatter_dimension=axis, tiled=True)
    total = lax.slice_in_dim(block, 0, 1, axis=axis)
    for k in range(1, count):
        piece = lax.slice_in_dim(block, count - k, count - k + 1, axis=axis)
        total = total + lax.ppermute(piece, "cand", [(j, (j + k) % count) for j in range(count)])
    return total


def gather_cand(block, axis):
    count = lax.axis_size("cand")
    if count > 8:
        return lax.all_gather(block, "cand", axis=axis, tiled=True)
    me = lax.axis_index("cand")
    parts = [block] + [
        lax.ppermute(block, "cand", [(j, (j + k) % count) for j in range(count)])
        for k in range(1, count)
    ]
    ordered = jnp.take(jnp.stack(parts, 0), (me - jnp.arange(count)) % count, axis=0)
    ordered = jnp.moveaxis(ordered, 0, axis)
    shape = block.shape[:axis] + (count * block.shape[axis],) + block.shape[axis + 1 :]
    return ordered.reshape(shape)


def sum_cand(block):
    count = lax.axis_size("cand")
    if count > 8:
        return lax.psum(block, "cand")
    total = block
    for k in range(1, count):
        total = total + lax.ppermute(block, "cand", [(j, (j + k) % count) for j in range(count)])
    return total


def scatter_cand(block, axis, total_type=None):
    count = lax.axis_size("cand")
    if count > 8:
        return lax.psum_scatter(block, "cand", scatter_dimension=axis, tiled=True)
    total_type = total_type or block.dtype
    me = lax.axis_index("cand")
    width = block.shape[axis] // count
    total = lax.dynamic_slice_in_dim(block, me * width, width, axis).astype(total_type)
    for k in range(1, count):
        piece = lax.dynamic_slice_in_dim(block, ((me + k) % count) * width, width, axis)
        moved = lax.ppermute(piece, "cand", [(j, (j + k) % count) for j in range(count)])
        total = total + moved.astype(total_type)
    return total


def gather_mp(block, axis):
    if lax.axis_size("mp") != 2:
        return lax.all_gather(block, "mp", axis=axis, tiled=True)
    other = lax.ppermute(block, "mp", [(0, 1), (1, 0)])
    return jnp.where(
        lax.axis_index("mp") == 0,
        jnp.concatenate([block, other], axis),
        jnp.concatenate([other, block], axis),
    )


def sum_query(block):
    if lax.axis_size("query") != 2:
        return lax.psum(block, "query")
    other = lax.ppermute(block, "query", [(0, 1), (1, 0)])
    return block.astype(jnp.float32) + other.astype(jnp.float32)


def local(
    tokens,
    lengths,
    teacher,
    w_first,
    w_out_first,
    gain_first,
    w_last,
    w_out_last,
    gain_last,
    w_score,
):
    lists, local_cands, seq_len, model_width = tokens.shape
    local_width = w_first.shape[2]
    local_heads = local_width // HEAD_DIM
    cand_count = local_cands * lax.axis_size("cand")
    query_count = lists * lax.axis_size("query")
    score_scale = HEAD_DIM ** (-0.5)
    positions = jnp.arange(seq_len)
    first_mask = positions == 0
    own_valid = positions[None, None, :] < lengths[:, :, None]
    local_ids = lax.axis_index("cand") * local_cands + jnp.arange(local_cands)
    if local_cands == 1 and lax.axis_size("cand") <= 8:
        slot_ids = (lax.axis_index("cand") - jnp.arange(cand_count)) % cand_count
    else:
        slot_ids = jnp.arange(cand_count)
    cross_valid = local_ids[:, None] != slot_ids[None, :]
    head_shape = (lists, local_cands, seq_len, local_heads, HEAD_DIM)
    cls_shape = (lists, cand_count, local_heads, HEAD_DIM)
    out_first_full = gather_mp(w_out_first, 0)
    last_full = gather_mp(w_last, 2)
    out_last_full = gather_mp(w_out_last, 0)
    cls_and_teacher = gather_slots(
        jnp.concatenate([tokens[:, :, 0].astype(jnp.float32), teacher[..., None]], -1), 1
    )
    cls_tokens = cls_and_teacher[..., :model_width].astype(jnp.bfloat16)
    teacher_all = cls_and_teacher[..., model_width]
    row_count = lists * local_cands * seq_len
    swap = [(0, 1), (1, 0)]
    paired_lists = lax.axis_size("query") == 2
    if paired_lists:
        other_tokens = lax.ppermute(tokens.reshape(row_count, model_width), "query", swap)
    projected = mixed("qcsd,kdf->kqcsf", tokens, w_first).astype(jnp.bfloat16)
    cls_projected = mixed("qcd,kdf->kqcf", cls_tokens, w_first[1:]).astype(jnp.bfloat16)
    gathered_keys = cls_projected[0]
    gathered_vals = cls_projected[1]
    first_query = projected[0].reshape(head_shape)
    first_keys = projected[1].reshape(head_shape)
    first_vals = projected[2].reshape(head_shape)
    cls_keys = gathered_keys.reshape(cls_shape)
    cls_vals = gathered_vals.reshape(cls_shape)
    own_scores = mixed("qcshe,qcthe->qchst", first_query, first_keys) * score_scale
    own_scores = jnp.where(own_valid[:, :, None, None, :], own_scores, NEGATIVE)
    cross_scores = mixed("qche,qdhe->qchd", first_query[:, :, 0], cls_keys) * score_scale
    cross_scores = jnp.where(cross_valid[None, :, None, :], cross_scores, NEGATIVE)
    own_prob, cross_prob = split_softmax(own_scores, cross_scores, first_mask)
    own_weight = own_prob.astype(jnp.bfloat16)
    cross_weight = cross_prob.astype(jnp.bfloat16)
    attended = mixed("qchst,qcthe->qcshe", own_weight, first_vals)
    attended_cls = mixed("qchd,qdhe->qche", cross_weight, cls_vals)
    attended = jnp.where(
        first_mask[None, None, :, None, None], attended + attended_cls[:, :, None], attended
    )
    first_mixed = attended.reshape(lists, local_cands, seq_len, local_width).astype(jnp.bfloat16)
    first_joined = lax.all_gather(first_mixed, "mp", axis=3, tiled=True)
    residual_first = tokens.astype(jnp.float32) + mixed(
        "qcsf,fd->qcsd", first_joined, out_first_full
    )
    normed_first, unit_first, inverse_first = norm_forward(residual_first, gain_first)
    hidden = normed_first.astype(jnp.bfloat16)
    last_query = mixed("qcd,df->qcf", hidden[:, :, 0], w_last[0]).astype(jnp.bfloat16)
    last_kv = mixed("qcsd,kdf->kqcsf", hidden, w_last[1:]).astype(jnp.bfloat16)
    gathered_kv_last = gather_slots(
        jnp.concatenate([last_kv[0][:, :, 0], last_kv[1][:, :, 0]], -1), 1
    )
    gathered_keys_last = gathered_kv_last[..., :local_width]
    gathered_vals_last = gathered_kv_last[..., local_width:]
    last_heads = last_query.reshape(lists, local_cands, local_heads, HEAD_DIM)
    last_keys = last_kv[0].reshape(head_shape)
    last_vals = last_kv[1].reshape(head_shape)
    cls_keys_last = gathered_keys_last.reshape(cls_shape)
    cls_vals_last = gathered_vals_last.reshape(cls_shape)
    own_last = mixed("qche,qcthe->qcht", last_heads, last_keys) * score_scale
    own_last = jnp.where(own_valid[:, :, None, :], own_last, NEGATIVE)
    cross_last = mixed("qche,qdhe->qchd", last_heads, cls_keys_last) * score_scale
    cross_last = jnp.where(cross_valid[None, :, None, :], cross_last, NEGATIVE)
    own_last_prob, cross_last_prob = row_softmax(own_last, cross_last)
    own_last_weight = own_last_prob.astype(jnp.bfloat16)
    cross_last_weight = cross_last_prob.astype(jnp.bfloat16)
    attended_last = mixed("qcht,qcthe->qche", own_last_weight, last_vals) + mixed(
        "qchd,qdhe->qche", cross_last_weight, cls_vals_last
    )
    last_mixed = attended_last.reshape(lists, local_cands, local_width).astype(jnp.bfloat16)
    last_joined = lax.all_gather(last_mixed, "mp", axis=2, tiled=True)
    residual_last = hidden[:, :, 0].astype(jnp.float32) + mixed(
        "qcf,fd->qcd", last_joined, out_last_full
    )
    normed_last, unit_last, inverse_last = norm_forward(residual_last, gain_last)
    scores = jnp.einsum("qcd,d->qc", normed_last, w_score, precision=lax.Precision.HIGHEST)
    score_exp = jnp.exp(scores)
    teacher_peak = jnp.max(teacher_all, 1)
    teacher_exp = jnp.exp(teacher - teacher_peak[:, None])
    teacher_totals = jnp.sum(jnp.exp(teacher_all - teacher_peak[:, None]), 1)
    score_totals = sum_cand(jnp.sum(score_exp, 1))
    student_prob = score_exp / score_totals[:, None]
    teacher_prob = teacher_exp / teacher_totals[:, None]
    score_grad = LOSS_SCALE * (student_prob - teacher_prob) / query_count
    grad_last = norm_backward(score_grad[..., None] * w_score, unit_last, inverse_last, gain_last)
    grad_last_low = grad_last.astype(jnp.bfloat16)
    grad_mixed_last = (
        mixed("qcd,fd->qcf", grad_last_low, w_out_last)
        .astype(jnp.bfloat16)
        .reshape(lists, local_cands, local_heads, HEAD_DIM)
    )
    own_dot = mixed("qche,qcthe->qcht", grad_mixed_last, last_vals)
    cross_dot = mixed("qche,qdhe->qchd", grad_mixed_last, cls_vals_last)
    centre = jnp.sum(own_last_prob * own_dot, -1, keepdims=True) + jnp.sum(
        cross_last_prob * cross_dot, -1, keepdims=True
    )
    own_slope = (own_last_prob * (own_dot - centre)).astype(jnp.bfloat16)
    cross_slope = (cross_last_prob * (cross_dot - centre)).astype(jnp.bfloat16)
    grad_query_last = (
        (
            (
                mixed("qcht,qcthe->qche", own_slope, last_keys)
                + mixed("qchd,qdhe->qche", cross_slope, cls_keys_last)
            )
            * score_scale
        )
        .astype(jnp.bfloat16)
        .reshape(lists, local_cands, local_width)
    )
    own_key_grad = (mixed("qcht,qche->qcthe", own_slope, last_heads) * score_scale).reshape(
        lists, local_cands, seq_len, local_width
    )
    own_val_grad = mixed("qcht,qche->qcthe", own_last_weight, grad_mixed_last).reshape(
        lists, local_cands, seq_len, local_width
    )
    cls_key_terms = (mixed("qchd,qche->qdhe", cross_slope, last_heads) * score_scale).reshape(
        lists, cand_count, local_width
    )
    cls_val_terms = mixed("qchd,qche->qdhe", cross_last_weight, grad_mixed_last).reshape(
        lists, cand_count, local_width
    )
    back_terms = scatter_slots(jnp.concatenate([cls_key_terms, cls_val_terms], -1), 1)
    back_keys = back_terms[..., :local_width]
    back_vals = back_terms[..., local_width:]
    first_cols = first_mask[None, None, :, None]
    key_grad = jnp.where(first_cols, own_key_grad + back_keys[:, :, None], own_key_grad).astype(
        jnp.bfloat16
    )
    val_grad = jnp.where(first_cols, own_val_grad + back_vals[:, :, None], own_val_grad).astype(
        jnp.bfloat16
    )
    joined = lax.all_gather(
        jnp.concatenate([key_grad, val_grad, grad_query_last[:, :, None]], 2),
        "mp",
        axis=3,
        tiled=True,
    )
    key_joined = joined[:, :, :seq_len]
    val_joined = joined[:, :, seq_len : 2 * seq_len]
    query_joined = joined[:, :, 2 * seq_len]
    summed_term = mixed("qcsf,df->qcsd", key_joined, last_full[1]) + mixed(
        "qcsf,df->qcsd", val_joined, last_full[2]
    )
    query_term = mixed("qcf,df->qcd", query_joined, last_full[0])
    summed_term = jnp.where(first_cols, summed_term + query_term[:, :, None], summed_term)
    grad_hidden = jnp.where(first_cols, summed_term + grad_last[:, :, None], summed_term)
    grad_first = norm_backward(grad_hidden, unit_first, inverse_first, gain_first).astype(
        jnp.bfloat16
    )
    grad_mixed_first = (
        mixed("qcsd,fd->qcsf", grad_first, w_out_first).astype(jnp.bfloat16).reshape(head_shape)
    )
    own_dot_first = mixed("qcshe,qcthe->qchst", grad_mixed_first, first_vals)
    cross_dot_first = mixed("qche,qdhe->qchd", grad_mixed_first[:, :, 0], cls_vals)
    own_part = jnp.sum(own_prob * own_dot_first, -1)
    row_part = own_part[..., 0] + jnp.sum(cross_prob * cross_dot_first, -1)
    centre_first = jnp.where(first_mask, row_part[..., None], own_part)
    own_slope_first = (own_prob * (own_dot_first - centre_first[..., None])).astype(jnp.bfloat16)
    cross_slope_first = (cross_prob * (cross_dot_first - row_part[..., None])).astype(jnp.bfloat16)
    query_grad = mixed("qchst,qcthe->qcshe", own_slope_first, first_keys)
    query_cls = mixed("qchd,qdhe->qche", cross_slope_first, cls_keys)
    query_grad = jnp.where(
        first_mask[None, None, :, None, None], query_grad + query_cls[:, :, None], query_grad
    )
    query_grad = (
        (query_grad * score_scale)
        .astype(jnp.bfloat16)
        .reshape(lists, local_cands, seq_len, local_width)
    )
    key_first = (mixed("qchst,qcshe->qcthe", own_slope_first, first_query) * score_scale).reshape(
        lists, local_cands, seq_len, local_width
    )
    val_first = mixed("qchst,qcshe->qcthe", own_weight, grad_mixed_first).reshape(
        lists, local_cands, seq_len, local_width
    )
    cls_key_first = (
        mixed("qchd,qche->qdhe", cross_slope_first, first_query[:, :, 0]) * score_scale
    ).reshape(lists, cand_count, local_width)
    cls_val_first = mixed("qchd,qche->qdhe", cross_weight, grad_mixed_first[:, :, 0]).reshape(
        lists, cand_count, local_width
    )
    key_first = key_first.astype(jnp.bfloat16)
    val_first = val_first.astype(jnp.bfloat16)
    stacked = jnp.stack([query_grad, key_first, val_first], 3).reshape(row_count, 3, local_width)
    cross_rows = lists * cand_count
    cross_stacked = jnp.stack(
        [jnp.zeros_like(cls_key_first), cls_key_first, cls_val_first], 2
    ).astype(jnp.bfloat16)
    all_rows = jnp.concatenate(
        [stacked, cross_stacked.reshape(cross_rows, 3, local_width)], 0
    )
    all_tokens = jnp.concatenate(
        [tokens.reshape(row_count, model_width), cls_tokens.reshape(cross_rows, model_width)], 0
    )
    if not paired_lists:
        partial_grad = lax.psum_scatter(
            mixed("rd,rkf->dkf", all_tokens, all_rows).astype(jnp.bfloat16),
            "cand",
            scatter_dimension=0,
            tiled=True,
        )
        return sum_query(partial_grad).astype(jnp.float32)
    half = 3 * local_width // 2
    side = lax.axis_index("query")
    flat_rows = all_rows.reshape(all_rows.shape[0], 3 * local_width)
    cls_flat = cls_tokens.reshape(cross_rows, model_width)
    own_half = lax.dynamic_slice_in_dim(flat_rows, side * half, half, 1)
    given_half = lax.dynamic_slice_in_dim(flat_rows, (1 - side) * half, half, 1)
    sent = lax.ppermute(
        jnp.concatenate([given_half.reshape(-1), cls_flat.reshape(-1)]), "query", swap
    )
    other_half = sent[: given_half.size].reshape(given_half.shape)
    other_cls = sent[given_half.size :].reshape(cls_flat.shape)
    paired = (
        mixed("rd,rf->df", all_tokens, own_half)
        + mixed("rd,rf->df", other_tokens, other_half[:row_count])
        + mixed("rd,rf->df", other_cls, other_half[row_count:])
    )
    reduced = scatter_cand(paired.astype(jnp.bfloat16), 0, jnp.float32).astype(jnp.bfloat16)
    partner = lax.ppermute(reduced, "query", swap)
    joined = jnp.where(
        side == 0,
        jnp.concatenate([reduced, partner], 1),
        jnp.concatenate([partner, reduced], 1),
    )
    return joined.reshape(joined.shape[0], 3, local_width).astype(jnp.float32)


def solution(mesh):
    return jax.shard_map(
        local,
        mesh=mesh,
        in_specs=(
            P(("groups", "query"), "cand", None, None),
            P(("groups", "query"), "cand"),
            P(("groups", "query"), "cand"),
            P(None, None, "mp"),
            P("mp", None),
            P(),
            P(None, None, "mp"),
            P("mp", None),
            P(),
            P(),
        ),
        out_specs=P(("groups", "cand"), None, "mp"),
        check_vma=False,
    )
```

```python
import jax
import jax.numpy as jnp
from jax import lax
from jax.sharding import PartitionSpec as P

HEAD_DIM = 64


EPSILON = 1e-05
LOSS_SCALE = 1024.0
NEGATIVE = -1e30


def mixed(pattern, former, latter):
    return jnp.einsum(pattern, former, latter, preferred_element_type=jnp.float32)


def norm_forward(matrix, scales):
    center = matrix - jnp.mean(matrix, -1, keepdims=True)
    inverse = lax.rsqrt(jnp.mean(center * center, -1, keepdims=True) + EPSILON)
    normed = center * inverse
    return (normed * scales, normed, inverse)


def norm_backward(incoming, normed, inverse, scales):
    scaled = incoming * scales
    return inverse * (
        scaled
        - jnp.mean(scaled, -1, keepdims=True)
        - normed * jnp.mean(scaled * normed, -1, keepdims=True)
    )


def split_softmax(own_scores, cross_scores, first_mask):
    own_peak = jnp.max(own_scores, -1)
    row_peak = jnp.maximum(own_peak[..., 0], jnp.max(cross_scores, -1))
    peak = jnp.where(first_mask, row_peak[..., None], own_peak)
    own_exp = jnp.exp(own_scores - peak[..., None])
    cross_exp = jnp.exp(cross_scores - row_peak[..., None])
    own_totals = jnp.sum(own_exp, -1)
    row_totals = own_totals[..., 0] + jnp.sum(cross_exp, -1)
    totals = jnp.where(first_mask, row_totals[..., None], own_totals)
    return (own_exp / totals[..., None], cross_exp / row_totals[..., None])


def row_softmax(own_scores, cross_scores):
    peak = jnp.maximum(jnp.max(own_scores, -1), jnp.max(cross_scores, -1))[..., None]
    own_exp = jnp.exp(own_scores - peak)
    cross_exp = jnp.exp(cross_scores - peak)
    totals = (jnp.sum(own_exp, -1) + jnp.sum(cross_exp, -1))[..., None]
    return (own_exp / totals, cross_exp / totals)


def gather_cand(block, axis):
    count = lax.axis_size("cand")
    if count > 8:
        return lax.all_gather(block, "cand", axis=axis, tiled=True)
    me = lax.axis_index("cand")
    parts = [block] + [
        lax.ppermute(block, "cand", [(j, (j + k) % count) for j in range(count)])
        for k in range(1, count)
    ]
    ordered = jnp.take(jnp.stack(parts, 0), (me - jnp.arange(count)) % count, axis=0)
    ordered = jnp.moveaxis(ordered, 0, axis)
    shape = block.shape[:axis] + (count * block.shape[axis],) + block.shape[axis + 1 :]
    return ordered.reshape(shape)


def sum_cand(block):
    count = lax.axis_size("cand")
    if count > 8:
        return lax.psum(block, "cand")
    total = block
    for k in range(1, count):
        total = total + lax.ppermute(block, "cand", [(j, (j + k) % count) for j in range(count)])
    return total


def scatter_cand(block, axis, total_type=None):
    count = lax.axis_size("cand")
    if count > 8:
        return lax.psum_scatter(block, "cand", scatter_dimension=axis, tiled=True)
    total_type = total_type or block.dtype
    me = lax.axis_index("cand")
    width = block.shape[axis] // count
    total = lax.dynamic_slice_in_dim(block, me * width, width, axis).astype(total_type)
    for k in range(1, count):
        piece = lax.dynamic_slice_in_dim(block, ((me + k) % count) * width, width, axis)
        moved = lax.ppermute(piece, "cand", [(j, (j + k) % count) for j in range(count)])
        total = total + moved.astype(total_type)
    return total


def gather_mp(block, axis):
    other = lax.ppermute(block, "mp", [(0, 1), (1, 0)])
    return jnp.concatenate([block, other], axis)


def sum_query(block):
    if lax.axis_size("query") != 2:
        return lax.psum(block, "query")
    other = lax.ppermute(block, "query", [(0, 1), (1, 0)])
    return block.astype(jnp.float32) + other.astype(jnp.float32)


def local(
    tokens,
    lengths,
    teacher,
    w_first,
    w_out_first,
    gain_first,
    w_last,
    w_out_last,
    gain_last,
    w_score,
):
    lists, local_cands, seq_len, model_width = tokens.shape
    local_width = w_first.shape[2]
    local_heads = local_width // HEAD_DIM
    cand_count = local_cands * lax.axis_size("cand")
    query_count = lists * lax.axis_size("query")
    score_scale = HEAD_DIM ** (-0.5)
    positions = jnp.arange(seq_len)
    first_mask = positions == 0
    own_valid = positions[None, None, :] < lengths[:, :, None]
    local_ids = lax.axis_index("cand") * local_cands + jnp.arange(local_cands)
    cross_valid = local_ids[:, None] != jnp.arange(cand_count)[None, :]
    head_shape = (lists, local_cands, seq_len, local_heads, HEAD_DIM)
    cls_shape = (lists, cand_count, local_heads, HEAD_DIM)
    out_first_full = gather_mp(w_out_first, 0)
    last_full = gather_mp(w_last, 2)
    out_last_full = gather_mp(w_out_last, 0)
    cls_and_teacher = gather_cand(
        jnp.concatenate([tokens[:, :, 0].astype(jnp.float32), teacher[..., None]], -1), 1
    )
    cls_tokens = cls_and_teacher[..., :model_width].astype(jnp.bfloat16)
    teacher_all = cls_and_teacher[..., model_width]
    row_count = lists * local_cands * seq_len
    swap = [(0, 1), (1, 0)]
    paired_lists = lax.axis_size("query") == 2
    if paired_lists:
        other_tokens = lax.ppermute(tokens.reshape(row_count, model_width), "query", swap)
    projected = mixed("qcsd,kdf->kqcsf", tokens, w_first).astype(jnp.bfloat16)
    cls_projected = mixed("qcd,kdf->kqcf", cls_tokens, w_first[1:]).astype(jnp.bfloat16)
    gathered_keys = cls_projected[0]
    gathered_vals = cls_projected[1]
    first_query = projected[0].reshape(head_shape)
    first_keys = projected[1].reshape(head_shape)
    first_vals = projected[2].reshape(head_shape)
    cls_keys = gathered_keys.reshape(cls_shape)
    cls_vals = gathered_vals.reshape(cls_shape)
    own_scores = mixed("qcshe,qcthe->qchst", first_query, first_keys) * score_scale
    own_scores = jnp.where(own_valid[:, :, None, None, :], own_scores, NEGATIVE)
    cross_scores = mixed("qche,qdhe->qchd", first_query[:, :, 0], cls_keys) * score_scale
    cross_scores = jnp.where(cross_valid[None, :, None, :], cross_scores, NEGATIVE)
    own_prob, cross_prob = split_softmax(own_scores, cross_scores, first_mask)
    own_weight = own_prob.astype(jnp.bfloat16)
    cross_weight = cross_prob.astype(jnp.bfloat16)
    attended = mixed("qchst,qcthe->qcshe", own_weight, first_vals)
    attended_cls = mixed("qchd,qdhe->qche", cross_weight, cls_vals)
    attended = jnp.where(
        first_mask[None, None, :, None, None], attended + attended_cls[:, :, None], attended
    )
    first_mixed = attended.reshape(lists, local_cands, seq_len, local_width).astype(jnp.bfloat16)
    first_joined = gather_mp(first_mixed, 3)
    residual_first = tokens.astype(jnp.float32) + mixed(
        "qcsf,fd->qcsd", first_joined, out_first_full
    )
    normed_first, unit_first, inverse_first = norm_forward(residual_first, gain_first)
    hidden = normed_first.astype(jnp.bfloat16)
    last_query = mixed("qcd,df->qcf", hidden[:, :, 0], w_last[0]).astype(jnp.bfloat16)
    last_kv = mixed("qcsd,kdf->kqcsf", hidden, w_last[1:]).astype(jnp.bfloat16)
    gathered_kv_last = gather_cand(
        jnp.concatenate([last_kv[0][:, :, 0], last_kv[1][:, :, 0]], -1), 1
    )
    gathered_keys_last = gathered_kv_last[..., :local_width]
    gathered_vals_last = gathered_kv_last[..., local_width:]
    last_heads = last_query.reshape(lists, local_cands, local_heads, HEAD_DIM)
    last_keys = last_kv[0].reshape(head_shape)
    last_vals = last_kv[1].reshape(head_shape)
    cls_keys_last = gathered_keys_last.reshape(cls_shape)
    cls_vals_last = gathered_vals_last.reshape(cls_shape)
    own_last = mixed("qche,qcthe->qcht", last_heads, last_keys) * score_scale
    own_last = jnp.where(own_valid[:, :, None, :], own_last, NEGATIVE)
    cross_last = mixed("qche,qdhe->qchd", last_heads, cls_keys_last) * score_scale
    cross_last = jnp.where(cross_valid[None, :, None, :], cross_last, NEGATIVE)
    own_last_prob, cross_last_prob = row_softmax(own_last, cross_last)
    own_last_weight = own_last_prob.astype(jnp.bfloat16)
    cross_last_weight = cross_last_prob.astype(jnp.bfloat16)
    attended_last = mixed("qcht,qcthe->qche", own_last_weight, last_vals) + mixed(
        "qchd,qdhe->qche", cross_last_weight, cls_vals_last
    )
    last_mixed = attended_last.reshape(lists, local_cands, local_width).astype(jnp.bfloat16)
    last_joined = gather_mp(last_mixed, 2)
    residual_last = hidden[:, :, 0].astype(jnp.float32) + mixed(
        "qcf,fd->qcd", last_joined, out_last_full
    )
    normed_last, unit_last, inverse_last = norm_forward(residual_last, gain_last)
    scores = jnp.einsum("qcd,d->qc", normed_last, w_score, precision=lax.Precision.HIGHEST)
    score_exp = jnp.exp(scores)
    teacher_peak = jnp.max(teacher_all, 1)
    teacher_exp = jnp.exp(teacher - teacher_peak[:, None])
    teacher_totals = jnp.sum(jnp.exp(teacher_all - teacher_peak[:, None]), 1)
    score_totals = sum_cand(jnp.sum(score_exp, 1))
    student_prob = score_exp / score_totals[:, None]
    teacher_prob = teacher_exp / teacher_totals[:, None]
    score_grad = LOSS_SCALE * (student_prob - teacher_prob) / query_count
    grad_last = norm_backward(score_grad[..., None] * w_score, unit_last, inverse_last, gain_last)
    grad_last_low = grad_last.astype(jnp.bfloat16)
    grad_mixed_last = (
        mixed("qcd,fd->qcf", grad_last_low, w_out_last)
        .astype(jnp.bfloat16)
        .reshape(lists, local_cands, local_heads, HEAD_DIM)
    )
    own_dot = mixed("qche,qcthe->qcht", grad_mixed_last, last_vals)
    cross_dot = mixed("qche,qdhe->qchd", grad_mixed_last, cls_vals_last)
    centre = jnp.sum(own_last_prob * own_dot, -1, keepdims=True) + jnp.sum(
        cross_last_prob * cross_dot, -1, keepdims=True
    )
    own_slope = (own_last_prob * (own_dot - centre)).astype(jnp.bfloat16)
    cross_slope = (cross_last_prob * (cross_dot - centre)).astype(jnp.bfloat16)
    grad_query_last = (
        (
            (
                mixed("qcht,qcthe->qche", own_slope, last_keys)
                + mixed("qchd,qdhe->qche", cross_slope, cls_keys_last)
            )
            * score_scale
        )
        .astype(jnp.bfloat16)
        .reshape(lists, local_cands, local_width)
    )
    own_key_grad = (mixed("qcht,qche->qcthe", own_slope, last_heads) * score_scale).reshape(
        lists, local_cands, seq_len, local_width
    )
    own_val_grad = mixed("qcht,qche->qcthe", own_last_weight, grad_mixed_last).reshape(
        lists, local_cands, seq_len, local_width
    )
    cls_key_terms = (mixed("qchd,qche->qdhe", cross_slope, last_heads) * score_scale).reshape(
        lists, cand_count, local_width
    )
    cls_val_terms = mixed("qchd,qche->qdhe", cross_last_weight, grad_mixed_last).reshape(
        lists, cand_count, local_width
    )
    back_terms = scatter_cand(jnp.concatenate([cls_key_terms, cls_val_terms], -1), 1)
    back_keys = back_terms[..., :local_width]
    back_vals = back_terms[..., local_width:]
    first_cols = first_mask[None, None, :, None]
    key_grad = jnp.where(first_cols, own_key_grad + back_keys[:, :, None], own_key_grad).astype(
        jnp.bfloat16
    )
    val_grad = jnp.where(first_cols, own_val_grad + back_vals[:, :, None], own_val_grad).astype(
        jnp.bfloat16
    )
    joined = gather_mp(jnp.concatenate([key_grad, val_grad, grad_query_last[:, :, None]], 2), 3)
    key_joined = joined[:, :, :seq_len]
    val_joined = joined[:, :, seq_len : 2 * seq_len]
    query_joined = joined[:, :, 2 * seq_len]
    summed_term = mixed("qcsf,df->qcsd", key_joined, last_full[1]) + mixed(
        "qcsf,df->qcsd", val_joined, last_full[2]
    )
    query_term = mixed("qcf,df->qcd", query_joined, last_full[0])
    summed_term = jnp.where(first_cols, summed_term + query_term[:, :, None], summed_term)
    grad_hidden = jnp.where(first_cols, summed_term + grad_last[:, :, None], summed_term)
    grad_first = norm_backward(grad_hidden, unit_first, inverse_first, gain_first).astype(
        jnp.bfloat16
    )
    grad_mixed_first = (
        mixed("qcsd,fd->qcsf", grad_first, w_out_first).astype(jnp.bfloat16).reshape(head_shape)
    )
    own_dot_first = mixed("qcshe,qcthe->qchst", grad_mixed_first, first_vals)
    cross_dot_first = mixed("qche,qdhe->qchd", grad_mixed_first[:, :, 0], cls_vals)
    own_part = jnp.sum(own_prob * own_dot_first, -1)
    row_part = own_part[..., 0] + jnp.sum(cross_prob * cross_dot_first, -1)
    centre_first = jnp.where(first_mask, row_part[..., None], own_part)
    own_slope_first = (own_prob * (own_dot_first - centre_first[..., None])).astype(jnp.bfloat16)
    cross_slope_first = (cross_prob * (cross_dot_first - row_part[..., None])).astype(jnp.bfloat16)
    query_grad = mixed("qchst,qcthe->qcshe", own_slope_first, first_keys)
    query_cls = mixed("qchd,qdhe->qche", cross_slope_first, cls_keys)
    query_grad = jnp.where(
        first_mask[None, None, :, None, None], query_grad + query_cls[:, :, None], query_grad
    )
    query_grad = (
        (query_grad * score_scale)
        .astype(jnp.bfloat16)
        .reshape(lists, local_cands, seq_len, local_width)
    )
    key_first = (mixed("qchst,qcshe->qcthe", own_slope_first, first_query) * score_scale).reshape(
        lists, local_cands, seq_len, local_width
    )
    val_first = mixed("qchst,qcshe->qcthe", own_weight, grad_mixed_first).reshape(
        lists, local_cands, seq_len, local_width
    )
    cls_key_first = (
        mixed("qchd,qche->qdhe", cross_slope_first, first_query[:, :, 0]) * score_scale
    ).reshape(lists, cand_count, local_width)
    cls_val_first = mixed("qchd,qche->qdhe", cross_weight, grad_mixed_first[:, :, 0]).reshape(
        lists, cand_count, local_width
    )
    key_first = key_first.astype(jnp.bfloat16)
    val_first = val_first.astype(jnp.bfloat16)
    stacked = jnp.stack([query_grad, key_first, val_first], 3).reshape(row_count, 3, local_width)
    cross_rows = lists * cand_count
    cross_stacked = jnp.stack(
        [jnp.zeros_like(cls_key_first), cls_key_first, cls_val_first], 2
    ).astype(jnp.bfloat16)
    all_rows = jnp.concatenate(
        [stacked, cross_stacked.reshape(cross_rows, 3, local_width)], 0
    )
    all_tokens = jnp.concatenate(
        [tokens.reshape(row_count, model_width), cls_tokens.reshape(cross_rows, model_width)], 0
    )
    if not paired_lists:
        partial_grad = lax.psum_scatter(
            mixed("rd,rkf->dkf", all_tokens, all_rows).astype(jnp.bfloat16),
            "cand",
            scatter_dimension=0,
            tiled=True,
        )
        return sum_query(partial_grad).astype(jnp.float32)
    half = 3 * local_width // 2
    side = lax.axis_index("query")
    flat_rows = all_rows.reshape(all_rows.shape[0], 3 * local_width)
    cls_flat = cls_tokens.reshape(cross_rows, model_width)
    own_half = lax.dynamic_slice_in_dim(flat_rows, side * half, half, 1)
    given_half = lax.dynamic_slice_in_dim(flat_rows, (1 - side) * half, half, 1)
    sent = lax.ppermute(
        jnp.concatenate([given_half.reshape(-1), cls_flat.reshape(-1)]), "query", swap
    )
    other_half = sent[: given_half.size].reshape(given_half.shape)
    other_cls = sent[given_half.size :].reshape(cls_flat.shape)
    paired = (
        mixed("rd,rf->df", all_tokens, own_half)
        + mixed("rd,rf->df", other_tokens, other_half[:row_count])
        + mixed("rd,rf->df", other_cls, other_half[row_count:])
    )
    reduced = scatter_cand(paired.astype(jnp.bfloat16), 0, jnp.float32).astype(jnp.bfloat16)
    partner = lax.ppermute(reduced, "query", swap)
    joined = jnp.where(
        side == 0,
        jnp.concatenate([reduced, partner], 1),
        jnp.concatenate([partner, reduced], 1),
    )
    return joined.reshape(joined.shape[0], 3, local_width).astype(jnp.float32)


def solution(mesh):
    return jax.shard_map(
        local,
        mesh=mesh,
        in_specs=(
            P(("groups", "query"), "cand", None, None),
            P(("groups", "query"), "cand"),
            P(("groups", "query"), "cand"),
            P(None, None, "mp"),
            P("mp", None),
            P(),
            P(None, None, "mp"),
            P("mp", None),
            P(),
            P(),
        ),
        out_specs=P(("groups", "cand"), None, "mp"),
        check_vma=False,
    )
```

```python
import jax
import jax.numpy as jnp
from jax import lax
from jax.sharding import PartitionSpec as P

HEAD_DIM = 64


EPSILON = 1e-05
LOSS_SCALE = 1024.0
NEGATIVE = -1e30


def mixed(pattern, former, latter):
    return jnp.einsum(pattern, former, latter, preferred_element_type=jnp.float32)


def norm_forward(matrix, scales):
    center = matrix - jnp.mean(matrix, -1, keepdims=True)
    inverse = lax.rsqrt(jnp.mean(center * center, -1, keepdims=True) + EPSILON)
    normed = center * inverse
    return (normed * scales, normed, inverse)


def norm_backward(incoming, normed, inverse, scales):
    scaled = incoming * scales
    return inverse * (
        scaled
        - jnp.mean(scaled, -1, keepdims=True)
        - normed * jnp.mean(scaled * normed, -1, keepdims=True)
    )


def split_softmax(own_scores, cross_scores, first_mask):
    own_peak = jnp.max(own_scores, -1)
    row_peak = jnp.maximum(own_peak[..., 0], jnp.max(cross_scores, -1))
    peak = jnp.where(first_mask, row_peak[..., None], own_peak)
    own_exp = jnp.exp(own_scores - peak[..., None])
    cross_exp = jnp.exp(cross_scores - row_peak[..., None])
    own_totals = jnp.sum(own_exp, -1)
    row_totals = own_totals[..., 0] + jnp.sum(cross_exp, -1)
    totals = jnp.where(first_mask, row_totals[..., None], own_totals)
    return (own_exp / totals[..., None], cross_exp / row_totals[..., None])


def row_softmax(own_scores, cross_scores):
    peak = jnp.maximum(jnp.max(own_scores, -1), jnp.max(cross_scores, -1))[..., None]
    own_exp = jnp.exp(own_scores - peak)
    cross_exp = jnp.exp(cross_scores - peak)
    totals = (jnp.sum(own_exp, -1) + jnp.sum(cross_exp, -1))[..., None]
    return (own_exp / totals, cross_exp / totals)


def gather_cand(block, axis):
    count = lax.axis_size("cand")
    if count > 8:
        return lax.all_gather(block, "cand", axis=axis, tiled=True)
    me = lax.axis_index("cand")
    parts = [block] + [
        lax.ppermute(block, "cand", [(j, (j + k) % count) for j in range(count)])
        for k in range(1, count)
    ]
    ordered = jnp.take(jnp.stack(parts, 0), (me - jnp.arange(count)) % count, axis=0)
    ordered = jnp.moveaxis(ordered, 0, axis)
    shape = block.shape[:axis] + (count * block.shape[axis],) + block.shape[axis + 1 :]
    return ordered.reshape(shape)


def sum_cand(block):
    count = lax.axis_size("cand")
    if count > 8:
        return lax.psum(block, "cand")
    total = block
    for k in range(1, count):
        total = total + lax.ppermute(block, "cand", [(j, (j + k) % count) for j in range(count)])
    return total


def scatter_cand(block, axis, total_type=None):
    count = lax.axis_size("cand")
    if count > 8:
        return lax.psum_scatter(block, "cand", scatter_dimension=axis, tiled=True)
    total_type = total_type or block.dtype
    me = lax.axis_index("cand")
    width = block.shape[axis] // count
    total = lax.dynamic_slice_in_dim(block, me * width, width, axis).astype(total_type)
    for k in range(1, count):
        piece = lax.dynamic_slice_in_dim(block, ((me + k) % count) * width, width, axis)
        moved = lax.ppermute(piece, "cand", [(j, (j + k) % count) for j in range(count)])
        total = total + moved.astype(total_type)
    return total


def gather_mp(block, axis):
    if lax.axis_size("mp") != 2:
        return lax.all_gather(block, "mp", axis=axis, tiled=True)
    other = lax.ppermute(block, "mp", [(0, 1), (1, 0)])
    return jnp.where(
        lax.axis_index("mp") == 0,
        jnp.concatenate([block, other], axis),
        jnp.concatenate([other, block], axis),
    )


def sum_query(block):
    if lax.axis_size("query") != 2:
        return lax.psum(block, "query")
    other = lax.ppermute(block, "query", [(0, 1), (1, 0)])
    return block.astype(jnp.float32) + other.astype(jnp.float32)


def local(
    tokens,
    lengths,
    teacher,
    w_first,
    w_out_first,
    gain_first,
    w_last,
    w_out_last,
    gain_last,
    w_score,
):
    lists, local_cands, seq_len, model_width = tokens.shape
    local_width = w_first.shape[2]
    local_heads = local_width // HEAD_DIM
    cand_count = local_cands * lax.axis_size("cand")
    query_count = lists * lax.axis_size("query")
    score_scale = HEAD_DIM ** (-0.5)
    positions = jnp.arange(seq_len)
    first_mask = positions == 0
    own_valid = positions[None, None, :] < lengths[:, :, None]
    local_ids = lax.axis_index("cand") * local_cands + jnp.arange(local_cands)
    cross_valid = local_ids[:, None] != jnp.arange(cand_count)[None, :]
    head_shape = (lists, local_cands, seq_len, local_heads, HEAD_DIM)
    cls_shape = (lists, cand_count, local_heads, HEAD_DIM)
    out_first_full = gather_mp(w_out_first, 0)
    other_last = lax.ppermute(w_last, "mp", [(0, 1), (1, 0)])
    out_last_full = gather_mp(w_out_last, 0)
    cls_and_teacher = gather_cand(
        jnp.concatenate([tokens[:, :, 0].astype(jnp.float32), teacher[..., None]], -1), 1
    )
    cls_tokens = cls_and_teacher[..., :model_width].astype(jnp.bfloat16)
    teacher_all = cls_and_teacher[..., model_width]
    row_count = lists * local_cands * seq_len
    swap = [(0, 1), (1, 0)]
    paired_lists = lax.axis_size("query") == 2
    if paired_lists:
        other_tokens = lax.ppermute(tokens.reshape(row_count, model_width), "query", swap)
    projected = mixed("qcsd,kdf->kqcsf", tokens, w_first).astype(jnp.bfloat16)
    cls_projected = mixed("qcd,kdf->kqcf", cls_tokens, w_first[1:]).astype(jnp.bfloat16)
    gathered_keys = cls_projected[0]
    gathered_vals = cls_projected[1]
    first_query = projected[0].reshape(head_shape)
    first_keys = projected[1].reshape(head_shape)
    first_vals = projected[2].reshape(head_shape)
    cls_keys = gathered_keys.reshape(cls_shape)
    cls_vals = gathered_vals.reshape(cls_shape)
    own_scores = mixed("qcshe,qcthe->qchst", first_query, first_keys) * score_scale
    own_scores = jnp.where(own_valid[:, :, None, None, :], own_scores, NEGATIVE)
    cross_scores = mixed("qche,qdhe->qchd", first_query[:, :, 0], cls_keys) * score_scale
    cross_scores = jnp.where(cross_valid[None, :, None, :], cross_scores, NEGATIVE)
    own_prob, cross_prob = split_softmax(own_scores, cross_scores, first_mask)
    own_weight = own_prob.astype(jnp.bfloat16)
    cross_weight = cross_prob.astype(jnp.bfloat16)
    attended = mixed("qchst,qcthe->qcshe", own_weight, first_vals)
    attended_cls = mixed("qchd,qdhe->qche", cross_weight, cls_vals)
    attended = jnp.where(
        first_mask[None, None, :, None, None], attended + attended_cls[:, :, None], attended
    )
    first_mixed = attended.reshape(lists, local_cands, seq_len, local_width).astype(jnp.bfloat16)
    first_joined = lax.all_gather(first_mixed, "mp", axis=3, tiled=True)
    residual_first = tokens.astype(jnp.float32) + mixed(
        "qcsf,fd->qcsd", first_joined, out_first_full
    )
    normed_first, unit_first, inverse_first = norm_forward(residual_first, gain_first)
    hidden = normed_first.astype(jnp.bfloat16)
    last_query = mixed("qcd,df->qcf", hidden[:, :, 0], w_last[0]).astype(jnp.bfloat16)
    last_kv = mixed("qcsd,kdf->kqcsf", hidden, w_last[1:]).astype(jnp.bfloat16)
    gathered_kv_last = gather_cand(
        jnp.concatenate([last_kv[0][:, :, 0], last_kv[1][:, :, 0]], -1), 1
    )
    gathered_keys_last = gathered_kv_last[..., :local_width]
    gathered_vals_last = gathered_kv_last[..., local_width:]
    last_heads = last_query.reshape(lists, local_cands, local_heads, HEAD_DIM)
    last_keys = last_kv[0].reshape(head_shape)
    last_vals = last_kv[1].reshape(head_shape)
    cls_keys_last = gathered_keys_last.reshape(cls_shape)
    cls_vals_last = gathered_vals_last.reshape(cls_shape)
    own_last = mixed("qche,qcthe->qcht", last_heads, last_keys) * score_scale
    own_last = jnp.where(own_valid[:, :, None, :], own_last, NEGATIVE)
    cross_last = mixed("qche,qdhe->qchd", last_heads, cls_keys_last) * score_scale
    cross_last = jnp.where(cross_valid[None, :, None, :], cross_last, NEGATIVE)
    own_last_prob, cross_last_prob = row_softmax(own_last, cross_last)
    own_last_weight = own_last_prob.astype(jnp.bfloat16)
    cross_last_weight = cross_last_prob.astype(jnp.bfloat16)
    attended_last = mixed("qcht,qcthe->qche", own_last_weight, last_vals) + mixed(
        "qchd,qdhe->qche", cross_last_weight, cls_vals_last
    )
    last_mixed = attended_last.reshape(lists, local_cands, local_width).astype(jnp.bfloat16)
    last_joined = lax.all_gather(last_mixed, "mp", axis=2, tiled=True)
    residual_last = hidden[:, :, 0].astype(jnp.float32) + mixed(
        "qcf,fd->qcd", last_joined, out_last_full
    )
    normed_last, unit_last, inverse_last = norm_forward(residual_last, gain_last)
    scores = jnp.einsum("qcd,d->qc", normed_last, w_score, precision=lax.Precision.HIGHEST)
    score_exp = jnp.exp(scores)
    teacher_peak = jnp.max(teacher_all, 1)
    teacher_exp = jnp.exp(teacher - teacher_peak[:, None])
    teacher_totals = jnp.sum(jnp.exp(teacher_all - teacher_peak[:, None]), 1)
    score_totals = sum_cand(jnp.sum(score_exp, 1))
    student_prob = score_exp / score_totals[:, None]
    teacher_prob = teacher_exp / teacher_totals[:, None]
    score_grad = LOSS_SCALE * (student_prob - teacher_prob) / query_count
    grad_last = norm_backward(score_grad[..., None] * w_score, unit_last, inverse_last, gain_last)
    grad_last_low = grad_last.astype(jnp.bfloat16)
    grad_mixed_last = (
        mixed("qcd,fd->qcf", grad_last_low, w_out_last)
        .astype(jnp.bfloat16)
        .reshape(lists, local_cands, local_heads, HEAD_DIM)
    )
    own_dot = mixed("qche,qcthe->qcht", grad_mixed_last, last_vals)
    cross_dot = mixed("qche,qdhe->qchd", grad_mixed_last, cls_vals_last)
    centre = jnp.sum(own_last_prob * own_dot, -1, keepdims=True) + jnp.sum(
        cross_last_prob * cross_dot, -1, keepdims=True
    )
    own_slope = (own_last_prob * (own_dot - centre)).astype(jnp.bfloat16)
    cross_slope = (cross_last_prob * (cross_dot - centre)).astype(jnp.bfloat16)
    grad_query_last = (
        (
            (
                mixed("qcht,qcthe->qche", own_slope, last_keys)
                + mixed("qchd,qdhe->qche", cross_slope, cls_keys_last)
            )
            * score_scale
        )
        .astype(jnp.bfloat16)
        .reshape(lists, local_cands, local_width)
    )
    own_key_grad = (mixed("qcht,qche->qcthe", own_slope, last_heads) * score_scale).reshape(
        lists, local_cands, seq_len, local_width
    )
    own_val_grad = mixed("qcht,qche->qcthe", own_last_weight, grad_mixed_last).reshape(
        lists, local_cands, seq_len, local_width
    )
    cls_key_terms = (mixed("qchd,qche->qdhe", cross_slope, last_heads) * score_scale).reshape(
        lists, cand_count, local_width
    )
    cls_val_terms = mixed("qchd,qche->qdhe", cross_last_weight, grad_mixed_last).reshape(
        lists, cand_count, local_width
    )
    back_terms = scatter_cand(jnp.concatenate([cls_key_terms, cls_val_terms], -1), 1)
    back_keys = back_terms[..., :local_width]
    back_vals = back_terms[..., local_width:]
    first_cols = first_mask[None, None, :, None]
    key_grad = jnp.where(first_cols, own_key_grad + back_keys[:, :, None], own_key_grad).astype(
        jnp.bfloat16
    )
    val_grad = jnp.where(first_cols, own_val_grad + back_vals[:, :, None], own_val_grad).astype(
        jnp.bfloat16
    )
    joined = lax.all_gather(
        jnp.concatenate([key_grad, val_grad, grad_query_last[:, :, None]], 2),
        "mp",
        axis=3,
        tiled=True,
    )
    partner = lax.dynamic_slice_in_dim(
        joined, (1 - lax.axis_index("mp")) * local_width, local_width, 3
    )
    summed_term = (
        mixed("qcsf,df->qcsd", key_grad, w_last[1])
        + mixed("qcsf,df->qcsd", val_grad, w_last[2])
        + mixed("qcsf,df->qcsd", partner[:, :, :seq_len], other_last[1])
        + mixed("qcsf,df->qcsd", partner[:, :, seq_len : 2 * seq_len], other_last[2])
    )
    query_term = mixed("qcf,df->qcd", grad_query_last, w_last[0]) + mixed(
        "qcf,df->qcd", partner[:, :, 2 * seq_len], other_last[0]
    )
    summed_term = jnp.where(first_cols, summed_term + query_term[:, :, None], summed_term)
    grad_hidden = jnp.where(first_cols, summed_term + grad_last[:, :, None], summed_term)
    grad_first = norm_backward(grad_hidden, unit_first, inverse_first, gain_first).astype(
        jnp.bfloat16
    )
    grad_mixed_first = (
        mixed("qcsd,fd->qcsf", grad_first, w_out_first).astype(jnp.bfloat16).reshape(head_shape)
    )
    own_dot_first = mixed("qcshe,qcthe->qchst", grad_mixed_first, first_vals)
    cross_dot_first = mixed("qche,qdhe->qchd", grad_mixed_first[:, :, 0], cls_vals)
    own_part = jnp.sum(own_prob * own_dot_first, -1)
    row_part = own_part[..., 0] + jnp.sum(cross_prob * cross_dot_first, -1)
    centre_first = jnp.where(first_mask, row_part[..., None], own_part)
    own_slope_first = (own_prob * (own_dot_first - centre_first[..., None])).astype(jnp.bfloat16)
    cross_slope_first = (cross_prob * (cross_dot_first - row_part[..., None])).astype(jnp.bfloat16)
    query_grad = mixed("qchst,qcthe->qcshe", own_slope_first, first_keys)
    query_cls = mixed("qchd,qdhe->qche", cross_slope_first, cls_keys)
    query_grad = jnp.where(
        first_mask[None, None, :, None, None], query_grad + query_cls[:, :, None], query_grad
    )
    query_grad = (
        (query_grad * score_scale)
        .astype(jnp.bfloat16)
        .reshape(lists, local_cands, seq_len, local_width)
    )
    key_first = (mixed("qchst,qcshe->qcthe", own_slope_first, first_query) * score_scale).reshape(
        lists, local_cands, seq_len, local_width
    )
    val_first = mixed("qchst,qcshe->qcthe", own_weight, grad_mixed_first).reshape(
        lists, local_cands, seq_len, local_width
    )
    cls_key_first = (
        mixed("qchd,qche->qdhe", cross_slope_first, first_query[:, :, 0]) * score_scale
    ).reshape(lists, cand_count, local_width)
    cls_val_first = mixed("qchd,qche->qdhe", cross_weight, grad_mixed_first[:, :, 0]).reshape(
        lists, cand_count, local_width
    )
    key_first = key_first.astype(jnp.bfloat16)
    val_first = val_first.astype(jnp.bfloat16)
    stacked = jnp.stack([query_grad, key_first, val_first], 3).reshape(row_count, 3, local_width)
    cross_rows = lists * cand_count
    cross_stacked = jnp.stack(
        [jnp.zeros_like(cls_key_first), cls_key_first, cls_val_first], 2
    ).astype(jnp.bfloat16)
    all_rows = jnp.concatenate(
        [stacked, cross_stacked.reshape(cross_rows, 3, local_width)], 0
    )
    all_tokens = jnp.concatenate(
        [tokens.reshape(row_count, model_width), cls_tokens.reshape(cross_rows, model_width)], 0
    )
    if not paired_lists:
        partial_grad = lax.psum_scatter(
            mixed("rd,rkf->dkf", all_tokens, all_rows).astype(jnp.bfloat16),
            "cand",
            scatter_dimension=0,
            tiled=True,
        )
        return sum_query(partial_grad).astype(jnp.float32)
    half = 3 * local_width // 2
    side = lax.axis_index("query")
    flat_rows = all_rows.reshape(all_rows.shape[0], 3 * local_width)
    cls_flat = cls_tokens.reshape(cross_rows, model_width)
    own_half = lax.dynamic_slice_in_dim(flat_rows, side * half, half, 1)
    given_half = lax.dynamic_slice_in_dim(flat_rows, (1 - side) * half, half, 1)
    sent = lax.ppermute(
        jnp.concatenate([given_half.reshape(-1), cls_flat.reshape(-1)]), "query", swap
    )
    other_half = sent[: given_half.size].reshape(given_half.shape)
    other_cls = sent[given_half.size :].reshape(cls_flat.shape)
    paired = (
        mixed("rd,rf->df", all_tokens, own_half)
        + mixed("rd,rf->df", other_tokens, other_half[:row_count])
        + mixed("rd,rf->df", other_cls, other_half[row_count:])
    )
    reduced = scatter_cand(paired.astype(jnp.bfloat16), 0, jnp.float32).astype(jnp.bfloat16)
    partner = lax.ppermute(reduced, "query", swap)
    joined = jnp.where(
        side == 0,
        jnp.concatenate([reduced, partner], 1),
        jnp.concatenate([partner, reduced], 1),
    )
    return joined.reshape(joined.shape[0], 3, local_width).astype(jnp.float32)


def solution(mesh):
    return jax.shard_map(
        local,
        mesh=mesh,
        in_specs=(
            P(("groups", "query"), "cand", None, None),
            P(("groups", "query"), "cand"),
            P(("groups", "query"), "cand"),
            P(None, None, "mp"),
            P("mp", None),
            P(),
            P(None, None, "mp"),
            P("mp", None),
            P(),
            P(),
        ),
        out_specs=P(("groups", "cand"), None, "mp"),
        check_vma=False,
    )
```

```python
import jax
import jax.numpy as jnp
from jax import lax
from jax.sharding import PartitionSpec as P

HEAD_DIM = 64


EPSILON = 1e-05
LOSS_SCALE = 1024.0
NEGATIVE = -1e30


def mixed(pattern, former, latter):
    return jnp.einsum(pattern, former, latter, preferred_element_type=jnp.float32)


def norm_forward(matrix, scales):
    center = matrix - jnp.mean(matrix, -1, keepdims=True)
    inverse = lax.rsqrt(jnp.mean(center * center, -1, keepdims=True) + EPSILON)
    normed = center * inverse
    return (normed * scales, normed, inverse)


def norm_backward(incoming, normed, inverse, scales):
    scaled = incoming * scales
    return inverse * (
        scaled
        - jnp.mean(scaled, -1, keepdims=True)
        - normed * jnp.mean(scaled * normed, -1, keepdims=True)
    )


def split_softmax(own_scores, cross_scores, first_mask):
    own_peak = jnp.max(own_scores, -1)
    row_peak = jnp.maximum(own_peak[..., 0], jnp.max(cross_scores, -1))
    peak = jnp.where(first_mask, row_peak[..., None], own_peak)
    own_exp = jnp.exp(own_scores - peak[..., None])
    cross_exp = jnp.exp(cross_scores - row_peak[..., None])
    own_totals = jnp.sum(own_exp, -1)
    row_totals = own_totals[..., 0] + jnp.sum(cross_exp, -1)
    totals = jnp.where(first_mask, row_totals[..., None], own_totals)
    return (own_exp / totals[..., None], cross_exp / row_totals[..., None])


def row_softmax(own_scores, cross_scores):
    peak = jnp.maximum(jnp.max(own_scores, -1), jnp.max(cross_scores, -1))[..., None]
    own_exp = jnp.exp(own_scores - peak)
    cross_exp = jnp.exp(cross_scores - peak)
    totals = (jnp.sum(own_exp, -1) + jnp.sum(cross_exp, -1))[..., None]
    return (own_exp / totals, cross_exp / totals)


def gather_cand(block, axis):
    count = lax.axis_size("cand")
    if count > 8:
        return lax.all_gather(block, "cand", axis=axis, tiled=True)
    me = lax.axis_index("cand")
    parts = [block] + [
        lax.ppermute(block, "cand", [(j, (j + k) % count) for j in range(count)])
        for k in range(1, count)
    ]
    ordered = jnp.take(jnp.stack(parts, 0), (me - jnp.arange(count)) % count, axis=0)
    ordered = jnp.moveaxis(ordered, 0, axis)
    shape = block.shape[:axis] + (count * block.shape[axis],) + block.shape[axis + 1 :]
    return ordered.reshape(shape)


def sum_cand(block):
    count = lax.axis_size("cand")
    if count > 8:
        return lax.psum(block, "cand")
    total = block
    for k in range(1, count):
        total = total + lax.ppermute(block, "cand", [(j, (j + k) % count) for j in range(count)])
    return total


def scatter_cand(block, axis, total_type=None):
    count = lax.axis_size("cand")
    if count > 8:
        return lax.psum_scatter(block, "cand", scatter_dimension=axis, tiled=True)
    total_type = total_type or block.dtype
    me = lax.axis_index("cand")
    width = block.shape[axis] // count
    total = lax.dynamic_slice_in_dim(block, me * width, width, axis).astype(total_type)
    for k in range(1, count):
        piece = lax.dynamic_slice_in_dim(block, ((me + k) % count) * width, width, axis)
        moved = lax.ppermute(piece, "cand", [(j, (j + k) % count) for j in range(count)])
        total = total + moved.astype(total_type)
    return total


def gather_mp(block, axis):
    if lax.axis_size("mp") != 2:
        return lax.all_gather(block, "mp", axis=axis, tiled=True)
    other = lax.ppermute(block, "mp", [(0, 1), (1, 0)])
    return jnp.where(
        lax.axis_index("mp") == 0,
        jnp.concatenate([block, other], axis),
        jnp.concatenate([other, block], axis),
    )


def sum_query(block):
    if lax.axis_size("query") != 2:
        return lax.psum(block, "query")
    other = lax.ppermute(block, "query", [(0, 1), (1, 0)])
    return block.astype(jnp.float32) + other.astype(jnp.float32)


def local(
    tokens,
    lengths,
    teacher,
    w_first,
    w_out_first,
    gain_first,
    w_last,
    w_out_last,
    gain_last,
    w_score,
):
    lists, local_cands, seq_len, model_width = tokens.shape
    local_width = w_first.shape[2]
    local_heads = local_width // HEAD_DIM
    cand_count = local_cands * lax.axis_size("cand")
    query_count = lists * lax.axis_size("query")
    score_scale = HEAD_DIM ** (-0.5)
    positions = jnp.arange(seq_len)
    first_mask = positions == 0
    own_valid = positions[None, None, :] < lengths[:, :, None]
    local_ids = lax.axis_index("cand") * local_cands + jnp.arange(local_cands)
    cross_valid = local_ids[:, None] != jnp.arange(cand_count)[None, :]
    head_shape = (lists, local_cands, seq_len, local_heads, HEAD_DIM)
    cls_shape = (lists, cand_count, local_heads, HEAD_DIM)
    swap = [(0, 1), (1, 0)]
    other_out_first = lax.ppermute(w_out_first, "mp", swap)
    last_full = gather_mp(w_last, 2)
    other_out_last = lax.ppermute(w_out_last, "mp", swap)
    partner_at = (1 - lax.axis_index("mp")) * local_width
    cls_and_teacher = gather_cand(
        jnp.concatenate([tokens[:, :, 0].astype(jnp.float32), teacher[..., None]], -1), 1
    )
    cls_tokens = cls_and_teacher[..., :model_width].astype(jnp.bfloat16)
    teacher_all = cls_and_teacher[..., model_width]
    row_count = lists * local_cands * seq_len
    swap = [(0, 1), (1, 0)]
    paired_lists = lax.axis_size("query") == 2
    if paired_lists:
        other_tokens = lax.ppermute(tokens.reshape(row_count, model_width), "query", swap)
    projected = mixed("qcsd,kdf->kqcsf", tokens, w_first).astype(jnp.bfloat16)
    cls_projected = mixed("qcd,kdf->kqcf", cls_tokens, w_first[1:]).astype(jnp.bfloat16)
    gathered_keys = cls_projected[0]
    gathered_vals = cls_projected[1]
    first_query = projected[0].reshape(head_shape)
    first_keys = projected[1].reshape(head_shape)
    first_vals = projected[2].reshape(head_shape)
    cls_keys = gathered_keys.reshape(cls_shape)
    cls_vals = gathered_vals.reshape(cls_shape)
    own_scores = mixed("qcshe,qcthe->qchst", first_query, first_keys) * score_scale
    own_scores = jnp.where(own_valid[:, :, None, None, :], own_scores, NEGATIVE)
    cross_scores = mixed("qche,qdhe->qchd", first_query[:, :, 0], cls_keys) * score_scale
    cross_scores = jnp.where(cross_valid[None, :, None, :], cross_scores, NEGATIVE)
    own_prob, cross_prob = split_softmax(own_scores, cross_scores, first_mask)
    own_weight = own_prob.astype(jnp.bfloat16)
    cross_weight = cross_prob.astype(jnp.bfloat16)
    attended = mixed("qchst,qcthe->qcshe", own_weight, first_vals)
    attended_cls = mixed("qchd,qdhe->qche", cross_weight, cls_vals)
    attended = jnp.where(
        first_mask[None, None, :, None, None], attended + attended_cls[:, :, None], attended
    )
    first_mixed = attended.reshape(lists, local_cands, seq_len, local_width).astype(jnp.bfloat16)
    first_joined = lax.all_gather(first_mixed, "mp", axis=3, tiled=True)
    residual_first = (
        tokens.astype(jnp.float32)
        + mixed("qcsf,fd->qcsd", first_mixed, w_out_first)
        + mixed(
            "qcsf,fd->qcsd",
            lax.dynamic_slice_in_dim(first_joined, partner_at, local_width, 3),
            other_out_first,
        )
    )
    normed_first, unit_first, inverse_first = norm_forward(residual_first, gain_first)
    hidden = normed_first.astype(jnp.bfloat16)
    last_query = mixed("qcd,df->qcf", hidden[:, :, 0], w_last[0]).astype(jnp.bfloat16)
    last_kv = mixed("qcsd,kdf->kqcsf", hidden, w_last[1:]).astype(jnp.bfloat16)
    gathered_kv_last = gather_cand(
        jnp.concatenate([last_kv[0][:, :, 0], last_kv[1][:, :, 0]], -1), 1
    )
    gathered_keys_last = gathered_kv_last[..., :local_width]
    gathered_vals_last = gathered_kv_last[..., local_width:]
    last_heads = last_query.reshape(lists, local_cands, local_heads, HEAD_DIM)
    last_keys = last_kv[0].reshape(head_shape)
    last_vals = last_kv[1].reshape(head_shape)
    cls_keys_last = gathered_keys_last.reshape(cls_shape)
    cls_vals_last = gathered_vals_last.reshape(cls_shape)
    own_last = mixed("qche,qcthe->qcht", last_heads, last_keys) * score_scale
    own_last = jnp.where(own_valid[:, :, None, :], own_last, NEGATIVE)
    cross_last = mixed("qche,qdhe->qchd", last_heads, cls_keys_last) * score_scale
    cross_last = jnp.where(cross_valid[None, :, None, :], cross_last, NEGATIVE)
    own_last_prob, cross_last_prob = row_softmax(own_last, cross_last)
    own_last_weight = own_last_prob.astype(jnp.bfloat16)
    cross_last_weight = cross_last_prob.astype(jnp.bfloat16)
    attended_last = mixed("qcht,qcthe->qche", own_last_weight, last_vals) + mixed(
        "qchd,qdhe->qche", cross_last_weight, cls_vals_last
    )
    last_mixed = attended_last.reshape(lists, local_cands, local_width).astype(jnp.bfloat16)
    last_joined = lax.all_gather(last_mixed, "mp", axis=2, tiled=True)
    residual_last = (
        hidden[:, :, 0].astype(jnp.float32)
        + mixed("qcf,fd->qcd", last_mixed, w_out_last)
        + mixed(
            "qcf,fd->qcd",
            lax.dynamic_slice_in_dim(last_joined, partner_at, local_width, 2),
            other_out_last,
        )
    )
    normed_last, unit_last, inverse_last = norm_forward(residual_last, gain_last)
    scores = jnp.einsum("qcd,d->qc", normed_last, w_score, precision=lax.Precision.HIGHEST)
    score_exp = jnp.exp(scores)
    teacher_peak = jnp.max(teacher_all, 1)
    teacher_exp = jnp.exp(teacher - teacher_peak[:, None])
    teacher_totals = jnp.sum(jnp.exp(teacher_all - teacher_peak[:, None]), 1)
    score_totals = sum_cand(jnp.sum(score_exp, 1))
    student_prob = score_exp / score_totals[:, None]
    teacher_prob = teacher_exp / teacher_totals[:, None]
    score_grad = LOSS_SCALE * (student_prob - teacher_prob) / query_count
    grad_last = norm_backward(score_grad[..., None] * w_score, unit_last, inverse_last, gain_last)
    grad_last_low = grad_last.astype(jnp.bfloat16)
    grad_mixed_last = (
        mixed("qcd,fd->qcf", grad_last_low, w_out_last)
        .astype(jnp.bfloat16)
        .reshape(lists, local_cands, local_heads, HEAD_DIM)
    )
    own_dot = mixed("qche,qcthe->qcht", grad_mixed_last, last_vals)
    cross_dot = mixed("qche,qdhe->qchd", grad_mixed_last, cls_vals_last)
    centre = jnp.sum(own_last_prob * own_dot, -1, keepdims=True) + jnp.sum(
        cross_last_prob * cross_dot, -1, keepdims=True
    )
    own_slope = (own_last_prob * (own_dot - centre)).astype(jnp.bfloat16)
    cross_slope = (cross_last_prob * (cross_dot - centre)).astype(jnp.bfloat16)
    grad_query_last = (
        (
            (
                mixed("qcht,qcthe->qche", own_slope, last_keys)
                + mixed("qchd,qdhe->qche", cross_slope, cls_keys_last)
            )
            * score_scale
        )
        .astype(jnp.bfloat16)
        .reshape(lists, local_cands, local_width)
    )
    own_key_grad = (mixed("qcht,qche->qcthe", own_slope, last_heads) * score_scale).reshape(
        lists, local_cands, seq_len, local_width
    )
    own_val_grad = mixed("qcht,qche->qcthe", own_last_weight, grad_mixed_last).reshape(
        lists, local_cands, seq_len, local_width
    )
    cls_key_terms = (mixed("qchd,qche->qdhe", cross_slope, last_heads) * score_scale).reshape(
        lists, cand_count, local_width
    )
    cls_val_terms = mixed("qchd,qche->qdhe", cross_last_weight, grad_mixed_last).reshape(
        lists, cand_count, local_width
    )
    back_terms = scatter_cand(jnp.concatenate([cls_key_terms, cls_val_terms], -1), 1)
    back_keys = back_terms[..., :local_width]
    back_vals = back_terms[..., local_width:]
    first_cols = first_mask[None, None, :, None]
    key_grad = jnp.where(first_cols, own_key_grad + back_keys[:, :, None], own_key_grad).astype(
        jnp.bfloat16
    )
    val_grad = jnp.where(first_cols, own_val_grad + back_vals[:, :, None], own_val_grad).astype(
        jnp.bfloat16
    )
    joined = lax.all_gather(
        jnp.concatenate([key_grad, val_grad, grad_query_last[:, :, None]], 2),
        "mp",
        axis=3,
        tiled=True,
    )
    key_joined = joined[:, :, :seq_len]
    val_joined = joined[:, :, seq_len : 2 * seq_len]
    query_joined = joined[:, :, 2 * seq_len]
    summed_term = mixed("qcsf,df->qcsd", key_joined, last_full[1]) + mixed(
        "qcsf,df->qcsd", val_joined, last_full[2]
    )
    query_term = mixed("qcf,df->qcd", query_joined, last_full[0])
    summed_term = jnp.where(first_cols, summed_term + query_term[:, :, None], summed_term)
    grad_hidden = jnp.where(first_cols, summed_term + grad_last[:, :, None], summed_term)
    grad_first = norm_backward(grad_hidden, unit_first, inverse_first, gain_first).astype(
        jnp.bfloat16
    )
    grad_mixed_first = (
        mixed("qcsd,fd->qcsf", grad_first, w_out_first).astype(jnp.bfloat16).reshape(head_shape)
    )
    own_dot_first = mixed("qcshe,qcthe->qchst", grad_mixed_first, first_vals)
    cross_dot_first = mixed("qche,qdhe->qchd", grad_mixed_first[:, :, 0], cls_vals)
    own_part = jnp.sum(own_prob * own_dot_first, -1)
    row_part = own_part[..., 0] + jnp.sum(cross_prob * cross_dot_first, -1)
    centre_first = jnp.where(first_mask, row_part[..., None], own_part)
    own_slope_first = (own_prob * (own_dot_first - centre_first[..., None])).astype(jnp.bfloat16)
    cross_slope_first = (cross_prob * (cross_dot_first - row_part[..., None])).astype(jnp.bfloat16)
    query_grad = mixed("qchst,qcthe->qcshe", own_slope_first, first_keys)
    query_cls = mixed("qchd,qdhe->qche", cross_slope_first, cls_keys)
    query_grad = jnp.where(
        first_mask[None, None, :, None, None], query_grad + query_cls[:, :, None], query_grad
    )
    query_grad = (
        (query_grad * score_scale)
        .astype(jnp.bfloat16)
        .reshape(lists, local_cands, seq_len, local_width)
    )
    key_first = (mixed("qchst,qcshe->qcthe", own_slope_first, first_query) * score_scale).reshape(
        lists, local_cands, seq_len, local_width
    )
    val_first = mixed("qchst,qcshe->qcthe", own_weight, grad_mixed_first).reshape(
        lists, local_cands, seq_len, local_width
    )
    cls_key_first = (
        mixed("qchd,qche->qdhe", cross_slope_first, first_query[:, :, 0]) * score_scale
    ).reshape(lists, cand_count, local_width)
    cls_val_first = mixed("qchd,qche->qdhe", cross_weight, grad_mixed_first[:, :, 0]).reshape(
        lists, cand_count, local_width
    )
    key_first = key_first.astype(jnp.bfloat16)
    val_first = val_first.astype(jnp.bfloat16)
    stacked = jnp.stack([query_grad, key_first, val_first], 3).reshape(row_count, 3, local_width)
    cross_rows = lists * cand_count
    cross_stacked = jnp.stack(
        [jnp.zeros_like(cls_key_first), cls_key_first, cls_val_first], 2
    ).astype(jnp.bfloat16)
    all_rows = jnp.concatenate(
        [stacked, cross_stacked.reshape(cross_rows, 3, local_width)], 0
    )
    all_tokens = jnp.concatenate(
        [tokens.reshape(row_count, model_width), cls_tokens.reshape(cross_rows, model_width)], 0
    )
    if not paired_lists:
        partial_grad = lax.psum_scatter(
            mixed("rd,rkf->dkf", all_tokens, all_rows).astype(jnp.bfloat16),
            "cand",
            scatter_dimension=0,
            tiled=True,
        )
        return sum_query(partial_grad).astype(jnp.float32)
    half = 3 * local_width // 2
    side = lax.axis_index("query")
    flat_rows = all_rows.reshape(all_rows.shape[0], 3 * local_width)
    cls_flat = cls_tokens.reshape(cross_rows, model_width)
    own_half = lax.dynamic_slice_in_dim(flat_rows, side * half, half, 1)
    given_half = lax.dynamic_slice_in_dim(flat_rows, (1 - side) * half, half, 1)
    sent = lax.ppermute(
        jnp.concatenate([given_half.reshape(-1), cls_flat.reshape(-1)]), "query", swap
    )
    other_half = sent[: given_half.size].reshape(given_half.shape)
    other_cls = sent[given_half.size :].reshape(cls_flat.shape)
    paired = (
        mixed("rd,rf->df", all_tokens, own_half)
        + mixed("rd,rf->df", other_tokens, other_half[:row_count])
        + mixed("rd,rf->df", other_cls, other_half[row_count:])
    )
    reduced = scatter_cand(paired.astype(jnp.bfloat16), 0, jnp.float32).astype(jnp.bfloat16)
    partner = lax.ppermute(reduced, "query", swap)
    joined = jnp.where(
        side == 0,
        jnp.concatenate([reduced, partner], 1),
        jnp.concatenate([partner, reduced], 1),
    )
    return joined.reshape(joined.shape[0], 3, local_width).astype(jnp.float32)


def solution(mesh):
    return jax.shard_map(
        local,
        mesh=mesh,
        in_specs=(
            P(("groups", "query"), "cand", None, None),
            P(("groups", "query"), "cand"),
            P(("groups", "query"), "cand"),
            P(None, None, "mp"),
            P("mp", None),
            P(),
            P(None, None, "mp"),
            P("mp", None),
            P(),
            P(),
        ),
        out_specs=P(("groups", "cand"), None, "mp"),
        check_vma=False,
    )
```

```python
import jax
import jax.numpy as jnp
from jax import lax
from jax.sharding import PartitionSpec as P

HEAD_DIM = 64


EPSILON = 1e-05
LOSS_SCALE = 1024.0
NEGATIVE = -1e30


def mixed(pattern, former, latter):
    return jnp.einsum(pattern, former, latter, preferred_element_type=jnp.float32)


def norm_forward(matrix, scales):
    center = matrix - jnp.mean(matrix, -1, keepdims=True)
    inverse = lax.rsqrt(jnp.mean(center * center, -1, keepdims=True) + EPSILON)
    normed = center * inverse
    return (normed * scales, normed, inverse)


def norm_backward(incoming, normed, inverse, scales):
    scaled = incoming * scales
    return inverse * (
        scaled
        - jnp.mean(scaled, -1, keepdims=True)
        - normed * jnp.mean(scaled * normed, -1, keepdims=True)
    )


def split_softmax(own_scores, cross_scores, first_mask):
    own_peak = jnp.max(own_scores, -1)
    row_peak = jnp.maximum(own_peak[..., 0], jnp.max(cross_scores, -1))
    peak = jnp.where(first_mask, row_peak[..., None], own_peak)
    own_exp = jnp.exp(own_scores - peak[..., None])
    cross_exp = jnp.exp(cross_scores - row_peak[..., None])
    own_totals = jnp.sum(own_exp, -1)
    row_totals = own_totals[..., 0] + jnp.sum(cross_exp, -1)
    totals = jnp.where(first_mask, row_totals[..., None], own_totals)
    return (own_exp / totals[..., None], cross_exp / row_totals[..., None])


def row_softmax(own_scores, cross_scores):
    peak = jnp.maximum(jnp.max(own_scores, -1), jnp.max(cross_scores, -1))[..., None]
    own_exp = jnp.exp(own_scores - peak)
    cross_exp = jnp.exp(cross_scores - peak)
    totals = (jnp.sum(own_exp, -1) + jnp.sum(cross_exp, -1))[..., None]
    return (own_exp / totals, cross_exp / totals)


def gather_cand(block, axis):
    count = lax.axis_size("cand")
    if count > 8:
        return lax.all_gather(block, "cand", axis=axis, tiled=True)
    me = lax.axis_index("cand")
    parts = [block] + [
        lax.ppermute(block, "cand", [(j, (j + k) % count) for j in range(count)])
        for k in range(1, count)
    ]
    ordered = jnp.take(jnp.stack(parts, 0), (me - jnp.arange(count)) % count, axis=0)
    ordered = jnp.moveaxis(ordered, 0, axis)
    shape = block.shape[:axis] + (count * block.shape[axis],) + block.shape[axis + 1 :]
    return ordered.reshape(shape)


def sum_cand(block):
    count = lax.axis_size("cand")
    if count > 8:
        return lax.psum(block, "cand")
    total = block
    for k in range(1, count):
        total = total + lax.ppermute(block, "cand", [(j, (j + k) % count) for j in range(count)])
    return total


def scatter_cand(block, axis, total_type=None):
    count = lax.axis_size("cand")
    if count > 8:
        return lax.psum_scatter(block, "cand", scatter_dimension=axis, tiled=True)
    total_type = total_type or block.dtype
    me = lax.axis_index("cand")
    width = block.shape[axis] // count
    total = lax.dynamic_slice_in_dim(block, me * width, width, axis).astype(total_type)
    for k in range(1, count):
        piece = lax.dynamic_slice_in_dim(block, ((me + k) % count) * width, width, axis)
        moved = lax.ppermute(piece, "cand", [(j, (j + k) % count) for j in range(count)])
        total = total + moved.astype(total_type)
    return total


def gather_mp(block, axis):
    if lax.axis_size("mp") != 2:
        return lax.all_gather(block, "mp", axis=axis, tiled=True)
    other = lax.ppermute(block, "mp", [(0, 1), (1, 0)])
    return jnp.where(
        lax.axis_index("mp") == 0,
        jnp.concatenate([block, other], axis),
        jnp.concatenate([other, block], axis),
    )


def sum_query(block):
    if lax.axis_size("query") != 2:
        return lax.psum(block, "query")
    other = lax.ppermute(block, "query", [(0, 1), (1, 0)])
    return block.astype(jnp.float32) + other.astype(jnp.float32)


def local(
    tokens,
    lengths,
    teacher,
    w_first,
    w_out_first,
    gain_first,
    w_last,
    w_out_last,
    gain_last,
    w_score,
):
    lists, local_cands, seq_len, model_width = tokens.shape
    local_width = w_first.shape[2]
    local_heads = local_width // HEAD_DIM
    cand_count = local_cands * lax.axis_size("cand")
    query_count = lists * lax.axis_size("query")
    score_scale = HEAD_DIM ** (-0.5)
    positions = jnp.arange(seq_len)
    first_mask = positions == 0
    own_valid = positions[None, None, :] < lengths[:, :, None]
    local_ids = lax.axis_index("cand") * local_cands + jnp.arange(local_cands)
    cross_valid = local_ids[:, None] != jnp.arange(cand_count)[None, :]
    head_shape = (lists, local_cands, seq_len, local_heads, HEAD_DIM)
    cls_shape = (lists, cand_count, local_heads, HEAD_DIM)
    out_first_full = gather_mp(w_out_first, 0)
    last_full = gather_mp(w_last, 2)
    out_last_full = gather_mp(w_out_last, 0)
    cls_and_teacher = gather_cand(
        jnp.concatenate([tokens[:, :, 0].astype(jnp.float32), teacher[..., None]], -1), 1
    )
    cls_tokens = cls_and_teacher[..., :model_width].astype(jnp.bfloat16)
    teacher_all = cls_and_teacher[..., model_width]
    row_count = lists * local_cands * seq_len
    swap = [(0, 1), (1, 0)]
    paired_lists = lax.axis_size("query") == 2
    if paired_lists:
        other_tokens = lax.ppermute(tokens.reshape(row_count, model_width), "query", swap)
    projected = mixed("qcsd,kdf->kqcsf", tokens, w_first).astype(jnp.bfloat16)
    cls_projected = mixed("qcd,kdf->kqcf", cls_tokens, w_first[1:]).astype(jnp.bfloat16)
    gathered_keys = cls_projected[0]
    gathered_vals = cls_projected[1]
    first_query = projected[0].reshape(head_shape)
    first_keys = projected[1].reshape(head_shape)
    first_vals = projected[2].reshape(head_shape)
    cls_keys = gathered_keys.reshape(cls_shape)
    cls_vals = gathered_vals.reshape(cls_shape)
    own_scores = mixed("qcshe,qcthe->qchst", first_query, first_keys) * score_scale
    own_scores = jnp.where(own_valid[:, :, None, None, :], own_scores, NEGATIVE)
    cross_scores = mixed("qche,qdhe->qchd", first_query[:, :, 0], cls_keys) * score_scale
    cross_scores = jnp.where(cross_valid[None, :, None, :], cross_scores, NEGATIVE)
    own_prob, cross_prob = split_softmax(own_scores, cross_scores, first_mask)
    own_weight = own_prob.astype(jnp.bfloat16)
    cross_weight = cross_prob.astype(jnp.bfloat16)
    attended = mixed("qchst,qcthe->qcshe", own_weight, first_vals)
    attended_cls = mixed("qchd,qdhe->qche", cross_weight, cls_vals)
    attended = jnp.where(
        first_mask[None, None, :, None, None], attended + attended_cls[:, :, None], attended
    )
    first_mixed = attended.reshape(lists, local_cands, seq_len, local_width).astype(jnp.bfloat16)
    first_joined = lax.all_gather(first_mixed, "mp", axis=3, tiled=True)
    residual_first = tokens.astype(jnp.float32) + mixed(
        "qcsf,fd->qcsd", first_joined, out_first_full
    )
    normed_first, unit_first, inverse_first = norm_forward(residual_first, gain_first)
    hidden = normed_first.astype(jnp.bfloat16)
    last_query = mixed("qcd,df->qcf", hidden[:, :, 0], w_last[0]).astype(jnp.bfloat16)
    last_kv = mixed("qcsd,kdf->kqcsf", hidden, w_last[1:]).astype(jnp.bfloat16)
    gathered_kv_last = gather_cand(
        jnp.concatenate([last_kv[0][:, :, 0], last_kv[1][:, :, 0]], -1), 1
    )
    gathered_keys_last = gathered_kv_last[..., :local_width]
    gathered_vals_last = gathered_kv_last[..., local_width:]
    last_heads = last_query.reshape(lists, local_cands, local_heads, HEAD_DIM)
    last_keys = last_kv[0].reshape(head_shape)
    last_vals = last_kv[1].reshape(head_shape)
    cls_keys_last = gathered_keys_last.reshape(cls_shape)
    cls_vals_last = gathered_vals_last.reshape(cls_shape)
    own_last = mixed("qche,qcthe->qcht", last_heads, last_keys) * score_scale
    own_last = jnp.where(own_valid[:, :, None, :], own_last, NEGATIVE)
    cross_last = mixed("qche,qdhe->qchd", last_heads, cls_keys_last) * score_scale
    cross_last = jnp.where(cross_valid[None, :, None, :], cross_last, NEGATIVE)
    own_last_prob, cross_last_prob = row_softmax(own_last, cross_last)
    own_last_weight = own_last_prob.astype(jnp.bfloat16)
    cross_last_weight = cross_last_prob.astype(jnp.bfloat16)
    attended_last = mixed("qcht,qcthe->qche", own_last_weight, last_vals) + mixed(
        "qchd,qdhe->qche", cross_last_weight, cls_vals_last
    )
    last_mixed = attended_last.reshape(lists, local_cands, local_width).astype(jnp.bfloat16)
    last_joined = lax.all_gather(last_mixed, "mp", axis=2, tiled=True)
    residual_last = hidden[:, :, 0].astype(jnp.float32) + mixed(
        "qcf,fd->qcd", last_joined, out_last_full
    )
    normed_last, unit_last, inverse_last = norm_forward(residual_last, gain_last)
    scores = jnp.einsum("qcd,d->qc", normed_last, w_score, precision=lax.Precision.HIGHEST)
    score_exp = jnp.exp(scores)
    teacher_peak = jnp.max(teacher_all, 1)
    teacher_exp = jnp.exp(teacher - teacher_peak[:, None])
    teacher_totals = jnp.sum(jnp.exp(teacher_all - teacher_peak[:, None]), 1)
    score_totals = sum_cand(jnp.sum(score_exp, 1))
    student_prob = score_exp / score_totals[:, None]
    teacher_prob = teacher_exp / teacher_totals[:, None]
    score_grad = LOSS_SCALE * (student_prob - teacher_prob) / query_count
    grad_last = norm_backward(score_grad[..., None] * w_score, unit_last, inverse_last, gain_last)
    grad_last_low = grad_last.astype(jnp.bfloat16)
    grad_mixed_last = (
        mixed("qcd,fd->qcf", grad_last_low, w_out_last)
        .astype(jnp.bfloat16)
        .reshape(lists, local_cands, local_heads, HEAD_DIM)
    )
    own_dot = mixed("qche,qcthe->qcht", grad_mixed_last, last_vals)
    cross_dot = mixed("qche,qdhe->qchd", grad_mixed_last, cls_vals_last)
    centre = jnp.sum(own_last_prob * own_dot, -1, keepdims=True) + jnp.sum(
        cross_last_prob * cross_dot, -1, keepdims=True
    )
    own_slope = (own_last_prob * (own_dot - centre)).astype(jnp.bfloat16)
    cross_slope = (cross_last_prob * (cross_dot - centre)).astype(jnp.bfloat16)
    grad_query_last = (
        (
            (
                mixed("qcht,qcthe->qche", own_slope, last_keys)
                + mixed("qchd,qdhe->qche", cross_slope, cls_keys_last)
            )
            * score_scale
        )
        .astype(jnp.bfloat16)
        .reshape(lists, local_cands, local_width)
    )
    own_key_grad = (mixed("qcht,qche->qcthe", own_slope, last_heads) * score_scale).reshape(
        lists, local_cands, seq_len, local_width
    )
    own_val_grad = mixed("qcht,qche->qcthe", own_last_weight, grad_mixed_last).reshape(
        lists, local_cands, seq_len, local_width
    )
    cls_key_terms = (mixed("qchd,qche->qdhe", cross_slope, last_heads) * score_scale).reshape(
        lists, cand_count, local_width
    )
    cls_val_terms = mixed("qchd,qche->qdhe", cross_last_weight, grad_mixed_last).reshape(
        lists, cand_count, local_width
    )
    back_terms = scatter_cand(jnp.concatenate([cls_key_terms, cls_val_terms], -1), 1)
    back_keys = back_terms[..., :local_width]
    back_vals = back_terms[..., local_width:]
    first_cols = first_mask[None, None, :, None]
    key_grad = jnp.where(first_cols, own_key_grad + back_keys[:, :, None], own_key_grad).astype(
        jnp.bfloat16
    )
    val_grad = jnp.where(first_cols, own_val_grad + back_vals[:, :, None], own_val_grad).astype(
        jnp.bfloat16
    )
    joined = lax.all_gather(
        jnp.concatenate([key_grad, val_grad, grad_query_last[:, :, None]], 2),
        "mp",
        axis=3,
        tiled=True,
    )
    key_joined = joined[:, :, :seq_len]
    val_joined = joined[:, :, seq_len : 2 * seq_len]
    query_joined = joined[:, :, 2 * seq_len]
    summed_term = mixed("qcsf,df->qcsd", key_joined, last_full[1]) + mixed(
        "qcsf,df->qcsd", val_joined, last_full[2]
    )
    query_term = mixed("qcf,df->qcd", query_joined, last_full[0])
    summed_term = jnp.where(first_cols, summed_term + query_term[:, :, None], summed_term)
    grad_hidden = jnp.where(first_cols, summed_term + grad_last[:, :, None], summed_term)
    grad_first = norm_backward(grad_hidden, unit_first, inverse_first, gain_first).astype(
        jnp.bfloat16
    )
    grad_mixed_first = (
        mixed("qcsd,fd->qcsf", grad_first, w_out_first).astype(jnp.bfloat16).reshape(head_shape)
    )
    own_dot_first = mixed("qcshe,qcthe->qchst", grad_mixed_first, first_vals)
    cross_dot_first = mixed("qche,qdhe->qchd", grad_mixed_first[:, :, 0], cls_vals)
    own_part = jnp.sum(own_prob * own_dot_first, -1)
    row_part = own_part[..., 0] + jnp.sum(cross_prob * cross_dot_first, -1)
    centre_first = jnp.where(first_mask, row_part[..., None], own_part)
    own_slope_first = (own_prob * (own_dot_first - centre_first[..., None])).astype(jnp.bfloat16)
    cross_slope_first = (cross_prob * (cross_dot_first - row_part[..., None])).astype(jnp.bfloat16)
    query_grad = mixed("qchst,qcthe->qcshe", own_slope_first, first_keys)
    query_cls = mixed("qchd,qdhe->qche", cross_slope_first, cls_keys)
    query_grad = jnp.where(
        first_mask[None, None, :, None, None], query_grad + query_cls[:, :, None], query_grad
    )
    query_grad = (
        (query_grad * score_scale)
        .astype(jnp.bfloat16)
        .reshape(lists, local_cands, seq_len, local_width)
    )
    key_first = (mixed("qchst,qcshe->qcthe", own_slope_first, first_query) * score_scale).reshape(
        lists, local_cands, seq_len, local_width
    )
    val_first = mixed("qchst,qcshe->qcthe", own_weight, grad_mixed_first).reshape(
        lists, local_cands, seq_len, local_width
    )
    cls_key_first = (
        mixed("qchd,qche->qdhe", cross_slope_first, first_query[:, :, 0]) * score_scale
    ).reshape(lists, cand_count, local_width)
    cls_val_first = mixed("qchd,qche->qdhe", cross_weight, grad_mixed_first[:, :, 0]).reshape(
        lists, cand_count, local_width
    )
    key_first = key_first.astype(jnp.bfloat16)
    val_first = val_first.astype(jnp.bfloat16)
    stacked = jnp.stack([query_grad, key_first, val_first], 3).reshape(row_count, 3, local_width)
    cross_rows = lists * cand_count
    cross_stacked = jnp.stack(
        [jnp.zeros_like(cls_key_first), cls_key_first, cls_val_first], 2
    ).astype(jnp.bfloat16)
    all_rows = jnp.concatenate(
        [stacked, cross_stacked.reshape(cross_rows, 3, local_width)], 0
    )
    all_tokens = jnp.concatenate(
        [tokens.reshape(row_count, model_width), cls_tokens.reshape(cross_rows, model_width)], 0
    )
    if not paired_lists:
        partial_grad = lax.psum_scatter(
            mixed("rd,rkf->dkf", all_tokens, all_rows).astype(jnp.bfloat16),
            "cand",
            scatter_dimension=0,
            tiled=True,
        )
        return sum_query(partial_grad).astype(jnp.float32)
    half = 3 * local_width // 2
    side = lax.axis_index("query")
    flat_rows = all_rows.reshape(all_rows.shape[0], 3 * local_width)
    cls_flat = cls_tokens.reshape(cross_rows, model_width)
    own_half = lax.dynamic_slice_in_dim(flat_rows, side * half, half, 1)
    given_half = lax.dynamic_slice_in_dim(flat_rows, (1 - side) * half, half, 1)
    sent = lax.ppermute(
        jnp.concatenate([given_half.reshape(-1), cls_flat.reshape(-1)]), "query", swap
    )
    other_half = sent[: given_half.size].reshape(given_half.shape)
    other_cls = sent[given_half.size :].reshape(cls_flat.shape)
    count = lax.axis_size("cand")
    width = model_width // count

    def block_for(member):
        start = member * width
        return (
            mixed("rd,rf->df", lax.dynamic_slice_in_dim(all_tokens, start, width, 1), own_half)
            + mixed(
                "rd,rf->df",
                lax.dynamic_slice_in_dim(other_tokens, start, width, 1),
                other_half[:row_count],
            )
            + mixed(
                "rd,rf->df",
                lax.dynamic_slice_in_dim(other_cls, start, width, 1),
                other_half[row_count:],
            )
        )

    if count > 8:
        paired = block_for(0) if count == 1 else jnp.concatenate(
            [block_for(b) for b in range(count)], 0
        )
        reduced = scatter_cand(paired.astype(jnp.bfloat16), 0, jnp.float32).astype(jnp.bfloat16)
    else:
        me = lax.axis_index("cand")
        moved = [
            lax.ppermute(
                block_for((me + k) % count).astype(jnp.bfloat16),
                "cand",
                [(j, (j + k) % count) for j in range(count)],
            )
            for k in range(1, count)
        ]
        total = block_for(me)
        for piece in moved:
            total = total + piece.astype(jnp.float32)
        reduced = total.astype(jnp.bfloat16)
    partner = lax.ppermute(reduced, "query", swap)
    joined = jnp.where(
        side == 0,
        jnp.concatenate([reduced, partner], 1),
        jnp.concatenate([partner, reduced], 1),
    )
    return joined.reshape(joined.shape[0], 3, local_width).astype(jnp.float32)


def solution(mesh):
    return jax.shard_map(
        local,
        mesh=mesh,
        in_specs=(
            P(("groups", "query"), "cand", None, None),
            P(("groups", "query"), "cand"),
            P(("groups", "query"), "cand"),
            P(None, None, "mp"),
            P("mp", None),
            P(),
            P(None, None, "mp"),
            P("mp", None),
            P(),
            P(),
        ),
        out_specs=P(("groups", "cand"), None, "mp"),
        check_vma=False,
    )
```

```python
import jax
import jax.numpy as jnp
from jax import lax
from jax.sharding import PartitionSpec as P

HEAD_DIM = 64


EPSILON = 1e-05
LOSS_SCALE = 1024.0
NEGATIVE = -1e30


def mixed(pattern, former, latter):
    return jnp.einsum(pattern, former, latter, preferred_element_type=jnp.float32)


def norm_forward(matrix, scales):
    center = matrix - jnp.mean(matrix, -1, keepdims=True)
    inverse = lax.rsqrt(jnp.mean(center * center, -1, keepdims=True) + EPSILON)
    normed = center * inverse
    return (normed * scales, normed, inverse)


def norm_backward(incoming, normed, inverse, scales):
    scaled = incoming * scales
    return inverse * (
        scaled
        - jnp.mean(scaled, -1, keepdims=True)
        - normed * jnp.mean(scaled * normed, -1, keepdims=True)
    )


def split_softmax(own_scores, cross_scores, first_mask):
    own_peak = jnp.max(own_scores, -1)
    row_peak = jnp.maximum(own_peak[..., 0], jnp.max(cross_scores, -1))
    peak = jnp.where(first_mask, row_peak[..., None], own_peak)
    own_exp = jnp.exp(own_scores - peak[..., None])
    cross_exp = jnp.exp(cross_scores - row_peak[..., None])
    own_totals = jnp.sum(own_exp, -1)
    row_totals = own_totals[..., 0] + jnp.sum(cross_exp, -1)
    totals = jnp.where(first_mask, row_totals[..., None], own_totals)
    return (own_exp / totals[..., None], cross_exp / row_totals[..., None])


def row_softmax(own_scores, cross_scores):
    peak = jnp.maximum(jnp.max(own_scores, -1), jnp.max(cross_scores, -1))[..., None]
    own_exp = jnp.exp(own_scores - peak)
    cross_exp = jnp.exp(cross_scores - peak)
    totals = (jnp.sum(own_exp, -1) + jnp.sum(cross_exp, -1))[..., None]
    return (own_exp / totals, cross_exp / totals)


def gather_cand(block, axis):
    count = lax.axis_size("cand")
    if count > 8:
        return lax.all_gather(block, "cand", axis=axis, tiled=True)
    me = lax.axis_index("cand")
    parts = [block] + [
        lax.ppermute(block, "cand", [(j, (j + k) % count) for j in range(count)])
        for k in range(1, count)
    ]
    ordered = jnp.take(jnp.stack(parts, 0), (me - jnp.arange(count)) % count, axis=0)
    ordered = jnp.moveaxis(ordered, 0, axis)
    shape = block.shape[:axis] + (count * block.shape[axis],) + block.shape[axis + 1 :]
    return ordered.reshape(shape)


def sum_cand(block):
    count = lax.axis_size("cand")
    if count > 8:
        return lax.psum(block, "cand")
    total = block
    for k in range(1, count):
        total = total + lax.ppermute(block, "cand", [(j, (j + k) % count) for j in range(count)])
    return total


def scatter_cand(block, axis, total_type=None):
    count = lax.axis_size("cand")
    if count > 8:
        return lax.psum_scatter(block, "cand", scatter_dimension=axis, tiled=True)
    total_type = total_type or block.dtype
    me = lax.axis_index("cand")
    width = block.shape[axis] // count
    total = lax.dynamic_slice_in_dim(block, me * width, width, axis).astype(total_type)
    for k in range(1, count):
        piece = lax.dynamic_slice_in_dim(block, ((me + k) % count) * width, width, axis)
        moved = lax.ppermute(piece, "cand", [(j, (j + k) % count) for j in range(count)])
        total = total + moved.astype(total_type)
    return total


def gather_mp(block, axis):
    if lax.axis_size("mp") != 2:
        return lax.all_gather(block, "mp", axis=axis, tiled=True)
    other = lax.ppermute(block, "mp", [(0, 1), (1, 0)])
    return jnp.where(
        lax.axis_index("mp") == 0,
        jnp.concatenate([block, other], axis),
        jnp.concatenate([other, block], axis),
    )


def sum_query(block):
    if lax.axis_size("query") != 2:
        return lax.psum(block, "query")
    other = lax.ppermute(block, "query", [(0, 1), (1, 0)])
    return block.astype(jnp.float32) + other.astype(jnp.float32)


def local(
    tokens,
    lengths,
    teacher,
    w_first,
    w_out_first,
    gain_first,
    w_last,
    w_out_last,
    gain_last,
    w_score,
):
    lists, local_cands, seq_len, model_width = tokens.shape
    local_width = w_first.shape[2]
    local_heads = local_width // HEAD_DIM
    cand_count = local_cands * lax.axis_size("cand")
    query_count = lists * lax.axis_size("query")
    score_scale = HEAD_DIM ** (-0.5)
    positions = jnp.arange(seq_len)
    first_mask = positions == 0
    own_valid = positions[None, None, :] < lengths[:, :, None]
    local_ids = lax.axis_index("cand") * local_cands + jnp.arange(local_cands)
    cross_valid = local_ids[:, None] != jnp.arange(cand_count)[None, :]
    head_shape = (lists, local_cands, seq_len, local_heads, HEAD_DIM)
    cls_shape = (lists, cand_count, local_heads, HEAD_DIM)
    out_first_full = gather_mp(w_out_first, 0)
    last_full = gather_mp(w_last, 2)
    out_last_full = gather_mp(w_out_last, 0)
    cls_and_teacher = gather_cand(
        jnp.concatenate([tokens[:, :, 0].astype(jnp.float32), teacher[..., None]], -1), 1
    )
    cls_tokens = cls_and_teacher[..., :model_width].astype(jnp.bfloat16)
    teacher_all = cls_and_teacher[..., model_width]
    row_count = lists * local_cands * seq_len
    swap = [(0, 1), (1, 0)]
    paired_lists = lax.axis_size("query") == 2
    if paired_lists:
        other_tokens = lax.ppermute(tokens.reshape(row_count, model_width), "query", swap)
    projected = mixed("qcsd,kdf->kqcsf", tokens, w_first).astype(jnp.bfloat16)
    cls_projected = mixed("qcd,kdf->kqcf", cls_tokens, w_first[1:]).astype(jnp.bfloat16)
    gathered_keys = cls_projected[0]
    gathered_vals = cls_projected[1]
    first_query = projected[0].reshape(head_shape)
    first_keys = projected[1].reshape(head_shape)
    first_vals = projected[2].reshape(head_shape)
    cls_keys = gathered_keys.reshape(cls_shape)
    cls_vals = gathered_vals.reshape(cls_shape)
    own_scores = mixed("qcshe,qcthe->qchst", first_query, first_keys) * score_scale
    own_scores = jnp.where(own_valid[:, :, None, None, :], own_scores, NEGATIVE)
    cross_scores = mixed("qche,qdhe->qchd", first_query[:, :, 0], cls_keys) * score_scale
    cross_scores = jnp.where(cross_valid[None, :, None, :], cross_scores, NEGATIVE)
    own_prob, cross_prob = split_softmax(own_scores, cross_scores, first_mask)
    own_weight = own_prob.astype(jnp.bfloat16)
    cross_weight = cross_prob.astype(jnp.bfloat16)
    attended = mixed("qchst,qcthe->qcshe", own_weight, first_vals)
    attended_cls = mixed("qchd,qdhe->qche", cross_weight, cls_vals)
    attended = jnp.where(
        first_mask[None, None, :, None, None], attended + attended_cls[:, :, None], attended
    )
    first_mixed = attended.reshape(lists, local_cands, seq_len, local_width).astype(jnp.bfloat16)
    first_joined = lax.all_gather(first_mixed, "mp", axis=3, tiled=True)
    residual_first = tokens.astype(jnp.float32) + mixed(
        "qcsf,fd->qcsd", first_joined, out_first_full
    )
    normed_first, unit_first, inverse_first = norm_forward(residual_first, gain_first)
    hidden = normed_first.astype(jnp.bfloat16)
    last_query = mixed("qcd,df->qcf", hidden[:, :, 0], w_last[0]).astype(jnp.bfloat16)
    last_kv = mixed("qcsd,kdf->kqcsf", hidden, w_last[1:]).astype(jnp.bfloat16)
    gathered_kv_last = gather_cand(
        jnp.concatenate([last_kv[0][:, :, 0], last_kv[1][:, :, 0]], -1), 1
    )
    gathered_keys_last = gathered_kv_last[..., :local_width]
    gathered_vals_last = gathered_kv_last[..., local_width:]
    last_heads = last_query.reshape(lists, local_cands, local_heads, HEAD_DIM)
    last_keys = last_kv[0].reshape(head_shape)
    last_vals = last_kv[1].reshape(head_shape)
    cls_keys_last = gathered_keys_last.reshape(cls_shape)
    cls_vals_last = gathered_vals_last.reshape(cls_shape)
    own_last = mixed("qche,qcthe->qcht", last_heads, last_keys) * score_scale
    own_last = jnp.where(own_valid[:, :, None, :], own_last, NEGATIVE)
    cross_last = mixed("qche,qdhe->qchd", last_heads, cls_keys_last) * score_scale
    cross_last = jnp.where(cross_valid[None, :, None, :], cross_last, NEGATIVE)
    own_last_prob, cross_last_prob = row_softmax(own_last, cross_last)
    own_last_weight = own_last_prob.astype(jnp.bfloat16)
    cross_last_weight = cross_last_prob.astype(jnp.bfloat16)
    attended_last = mixed("qcht,qcthe->qche", own_last_weight, last_vals) + mixed(
        "qchd,qdhe->qche", cross_last_weight, cls_vals_last
    )
    last_mixed = attended_last.reshape(lists, local_cands, local_width).astype(jnp.bfloat16)
    last_joined = lax.all_gather(last_mixed, "mp", axis=2, tiled=True)
    residual_last = hidden[:, :, 0].astype(jnp.float32) + mixed(
        "qcf,fd->qcd", last_joined, out_last_full
    )
    normed_last, unit_last, inverse_last = norm_forward(residual_last, gain_last)
    scores = jnp.einsum("qcd,d->qc", normed_last, w_score, precision=lax.Precision.HIGHEST)
    score_exp = jnp.exp(scores)
    teacher_peak = jnp.max(teacher_all, 1)
    teacher_exp = jnp.exp(teacher - teacher_peak[:, None])
    teacher_totals = jnp.sum(jnp.exp(teacher_all - teacher_peak[:, None]), 1)
    score_totals = sum_cand(jnp.sum(score_exp, 1))
    student_prob = score_exp / score_totals[:, None]
    teacher_prob = teacher_exp / teacher_totals[:, None]
    score_grad = LOSS_SCALE * (student_prob - teacher_prob) / query_count
    grad_last = norm_backward(score_grad[..., None] * w_score, unit_last, inverse_last, gain_last)
    grad_last_low = grad_last.astype(jnp.bfloat16)
    grad_mixed_last = (
        mixed("qcd,fd->qcf", grad_last_low, w_out_last)
        .astype(jnp.bfloat16)
        .reshape(lists, local_cands, local_heads, HEAD_DIM)
    )
    own_dot = mixed("qche,qcthe->qcht", grad_mixed_last, last_vals)
    cross_dot = mixed("qche,qdhe->qchd", grad_mixed_last, cls_vals_last)
    centre = jnp.sum(own_last_prob * own_dot, -1, keepdims=True) + jnp.sum(
        cross_last_prob * cross_dot, -1, keepdims=True
    )
    own_slope = (own_last_prob * (own_dot - centre)).astype(jnp.bfloat16)
    cross_slope = (cross_last_prob * (cross_dot - centre)).astype(jnp.bfloat16)
    grad_query_last = (
        (
            (
                mixed("qcht,qcthe->qche", own_slope, last_keys)
                + mixed("qchd,qdhe->qche", cross_slope, cls_keys_last)
            )
            * score_scale
        )
        .astype(jnp.bfloat16)
        .reshape(lists, local_cands, local_width)
    )
    own_key_grad = (mixed("qcht,qche->qcthe", own_slope, last_heads) * score_scale).reshape(
        lists, local_cands, seq_len, local_width
    )
    own_val_grad = mixed("qcht,qche->qcthe", own_last_weight, grad_mixed_last).reshape(
        lists, local_cands, seq_len, local_width
    )
    cls_key_terms = (mixed("qchd,qche->qdhe", cross_slope, last_heads) * score_scale).reshape(
        lists, cand_count, local_width
    )
    cls_val_terms = mixed("qchd,qche->qdhe", cross_last_weight, grad_mixed_last).reshape(
        lists, cand_count, local_width
    )
    back_terms = scatter_cand(jnp.concatenate([cls_key_terms, cls_val_terms], -1), 1)
    back_keys = back_terms[..., :local_width]
    back_vals = back_terms[..., local_width:]
    first_cols = first_mask[None, None, :, None]
    key_grad = jnp.where(first_cols, own_key_grad + back_keys[:, :, None], own_key_grad).astype(
        jnp.bfloat16
    )
    val_grad = jnp.where(first_cols, own_val_grad + back_vals[:, :, None], own_val_grad).astype(
        jnp.bfloat16
    )
    joined = lax.all_gather(
        jnp.concatenate([key_grad, val_grad, grad_query_last[:, :, None]], 2),
        "mp",
        axis=3,
        tiled=True,
    )
    key_joined = joined[:, :, :seq_len]
    val_joined = joined[:, :, seq_len : 2 * seq_len]
    query_joined = joined[:, :, 2 * seq_len]
    summed_term = mixed("qcsf,df->qcsd", key_joined, last_full[1]) + mixed(
        "qcsf,df->qcsd", val_joined, last_full[2]
    )
    query_term = mixed("qcf,df->qcd", query_joined, last_full[0])
    summed_term = jnp.where(first_cols, summed_term + query_term[:, :, None], summed_term)
    grad_hidden = jnp.where(first_cols, summed_term + grad_last[:, :, None], summed_term)
    grad_first = norm_backward(grad_hidden, unit_first, inverse_first, gain_first).astype(
        jnp.bfloat16
    )
    grad_mixed_first = (
        mixed("qcsd,fd->qcsf", grad_first, w_out_first).astype(jnp.bfloat16).reshape(head_shape)
    )
    own_dot_first = mixed("qcshe,qcthe->qchst", grad_mixed_first, first_vals)
    cross_dot_first = mixed("qche,qdhe->qchd", grad_mixed_first[:, :, 0], cls_vals)
    own_part = jnp.sum(own_prob * own_dot_first, -1)
    row_part = own_part[..., 0] + jnp.sum(cross_prob * cross_dot_first, -1)
    centre_first = jnp.where(first_mask, row_part[..., None], own_part)
    own_slope_first = (own_prob * (own_dot_first - centre_first[..., None])).astype(jnp.bfloat16)
    cross_slope_first = (cross_prob * (cross_dot_first - row_part[..., None])).astype(jnp.bfloat16)
    query_grad = mixed("qchst,qcthe->qcshe", own_slope_first, first_keys)
    query_cls = mixed("qchd,qdhe->qche", cross_slope_first, cls_keys)
    query_grad = jnp.where(
        first_mask[None, None, :, None, None], query_grad + query_cls[:, :, None], query_grad
    )
    query_grad = (
        (query_grad * score_scale)
        .astype(jnp.bfloat16)
        .reshape(lists, local_cands, seq_len, local_width)
    )
    key_first = (mixed("qchst,qcshe->qcthe", own_slope_first, first_query) * score_scale).reshape(
        lists, local_cands, seq_len, local_width
    )
    val_first = mixed("qchst,qcshe->qcthe", own_weight, grad_mixed_first).reshape(
        lists, local_cands, seq_len, local_width
    )
    cls_key_first = (
        mixed("qchd,qche->qdhe", cross_slope_first, first_query[:, :, 0]) * score_scale
    ).reshape(lists, cand_count, local_width)
    cls_val_first = mixed("qchd,qche->qdhe", cross_weight, grad_mixed_first[:, :, 0]).reshape(
        lists, cand_count, local_width
    )
    key_first = key_first.astype(jnp.bfloat16)
    val_first = val_first.astype(jnp.bfloat16)
    stacked = jnp.stack([query_grad, key_first, val_first], 3).reshape(row_count, 3, local_width)
    cross_rows = lists * cand_count
    cross_stacked = jnp.stack(
        [jnp.zeros_like(cls_key_first), cls_key_first, cls_val_first], 2
    ).astype(jnp.bfloat16)
    all_rows = jnp.concatenate(
        [stacked, cross_stacked.reshape(cross_rows, 3, local_width)], 0
    )
    all_tokens = jnp.concatenate(
        [tokens.reshape(row_count, model_width), cls_tokens.reshape(cross_rows, model_width)], 0
    )
    if not paired_lists:
        partial_grad = lax.psum_scatter(
            mixed("rd,rkf->dkf", all_tokens, all_rows).astype(jnp.bfloat16),
            "cand",
            scatter_dimension=0,
            tiled=True,
        )
        return sum_query(partial_grad).astype(jnp.float32)
    half = 3 * local_width // 2
    side = lax.axis_index("query")
    flat_rows = all_rows.reshape(all_rows.shape[0], 3 * local_width)
    cls_flat = cls_tokens.reshape(cross_rows, model_width)
    own_half = lax.dynamic_slice_in_dim(flat_rows, side * half, half, 1)
    given_half = lax.dynamic_slice_in_dim(flat_rows, (1 - side) * half, half, 1)
    sent = lax.ppermute(
        jnp.concatenate([given_half.reshape(-1), cls_flat.reshape(-1)]), "query", swap
    )
    other_half = sent[: given_half.size].reshape(given_half.shape)
    other_cls = sent[given_half.size :].reshape(cls_flat.shape)
    paired = (
        mixed("rd,rf->df", all_tokens, own_half)
        + mixed("rd,rf->df", other_tokens, other_half[:row_count])
        + mixed("rd,rf->df", other_cls, other_half[row_count:])
    )
    reduced = scatter_cand(paired.astype(jnp.bfloat16), 0, jnp.float32).astype(jnp.bfloat16)
    partner = lax.ppermute(reduced, "query", swap)
    joined = jnp.zeros((reduced.shape[0], 2 * half), jnp.float32)
    joined = lax.dynamic_update_slice_in_dim(joined, reduced.astype(jnp.float32), side * half, 1)
    joined = lax.dynamic_update_slice_in_dim(
        joined, partner.astype(jnp.float32), (1 - side) * half, 1
    )
    return joined.reshape(joined.shape[0], 3, local_width)


def solution(mesh):
    return jax.shard_map(
        local,
        mesh=mesh,
        in_specs=(
            P(("groups", "query"), "cand", None, None),
            P(("groups", "query"), "cand"),
            P(("groups", "query"), "cand"),
            P(None, None, "mp"),
            P("mp", None),
            P(),
            P(None, None, "mp"),
            P("mp", None),
            P(),
            P(),
        ),
        out_specs=P(("groups", "cand"), None, "mp"),
        check_vma=False,
    )
```
